32 devices in a mesh: seq: 8 (over z, y), fsdp: 4 (over x, core).
Axes of the slice: x: 2, y: 2, z: 4, core: 2. Of those that a mesh axis runs over, the one named last changes fastest.
Arguments:
- layer_input: bfloat16 [2, 4, 1024, 768], P(None, 'fsdp', 'seq'), may hold values from -6 to 6
- history: bfloat16 [4, 2, 4, 1024, 768], P(None, None, 'fsdp', 'seq'), may hold values from -6 to 6
- cotangent: bfloat16 [2, 4, 1024, 768], P(None, 'fsdp', 'seq'), may hold values from -6 to 6
- lengths: int32 [2, 4], P(None, 'fsdp'), may hold values from 256 to 1024, as said below
- w_qkv: bfloat16 [768, 2304], P(('seq', 'fsdp')), may hold values from -0.21875 to 0.21875
- w_out: bfloat16 [768, 768], P(('seq', 'fsdp')), may hold values from -1 to 1
- w_up: bfloat16 [768, 3072], P(('seq', 'fsdp')), may hold values from -0.21875 to 0.21875
- w_down: bfloat16 [3072, 768], P(('seq', 'fsdp')), may hold values from -0.109375 to 0.109375
- ln_gains: bfloat16 [768, 2], P(('seq', 'fsdp')), may hold values from 0.5 to 1.5
- ln_biases: bfloat16 [768, 2], P(('seq', 'fsdp')), may hold values from -0.5 to 0.5
- depth_weights: float32 [5], replicated, may hold values from 0.3 to 1
Outputs:
- next_input: bfloat16 [2, 4, 1024, 768], P(None, 'fsdp', 'seq')
- grad_input: bfloat16 [2, 4, 1024, 768], P(None, 'fsdp', 'seq')
- grad_history: bfloat16 [4, 2, 4, 1024, 768], P(None, None, 'fsdp', 'seq')
- grad_w_qkv: float32 [768, 2304], P(('seq', 'fsdp'))
- grad_w_out: float32 [768, 768], P(('seq', 'fsdp'))
- grad_w_up: float32 [768, 3072], P(('seq', 'fsdp'))
- grad_w_down: float32 [3072, 768], P(('seq', 'fsdp'))
- grad_ln_gains: float32 [768, 2], P(('seq', 'fsdp'))
- grad_ln_biases: float32 [768, 2], P(('seq', 'fsdp'))
- grad_depth: float32 [5], replicated
The draws below stay inside these ranges and needn't reach their ends.
Inputs may be any that keep to these rules, and one draw needn't show every extreme that they name: Each slot holds one sequence of lengths[m, s] tokens at its start and padding after it; the first slot of every micro-batch is full.
All inputs are finite; a program needn't handle non-finite values.
Results may differ from the reference program's by a relative error of at most 0.015.
Values may be sent and summed in bfloat16 or wider, within the bound.
No kernel may reach another device: no remote copies, remote signals or barrier semaphores. Data moves between devices by JAX's collectives and lax.ppermute only.
A program may use at most 192 MiB of HBM per device.

```python
import jax
import jax.numpy as jnp
from jax import lax

D = 768
HEADS = 12
HEAD = 64
FF = 3072
MB = 2
SLOT = 1024
SLOTS = 4


def draw_lengths(key, part):
    drawn = jax.random.randint(key, (MB, SLOTS), SLOT // 4, SLOT + 1)
    return drawn.at[:, 0].set(SLOT).astype(jnp.int32)


def shard_levels(stream_key, shape, cuts, least, largest):
    gain, own = 1.0, jax.random.fold_in(stream_key, 6)
    for axis_at, shards_of in cuts:
        draws = jnp.exp(jax.random.uniform(jax.random.fold_in(own, axis_at), (shards_of,), jnp.float32, least / len(cuts), largest / len(cuts)))
        gain = gain * jnp.repeat(draws, shape[axis_at] // shards_of).reshape([-1 if axis == axis_at else 1 for axis in range(len(shape))])
    return gain


def noise(own_key, dims, deviation, reach, cuts=(), held_as=jnp.bfloat16):
    level = shard_levels(own_key, dims, cuts, -0.22, 0.18) if cuts else 1.0
    entries = jax.random.normal(own_key, dims, jnp.float32) * deviation * level
    return jnp.minimum(jnp.maximum(entries, -reach), reach).astype(held_as)


def setup_inputs(seed: int = 0) -> dict:
    splits = jax.random.split(jax.random.key(seed), 12)
    return {
        "layer_input": noise(splits[0], (MB, SLOTS, SLOT, D), 1.0, 6.0, ((1, 4), (2, 8))),
        "history": noise(splits[1], (4, MB, SLOTS, SLOT, D), 1.0, 6.0, ((2, 4), (3, 8))),
        "cotangent": noise(splits[2], (MB, SLOTS, SLOT, D), 1.0, 6.0, ((1, 4), (2, 8))),
        "lengths": draw_lengths(jax.random.fold_in(splits[11], 71), 0),
        "w_qkv": noise(splits[4], (D, 3 * D), D ** -0.5, 0.21875, ((0, 32),)),
        "w_out": noise(splits[5], (D, D), (D // 24) ** -0.5, 1.0, ((0, 32),)),
        "w_up": noise(splits[6], (D, FF), D ** -0.5, 0.21875, ((0, 32),)),
        "w_down": noise(splits[7], (FF, D), FF ** -0.5, 0.109375, ((0, 32),)),
        "ln_gains": jnp.clip(1.0 + 0.1 * jax.random.normal(splits[8], (D, 2), jnp.float32), 0.5, 1.5).astype(jnp.bfloat16),
        "ln_biases": jnp.clip(jax.random.uniform(splits[9], (D, 2), jnp.float32, -0.5, 0.5) * shard_levels(splits[9], (D, 2), ((0, 32),), -0.4, 0.0), -0.5, 0.5).astype(jnp.bfloat16),
        "depth_weights": jnp.clip(jax.random.uniform(splits[10], (5,), jnp.float32, 0.3, 1.0), 0.3, 1.0),
    }


@jax.custom_vjp
def low(v):
    return lax.optimization_barrier(v.astype(jnp.bfloat16)).astype(jnp.float32)

@jax.custom_vjp
def low_back(v):
    return v

def low_keep(v):
    return (low(v), None)

def low_pass(kept, grad):
    return (grad,)

def back_keep(v):
    return (v, None)

def back_low(kept, grad):
    return (low(grad),)
low.defvjp(low_keep, low_pass)
low_back.defvjp(back_keep, back_low)
epsilon = 1e-05

def layer_norm(values, gain_vector, bias_vector):
    center = values - lax.optimization_barrier(jnp.mean(values, axis=-1, keepdims=True))
    spread = lax.optimization_barrier(jnp.mean(center * center, axis=-1, keepdims=True))
    return center * lax.rsqrt(spread + epsilon) * gain_vector + bias_vector

def rotary_tables(positions):
    half_width = HEAD // 2
    frequencies = 10000.0 ** (-jnp.arange(half_width, dtype=jnp.float32) / half_width)
    angles = positions.astype(jnp.float32)[:, None] * frequencies[None, :]
    return (jnp.cos(angles)[:, None, :], jnp.sin(angles)[:, None, :])

def rotate(values, cosine_part, sine_part):
    row_count = values.shape[0]
    shaped = values.reshape(row_count, HEADS, HEAD)
    half_width = HEAD // 2
    first_half = shaped[..., :half_width]
    second_half = shaped[..., half_width:]
    turned = jnp.concatenate([first_half * cosine_part - second_half * sine_part, second_half * cosine_part + first_half * sine_part], axis=-1)
    return turned.reshape(row_count, HEADS * HEAD)

def attention(queries, keys, values, length):
    query_block = min(512, SLOT)
    shaped_keys = keys.reshape(SLOT, HEADS, HEAD)
    shaped_values = values.reshape(SLOT, HEADS, HEAD)
    key_positions = jnp.arange(SLOT, dtype=jnp.int32)
    factor = HEAD ** (-0.5)

    def one_block(block_index):
        first_row = (block_index * query_block).astype(jnp.int32)
        block_queries = lax.dynamic_slice_in_dim(queries, first_row, query_block, 0).reshape(query_block, HEADS, HEAD)
        scores = jnp.einsum('qhd,khd->hqk', block_queries, shaped_keys, precision=lax.Precision.HIGHEST) * factor
        query_positions = first_row + jnp.arange(query_block, dtype=jnp.int32)
        allowed = (key_positions[None, :] <= query_positions[:, None]) & (key_positions[None, :] < length)
        scores = low_back(jnp.where(allowed[None], scores, -1000000000.0))
        weights = jax.nn.softmax(scores, axis=-1)
        combined = jnp.einsum('hqk,khd->qhd', low(weights), shaped_values, precision=lax.Precision.HIGHEST)
        return combined.reshape(query_block, HEADS * HEAD)
    blocks = lax.map(jax.checkpoint(one_block), jnp.arange(SLOT // query_block, dtype=jnp.int32))
    return blocks.reshape(SLOT, HEADS * HEAD)

def layer(inputs, earlier, w_qkv, w_out, w_up, w_down, ln_gains, ln_biases, depth_weights, length):
    precise = lax.Precision.HIGHEST
    cosine_part, sine_part = rotary_tables(jnp.arange(SLOT, dtype=jnp.int32))
    first_low = low(layer_norm(inputs, ln_gains[:, 0], ln_biases[:, 0]))
    projected = low_back(jnp.dot(first_low, w_qkv, precision=precise))
    queries = low(rotate(projected[:, :D], cosine_part, sine_part))
    keys = low(rotate(projected[:, D:2 * D], cosine_part, sine_part))
    values = low(projected[:, 2 * D:])
    attended = low(low_back(attention(queries, keys, values, length)))
    residual = inputs + low_back(jnp.dot(attended, w_out, precision=precise))
    second_low = low(layer_norm(residual, ln_gains[:, 1], ln_biases[:, 1]))
    hidden = low_back(jnp.dot(second_low, w_up, precision=precise))
    hidden_low = low(jax.nn.gelu(hidden, approximate=True))
    block_out = residual + low_back(jnp.dot(hidden_low, w_down, precision=precise))
    return depth_weights[4] * block_out + jnp.einsum('j,jrd->rd', depth_weights[:4], earlier, precision=precise)

def reference(layer_input, history, cotangent, lengths, w_qkv, w_out, w_up, w_down, ln_gains, ln_biases, depth_weights):
    slots_all = MB * SLOTS
    flat_input = layer_input.reshape(slots_all, SLOT, D)
    flat_hist = jnp.moveaxis(history.reshape(4, slots_all, SLOT, D), 0, 1)
    flat_cot = cotangent.reshape(slots_all, SLOT, D)
    flat_len = lengths.reshape(slots_all).astype(jnp.int32)
    params = tuple((weight_array.astype(jnp.float32) for weight_array in (w_qkv, w_out, w_up, w_down, ln_gains, ln_biases, depth_weights)))

    def one_slot(summed, inputs):
        slot_input, slot_hist, slot_cot, slot_len = inputs

        def forward(inner_input, inner_hist, *weights):
            return layer(inner_input, inner_hist, *weights, slot_len)
        result, pullback = jax.vjp(forward, slot_input.astype(jnp.float32), slot_hist.astype(jnp.float32), *params)
        usable = (jnp.arange(SLOT, dtype=jnp.int32) < slot_len)[:, None]
        pulled = pullback(jnp.where(usable, slot_cot.astype(jnp.float32), jnp.float32(0.0)))
        summed = tuple((former + latter for former, latter in zip(summed, pulled[2:])))
        return (summed, (result.astype(jnp.bfloat16), pulled[0].astype(jnp.bfloat16), pulled[1].astype(jnp.bfloat16)))
    initial = tuple((jnp.zeros_like(weight_array) for weight_array in params))
    summed, (next_rows, input_rows, hist_rows) = lax.scan(one_slot, initial, (flat_input, flat_hist, flat_cot, flat_len))
    next_input = next_rows.reshape(MB, SLOTS, SLOT, D)
    grad_input = input_rows.reshape(MB, SLOTS, SLOT, D)
    grad_history = jnp.moveaxis(hist_rows, 1, 0).reshape(4, MB, SLOTS, SLOT, D)
    return (next_input, grad_input, grad_history, summed[0], summed[1], summed[2], summed[3], summed[4], summed[5], summed[6])
```

```python
from functools import partial
import math

import jax
import jax.numpy as jnp
from jax import lax
from jax.sharding import PartitionSpec as P

HEADS = 12
HEAD = 64


epsilon = 1e-05
masked_value = -1e30


def layer_norm(values, gain_vector, bias_vector):
    center = values - jnp.mean(values, axis=-1, keepdims=True)
    spread = jnp.mean(center * center, axis=-1, keepdims=True)
    return center * lax.rsqrt(spread + epsilon) * gain_vector + bias_vector


def rotary_tables(positions):
    half_width = HEAD // 2
    frequencies = 10000.0 ** (-jnp.arange(half_width, dtype=jnp.float32) / half_width)
    angles = positions.astype(jnp.float32)[:, None] * frequencies[None, :]
    return (jnp.cos(angles)[:, None, :], jnp.sin(angles)[:, None, :])


def rotate(values, cosine_part, sine_part):
    row_count = values.shape[0]
    shaped = values.reshape(row_count, HEADS, HEAD)
    half_width = HEAD // 2
    first_half = shaped[..., :half_width]
    second_half = shaped[..., half_width:]
    turned = jnp.concatenate(
        [
            first_half * cosine_part - second_half * sine_part,
            second_half * cosine_part + first_half * sine_part,
        ],
        axis=-1,
    )
    return turned.reshape(row_count, HEADS * HEAD)


def block_scores(queries3, keys3, query_pos, key_pos, length):
    scores = jnp.einsum(
        "rhd,khd->hrk", queries3, keys3, preferred_element_type=jnp.float32
    ) * HEAD ** (-0.5)
    allowed = (key_pos[None, :] <= query_pos[:, None]) & (key_pos[None, :] < length)
    return (scores, allowed[None])


def row_totals(queries3, keys3, query_pos, length, key_block):
    row_count = queries3.shape[0]

    def row_advance(state, block_index):
        running_top, running_sum = state
        first_key = block_index * key_block
        keys_part = lax.dynamic_slice_in_dim(keys3, first_key, key_block, 0)
        key_pos = first_key + jnp.arange(key_block, dtype=jnp.int32)
        scores, allowed = block_scores(queries3, keys_part, query_pos, key_pos, length)
        masked = jnp.where(allowed, scores, masked_value)
        new_top = jnp.maximum(running_top, jnp.max(masked, axis=-1))
        kept_terms = jnp.where(allowed, jnp.exp(masked - new_top[..., None]), 0.0)
        running_sum = running_sum * jnp.exp(running_top - new_top) + jnp.sum(kept_terms, axis=-1)
        return ((new_top, running_sum), None)

    initial = (
        jnp.full((HEADS, row_count), masked_value, jnp.float32),
        jnp.zeros((HEADS, row_count), jnp.float32),
    )
    (row_tops, row_sums), _ = lax.scan(
        row_advance, initial, jnp.arange(keys3.shape[0] // key_block, dtype=jnp.int32)
    )
    return row_tops + jnp.log(row_sums)


def attend(queries3, keys3, values3, query_pos, length, key_block, log_total):

    def attend_advance(running, block_index):
        first_key = block_index * key_block
        keys_part = lax.dynamic_slice_in_dim(keys3, first_key, key_block, 0)
        values_part = lax.dynamic_slice_in_dim(values3, first_key, key_block, 0)
        key_pos = first_key + jnp.arange(key_block, dtype=jnp.int32)
        scores, allowed = block_scores(queries3, keys_part, query_pos, key_pos, length)
        probabilities = jnp.where(allowed, jnp.exp(scores - log_total[..., None]), 0.0).astype(
            jnp.bfloat16
        )
        return (
            running
            + jnp.einsum(
                "hrk,khd->rhd", probabilities, values_part, preferred_element_type=jnp.float32
            ),
            None,
        )

    initial = jnp.zeros(queries3.shape, jnp.float32)
    result, _ = lax.scan(
        attend_advance, initial, jnp.arange(keys3.shape[0] // key_block, dtype=jnp.int32)
    )
    return result


def query_grads(
    queries3, grads3, keys3, values3, query_pos, length, key_block, log_total, row_delta
):

    def query_advance(running, block_index):
        first_key = block_index * key_block
        keys_part = lax.dynamic_slice_in_dim(keys3, first_key, key_block, 0)
        values_part = lax.dynamic_slice_in_dim(values3, first_key, key_block, 0)
        key_pos = first_key + jnp.arange(key_block, dtype=jnp.int32)
        scores, allowed = block_scores(queries3, keys_part, query_pos, key_pos, length)
        probabilities = jnp.where(allowed, jnp.exp(scores - log_total[..., None]), 0.0)
        prob_grad = jnp.einsum(
            "rhd,khd->hrk", grads3, values_part, preferred_element_type=jnp.float32
        )
        score_low = (probabilities * (prob_grad - row_delta[..., None])).astype(jnp.bfloat16)
        return (
            running
            + jnp.einsum("hrk,khd->rhd", score_low, keys_part, preferred_element_type=jnp.float32),
            None,
        )

    initial = jnp.zeros(queries3.shape, jnp.float32)
    result, _ = lax.scan(
        query_advance, initial, jnp.arange(keys3.shape[0] // key_block, dtype=jnp.int32)
    )
    return result * HEAD ** (-0.5)


def key_side(queries3, grads3, log_part, delta_part, query_pos, keys3, values3, key_pos, length):
    key_count = keys3.shape[0]
    scores, allowed = block_scores(queries3, keys3, query_pos, key_pos, length)
    probabilities = jnp.where(allowed, jnp.exp(scores - log_part[..., None]), 0.0)
    prob_grad = jnp.einsum("rhd,khd->hrk", grads3, values3, preferred_element_type=jnp.float32)
    score_low = (probabilities * (prob_grad - delta_part[..., None])).astype(jnp.bfloat16)
    value_grad = jnp.einsum(
        "hrk,rhd->khd",
        probabilities.astype(jnp.bfloat16),
        grads3,
        preferred_element_type=jnp.float32,
    )
    key_grad = jnp.einsum(
        "hrk,rhd->khd", score_low, queries3, preferred_element_type=jnp.float32
    ) * HEAD ** (-0.5)
    return jnp.concatenate(
        [key_grad.reshape(key_count, HEADS * HEAD), value_grad.reshape(key_count, HEADS * HEAD)],
        axis=1,
    )


def local(
    layer_input,
    history,
    cotangent,
    lengths,
    w_qkv,
    w_out,
    w_up,
    w_down,
    ln_gains,
    ln_biases,
    depth_weights,
):
    batches = layer_input.shape[0]
    row_count = layer_input.shape[2]
    model_width = layer_input.shape[3]
    ff_width = w_up.shape[1]
    shard_rows = w_qkv.shape[0]
    slot_len = row_count * lax.axis_size("seq")
    key_block = min(1024, slot_len)
    positions = lax.axis_index("seq") * row_count + jnp.arange(row_count, dtype=jnp.int32)
    cosine_part, sine_part = rotary_tables(positions)
    gelu_tanh = partial(jax.nn.gelu, approximate=True)
    lane_pad = 128 - 4
    widths = (3 * model_width, model_width, ff_width, ff_width, 2, 2, lane_pad)
    offsets = [0]
    for width in widths:
        offsets.append(offsets[-1] + width)

    def pieces(packed_rows):
        return [packed_rows[:, offsets[i] : offsets[i + 1]] for i in range(len(widths))]

    packed = jnp.concatenate(
        [
            w_qkv,
            w_out,
            w_up,
            w_down.reshape(shard_rows, ff_width),
            ln_gains,
            ln_biases,
            jnp.zeros((shard_rows, lane_pad), w_qkv.dtype),
        ],
        axis=1,
    )
    gathered = lax.all_gather(packed, ("seq", "fsdp"), axis=0, tiled=True)
    full_qkv, full_out, full_up, down_rows, gain_rows, bias_rows, _ = pieces(gathered)
    full_down = down_rows.reshape(ff_width, model_width)
    norm_gains = gain_rows.astype(jnp.float32)
    norm_biases = bias_rows.astype(jnp.float32)

    depth_terms = jnp.zeros((5,), jnp.float32)
    forward_parts = []
    own_kv = []
    for micro in range(batches):
        inputs = layer_input[micro, 0].astype(jnp.float32)
        first_low = layer_norm(inputs, norm_gains[:, 0], norm_biases[:, 0]).astype(jnp.bfloat16)
        projected = jnp.dot(first_low, full_qkv, preferred_element_type=jnp.float32)
        queries = (
            rotate(projected[:, :model_width], cosine_part, sine_part)
            .astype(jnp.bfloat16)
            .reshape(row_count, HEADS, HEAD)
        )
        keys_own = rotate(
            projected[:, model_width : 2 * model_width], cosine_part, sine_part
        ).astype(jnp.bfloat16)
        values_own = projected[:, 2 * model_width :].astype(jnp.bfloat16)
        forward_parts.append((inputs, first_low, queries))
        own_kv.append(jnp.concatenate([keys_own, values_own], axis=1))
    kv_all = lax.all_gather(jnp.stack(own_kv), "seq", axis=1, tiled=True)

    key_value_parts = []
    later_parts = []
    totals = None
    next_rows = []
    history_grads = []
    for micro in range(batches):
        inputs, first_low, queries = forward_parts[micro]
        keys3 = kv_all[micro, :, :model_width].reshape(slot_len, HEADS, HEAD)
        values3 = kv_all[micro, :, model_width:].reshape(slot_len, HEADS, HEAD)
        length = lengths[micro, 0]
        usable = (positions < length)[:, None]
        earlier = history[:, micro, 0].astype(jnp.float32)
        grad_next = jnp.where(usable, cotangent[micro, 0].astype(jnp.float32), 0.0)
        log_total = row_totals(queries, keys3, positions, length, key_block)
        attended = attend(queries, keys3, values3, positions, length, key_block, log_total)
        attended_low = attended.reshape(row_count, model_width).astype(jnp.bfloat16)
        residual = inputs + jnp.dot(attended_low, full_out, preferred_element_type=jnp.float32)
        second_low = layer_norm(residual, norm_gains[:, 1], norm_biases[:, 1]).astype(jnp.bfloat16)
        hidden = jnp.dot(second_low, full_up, preferred_element_type=jnp.float32)
        hidden_low = gelu_tanh(hidden).astype(jnp.bfloat16)
        block_out = residual + jnp.dot(hidden_low, full_down, preferred_element_type=jnp.float32)
        combined = depth_weights[4] * block_out + jnp.einsum(
            "j,jrd->rd", depth_weights[:4], earlier
        )
        next_rows.append(combined.astype(jnp.bfloat16))
        history_grads.append((depth_weights[:4, None, None] * grad_next[None]).astype(jnp.bfloat16))
        depth_terms = depth_terms + jnp.concatenate(
            [jnp.einsum("jrd,rd->j", earlier, grad_next), jnp.sum(block_out * grad_next)[None]]
        )
        out_grad = depth_weights[4] * grad_next
        out_low = out_grad.astype(jnp.bfloat16)
        grad_down = jnp.einsum("rf,rd->fd", hidden_low, out_low, preferred_element_type=jnp.float32)
        hidden_grad = jnp.einsum(
            "rd,fd->rf", out_low, full_down, preferred_element_type=jnp.float32
        )
        _, gelu_pullback = jax.vjp(gelu_tanh, hidden)
        up_low = gelu_pullback(hidden_grad)[0].astype(jnp.bfloat16)
        grad_up = jnp.einsum("rd,rf->df", second_low, up_low, preferred_element_type=jnp.float32)
        second_grad = jnp.einsum("rf,df->rd", up_low, full_up, preferred_element_type=jnp.float32)
        _, second_pullback = jax.vjp(layer_norm, residual, norm_gains[:, 1], norm_biases[:, 1])
        residual_part, gain_two, bias_two = second_pullback(second_grad)
        residual_grad = out_grad + residual_part
        branch_low = residual_grad.astype(jnp.bfloat16)
        grad_outproj = jnp.einsum(
            "rc,rd->cd", attended_low, branch_low, preferred_element_type=jnp.float32
        )
        attended_grad = jnp.einsum(
            "rd,cd->rc", branch_low, full_out, preferred_element_type=jnp.float32
        ).astype(jnp.bfloat16)
        attended_grad3 = attended_grad.reshape(row_count, HEADS, HEAD)
        row_delta = jnp.einsum("rhd,rhd->hr", attended_grad3.astype(jnp.float32), attended)
        query_grad = query_grads(
            queries,
            attended_grad3,
            keys3,
            values3,
            positions,
            length,
            key_block,
            log_total,
            row_delta,
        )
        sub_rows = math.gcd(slot_len, key_block)

        def one_piece(piece_index):
            first_key = piece_index * sub_rows
            keys_part = lax.dynamic_slice_in_dim(keys3, first_key, sub_rows, 0)
            values_part = lax.dynamic_slice_in_dim(values3, first_key, sub_rows, 0)
            key_pos = first_key + jnp.arange(sub_rows, dtype=jnp.int32)
            return key_side(
                queries,
                attended_grad3,
                log_total,
                row_delta,
                positions,
                keys_part,
                values_part,
                key_pos,
                length,
            )

        pieces_out = lax.map(one_piece, jnp.arange(slot_len // sub_rows, dtype=jnp.int32))
        key_value_parts.append(
            pieces_out.reshape(slot_len, 2 * model_width).astype(jnp.bfloat16)
        )
        later_parts.append((residual_grad, query_grad))
        micro_grads = (grad_outproj, grad_up, grad_down, gain_two, bias_two)
        totals = (
            micro_grads
            if totals is None
            else tuple((former + latter for former, latter in zip(totals, micro_grads)))
        )
    key_value_all = lax.psum_scatter(
        jnp.stack(key_value_parts), "seq", scatter_dimension=1, tiled=True
    ).astype(jnp.float32)

    input_grads = []
    first_totals = None
    for micro in range(batches):
        inputs, first_low, queries = forward_parts[micro]
        residual_grad, query_grad = later_parts[micro]
        key_grad = key_value_all[micro, :, :model_width]
        value_grad = key_value_all[micro, :, model_width:]
        qkv_low = jnp.concatenate(
            [
                rotate(query_grad.reshape(row_count, model_width), cosine_part, -sine_part),
                rotate(key_grad, cosine_part, -sine_part),
                value_grad,
            ],
            axis=1,
        ).astype(jnp.bfloat16)
        grad_qkv = jnp.einsum("rd,rc->dc", first_low, qkv_low, preferred_element_type=jnp.float32)
        first_grad = jnp.einsum("rc,dc->rd", qkv_low, full_qkv, preferred_element_type=jnp.float32)
        _, first_pullback = jax.vjp(layer_norm, inputs, norm_gains[:, 0], norm_biases[:, 0])
        input_part, gain_one, bias_one = first_pullback(first_grad)
        input_grads.append((residual_grad + input_part).astype(jnp.bfloat16))
        micro_first = (grad_qkv, gain_one, bias_one)
        first_totals = (
            micro_first
            if first_totals is None
            else tuple((former + latter for former, latter in zip(first_totals, micro_first)))
        )
    grad_outproj, grad_up, grad_down, gain_two, bias_two = totals
    grad_qkv, gain_one, bias_one = first_totals
    packed_grads = jnp.concatenate(
        [
            grad_qkv,
            grad_outproj,
            grad_up,
            grad_down.reshape(model_width, ff_width),
            jnp.stack([gain_one, gain_two], axis=1),
            jnp.stack([bias_one, bias_two], axis=1),
            jnp.zeros((model_width, lane_pad), jnp.float32),
        ],
        axis=1,
    )
    device_count = model_width // shard_rows
    scattered = lax.psum_scatter(
        packed_grads.reshape(device_count, shard_rows, offsets[-1]),
        ("seq", "fsdp"),
        scatter_dimension=0,
        tiled=False,
    )
    owned = pieces(scattered)
    owned = owned[:6]
    owned[3] = owned[3].reshape(-1, model_width)
    depth_total = lax.psum(depth_terms, ("seq", "fsdp"))
    next_input = jnp.stack(next_rows)[:, None]
    grad_input = jnp.stack(input_grads)[:, None]
    grad_history = jnp.stack(history_grads, axis=1)[:, :, None]
    return (next_input, grad_input, grad_history, *owned, depth_total)


def solution(mesh):
    in_specs = (
        P(None, "fsdp", "seq", None),
        P(None, None, "fsdp", "seq", None),
        P(None, "fsdp", "seq", None),
        P(None, "fsdp"),
        P(("seq", "fsdp"), None),
        P(("seq", "fsdp"), None),
        P(("seq", "fsdp"), None),
        P(("seq", "fsdp"), None),
        P(("seq", "fsdp"), None),
        P(("seq", "fsdp"), None),
        P(),
    )
    out_specs = (
        P(None, "fsdp", "seq", None),
        P(None, "fsdp", "seq", None),
        P(None, None, "fsdp", "seq", None),
        P(("seq", "fsdp"), None),
        P(("seq", "fsdp"), None),
        P(("seq", "fsdp"), None),
        P(("seq", "fsdp"), None),
        P(("seq", "fsdp"), None),
        P(("seq", "fsdp"), None),
        P(),
    )
    return jax.shard_map(local, mesh=mesh, in_specs=in_specs, out_specs=out_specs, check_vma=False)
```

```python
from functools import partial
import math

import jax
import jax.numpy as jnp
from jax import lax
from jax.sharding import PartitionSpec as P

HEADS = 12
HEAD = 64


epsilon = 1e-05
masked_value = -1e30


def layer_norm(values, gain_vector, bias_vector):
    center = values - jnp.mean(values, axis=-1, keepdims=True)
    spread = jnp.mean(center * center, axis=-1, keepdims=True)
    return center * lax.rsqrt(spread + epsilon) * gain_vector + bias_vector


def rotary_tables(positions):
    half_width = HEAD // 2
    frequencies = 10000.0 ** (-jnp.arange(half_width, dtype=jnp.float32) / half_width)
    angles = positions.astype(jnp.float32)[:, None] * frequencies[None, :]
    return (jnp.cos(angles)[:, None, :], jnp.sin(angles)[:, None, :])


def rotate(values, cosine_part, sine_part):
    row_count = values.shape[0]
    shaped = values.reshape(row_count, HEADS, HEAD)
    half_width = HEAD // 2
    first_half = shaped[..., :half_width]
    second_half = shaped[..., half_width:]
    turned = jnp.concatenate(
        [
            first_half * cosine_part - second_half * sine_part,
            second_half * cosine_part + first_half * sine_part,
        ],
        axis=-1,
    )
    return turned.reshape(row_count, HEADS * HEAD)


def block_scores(queries3, keys3, query_pos, key_pos, length):
    scores = jnp.einsum(
        "rhd,khd->hrk", queries3, keys3, preferred_element_type=jnp.float32
    ) * HEAD ** (-0.5)
    allowed = (key_pos[None, :] <= query_pos[:, None]) & (key_pos[None, :] < length)
    return (scores, allowed[None])


def row_totals(queries3, keys3, query_pos, length, key_block):
    row_count = queries3.shape[0]

    def row_advance(state, block_index):
        running_top, running_sum = state
        first_key = block_index * key_block
        keys_part = lax.dynamic_slice_in_dim(keys3, first_key, key_block, 0)
        key_pos = first_key + jnp.arange(key_block, dtype=jnp.int32)
        scores, allowed = block_scores(queries3, keys_part, query_pos, key_pos, length)
        masked = jnp.where(allowed, scores, masked_value)
        new_top = jnp.maximum(running_top, jnp.max(masked, axis=-1))
        kept_terms = jnp.where(allowed, jnp.exp(masked - new_top[..., None]), 0.0)
        running_sum = running_sum * jnp.exp(running_top - new_top) + jnp.sum(kept_terms, axis=-1)
        return ((new_top, running_sum), None)

    initial = (
        jnp.full((HEADS, row_count), masked_value, jnp.float32),
        jnp.zeros((HEADS, row_count), jnp.float32),
    )
    (row_tops, row_sums), _ = lax.scan(
        row_advance, initial, jnp.arange(keys3.shape[0] // key_block, dtype=jnp.int32)
    )
    return row_tops + jnp.log(row_sums)


def attend(queries3, keys3, values3, query_pos, length, key_block, log_total):

    def attend_advance(running, block_index):
        first_key = block_index * key_block
        keys_part = lax.dynamic_slice_in_dim(keys3, first_key, key_block, 0)
        values_part = lax.dynamic_slice_in_dim(values3, first_key, key_block, 0)
        key_pos = first_key + jnp.arange(key_block, dtype=jnp.int32)
        scores, allowed = block_scores(queries3, keys_part, query_pos, key_pos, length)
        probabilities = jnp.where(allowed, jnp.exp(scores - log_total[..., None]), 0.0).astype(
            jnp.bfloat16
        )
        return (
            running
            + jnp.einsum(
                "hrk,khd->rhd", probabilities, values_part, preferred_element_type=jnp.float32
            ),
            None,
        )

    initial = jnp.zeros(queries3.shape, jnp.float32)
    result, _ = lax.scan(
        attend_advance, initial, jnp.arange(keys3.shape[0] // key_block, dtype=jnp.int32)
    )
    return result


def query_grads(
    queries3, grads3, keys3, values3, query_pos, length, key_block, log_total, row_delta
):

    def query_advance(running, block_index):
        first_key = block_index * key_block
        keys_part = lax.dynamic_slice_in_dim(keys3, first_key, key_block, 0)
        values_part = lax.dynamic_slice_in_dim(values3, first_key, key_block, 0)
        key_pos = first_key + jnp.arange(key_block, dtype=jnp.int32)
        scores, allowed = block_scores(queries3, keys_part, query_pos, key_pos, length)
        probabilities = jnp.where(allowed, jnp.exp(scores - log_total[..., None]), 0.0)
        prob_grad = jnp.einsum(
            "rhd,khd->hrk", grads3, values_part, preferred_element_type=jnp.float32
        )
        score_low = (probabilities * (prob_grad - row_delta[..., None])).astype(jnp.bfloat16)
        return (
            running
            + jnp.einsum("hrk,khd->rhd", score_low, keys_part, preferred_element_type=jnp.float32),
            None,
        )

    initial = jnp.zeros(queries3.shape, jnp.float32)
    result, _ = lax.scan(
        query_advance, initial, jnp.arange(keys3.shape[0] // key_block, dtype=jnp.int32)
    )
    return result * HEAD ** (-0.5)


def key_side(queries3, grads3, log_part, delta_part, query_pos, keys3, values3, key_pos, length):
    key_count = keys3.shape[0]
    scores, allowed = block_scores(queries3, keys3, query_pos, key_pos, length)
    probabilities = jnp.where(allowed, jnp.exp(scores - log_part[..., None]), 0.0)
    prob_grad = jnp.einsum("rhd,khd->hrk", grads3, values3, preferred_element_type=jnp.float32)
    score_low = (probabilities * (prob_grad - delta_part[..., None])).astype(jnp.bfloat16)
    value_grad = jnp.einsum(
        "hrk,rhd->khd",
        probabilities.astype(jnp.bfloat16),
        grads3,
        preferred_element_type=jnp.float32,
    )
    key_grad = jnp.einsum(
        "hrk,rhd->khd", score_low, queries3, preferred_element_type=jnp.float32
    ) * HEAD ** (-0.5)
    return jnp.concatenate(
        [key_grad.reshape(key_count, HEADS * HEAD), value_grad.reshape(key_count, HEADS * HEAD)],
        axis=1,
    )


def local(
    layer_input,
    history,
    cotangent,
    lengths,
    w_qkv,
    w_out,
    w_up,
    w_down,
    ln_gains,
    ln_biases,
    depth_weights,
):
    batches = layer_input.shape[0]
    row_count = layer_input.shape[2]
    model_width = layer_input.shape[3]
    ff_width = w_up.shape[1]
    shard_rows = w_qkv.shape[0]
    slot_len = row_count * lax.axis_size("seq")
    key_block = min(1024, slot_len)
    positions = lax.axis_index("seq") * row_count + jnp.arange(row_count, dtype=jnp.int32)
    cosine_part, sine_part = rotary_tables(positions)
    gelu_tanh = partial(jax.nn.gelu, approximate=True)
    lane_pad = 128 - 4
    widths = (3 * model_width, model_width, ff_width, ff_width, 2, 2, lane_pad)
    offsets = [0]
    for width in widths:
        offsets.append(offsets[-1] + width)

    def pieces(packed_rows):
        return [packed_rows[:, offsets[i] : offsets[i + 1]] for i in range(len(widths))]

    packed = jnp.concatenate(
        [
            w_qkv,
            w_out,
            w_up,
            w_down.reshape(shard_rows, ff_width),
            ln_gains,
            ln_biases,
            jnp.zeros((shard_rows, lane_pad), w_qkv.dtype),
        ],
        axis=1,
    )
    gathered = lax.all_gather(packed, ("seq", "fsdp"), axis=0, tiled=True)
    full_qkv, full_out, full_up, down_rows, gain_rows, bias_rows, _ = pieces(gathered)
    full_down = down_rows.reshape(ff_width, model_width)
    norm_gains = gain_rows.astype(jnp.float32)
    norm_biases = bias_rows.astype(jnp.float32)

    depth_terms = jnp.zeros((5,), jnp.float32)
    forward_parts = []
    own_kv = []
    for micro in range(batches):
        inputs = layer_input[micro, 0].astype(jnp.float32)
        first_low = layer_norm(inputs, norm_gains[:, 0], norm_biases[:, 0]).astype(jnp.bfloat16)
        projected = jnp.dot(first_low, full_qkv, preferred_element_type=jnp.float32)
        queries = (
            rotate(projected[:, :model_width], cosine_part, sine_part)
            .astype(jnp.bfloat16)
            .reshape(row_count, HEADS, HEAD)
        )
        keys_own = rotate(
            projected[:, model_width : 2 * model_width], cosine_part, sine_part
        ).astype(jnp.bfloat16)
        values_own = projected[:, 2 * model_width :].astype(jnp.bfloat16)
        forward_parts.append((inputs, first_low, queries))
        own_kv.append(jnp.concatenate([keys_own, values_own], axis=1))
    kv_all = lax.all_gather(jnp.stack(own_kv, axis=1), "seq", axis=0, tiled=True)

    key_value_parts = []
    later_parts = []
    totals = None
    next_rows = []
    history_grads = []
    for micro in range(batches):
        inputs, first_low, queries = forward_parts[micro]
        keys3 = kv_all[:, micro, :model_width].reshape(slot_len, HEADS, HEAD)
        values3 = kv_all[:, micro, model_width:].reshape(slot_len, HEADS, HEAD)
        length = lengths[micro, 0]
        usable = (positions < length)[:, None]
        earlier = history[:, micro, 0].astype(jnp.float32)
        grad_next = jnp.where(usable, cotangent[micro, 0].astype(jnp.float32), 0.0)
        log_total = row_totals(queries, keys3, positions, length, key_block)
        attended = attend(queries, keys3, values3, positions, length, key_block, log_total)
        attended_low = attended.reshape(row_count, model_width).astype(jnp.bfloat16)
        residual = inputs + jnp.dot(attended_low, full_out, preferred_element_type=jnp.float32)
        second_low = layer_norm(residual, norm_gains[:, 1], norm_biases[:, 1]).astype(jnp.bfloat16)
        hidden = jnp.dot(second_low, full_up, preferred_element_type=jnp.float32)
        hidden_low = gelu_tanh(hidden).astype(jnp.bfloat16)
        block_out = residual + jnp.dot(hidden_low, full_down, preferred_element_type=jnp.float32)
        combined = depth_weights[4] * block_out + jnp.einsum(
            "j,jrd->rd", depth_weights[:4], earlier
        )
        next_rows.append(combined.astype(jnp.bfloat16))
        history_grads.append((depth_weights[:4, None, None] * grad_next[None]).astype(jnp.bfloat16))
        depth_terms = depth_terms + jnp.concatenate(
            [jnp.einsum("jrd,rd->j", earlier, grad_next), jnp.sum(block_out * grad_next)[None]]
        )
        out_grad = depth_weights[4] * grad_next
        out_low = out_grad.astype(jnp.bfloat16)
        grad_down = jnp.einsum("rf,rd->fd", hidden_low, out_low, preferred_element_type=jnp.float32)
        hidden_grad = jnp.einsum(
            "rd,fd->rf", out_low, full_down, preferred_element_type=jnp.float32
        )
        _, gelu_pullback = jax.vjp(gelu_tanh, hidden)
        up_low = gelu_pullback(hidden_grad)[0].astype(jnp.bfloat16)
        grad_up = jnp.einsum("rd,rf->df", second_low, up_low, preferred_element_type=jnp.float32)
        second_grad = jnp.einsum("rf,df->rd", up_low, full_up, preferred_element_type=jnp.float32)
        _, second_pullback = jax.vjp(layer_norm, residual, norm_gains[:, 1], norm_biases[:, 1])
        residual_part, gain_two, bias_two = second_pullback(second_grad)
        residual_grad = out_grad + residual_part
        branch_low = residual_grad.astype(jnp.bfloat16)
        grad_outproj = jnp.einsum(
            "rc,rd->cd", attended_low, branch_low, preferred_element_type=jnp.float32
        )
        attended_grad = jnp.einsum(
            "rd,cd->rc", branch_low, full_out, preferred_element_type=jnp.float32
        ).astype(jnp.bfloat16)
        attended_grad3 = attended_grad.reshape(row_count, HEADS, HEAD)
        row_delta = jnp.einsum("rhd,rhd->hr", attended_grad3.astype(jnp.float32), attended)
        query_grad = query_grads(
            queries,
            attended_grad3,
            keys3,
            values3,
            positions,
            length,
            key_block,
            log_total,
            row_delta,
        )
        sub_rows = math.gcd(slot_len, key_block)

        def one_piece(piece_index):
            first_key = piece_index * sub_rows
            keys_part = lax.dynamic_slice_in_dim(keys3, first_key, sub_rows, 0)
            values_part = lax.dynamic_slice_in_dim(values3, first_key, sub_rows, 0)
            key_pos = first_key + jnp.arange(sub_rows, dtype=jnp.int32)
            return key_side(
                queries,
                attended_grad3,
                log_total,
                row_delta,
                positions,
                keys_part,
                values_part,
                key_pos,
                length,
            )

        pieces_out = lax.map(one_piece, jnp.arange(slot_len // sub_rows, dtype=jnp.int32))
        key_value_parts.append(
            pieces_out.reshape(slot_len, 2 * model_width).astype(jnp.bfloat16)
        )
        later_parts.append((residual_grad, query_grad))
        micro_grads = (grad_outproj, grad_up, grad_down, gain_two, bias_two)
        totals = (
            micro_grads
            if totals is None
            else tuple((former + latter for former, latter in zip(totals, micro_grads)))
        )
    key_value_all = lax.psum_scatter(
        jnp.stack(key_value_parts, axis=1), "seq", scatter_dimension=0, tiled=True
    ).astype(jnp.float32)

    input_grads = []
    first_totals = None
    for micro in range(batches):
        inputs, first_low, queries = forward_parts[micro]
        residual_grad, query_grad = later_parts[micro]
        key_grad = key_value_all[:, micro, :model_width]
        value_grad = key_value_all[:, micro, model_width:]
        qkv_low = jnp.concatenate(
            [
                rotate(query_grad.reshape(row_count, model_width), cosine_part, -sine_part),
                rotate(key_grad, cosine_part, -sine_part),
                value_grad,
            ],
            axis=1,
        ).astype(jnp.bfloat16)
        grad_qkv = jnp.einsum("rd,rc->dc", first_low, qkv_low, preferred_element_type=jnp.float32)
        first_grad = jnp.einsum("rc,dc->rd", qkv_low, full_qkv, preferred_element_type=jnp.float32)
        _, first_pullback = jax.vjp(layer_norm, inputs, norm_gains[:, 0], norm_biases[:, 0])
        input_part, gain_one, bias_one = first_pullback(first_grad)
        input_grads.append((residual_grad + input_part).astype(jnp.bfloat16))
        micro_first = (grad_qkv, gain_one, bias_one)
        first_totals = (
            micro_first
            if first_totals is None
            else tuple((former + latter for former, latter in zip(first_totals, micro_first)))
        )
    grad_outproj, grad_up, grad_down, gain_two, bias_two = totals
    grad_qkv, gain_one, bias_one = first_totals
    packed_grads = jnp.concatenate(
        [
            grad_qkv,
            grad_outproj,
            grad_up,
            grad_down.reshape(model_width, ff_width),
            jnp.stack([gain_one, gain_two], axis=1),
            jnp.stack([bias_one, bias_two], axis=1),
            jnp.zeros((model_width, lane_pad), jnp.float32),
        ],
        axis=1,
    )
    device_count = model_width // shard_rows
    scattered = lax.psum_scatter(
        packed_grads.astype(jnp.bfloat16).reshape(device_count, shard_rows, offsets[-1]),
        ("seq", "fsdp"),
        scatter_dimension=0,
        tiled=False,
    )
    owned = pieces(scattered.astype(jnp.float32))
    owned = owned[:6]
    owned[3] = owned[3].reshape(-1, model_width)
    depth_total = lax.psum(depth_terms, ("seq", "fsdp"))
    next_input = jnp.stack(next_rows)[:, None]
    grad_input = jnp.stack(input_grads)[:, None]
    grad_history = jnp.stack(history_grads, axis=1)[:, :, None]
    return (next_input, grad_input, grad_history, *owned, depth_total)


def solution(mesh):
    in_specs = (
        P(None, "fsdp", "seq", None),
        P(None, None, "fsdp", "seq", None),
        P(None, "fsdp", "seq", None),
        P(None, "fsdp"),
        P(("seq", "fsdp"), None),
        P(("seq", "fsdp"), None),
        P(("seq", "fsdp"), None),
        P(("seq", "fsdp"), None),
        P(("seq", "fsdp"), None),
        P(("seq", "fsdp"), None),
        P(),
    )
    out_specs = (
        P(None, "fsdp", "seq", None),
        P(None, "fsdp", "seq", None),
        P(None, None, "fsdp", "seq", None),
        P(("seq", "fsdp"), None),
        P(("seq", "fsdp"), None),
        P(("seq", "fsdp"), None),
        P(("seq", "fsdp"), None),
        P(("seq", "fsdp"), None),
        P(("seq", "fsdp"), None),
        P(),
    )
    return jax.shard_map(local, mesh=mesh, in_specs=in_specs, out_specs=out_specs, check_vma=False)
```

```python
from functools import partial
import math

import jax
import jax.numpy as jnp
from jax import lax
from jax.sharding import PartitionSpec as P

HEADS = 12
HEAD = 64


epsilon = 1e-05
masked_value = -1e30


def layer_norm(values, gain_vector, bias_vector):
    center = values - jnp.mean(values, axis=-1, keepdims=True)
    spread = jnp.mean(center * center, axis=-1, keepdims=True)
    return center * lax.rsqrt(spread + epsilon) * gain_vector + bias_vector


def rotary_tables(positions):
    half_width = HEAD // 2
    frequencies = 10000.0 ** (-jnp.arange(half_width, dtype=jnp.float32) / half_width)
    angles = positions.astype(jnp.float32)[:, None] * frequencies[None, :]
    return (jnp.cos(angles)[:, None, :], jnp.sin(angles)[:, None, :])


def rotate(values, cosine_part, sine_part):
    row_count = values.shape[0]
    shaped = values.reshape(row_count, HEADS, HEAD)
    half_width = HEAD // 2
    first_half = shaped[..., :half_width]
    second_half = shaped[..., half_width:]
    turned = jnp.concatenate(
        [
            first_half * cosine_part - second_half * sine_part,
            second_half * cosine_part + first_half * sine_part,
        ],
        axis=-1,
    )
    return turned.reshape(row_count, HEADS * HEAD)


def block_scores(queries3, keys3, query_pos, key_pos, length):
    scores = jnp.einsum(
        "rhd,khd->hrk", queries3, keys3, preferred_element_type=jnp.float32
    ) * HEAD ** (-0.5)
    allowed = (key_pos[None, :] <= query_pos[:, None]) & (key_pos[None, :] < length)
    return (scores, allowed[None])


def row_totals(queries3, keys3, query_pos, length, key_block):
    row_count = queries3.shape[0]

    def row_advance(state, block_index):
        running_top, running_sum = state
        first_key = block_index * key_block
        keys_part = lax.dynamic_slice_in_dim(keys3, first_key, key_block, 0)
        key_pos = first_key + jnp.arange(key_block, dtype=jnp.int32)
        scores, allowed = block_scores(queries3, keys_part, query_pos, key_pos, length)
        masked = jnp.where(allowed, scores, masked_value)
        new_top = jnp.maximum(running_top, jnp.max(masked, axis=-1))
        kept_terms = jnp.where(allowed, jnp.exp(masked - new_top[..., None]), 0.0)
        running_sum = running_sum * jnp.exp(running_top - new_top) + jnp.sum(kept_terms, axis=-1)
        return ((new_top, running_sum), None)

    initial = (
        jnp.full((HEADS, row_count), masked_value, jnp.float32),
        jnp.zeros((HEADS, row_count), jnp.float32),
    )
    (row_tops, row_sums), _ = lax.scan(
        row_advance, initial, jnp.arange(keys3.shape[0] // key_block, dtype=jnp.int32)
    )
    return row_tops + jnp.log(row_sums)


def attend(queries3, keys3, values3, query_pos, length, key_block, log_total):

    def attend_advance(running, block_index):
        first_key = block_index * key_block
        keys_part = lax.dynamic_slice_in_dim(keys3, first_key, key_block, 0)
        values_part = lax.dynamic_slice_in_dim(values3, first_key, key_block, 0)
        key_pos = first_key + jnp.arange(key_block, dtype=jnp.int32)
        scores, allowed = block_scores(queries3, keys_part, query_pos, key_pos, length)
        probabilities = jnp.where(allowed, jnp.exp(scores - log_total[..., None]), 0.0).astype(
            jnp.bfloat16
        )
        return (
            running
            + jnp.einsum(
                "hrk,khd->rhd", probabilities, values_part, preferred_element_type=jnp.float32
            ),
            None,
        )

    initial = jnp.zeros(queries3.shape, jnp.float32)
    result, _ = lax.scan(
        attend_advance, initial, jnp.arange(keys3.shape[0] // key_block, dtype=jnp.int32)
    )
    return result


def query_grads(
    queries3, grads3, keys3, values3, query_pos, length, key_block, log_total, row_delta
):

    def query_advance(running, block_index):
        first_key = block_index * key_block
        keys_part = lax.dynamic_slice_in_dim(keys3, first_key, key_block, 0)
        values_part = lax.dynamic_slice_in_dim(values3, first_key, key_block, 0)
        key_pos = first_key + jnp.arange(key_block, dtype=jnp.int32)
        scores, allowed = block_scores(queries3, keys_part, query_pos, key_pos, length)
        probabilities = jnp.where(allowed, jnp.exp(scores - log_total[..., None]), 0.0)
        prob_grad = jnp.einsum(
            "rhd,khd->hrk", grads3, values_part, preferred_element_type=jnp.float32
        )
        score_low = (probabilities * (prob_grad - row_delta[..., None])).astype(jnp.bfloat16)
        return (
            running
            + jnp.einsum("hrk,khd->rhd", score_low, keys_part, preferred_element_type=jnp.float32),
            None,
        )

    initial = jnp.zeros(queries3.shape, jnp.float32)
    result, _ = lax.scan(
        query_advance, initial, jnp.arange(keys3.shape[0] // key_block, dtype=jnp.int32)
    )
    return result * HEAD ** (-0.5)


def key_side(queries3, grads3, log_part, delta_part, query_pos, keys3, values3, key_pos, length):
    key_count = keys3.shape[0]
    scores, allowed = block_scores(queries3, keys3, query_pos, key_pos, length)
    probabilities = jnp.where(allowed, jnp.exp(scores - log_part[..., None]), 0.0)
    prob_grad = jnp.einsum("rhd,khd->hrk", grads3, values3, preferred_element_type=jnp.float32)
    score_low = (probabilities * (prob_grad - delta_part[..., None])).astype(jnp.bfloat16)
    value_grad = jnp.einsum(
        "hrk,rhd->khd",
        probabilities.astype(jnp.bfloat16),
        grads3,
        preferred_element_type=jnp.float32,
    )
    key_grad = jnp.einsum(
        "hrk,rhd->khd", score_low, queries3, preferred_element_type=jnp.float32
    ) * HEAD ** (-0.5)
    return jnp.concatenate(
        [key_grad.reshape(key_count, HEADS * HEAD), value_grad.reshape(key_count, HEADS * HEAD)],
        axis=1,
    )


def slot_attention(queries3, keys3, values3, query_pos, length):
    key_pos = jnp.arange(keys3.shape[0], dtype=jnp.int32)
    scores, allowed = block_scores(queries3, keys3, query_pos, key_pos, length)
    masked = jnp.where(allowed, scores, masked_value)
    top = jnp.max(masked, axis=-1)
    kept_terms = jnp.where(allowed, jnp.exp(masked - top[..., None]), 0.0)
    log_total = top + jnp.log(jnp.sum(kept_terms, axis=-1))
    probabilities = jnp.where(allowed, jnp.exp(scores - log_total[..., None]), 0.0)
    probabilities_low = probabilities.astype(jnp.bfloat16)
    attended = jnp.einsum(
        "hrk,khd->rhd", probabilities_low, values3, preferred_element_type=jnp.float32
    )
    return attended, probabilities, probabilities_low


def slot_attention_grads(queries3, keys3, values3, grads3, attended, probabilities, probabilities_low):
    prob_grad = jnp.einsum("rhd,khd->hrk", grads3, values3, preferred_element_type=jnp.float32)
    row_delta = jnp.einsum("rhd,rhd->hr", grads3.astype(jnp.float32), attended)
    score_low = (probabilities * (prob_grad - row_delta[..., None])).astype(jnp.bfloat16)
    query_grad = jnp.einsum(
        "hrk,khd->rhd", score_low, keys3, preferred_element_type=jnp.float32
    ) * HEAD ** (-0.5)
    key_grad = jnp.einsum(
        "hrk,rhd->khd", score_low, queries3, preferred_element_type=jnp.float32
    ) * HEAD ** (-0.5)
    value_grad = jnp.einsum(
        "hrk,rhd->khd", probabilities_low, grads3, preferred_element_type=jnp.float32
    )
    return query_grad, key_grad, value_grad


def local(
    layer_input,
    history,
    cotangent,
    lengths,
    w_qkv,
    w_out,
    w_up,
    w_down,
    ln_gains,
    ln_biases,
    depth_weights,
):
    batches = layer_input.shape[0]
    row_count = layer_input.shape[2]
    model_width = layer_input.shape[3]
    ff_width = w_up.shape[1]
    shard_rows = w_qkv.shape[0]
    all_rows = batches * row_count
    slot_len = row_count * lax.axis_size("seq")
    positions = lax.axis_index("seq") * row_count + jnp.arange(row_count, dtype=jnp.int32)
    cosine_part, sine_part = rotary_tables(jnp.tile(positions, batches))
    gelu_tanh = partial(jax.nn.gelu, approximate=True)
    lane_pad = 128 - 4
    widths = (3 * model_width, model_width, ff_width, ff_width, 2, 2, lane_pad)
    offsets = [0]
    for width in widths:
        offsets.append(offsets[-1] + width)

    def pieces(packed_rows):
        return [packed_rows[:, offsets[i] : offsets[i + 1]] for i in range(len(widths))]

    packed = jnp.concatenate(
        [
            w_qkv,
            w_out,
            w_up,
            w_down.reshape(shard_rows, ff_width),
            ln_gains,
            ln_biases,
            jnp.zeros((shard_rows, lane_pad), w_qkv.dtype),
        ],
        axis=1,
    )
    gathered = lax.all_gather(packed, ("seq", "fsdp"), axis=0, tiled=True)
    full_qkv, full_out, full_up, down_rows, gain_rows, bias_rows, _ = pieces(gathered)
    full_down = down_rows.reshape(ff_width, model_width)
    norm_gains = gain_rows.astype(jnp.float32)
    norm_biases = bias_rows.astype(jnp.float32)

    slot_lengths = lengths[:, 0]
    inputs = layer_input[:, 0].reshape(all_rows, model_width).astype(jnp.float32)
    first_low = layer_norm(inputs, norm_gains[:, 0], norm_biases[:, 0]).astype(jnp.bfloat16)
    projected = jnp.dot(first_low, full_qkv, preferred_element_type=jnp.float32)
    queries = rotate(projected[:, :model_width], cosine_part, sine_part).astype(jnp.bfloat16)
    keys_own = rotate(
        projected[:, model_width : 2 * model_width], cosine_part, sine_part
    ).astype(jnp.bfloat16)
    values_own = projected[:, 2 * model_width :].astype(jnp.bfloat16)
    own_kv = jnp.concatenate([keys_own, values_own], axis=1).reshape(
        batches, row_count, 2 * model_width
    )
    kv_all = lax.all_gather(jnp.swapaxes(own_kv, 0, 1), "seq", axis=0, tiled=True)
    keys4 = jnp.swapaxes(kv_all[:, :, :model_width], 0, 1).reshape(batches, slot_len, HEADS, HEAD)
    values4 = jnp.swapaxes(kv_all[:, :, model_width:], 0, 1).reshape(
        batches, slot_len, HEADS, HEAD
    )
    queries4 = queries.reshape(batches, row_count, HEADS, HEAD)
    attended4, probabilities, probabilities_low = jax.vmap(
        slot_attention, in_axes=(0, 0, 0, None, 0)
    )(queries4, keys4, values4, positions, slot_lengths)
    attended_low = attended4.reshape(all_rows, model_width).astype(jnp.bfloat16)
    residual = inputs + jnp.dot(attended_low, full_out, preferred_element_type=jnp.float32)
    second_low = layer_norm(residual, norm_gains[:, 1], norm_biases[:, 1]).astype(jnp.bfloat16)
    hidden = jnp.dot(second_low, full_up, preferred_element_type=jnp.float32)
    hidden_low = gelu_tanh(hidden).astype(jnp.bfloat16)
    block_out = residual + jnp.dot(hidden_low, full_down, preferred_element_type=jnp.float32)
    earlier = history[:, :, 0].reshape(4, all_rows, model_width).astype(jnp.float32)
    usable = (positions[None, :] < slot_lengths[:, None]).reshape(all_rows, 1)
    grad_next = jnp.where(
        usable, cotangent[:, 0].reshape(all_rows, model_width).astype(jnp.float32), 0.0
    )
    combined = depth_weights[4] * block_out + jnp.einsum("j,jrd->rd", depth_weights[:4], earlier)
    next_input = combined.astype(jnp.bfloat16).reshape(batches, 1, row_count, model_width)
    grad_history = (depth_weights[:4, None, None] * grad_next[None]).astype(jnp.bfloat16)
    grad_history = grad_history.reshape(4, batches, 1, row_count, model_width)
    depth_terms = jnp.concatenate(
        [jnp.einsum("jrd,rd->j", earlier, grad_next), jnp.sum(block_out * grad_next)[None]]
    )
    out_grad = depth_weights[4] * grad_next
    out_low = out_grad.astype(jnp.bfloat16)
    hidden_grad = jnp.einsum("rd,fd->rf", out_low, full_down, preferred_element_type=jnp.float32)
    _, gelu_pullback = jax.vjp(gelu_tanh, hidden)
    up_low = gelu_pullback(hidden_grad)[0].astype(jnp.bfloat16)
    second_grad = jnp.einsum("rf,df->rd", up_low, full_up, preferred_element_type=jnp.float32)
    _, second_pullback = jax.vjp(layer_norm, residual, norm_gains[:, 1], norm_biases[:, 1])
    residual_part, gain_two, bias_two = second_pullback(second_grad)
    residual_grad = out_grad + residual_part
    branch_low = residual_grad.astype(jnp.bfloat16)
    attended_grad = jnp.einsum(
        "rd,cd->rc", branch_low, full_out, preferred_element_type=jnp.float32
    ).astype(jnp.bfloat16)
    query_grad4, key_grad4, value_grad4 = jax.vmap(slot_attention_grads)(
        queries4,
        keys4,
        values4,
        attended_grad.reshape(batches, row_count, HEADS, HEAD),
        attended4,
        probabilities,
        probabilities_low,
    )
    key_value_parts = jnp.concatenate(
        [
            key_grad4.reshape(batches, slot_len, model_width),
            value_grad4.reshape(batches, slot_len, model_width),
        ],
        axis=2,
    ).astype(jnp.bfloat16)
    key_value_all = lax.psum_scatter(
        jnp.swapaxes(key_value_parts, 0, 1), "seq", scatter_dimension=0, tiled=True
    )
    key_value_all = jnp.swapaxes(key_value_all, 0, 1).reshape(all_rows, 2 * model_width)
    key_value_all = key_value_all.astype(jnp.float32)
    grad_down = jnp.einsum("rf,rd->fd", hidden_low, out_low, preferred_element_type=jnp.float32)
    grad_up = jnp.einsum("rd,rf->df", second_low, up_low, preferred_element_type=jnp.float32)
    grad_outproj = jnp.einsum(
        "rc,rd->cd", attended_low, branch_low, preferred_element_type=jnp.float32
    )
    qkv_low = jnp.concatenate(
        [
            rotate(query_grad4.reshape(all_rows, model_width), cosine_part, -sine_part),
            rotate(key_value_all[:, :model_width], cosine_part, -sine_part),
            key_value_all[:, model_width:],
        ],
        axis=1,
    ).astype(jnp.bfloat16)
    grad_qkv = jnp.einsum("rd,rc->dc", first_low, qkv_low, preferred_element_type=jnp.float32)
    first_grad = jnp.einsum("rc,dc->rd", qkv_low, full_qkv, preferred_element_type=jnp.float32)
    _, first_pullback = jax.vjp(layer_norm, inputs, norm_gains[:, 0], norm_biases[:, 0])
    input_part, gain_one, bias_one = first_pullback(first_grad)
    grad_input = (residual_grad + input_part).astype(jnp.bfloat16)
    grad_input = grad_input.reshape(batches, 1, row_count, model_width)
    packed_grads = jnp.concatenate(
        [
            grad_qkv.astype(jnp.bfloat16),
            grad_outproj.astype(jnp.bfloat16),
            grad_up.astype(jnp.bfloat16),
            grad_down.reshape(model_width, ff_width).astype(jnp.bfloat16),
            jnp.stack([gain_one, gain_two], axis=1).astype(jnp.bfloat16),
            jnp.stack([bias_one, bias_two], axis=1).astype(jnp.bfloat16),
            jnp.zeros((model_width, lane_pad), jnp.bfloat16),
        ],
        axis=1,
    )
    device_count = model_width // shard_rows
    scattered = lax.psum_scatter(
        packed_grads.reshape(device_count, shard_rows, offsets[-1]),
        ("seq", "fsdp"),
        scatter_dimension=0,
        tiled=False,
    )
    owned = pieces(scattered.astype(jnp.float32))[:6]
    owned[3] = owned[3].reshape(-1, model_width)
    depth_total = lax.psum(depth_terms, ("seq", "fsdp"))
    return (next_input, grad_input, grad_history, *owned, depth_total)


def solution(mesh):
    in_specs = (
        P(None, "fsdp", "seq", None),
        P(None, None, "fsdp", "seq", None),
        P(None, "fsdp", "seq", None),
        P(None, "fsdp"),
        P(("seq", "fsdp"), None),
        P(("seq", "fsdp"), None),
        P(("seq", "fsdp"), None),
        P(("seq", "fsdp"), None),
        P(("seq", "fsdp"), None),
        P(("seq", "fsdp"), None),
        P(),
    )
    out_specs = (
        P(None, "fsdp", "seq", None),
        P(None, "fsdp", "seq", None),
        P(None, None, "fsdp", "seq", None),
        P(("seq", "fsdp"), None),
        P(("seq", "fsdp"), None),
        P(("seq", "fsdp"), None),
        P(("seq", "fsdp"), None),
        P(("seq", "fsdp"), None),
        P(("seq", "fsdp"), None),
        P(),
    )
    return jax.shard_map(local, mesh=mesh, in_specs=in_specs, out_specs=out_specs, check_vma=False)
```

```python
from functools import partial
import math

import jax
import jax.numpy as jnp
from jax import lax
from jax.sharding import PartitionSpec as P

HEADS = 12
HEAD = 64


epsilon = 1e-05
masked_value = -1e30


def layer_norm(values, gain_vector, bias_vector):
    center = values - jnp.mean(values, axis=-1, keepdims=True)
    spread = jnp.mean(center * center, axis=-1, keepdims=True)
    return center * lax.rsqrt(spread + epsilon) * gain_vector + bias_vector


def rotary_tables(positions):
    half_width = HEAD // 2
    frequencies = 10000.0 ** (-jnp.arange(half_width, dtype=jnp.float32) / half_width)
    angles = positions.astype(jnp.float32)[:, None] * frequencies[None, :]
    return (jnp.cos(angles)[:, None, :], jnp.sin(angles)[:, None, :])


def rotate(values, cosine_part, sine_part):
    row_count = values.shape[0]
    shaped = values.reshape(row_count, HEADS, HEAD)
    half_width = HEAD // 2
    first_half = shaped[..., :half_width]
    second_half = shaped[..., half_width:]
    turned = jnp.concatenate(
        [
            first_half * cosine_part - second_half * sine_part,
            second_half * cosine_part + first_half * sine_part,
        ],
        axis=-1,
    )
    return turned.reshape(row_count, HEADS * HEAD)


def block_scores(queries3, keys3, query_pos, key_pos, length):
    scores = jnp.einsum(
        "rhd,khd->hrk", queries3, keys3, preferred_element_type=jnp.float32
    ) * HEAD ** (-0.5)
    allowed = (key_pos[None, :] <= query_pos[:, None]) & (key_pos[None, :] < length)
    return (scores, allowed[None])


def row_totals(queries3, keys3, query_pos, length, key_block):
    row_count = queries3.shape[0]

    def row_advance(state, block_index):
        running_top, running_sum = state
        first_key = block_index * key_block
        keys_part = lax.dynamic_slice_in_dim(keys3, first_key, key_block, 0)
        key_pos = first_key + jnp.arange(key_block, dtype=jnp.int32)
        scores, allowed = block_scores(queries3, keys_part, query_pos, key_pos, length)
        masked = jnp.where(allowed, scores, masked_value)
        new_top = jnp.maximum(running_top, jnp.max(masked, axis=-1))
        kept_terms = jnp.where(allowed, jnp.exp(masked - new_top[..., None]), 0.0)
        running_sum = running_sum * jnp.exp(running_top - new_top) + jnp.sum(kept_terms, axis=-1)
        return ((new_top, running_sum), None)

    initial = (
        jnp.full((HEADS, row_count), masked_value, jnp.float32),
        jnp.zeros((HEADS, row_count), jnp.float32),
    )
    (row_tops, row_sums), _ = lax.scan(
        row_advance, initial, jnp.arange(keys3.shape[0] // key_block, dtype=jnp.int32)
    )
    return row_tops + jnp.log(row_sums)


def attend(queries3, keys3, values3, query_pos, length, key_block, log_total):

    def attend_advance(running, block_index):
        first_key = block_index * key_block
        keys_part = lax.dynamic_slice_in_dim(keys3, first_key, key_block, 0)
        values_part = lax.dynamic_slice_in_dim(values3, first_key, key_block, 0)
        key_pos = first_key + jnp.arange(key_block, dtype=jnp.int32)
        scores, allowed = block_scores(queries3, keys_part, query_pos, key_pos, length)
        probabilities = jnp.where(allowed, jnp.exp(scores - log_total[..., None]), 0.0).astype(
            jnp.bfloat16
        )
        return (
            running
            + jnp.einsum(
                "hrk,khd->rhd", probabilities, values_part, preferred_element_type=jnp.float32
            ),
            None,
        )

    initial = jnp.zeros(queries3.shape, jnp.float32)
    result, _ = lax.scan(
        attend_advance, initial, jnp.arange(keys3.shape[0] // key_block, dtype=jnp.int32)
    )
    return result


def query_grads(
    queries3, grads3, keys3, values3, query_pos, length, key_block, log_total, row_delta
):

    def query_advance(running, block_index):
        first_key = block_index * key_block
        keys_part = lax.dynamic_slice_in_dim(keys3, first_key, key_block, 0)
        values_part = lax.dynamic_slice_in_dim(values3, first_key, key_block, 0)
        key_pos = first_key + jnp.arange(key_block, dtype=jnp.int32)
        scores, allowed = block_scores(queries3, keys_part, query_pos, key_pos, length)
        probabilities = jnp.where(allowed, jnp.exp(scores - log_total[..., None]), 0.0)
        prob_grad = jnp.einsum(
            "rhd,khd->hrk", grads3, values_part, preferred_element_type=jnp.float32
        )
        score_low = (probabilities * (prob_grad - row_delta[..., None])).astype(jnp.bfloat16)
        return (
            running
            + jnp.einsum("hrk,khd->rhd", score_low, keys_part, preferred_element_type=jnp.float32),
            None,
        )

    initial = jnp.zeros(queries3.shape, jnp.float32)
    result, _ = lax.scan(
        query_advance, initial, jnp.arange(keys3.shape[0] // key_block, dtype=jnp.int32)
    )
    return result * HEAD ** (-0.5)


def key_side(queries3, grads3, log_part, delta_part, query_pos, keys3, values3, key_pos, length):
    key_count = keys3.shape[0]
    scores, allowed = block_scores(queries3, keys3, query_pos, key_pos, length)
    probabilities = jnp.where(allowed, jnp.exp(scores - log_part[..., None]), 0.0)
    prob_grad = jnp.einsum("rhd,khd->hrk", grads3, values3, preferred_element_type=jnp.float32)
    score_low = (probabilities * (prob_grad - delta_part[..., None])).astype(jnp.bfloat16)
    value_grad = jnp.einsum(
        "hrk,rhd->khd",
        probabilities.astype(jnp.bfloat16),
        grads3,
        preferred_element_type=jnp.float32,
    )
    key_grad = jnp.einsum(
        "hrk,rhd->khd", score_low, queries3, preferred_element_type=jnp.float32
    ) * HEAD ** (-0.5)
    return jnp.concatenate(
        [key_grad.reshape(key_count, HEADS * HEAD), value_grad.reshape(key_count, HEADS * HEAD)],
        axis=1,
    )


def slot_attention(queries3, keys3, values3, query_pos, length):
    key_pos = jnp.arange(keys3.shape[0], dtype=jnp.int32)
    scores, allowed = block_scores(queries3, keys3, query_pos, key_pos, length)
    masked = jnp.where(allowed, scores, masked_value)
    top = jnp.max(masked, axis=-1)
    kept_terms = jnp.where(allowed, jnp.exp(masked - top[..., None]), 0.0)
    log_total = top + jnp.log(jnp.sum(kept_terms, axis=-1))
    probabilities = jnp.where(allowed, jnp.exp(scores - log_total[..., None]), 0.0)
    probabilities_low = probabilities.astype(jnp.bfloat16)
    attended = jnp.einsum(
        "hrk,khd->rhd", probabilities_low, values3, preferred_element_type=jnp.float32
    )
    return attended, probabilities, probabilities_low


def slot_attention_grads(queries3, keys3, values3, grads3, attended, probabilities, probabilities_low):
    prob_grad = jnp.einsum("rhd,khd->hrk", grads3, values3, preferred_element_type=jnp.float32)
    row_delta = jnp.einsum("rhd,rhd->hr", grads3.astype(jnp.float32), attended)
    score_low = (probabilities * (prob_grad - row_delta[..., None])).astype(jnp.bfloat16)
    query_grad = jnp.einsum(
        "hrk,khd->rhd", score_low, keys3, preferred_element_type=jnp.float32
    ) * HEAD ** (-0.5)
    key_grad = jnp.einsum(
        "hrk,rhd->khd", score_low, queries3, preferred_element_type=jnp.float32
    ) * HEAD ** (-0.5)
    value_grad = jnp.einsum(
        "hrk,rhd->khd", probabilities_low, grads3, preferred_element_type=jnp.float32
    )
    return query_grad, key_grad, value_grad


def local(
    layer_input,
    history,
    cotangent,
    lengths,
    w_qkv,
    w_out,
    w_up,
    w_down,
    ln_gains,
    ln_biases,
    depth_weights,
):
    batches = layer_input.shape[0]
    row_count = layer_input.shape[2]
    model_width = layer_input.shape[3]
    ff_width = w_up.shape[1]
    shard_rows = w_qkv.shape[0]
    all_rows = batches * row_count
    slot_len = row_count * lax.axis_size("seq")
    positions = lax.axis_index("seq") * row_count + jnp.arange(row_count, dtype=jnp.int32)
    cosine_part, sine_part = rotary_tables(jnp.tile(positions, batches))
    gelu_tanh = partial(jax.nn.gelu, approximate=True)
    lane_pad = 128 - 4
    widths = (3 * model_width, model_width, ff_width, ff_width, 2, 2, lane_pad)
    offsets = [0]
    for width in widths:
        offsets.append(offsets[-1] + width)

    def pieces(packed_rows):
        return [packed_rows[:, offsets[i] : offsets[i + 1]] for i in range(len(widths))]

    packed = jnp.concatenate(
        [
            w_qkv,
            w_out,
            w_up,
            w_down.reshape(shard_rows, ff_width),
            ln_gains,
            ln_biases,
            jnp.zeros((shard_rows, lane_pad), w_qkv.dtype),
        ],
        axis=1,
    )
    gathered = lax.all_gather(packed, ("seq", "fsdp"), axis=0, tiled=True)
    full_qkv, full_out, full_up, down_rows, gain_rows, bias_rows, _ = pieces(gathered)
    full_down = down_rows.reshape(ff_width, model_width)
    norm_gains = gain_rows.astype(jnp.float32)
    norm_biases = bias_rows.astype(jnp.float32)

    slot_lengths = lengths[:, 0]
    inputs = layer_input[:, 0].reshape(all_rows, model_width).astype(jnp.float32)
    first_low = layer_norm(inputs, norm_gains[:, 0], norm_biases[:, 0]).astype(jnp.bfloat16)
    projected = jnp.dot(first_low, full_qkv, preferred_element_type=jnp.float32)
    queries = rotate(projected[:, :model_width], cosine_part, sine_part).astype(jnp.bfloat16)
    keys_own = rotate(
        projected[:, model_width : 2 * model_width], cosine_part, sine_part
    ).astype(jnp.bfloat16)
    values_own = projected[:, 2 * model_width :].astype(jnp.bfloat16)
    own_kv = jnp.concatenate([keys_own, values_own], axis=1).reshape(
        batches, row_count, 2 * model_width
    )
    kv_all = lax.all_gather(jnp.swapaxes(own_kv, 0, 1), "seq", axis=0, tiled=True)
    keys4 = jnp.swapaxes(kv_all[:, :, :model_width], 0, 1).reshape(batches, slot_len, HEADS, HEAD)
    values4 = jnp.swapaxes(kv_all[:, :, model_width:], 0, 1).reshape(
        batches, slot_len, HEADS, HEAD
    )
    queries4 = queries.reshape(batches, row_count, HEADS, HEAD)
    attended4, probabilities, probabilities_low = jax.vmap(
        slot_attention, in_axes=(0, 0, 0, None, 0)
    )(queries4, keys4, values4, positions, slot_lengths)
    attended_low = attended4.reshape(all_rows, model_width).astype(jnp.bfloat16)
    residual = inputs + jnp.dot(attended_low, full_out, preferred_element_type=jnp.float32)
    second_low = layer_norm(residual, norm_gains[:, 1], norm_biases[:, 1]).astype(jnp.bfloat16)
    hidden = jnp.dot(second_low, full_up, preferred_element_type=jnp.float32)
    hidden_low = gelu_tanh(hidden).astype(jnp.bfloat16)
    block_out = residual + jnp.dot(hidden_low, full_down, preferred_element_type=jnp.float32)
    earlier = history[:, :, 0].reshape(4, all_rows, model_width).astype(jnp.float32)
    usable = (positions[None, :] < slot_lengths[:, None]).reshape(all_rows, 1)
    grad_next = jnp.where(
        usable, cotangent[:, 0].reshape(all_rows, model_width).astype(jnp.float32), 0.0
    )
    combined = depth_weights[4] * block_out + jnp.einsum("j,jrd->rd", depth_weights[:4], earlier)
    next_input = combined.astype(jnp.bfloat16).reshape(batches, 1, row_count, model_width)
    grad_history = (depth_weights[:4, None, None] * grad_next[None]).astype(jnp.bfloat16)
    grad_history = grad_history.reshape(4, batches, 1, row_count, model_width)
    depth_terms = jnp.concatenate(
        [jnp.einsum("jrd,rd->j", earlier, grad_next), jnp.sum(block_out * grad_next)[None]]
    )
    out_grad = depth_weights[4] * grad_next
    out_low = out_grad.astype(jnp.bfloat16)
    hidden_grad = jnp.einsum("rd,fd->rf", out_low, full_down, preferred_element_type=jnp.float32)
    _, gelu_pullback = jax.vjp(gelu_tanh, hidden)
    up_low = gelu_pullback(hidden_grad)[0].astype(jnp.bfloat16)
    second_grad = jnp.einsum("rf,df->rd", up_low, full_up, preferred_element_type=jnp.float32)
    _, second_pullback = jax.vjp(layer_norm, residual, norm_gains[:, 1], norm_biases[:, 1])
    residual_part, gain_two, bias_two = second_pullback(second_grad)
    residual_grad = out_grad + residual_part
    branch_low = residual_grad.astype(jnp.bfloat16)
    attended_grad = jnp.einsum(
        "rd,cd->rc", branch_low, full_out, preferred_element_type=jnp.float32
    ).astype(jnp.bfloat16)
    query_grad4, key_grad4, value_grad4 = jax.vmap(slot_attention_grads)(
        queries4,
        keys4,
        values4,
        attended_grad.reshape(batches, row_count, HEADS, HEAD),
        attended4,
        probabilities,
        probabilities_low,
    )
    key_value_parts = jnp.concatenate(
        [
            key_grad4.reshape(batches, slot_len, model_width),
            value_grad4.reshape(batches, slot_len, model_width),
        ],
        axis=2,
    ).astype(jnp.bfloat16)
    key_value_all = lax.psum_scatter(
        jnp.swapaxes(key_value_parts, 0, 1), "seq", scatter_dimension=0, tiled=True
    )
    key_value_all = jnp.swapaxes(key_value_all, 0, 1).reshape(all_rows, 2 * model_width)
    key_value_all = key_value_all.astype(jnp.float32)
    grad_down = jnp.einsum("rf,rd->fd", hidden_low, out_low, preferred_element_type=jnp.float32)
    grad_up = jnp.einsum("rd,rf->df", second_low, up_low, preferred_element_type=jnp.float32)
    grad_outproj = jnp.einsum(
        "rc,rd->cd", attended_low, branch_low, preferred_element_type=jnp.float32
    )
    qkv_low = jnp.concatenate(
        [
            rotate(query_grad4.reshape(all_rows, model_width), cosine_part, -sine_part),
            rotate(key_value_all[:, :model_width], cosine_part, -sine_part),
            key_value_all[:, model_width:],
        ],
        axis=1,
    ).astype(jnp.bfloat16)
    grad_qkv = jnp.einsum("rd,rc->dc", first_low, qkv_low, preferred_element_type=jnp.float32)
    first_grad = jnp.einsum("rc,dc->rd", qkv_low, full_qkv, preferred_element_type=jnp.float32)
    _, first_pullback = jax.vjp(layer_norm, inputs, norm_gains[:, 0], norm_biases[:, 0])
    input_part, gain_one, bias_one = first_pullback(first_grad)
    grad_input = (residual_grad + input_part).astype(jnp.bfloat16)
    grad_input = grad_input.reshape(batches, 1, row_count, model_width)
    packed_grads = jnp.concatenate(
        [
            grad_qkv,
            grad_outproj,
            grad_up,
            grad_down.reshape(model_width, ff_width),
            jnp.stack([gain_one, gain_two], axis=1),
            jnp.stack([bias_one, bias_two], axis=1),
            jnp.zeros((model_width, lane_pad), jnp.float32),
        ],
        axis=1,
    ).astype(jnp.bfloat16)
    device_count = model_width // shard_rows
    scattered = lax.psum_scatter(
        packed_grads.reshape(device_count, shard_rows, offsets[-1]),
        ("seq", "fsdp"),
        scatter_dimension=0,
        tiled=False,
    )
    owned = pieces(scattered.astype(jnp.float32))[:6]
    owned[3] = owned[3].reshape(-1, model_width)
    depth_total = lax.psum(depth_terms, ("seq", "fsdp"))
    return (next_input, grad_input, grad_history, *owned, depth_total)


def solution(mesh):
    in_specs = (
        P(None, "fsdp", "seq", None),
        P(None, None, "fsdp", "seq", None),
        P(None, "fsdp", "seq", None),
        P(None, "fsdp"),
        P(("seq", "fsdp"), None),
        P(("seq", "fsdp"), None),
        P(("seq", "fsdp"), None),
        P(("seq", "fsdp"), None),
        P(("seq", "fsdp"), None),
        P(("seq", "fsdp"), None),
        P(),
    )
    out_specs = (
        P(None, "fsdp", "seq", None),
        P(None, "fsdp", "seq", None),
        P(None, None, "fsdp", "seq", None),
        P(("seq", "fsdp"), None),
        P(("seq", "fsdp"), None),
        P(("seq", "fsdp"), None),
        P(("seq", "fsdp"), None),
        P(("seq", "fsdp"), None),
        P(("seq", "fsdp"), None),
        P(),
    )
    return jax.shard_map(local, mesh=mesh, in_specs=in_specs, out_specs=out_specs, check_vma=False)
```

```python
from functools import partial
import math

import jax
import jax.numpy as jnp
from jax import lax
from jax.sharding import PartitionSpec as P
from jax.experimental.layout import Layout, with_layout_constraint

HEADS = 12
HEAD = 64


epsilon = 1e-05
masked_value = -1e30


def layer_norm(values, gain_vector, bias_vector):
    center = values - jnp.mean(values, axis=-1, keepdims=True)
    spread = jnp.mean(center * center, axis=-1, keepdims=True)
    return center * lax.rsqrt(spread + epsilon) * gain_vector + bias_vector


def rotary_tables(positions):
    half_width = HEAD // 2
    frequencies = 10000.0 ** (-jnp.arange(half_width, dtype=jnp.float32) / half_width)
    angles = positions.astype(jnp.float32)[:, None] * frequencies[None, :]
    return (jnp.cos(angles)[:, None, :], jnp.sin(angles)[:, None, :])


def rotate(values, cosine_part, sine_part):
    row_count = values.shape[0]
    shaped = values.reshape(row_count, HEADS, HEAD)
    half_width = HEAD // 2
    first_half = shaped[..., :half_width]
    second_half = shaped[..., half_width:]
    turned = jnp.concatenate(
        [
            first_half * cosine_part - second_half * sine_part,
            second_half * cosine_part + first_half * sine_part,
        ],
        axis=-1,
    )
    return turned.reshape(row_count, HEADS * HEAD)


def block_scores(queries3, keys3, query_pos, key_pos, length):
    scores = jnp.einsum(
        "rhd,khd->hrk", queries3, keys3, preferred_element_type=jnp.float32
    ) * HEAD ** (-0.5)
    allowed = (key_pos[None, :] <= query_pos[:, None]) & (key_pos[None, :] < length)
    return (scores, allowed[None])


def row_totals(queries3, keys3, query_pos, length, key_block):
    row_count = queries3.shape[0]

    def row_advance(state, block_index):
        running_top, running_sum = state
        first_key = block_index * key_block
        keys_part = lax.dynamic_slice_in_dim(keys3, first_key, key_block, 0)
        key_pos = first_key + jnp.arange(key_block, dtype=jnp.int32)
        scores, allowed = block_scores(queries3, keys_part, query_pos, key_pos, length)
        masked = jnp.where(allowed, scores, masked_value)
        new_top = jnp.maximum(running_top, jnp.max(masked, axis=-1))
        kept_terms = jnp.where(allowed, jnp.exp(masked - new_top[..., None]), 0.0)
        running_sum = running_sum * jnp.exp(running_top - new_top) + jnp.sum(kept_terms, axis=-1)
        return ((new_top, running_sum), None)

    initial = (
        jnp.full((HEADS, row_count), masked_value, jnp.float32),
        jnp.zeros((HEADS, row_count), jnp.float32),
    )
    (row_tops, row_sums), _ = lax.scan(
        row_advance, initial, jnp.arange(keys3.shape[0] // key_block, dtype=jnp.int32)
    )
    return row_tops + jnp.log(row_sums)


def attend(queries3, keys3, values3, query_pos, length, key_block, log_total):

    def attend_advance(running, block_index):
        first_key = block_index * key_block
        keys_part = lax.dynamic_slice_in_dim(keys3, first_key, key_block, 0)
        values_part = lax.dynamic_slice_in_dim(values3, first_key, key_block, 0)
        key_pos = first_key + jnp.arange(key_block, dtype=jnp.int32)
        scores, allowed = block_scores(queries3, keys_part, query_pos, key_pos, length)
        probabilities = jnp.where(allowed, jnp.exp(scores - log_total[..., None]), 0.0).astype(
            jnp.bfloat16
        )
        return (
            running
            + jnp.einsum(
                "hrk,khd->rhd", probabilities, values_part, preferred_element_type=jnp.float32
            ),
            None,
        )

    initial = jnp.zeros(queries3.shape, jnp.float32)
    result, _ = lax.scan(
        attend_advance, initial, jnp.arange(keys3.shape[0] // key_block, dtype=jnp.int32)
    )
    return result


def query_grads(
    queries3, grads3, keys3, values3, query_pos, length, key_block, log_total, row_delta
):

    def query_advance(running, block_index):
        first_key = block_index * key_block
        keys_part = lax.dynamic_slice_in_dim(keys3, first_key, key_block, 0)
        values_part = lax.dynamic_slice_in_dim(values3, first_key, key_block, 0)
        key_pos = first_key + jnp.arange(key_block, dtype=jnp.int32)
        scores, allowed = block_scores(queries3, keys_part, query_pos, key_pos, length)
        probabilities = jnp.where(allowed, jnp.exp(scores - log_total[..., None]), 0.0)
        prob_grad = jnp.einsum(
            "rhd,khd->hrk", grads3, values_part, preferred_element_type=jnp.float32
        )
        score_low = (probabilities * (prob_grad - row_delta[..., None])).astype(jnp.bfloat16)
        return (
            running
            + jnp.einsum("hrk,khd->rhd", score_low, keys_part, preferred_element_type=jnp.float32),
            None,
        )

    initial = jnp.zeros(queries3.shape, jnp.float32)
    result, _ = lax.scan(
        query_advance, initial, jnp.arange(keys3.shape[0] // key_block, dtype=jnp.int32)
    )
    return result * HEAD ** (-0.5)


def key_side(queries3, grads3, log_part, delta_part, query_pos, keys3, values3, key_pos, length):
    key_count = keys3.shape[0]
    scores, allowed = block_scores(queries3, keys3, query_pos, key_pos, length)
    probabilities = jnp.where(allowed, jnp.exp(scores - log_part[..., None]), 0.0)
    prob_grad = jnp.einsum("rhd,khd->hrk", grads3, values3, preferred_element_type=jnp.float32)
    score_low = (probabilities * (prob_grad - delta_part[..., None])).astype(jnp.bfloat16)
    value_grad = jnp.einsum(
        "hrk,rhd->khd",
        probabilities.astype(jnp.bfloat16),
        grads3,
        preferred_element_type=jnp.float32,
    )
    key_grad = jnp.einsum(
        "hrk,rhd->khd", score_low, queries3, preferred_element_type=jnp.float32
    ) * HEAD ** (-0.5)
    return jnp.concatenate(
        [key_grad.reshape(key_count, HEADS * HEAD), value_grad.reshape(key_count, HEADS * HEAD)],
        axis=1,
    )


def slot_attention(queries3, keys3, values3, query_pos, length):
    key_pos = jnp.arange(keys3.shape[0], dtype=jnp.int32)
    scores, allowed = block_scores(queries3, keys3, query_pos, key_pos, length)
    masked = jnp.where(allowed, scores, masked_value)
    top = jnp.max(masked, axis=-1)
    kept_terms = jnp.where(allowed, jnp.exp(masked - top[..., None]), 0.0)
    log_total = top + jnp.log(jnp.sum(kept_terms, axis=-1))
    probabilities = jnp.where(allowed, jnp.exp(scores - log_total[..., None]), 0.0)
    probabilities_low = probabilities.astype(jnp.bfloat16)
    attended = jnp.einsum(
        "hrk,khd->rhd", probabilities_low, values3, preferred_element_type=jnp.float32
    )
    return attended, probabilities, probabilities_low


def slot_attention_grads(queries3, keys3, values3, grads3, attended, probabilities, probabilities_low):
    prob_grad = jnp.einsum("rhd,khd->hrk", grads3, values3, preferred_element_type=jnp.float32)
    row_delta = jnp.einsum("rhd,rhd->hr", grads3.astype(jnp.float32), attended)
    score_low = (probabilities * (prob_grad - row_delta[..., None])).astype(jnp.bfloat16)
    query_grad = jnp.einsum(
        "hrk,khd->rhd", score_low, keys3, preferred_element_type=jnp.float32
    ) * HEAD ** (-0.5)
    key_grad = jnp.einsum(
        "hrk,rhd->khd", score_low, queries3, preferred_element_type=jnp.float32
    ) * HEAD ** (-0.5)
    value_grad = jnp.einsum(
        "hrk,rhd->khd", probabilities_low, grads3, preferred_element_type=jnp.float32
    )
    return query_grad, key_grad, value_grad


def local(
    layer_input,
    history,
    cotangent,
    lengths,
    w_qkv,
    w_out,
    w_up,
    w_down,
    ln_gains,
    ln_biases,
    depth_weights,
):
    batches = layer_input.shape[0]
    row_count = layer_input.shape[2]
    model_width = layer_input.shape[3]
    ff_width = w_up.shape[1]
    shard_rows = w_qkv.shape[0]
    all_rows = batches * row_count
    slot_len = row_count * lax.axis_size("seq")
    positions = lax.axis_index("seq") * row_count + jnp.arange(row_count, dtype=jnp.int32)
    cosine_part, sine_part = rotary_tables(jnp.tile(positions, batches))
    gelu_tanh = partial(jax.nn.gelu, approximate=True)
    lane_pad = 128 - 4
    widths = (3 * model_width, 2, 2, lane_pad, model_width, ff_width, ff_width)
    offsets = [0]
    for width in widths:
        offsets.append(offsets[-1] + width)
    late_width = offsets[4]

    def pieces(packed_rows):
        return [packed_rows[:, offsets[i] : offsets[i + 1]] for i in range(len(widths))]

    packed = jnp.concatenate(
        [
            w_qkv,
            ln_gains,
            ln_biases,
            jnp.zeros((shard_rows, lane_pad), w_qkv.dtype),
            w_out,
            w_up,
            w_down.reshape(shard_rows, ff_width),
        ],
        axis=1,
    )
    gathered = lax.all_gather(packed, ("seq", "fsdp"), axis=0, tiled=True)
    full_qkv, gain_rows, bias_rows, _, full_out, full_up, down_rows = pieces(gathered)
    full_down = down_rows.reshape(ff_width, model_width)
    norm_gains = gain_rows.astype(jnp.float32)
    norm_biases = bias_rows.astype(jnp.float32)

    slot_lengths = lengths[:, 0]
    inputs = layer_input[:, 0].reshape(all_rows, model_width).astype(jnp.float32)
    first_low = layer_norm(inputs, norm_gains[:, 0], norm_biases[:, 0]).astype(jnp.bfloat16)
    projected = jnp.dot(first_low, full_qkv, preferred_element_type=jnp.float32)
    queries = rotate(projected[:, :model_width], cosine_part, sine_part).astype(jnp.bfloat16)
    keys_own = rotate(
        projected[:, model_width : 2 * model_width], cosine_part, sine_part
    ).astype(jnp.bfloat16)
    values_own = projected[:, 2 * model_width :].astype(jnp.bfloat16)
    own_kv = jnp.concatenate([keys_own, values_own], axis=1).reshape(
        batches, row_count, 2 * model_width
    )
    queries4 = queries.reshape(batches, row_count, HEADS, HEAD)
    earlier = history[:, :, 0].reshape(4, all_rows, model_width).astype(jnp.float32)
    usable = (positions[None, :] < slot_lengths[:, None]).reshape(all_rows, 1)
    grad_next = jnp.where(
        usable, cotangent[:, 0].reshape(all_rows, model_width).astype(jnp.float32), 0.0
    )
    history_part = jnp.einsum("j,jrd->rd", depth_weights[:4], earlier)
    grad_history = (depth_weights[:4, None, None] * grad_next[None]).astype(jnp.bfloat16)
    grad_history = grad_history.reshape(4, batches, 1, row_count, model_width)
    out_grad = depth_weights[4] * grad_next
    out_low = out_grad.astype(jnp.bfloat16)

    per_micro = []
    for micro in range(batches):
        rows = slice(micro * row_count, (micro + 1) * row_count)
        kv_all = lax.all_gather(own_kv[micro], "seq", axis=0, tiled=True)
        keys3 = kv_all[:, :model_width].reshape(slot_len, HEADS, HEAD)
        values3 = kv_all[:, model_width:].reshape(slot_len, HEADS, HEAD)
        attended3, probabilities, probabilities_low = slot_attention(
            queries4[micro], keys3, values3, positions, slot_lengths[micro]
        )
        attended_low = attended3.reshape(row_count, model_width).astype(jnp.bfloat16)
        residual = inputs[rows] + jnp.dot(
            attended_low, full_out, preferred_element_type=jnp.float32
        )
        second_low = layer_norm(residual, norm_gains[:, 1], norm_biases[:, 1]).astype(
            jnp.bfloat16
        )
        hidden = jnp.dot(second_low, full_up, preferred_element_type=jnp.float32)
        hidden_low = gelu_tanh(hidden).astype(jnp.bfloat16)
        block_out = residual + jnp.dot(hidden_low, full_down, preferred_element_type=jnp.float32)
        hidden_grad = jnp.einsum(
            "rd,fd->rf", out_low[rows], full_down, preferred_element_type=jnp.float32
        )
        _, gelu_pullback = jax.vjp(gelu_tanh, hidden)
        up_low = gelu_pullback(hidden_grad)[0].astype(jnp.bfloat16)
        second_grad = jnp.einsum("rf,df->rd", up_low, full_up, preferred_element_type=jnp.float32)
        _, second_pullback = jax.vjp(layer_norm, residual, norm_gains[:, 1], norm_biases[:, 1])
        residual_part, gain_two, bias_two = second_pullback(second_grad)
        residual_grad = out_grad[rows] + residual_part
        branch_low = residual_grad.astype(jnp.bfloat16)
        attended_grad = jnp.einsum(
            "rd,cd->rc", branch_low, full_out, preferred_element_type=jnp.float32
        ).astype(jnp.bfloat16)
        query_grad3, key_grad3, value_grad3 = slot_attention_grads(
            queries4[micro],
            keys3,
            values3,
            attended_grad.reshape(row_count, HEADS, HEAD),
            attended3,
            probabilities,
            probabilities_low,
        )
        key_value_part = jnp.concatenate(
            [key_grad3.reshape(slot_len, model_width), value_grad3.reshape(slot_len, model_width)],
            axis=1,
        ).astype(jnp.bfloat16)
        key_value_own = lax.psum_scatter(key_value_part, "seq", scatter_dimension=0, tiled=True)
        per_micro.append(
            (
                attended_low,
                block_out,
                second_low,
                hidden_low,
                up_low,
                gain_two,
                bias_two,
                residual_grad,
                branch_low,
                query_grad3.reshape(row_count, model_width),
                key_value_own.astype(jnp.float32),
            )
        )
    (
        attended_low,
        block_out,
        second_low,
        hidden_low,
        up_low,
        gain_two,
        bias_two,
        residual_grad,
        branch_low,
        query_grad,
        key_value_all,
    ) = [
        jnp.concatenate(parts, axis=0) if parts[0].ndim == 2 else sum(parts[1:], parts[0])
        for parts in zip(*per_micro)
    ]
    combined = depth_weights[4] * block_out + history_part
    next_input = combined.astype(jnp.bfloat16).reshape(batches, 1, row_count, model_width)
    depth_terms = jnp.concatenate(
        [jnp.einsum("jrd,rd->j", earlier, grad_next), jnp.sum(block_out * grad_next)[None]]
    )
    grad_down = jnp.einsum("rf,rd->fd", hidden_low, out_low, preferred_element_type=jnp.float32)
    grad_up = jnp.einsum("rd,rf->df", second_low, up_low, preferred_element_type=jnp.float32)
    grad_outproj = jnp.einsum(
        "rc,rd->cd", attended_low, branch_low, preferred_element_type=jnp.float32
    )
    early_grads = jnp.concatenate(
        [
            jnp.zeros((model_width, late_width), jnp.float32),
            grad_outproj,
            grad_up,
            grad_down.reshape(model_width, ff_width),
        ],
        axis=1,
    ).astype(jnp.bfloat16)
    qkv_low = jnp.concatenate(
        [
            rotate(query_grad, cosine_part, -sine_part),
            rotate(key_value_all[:, :model_width], cosine_part, -sine_part),
            key_value_all[:, model_width:],
        ],
        axis=1,
    ).astype(jnp.bfloat16)
    grad_qkv = jnp.einsum("rd,rc->dc", first_low, qkv_low, preferred_element_type=jnp.float32)
    first_grad = jnp.einsum("rc,dc->rd", qkv_low, full_qkv, preferred_element_type=jnp.float32)
    _, first_pullback = jax.vjp(layer_norm, inputs, norm_gains[:, 0], norm_biases[:, 0])
    input_part, gain_one, bias_one = first_pullback(first_grad)
    grad_input = (residual_grad + input_part).astype(jnp.bfloat16)
    grad_input = grad_input.reshape(batches, 1, row_count, model_width)
    late_grads = jnp.concatenate(
        [
            grad_qkv,
            jnp.stack([gain_one, gain_two], axis=1),
            jnp.stack([bias_one, bias_two], axis=1),
            jnp.zeros((model_width, lane_pad), jnp.float32),
        ],
        axis=1,
    ).astype(jnp.bfloat16)
    packed_grads = lax.dynamic_update_slice(early_grads, late_grads, (0, 0))
    device_count = model_width // shard_rows
    row_major = Layout(major_to_minor=(0, 1, 2))
    scattered = lax.psum_scatter(
        with_layout_constraint(
            packed_grads.reshape(device_count, shard_rows, offsets[-1]), row_major
        ),
        ("seq", "fsdp"),
        scatter_dimension=0,
        tiled=False,
    )
    scattered = with_layout_constraint(scattered, Layout(major_to_minor=(0, 1)))
    full_pieces = pieces(scattered.astype(jnp.float32))
    owned = [
        full_pieces[0],
        full_pieces[4],
        full_pieces[5],
        full_pieces[6].reshape(-1, model_width),
        full_pieces[1],
        full_pieces[2],
    ]
    depth_total = lax.psum(depth_terms, ("seq", "fsdp"))
    return (next_input, grad_input, grad_history, *owned, depth_total)


def solution(mesh):
    in_specs = (
        P(None, "fsdp", "seq", None),
        P(None, None, "fsdp", "seq", None),
        P(None, "fsdp", "seq", None),
        P(None, "fsdp"),
        P(("seq", "fsdp"), None),
        P(("seq", "fsdp"), None),
        P(("seq", "fsdp"), None),
        P(("seq", "fsdp"), None),
        P(("seq", "fsdp"), None),
        P(("seq", "fsdp"), None),
        P(),
    )
    out_specs = (
        P(None, "fsdp", "seq", None),
        P(None, "fsdp", "seq", None),
        P(None, None, "fsdp", "seq", None),
        P(("seq", "fsdp"), None),
        P(("seq", "fsdp"), None),
        P(("seq", "fsdp"), None),
        P(("seq", "fsdp"), None),
        P(("seq", "fsdp"), None),
        P(("seq", "fsdp"), None),
        P(),
    )
    return jax.shard_map(local, mesh=mesh, in_specs=in_specs, out_specs=out_specs, check_vma=False)
```

```python
from functools import partial
import math

import jax
import jax.numpy as jnp
from jax import lax
from jax.sharding import PartitionSpec as P
from jax.experimental.layout import Layout, with_layout_constraint

HEADS = 12
HEAD = 64


epsilon = 1e-05
masked_value = -1e30


def layer_norm(values, gain_vector, bias_vector):
    center = values - jnp.mean(values, axis=-1, keepdims=True)
    spread = jnp.mean(center * center, axis=-1, keepdims=True)
    return center * lax.rsqrt(spread + epsilon) * gain_vector + bias_vector


def rotary_tables(positions):
    half_width = HEAD // 2
    frequencies = 10000.0 ** (-jnp.arange(half_width, dtype=jnp.float32) / half_width)
    angles = positions.astype(jnp.float32)[:, None] * frequencies[None, :]
    return (jnp.cos(angles)[:, None, :], jnp.sin(angles)[:, None, :])


def rotate(values, cosine_part, sine_part):
    row_count = values.shape[0]
    shaped = values.reshape(row_count, HEADS, HEAD)
    half_width = HEAD // 2
    first_half = shaped[..., :half_width]
    second_half = shaped[..., half_width:]
    turned = jnp.concatenate(
        [
            first_half * cosine_part - second_half * sine_part,
            second_half * cosine_part + first_half * sine_part,
        ],
        axis=-1,
    )
    return turned.reshape(row_count, HEADS * HEAD)


def block_scores(queries3, keys3, query_pos, key_pos, length):
    scores = jnp.einsum(
        "rhd,khd->hrk", queries3, keys3, preferred_element_type=jnp.float32
    ) * HEAD ** (-0.5)
    allowed = (key_pos[None, :] <= query_pos[:, None]) & (key_pos[None, :] < length)
    return (scores, allowed[None])


def row_totals(queries3, keys3, query_pos, length, key_block):
    row_count = queries3.shape[0]

    def row_advance(state, block_index):
        running_top, running_sum = state
        first_key = block_index * key_block
        keys_part = lax.dynamic_slice_in_dim(keys3, first_key, key_block, 0)
        key_pos = first_key + jnp.arange(key_block, dtype=jnp.int32)
        scores, allowed = block_scores(queries3, keys_part, query_pos, key_pos, length)
        masked = jnp.where(allowed, scores, masked_value)
        new_top = jnp.maximum(running_top, jnp.max(masked, axis=-1))
        kept_terms = jnp.where(allowed, jnp.exp(masked - new_top[..., None]), 0.0)
        running_sum = running_sum * jnp.exp(running_top - new_top) + jnp.sum(kept_terms, axis=-1)
        return ((new_top, running_sum), None)

    initial = (
        jnp.full((HEADS, row_count), masked_value, jnp.float32),
        jnp.zeros((HEADS, row_count), jnp.float32),
    )
    (row_tops, row_sums), _ = lax.scan(
        row_advance, initial, jnp.arange(keys3.shape[0] // key_block, dtype=jnp.int32)
    )
    return row_tops + jnp.log(row_sums)


def attend(queries3, keys3, values3, query_pos, length, key_block, log_total):

    def attend_advance(running, block_index):
        first_key = block_index * key_block
        keys_part = lax.dynamic_slice_in_dim(keys3, first_key, key_block, 0)
        values_part = lax.dynamic_slice_in_dim(values3, first_key, key_block, 0)
        key_pos = first_key + jnp.arange(key_block, dtype=jnp.int32)
        scores, allowed = block_scores(queries3, keys_part, query_pos, key_pos, length)
        probabilities = jnp.where(allowed, jnp.exp(scores - log_total[..., None]), 0.0).astype(
            jnp.bfloat16
        )
        return (
            running
            + jnp.einsum(
                "hrk,khd->rhd", probabilities, values_part, preferred_element_type=jnp.float32
            ),
            None,
        )

    initial = jnp.zeros(queries3.shape, jnp.float32)
    result, _ = lax.scan(
        attend_advance, initial, jnp.arange(keys3.shape[0] // key_block, dtype=jnp.int32)
    )
    return result


def query_grads(
    queries3, grads3, keys3, values3, query_pos, length, key_block, log_total, row_delta
):

    def query_advance(running, block_index):
        first_key = block_index * key_block
        keys_part = lax.dynamic_slice_in_dim(keys3, first_key, key_block, 0)
        values_part = lax.dynamic_slice_in_dim(values3, first_key, key_block, 0)
        key_pos = first_key + jnp.arange(key_block, dtype=jnp.int32)
        scores, allowed = block_scores(queries3, keys_part, query_pos, key_pos, length)
        probabilities = jnp.where(allowed, jnp.exp(scores - log_total[..., None]), 0.0)
        prob_grad = jnp.einsum(
            "rhd,khd->hrk", grads3, values_part, preferred_element_type=jnp.float32
        )
        score_low = (probabilities * (prob_grad - row_delta[..., None])).astype(jnp.bfloat16)
        return (
            running
            + jnp.einsum("hrk,khd->rhd", score_low, keys_part, preferred_element_type=jnp.float32),
            None,
        )

    initial = jnp.zeros(queries3.shape, jnp.float32)
    result, _ = lax.scan(
        query_advance, initial, jnp.arange(keys3.shape[0] // key_block, dtype=jnp.int32)
    )
    return result * HEAD ** (-0.5)


def key_side(queries3, grads3, log_part, delta_part, query_pos, keys3, values3, key_pos, length):
    key_count = keys3.shape[0]
    scores, allowed = block_scores(queries3, keys3, query_pos, key_pos, length)
    probabilities = jnp.where(allowed, jnp.exp(scores - log_part[..., None]), 0.0)
    prob_grad = jnp.einsum("rhd,khd->hrk", grads3, values3, preferred_element_type=jnp.float32)
    score_low = (probabilities * (prob_grad - delta_part[..., None])).astype(jnp.bfloat16)
    value_grad = jnp.einsum(
        "hrk,rhd->khd",
        probabilities.astype(jnp.bfloat16),
        grads3,
        preferred_element_type=jnp.float32,
    )
    key_grad = jnp.einsum(
        "hrk,rhd->khd", score_low, queries3, preferred_element_type=jnp.float32
    ) * HEAD ** (-0.5)
    return jnp.concatenate(
        [key_grad.reshape(key_count, HEADS * HEAD), value_grad.reshape(key_count, HEADS * HEAD)],
        axis=1,
    )


def slot_attention(queries3, keys3, values3, query_pos, length):
    key_pos = jnp.arange(keys3.shape[0], dtype=jnp.int32)
    scores, allowed = block_scores(queries3, keys3, query_pos, key_pos, length)
    masked = jnp.where(allowed, scores, masked_value)
    top = jnp.max(masked, axis=-1)
    kept_terms = jnp.where(allowed, jnp.exp(masked - top[..., None]), 0.0)
    log_total = top + jnp.log(jnp.sum(kept_terms, axis=-1))
    probabilities = jnp.where(allowed, jnp.exp(scores - log_total[..., None]), 0.0)
    probabilities_low = probabilities.astype(jnp.bfloat16)
    attended = jnp.einsum(
        "hrk,khd->rhd", probabilities_low, values3, preferred_element_type=jnp.float32
    )
    return attended, probabilities, probabilities_low


def slot_attention_grads(queries3, keys3, values3, grads3, attended, probabilities, probabilities_low):
    prob_grad = jnp.einsum("rhd,khd->hrk", grads3, values3, preferred_element_type=jnp.float32)
    row_delta = jnp.einsum("rhd,rhd->hr", grads3.astype(jnp.float32), attended)
    score_low = (probabilities * (prob_grad - row_delta[..., None])).astype(jnp.bfloat16)
    query_grad = jnp.einsum(
        "hrk,khd->rhd", score_low, keys3, preferred_element_type=jnp.float32
    ) * HEAD ** (-0.5)
    key_grad = jnp.einsum(
        "hrk,rhd->khd", score_low, queries3, preferred_element_type=jnp.float32
    ) * HEAD ** (-0.5)
    value_grad = jnp.einsum(
        "hrk,rhd->khd", probabilities_low, grads3, preferred_element_type=jnp.float32
    )
    return query_grad, key_grad, value_grad


def local(
    layer_input,
    history,
    cotangent,
    lengths,
    w_qkv,
    w_out,
    w_up,
    w_down,
    ln_gains,
    ln_biases,
    depth_weights,
):
    batches = layer_input.shape[0]
    row_count = layer_input.shape[2]
    model_width = layer_input.shape[3]
    ff_width = w_up.shape[1]
    shard_rows = w_qkv.shape[0]
    all_rows = batches * row_count
    slot_len = row_count * lax.axis_size("seq")
    positions = lax.axis_index("seq") * row_count + jnp.arange(row_count, dtype=jnp.int32)
    cosine_part, sine_part = rotary_tables(jnp.tile(positions, batches))
    gelu_tanh = partial(jax.nn.gelu, approximate=True)
    lane_pad = 128 - 4
    widths = (3 * model_width, 2, 2, lane_pad, model_width, ff_width, ff_width)
    offsets = [0]
    for width in widths:
        offsets.append(offsets[-1] + width)
    late_width = offsets[4]

    def pieces(packed_rows):
        return [packed_rows[:, offsets[i] : offsets[i + 1]] for i in range(len(widths))]

    packed = jnp.concatenate(
        [
            w_qkv,
            ln_gains,
            ln_biases,
            jnp.zeros((shard_rows, lane_pad), w_qkv.dtype),
            w_out,
            w_up,
            w_down.reshape(shard_rows, ff_width),
        ],
        axis=1,
    )
    gathered = lax.all_gather(packed, ("seq", "fsdp"), axis=0, tiled=True)
    full_qkv, gain_rows, bias_rows, _, full_out, full_up, down_rows = pieces(gathered)
    full_down = down_rows.reshape(ff_width, model_width)
    norm_gains = gain_rows.astype(jnp.float32)
    norm_biases = bias_rows.astype(jnp.float32)

    slot_lengths = lengths[:, 0]
    inputs = layer_input[:, 0].reshape(all_rows, model_width).astype(jnp.float32)
    first_low = layer_norm(inputs, norm_gains[:, 0], norm_biases[:, 0]).astype(jnp.bfloat16)
    projected = jnp.dot(first_low, full_qkv, preferred_element_type=jnp.float32)
    queries = rotate(projected[:, :model_width], cosine_part, sine_part).astype(jnp.bfloat16)
    keys_own = rotate(
        projected[:, model_width : 2 * model_width], cosine_part, sine_part
    ).astype(jnp.bfloat16)
    values_own = projected[:, 2 * model_width :].astype(jnp.bfloat16)
    own_kv = jnp.concatenate([keys_own, values_own], axis=1).reshape(
        batches, row_count, 2 * model_width
    )
    queries4 = queries.reshape(batches, row_count, HEADS, HEAD)
    earlier = history[:, :, 0].reshape(4, all_rows, model_width).astype(jnp.float32)
    usable = (positions[None, :] < slot_lengths[:, None]).reshape(all_rows, 1)
    grad_next = jnp.where(
        usable, cotangent[:, 0].reshape(all_rows, model_width).astype(jnp.float32), 0.0
    )
    history_part = jnp.einsum("j,jrd->rd", depth_weights[:4], earlier)
    grad_history = (depth_weights[:4, None, None] * grad_next[None]).astype(jnp.bfloat16)
    grad_history = grad_history.reshape(4, batches, 1, row_count, model_width)
    out_grad = depth_weights[4] * grad_next
    out_low = out_grad.astype(jnp.bfloat16)

    kv_all = lax.all_gather(jnp.swapaxes(own_kv, 0, 1), "seq", axis=0, tiled=True)
    keys4 = jnp.swapaxes(kv_all[:, :, :model_width], 0, 1).reshape(batches, slot_len, HEADS, HEAD)
    values4 = jnp.swapaxes(kv_all[:, :, model_width:], 0, 1).reshape(
        batches, slot_len, HEADS, HEAD
    )
    attended4, probabilities, probabilities_low = jax.vmap(
        slot_attention, in_axes=(0, 0, 0, None, 0)
    )(queries4, keys4, values4, positions, slot_lengths)
    attended_low = attended4.reshape(all_rows, model_width).astype(jnp.bfloat16)
    residual = inputs + jnp.dot(attended_low, full_out, preferred_element_type=jnp.float32)
    second_low = layer_norm(residual, norm_gains[:, 1], norm_biases[:, 1]).astype(jnp.bfloat16)
    hidden = jnp.dot(second_low, full_up, preferred_element_type=jnp.float32)
    hidden_low = gelu_tanh(hidden).astype(jnp.bfloat16)
    block_out = residual + jnp.dot(hidden_low, full_down, preferred_element_type=jnp.float32)
    hidden_grad = jnp.einsum("rd,fd->rf", out_low, full_down, preferred_element_type=jnp.float32)
    _, gelu_pullback = jax.vjp(gelu_tanh, hidden)
    up_low = gelu_pullback(hidden_grad)[0].astype(jnp.bfloat16)
    second_grad = jnp.einsum("rf,df->rd", up_low, full_up, preferred_element_type=jnp.float32)
    _, second_pullback = jax.vjp(layer_norm, residual, norm_gains[:, 1], norm_biases[:, 1])
    residual_part, gain_two, bias_two = second_pullback(second_grad)
    residual_grad = out_grad + residual_part
    branch_low = residual_grad.astype(jnp.bfloat16)
    attended_grad = jnp.einsum(
        "rd,cd->rc", branch_low, full_out, preferred_element_type=jnp.float32
    ).astype(jnp.bfloat16)
    query_grad4, key_grad4, value_grad4 = jax.vmap(slot_attention_grads)(
        queries4,
        keys4,
        values4,
        attended_grad.reshape(batches, row_count, HEADS, HEAD),
        attended4,
        probabilities,
        probabilities_low,
    )
    key_value_parts = jnp.concatenate(
        [
            key_grad4.reshape(batches, slot_len, model_width),
            value_grad4.reshape(batches, slot_len, model_width),
        ],
        axis=2,
    ).astype(jnp.bfloat16)
    key_value_all = lax.psum_scatter(
        jnp.swapaxes(key_value_parts, 0, 1), "seq", scatter_dimension=0, tiled=True
    )
    key_value_all = jnp.swapaxes(key_value_all, 0, 1).reshape(all_rows, 2 * model_width)
    key_value_all = key_value_all.astype(jnp.float32)
    query_grad = query_grad4.reshape(all_rows, model_width)
    combined = depth_weights[4] * block_out + history_part
    next_input = combined.astype(jnp.bfloat16).reshape(batches, 1, row_count, model_width)
    depth_terms = jnp.concatenate(
        [jnp.einsum("jrd,rd->j", earlier, grad_next), jnp.sum(block_out * grad_next)[None]]
    )
    grad_down = jnp.einsum("rf,rd->fd", hidden_low, out_low, preferred_element_type=jnp.float32)
    grad_up = jnp.einsum("rd,rf->df", second_low, up_low, preferred_element_type=jnp.float32)
    grad_outproj = jnp.einsum(
        "rc,rd->cd", attended_low, branch_low, preferred_element_type=jnp.float32
    )
    early_grads = jnp.concatenate(
        [
            jnp.zeros((model_width, late_width), jnp.float32),
            grad_outproj,
            grad_up,
            grad_down.reshape(model_width, ff_width),
        ],
        axis=1,
    ).astype(jnp.bfloat16)
    qkv_low = jnp.concatenate(
        [
            rotate(query_grad, cosine_part, -sine_part),
            rotate(key_value_all[:, :model_width], cosine_part, -sine_part),
            key_value_all[:, model_width:],
        ],
        axis=1,
    ).astype(jnp.bfloat16)
    grad_qkv = jnp.einsum("rd,rc->dc", first_low, qkv_low, preferred_element_type=jnp.float32)
    first_grad = jnp.einsum("rc,dc->rd", qkv_low, full_qkv, preferred_element_type=jnp.float32)
    _, first_pullback = jax.vjp(layer_norm, inputs, norm_gains[:, 0], norm_biases[:, 0])
    input_part, gain_one, bias_one = first_pullback(first_grad)
    grad_input = (residual_grad + input_part).astype(jnp.bfloat16)
    grad_input = grad_input.reshape(batches, 1, row_count, model_width)
    late_grads = jnp.concatenate(
        [
            grad_qkv,
            jnp.stack([gain_one, gain_two], axis=1),
            jnp.stack([bias_one, bias_two], axis=1),
            jnp.zeros((model_width, lane_pad), jnp.float32),
        ],
        axis=1,
    ).astype(jnp.bfloat16)
    packed_grads = lax.dynamic_update_slice(early_grads, late_grads, (0, 0))
    device_count = model_width // shard_rows
    row_major = Layout(major_to_minor=(0, 1, 2))
    scattered = lax.psum_scatter(
        with_layout_constraint(
            packed_grads.reshape(device_count, shard_rows, offsets[-1]), row_major
        ),
        ("seq", "fsdp"),
        scatter_dimension=0,
        tiled=False,
    )
    scattered = with_layout_constraint(scattered, Layout(major_to_minor=(0, 1)))
    full_pieces = pieces(scattered.astype(jnp.float32))
    owned = [
        full_pieces[0],
        full_pieces[4],
        full_pieces[5],
        full_pieces[6].reshape(-1, model_width),
        full_pieces[1],
        full_pieces[2],
    ]
    depth_total = lax.psum(depth_terms, ("seq", "fsdp"))
    return (next_input, grad_input, grad_history, *owned, depth_total)


def solution(mesh):
    in_specs = (
        P(None, "fsdp", "seq", None),
        P(None, None, "fsdp", "seq", None),
        P(None, "fsdp", "seq", None),
        P(None, "fsdp"),
        P(("seq", "fsdp"), None),
        P(("seq", "fsdp"), None),
        P(("seq", "fsdp"), None),
        P(("seq", "fsdp"), None),
        P(("seq", "fsdp"), None),
        P(("seq", "fsdp"), None),
        P(),
    )
    out_specs = (
        P(None, "fsdp", "seq", None),
        P(None, "fsdp", "seq", None),
        P(None, None, "fsdp", "seq", None),
        P(("seq", "fsdp"), None),
        P(("seq", "fsdp"), None),
        P(("seq", "fsdp"), None),
        P(("seq", "fsdp"), None),
        P(("seq", "fsdp"), None),
        P(("seq", "fsdp"), None),
        P(),
    )
    return jax.shard_map(local, mesh=mesh, in_specs=in_specs, out_specs=out_specs, check_vma=False)
```

```python
from functools import partial
import math

import jax
import jax.numpy as jnp
from jax import lax
from jax.sharding import PartitionSpec as P
from jax.experimental.layout import Layout, with_layout_constraint
from jax.experimental import pallas as pl
from jax.experimental.pallas import tpu as pltpu

HEADS = 12
HEAD = 64


epsilon = 1e-05
masked_value = -1e30


def layer_norm(values, gain_vector, bias_vector):
    center = values - jnp.mean(values, axis=-1, keepdims=True)
    spread = jnp.mean(center * center, axis=-1, keepdims=True)
    return center * lax.rsqrt(spread + epsilon) * gain_vector + bias_vector


def rotary_tables(positions):
    half_width = HEAD // 2
    frequencies = 10000.0 ** (-jnp.arange(half_width, dtype=jnp.float32) / half_width)
    angles = positions.astype(jnp.float32)[:, None] * frequencies[None, :]
    return (jnp.cos(angles)[:, None, :], jnp.sin(angles)[:, None, :])


def rotate(values, cosine_part, sine_part):
    row_count = values.shape[0]
    shaped = values.reshape(row_count, HEADS, HEAD)
    half_width = HEAD // 2
    first_half = shaped[..., :half_width]
    second_half = shaped[..., half_width:]
    turned = jnp.concatenate(
        [
            first_half * cosine_part - second_half * sine_part,
            second_half * cosine_part + first_half * sine_part,
        ],
        axis=-1,
    )
    return turned.reshape(row_count, HEADS * HEAD)


def block_scores(queries3, keys3, query_pos, key_pos, length):
    scores = jnp.einsum(
        "rhd,khd->hrk", queries3, keys3, preferred_element_type=jnp.float32
    ) * HEAD ** (-0.5)
    allowed = (key_pos[None, :] <= query_pos[:, None]) & (key_pos[None, :] < length)
    return (scores, allowed[None])


def row_totals(queries3, keys3, query_pos, length, key_block):
    row_count = queries3.shape[0]

    def row_advance(state, block_index):
        running_top, running_sum = state
        first_key = block_index * key_block
        keys_part = lax.dynamic_slice_in_dim(keys3, first_key, key_block, 0)
        key_pos = first_key + jnp.arange(key_block, dtype=jnp.int32)
        scores, allowed = block_scores(queries3, keys_part, query_pos, key_pos, length)
        masked = jnp.where(allowed, scores, masked_value)
        new_top = jnp.maximum(running_top, jnp.max(masked, axis=-1))
        kept_terms = jnp.where(allowed, jnp.exp(masked - new_top[..., None]), 0.0)
        running_sum = running_sum * jnp.exp(running_top - new_top) + jnp.sum(kept_terms, axis=-1)
        return ((new_top, running_sum), None)

    initial = (
        jnp.full((HEADS, row_count), masked_value, jnp.float32),
        jnp.zeros((HEADS, row_count), jnp.float32),
    )
    (row_tops, row_sums), _ = lax.scan(
        row_advance, initial, jnp.arange(keys3.shape[0] // key_block, dtype=jnp.int32)
    )
    return row_tops + jnp.log(row_sums)


def attend(queries3, keys3, values3, query_pos, length, key_block, log_total):

    def attend_advance(running, block_index):
        first_key = block_index * key_block
        keys_part = lax.dynamic_slice_in_dim(keys3, first_key, key_block, 0)
        values_part = lax.dynamic_slice_in_dim(values3, first_key, key_block, 0)
        key_pos = first_key + jnp.arange(key_block, dtype=jnp.int32)
        scores, allowed = block_scores(queries3, keys_part, query_pos, key_pos, length)
        probabilities = jnp.where(allowed, jnp.exp(scores - log_total[..., None]), 0.0).astype(
            jnp.bfloat16
        )
        return (
            running
            + jnp.einsum(
                "hrk,khd->rhd", probabilities, values_part, preferred_element_type=jnp.float32
            ),
            None,
        )

    initial = jnp.zeros(queries3.shape, jnp.float32)
    result, _ = lax.scan(
        attend_advance, initial, jnp.arange(keys3.shape[0] // key_block, dtype=jnp.int32)
    )
    return result


def query_grads(
    queries3, grads3, keys3, values3, query_pos, length, key_block, log_total, row_delta
):

    def query_advance(running, block_index):
        first_key = block_index * key_block
        keys_part = lax.dynamic_slice_in_dim(keys3, first_key, key_block, 0)
        values_part = lax.dynamic_slice_in_dim(values3, first_key, key_block, 0)
        key_pos = first_key + jnp.arange(key_block, dtype=jnp.int32)
        scores, allowed = block_scores(queries3, keys_part, query_pos, key_pos, length)
        probabilities = jnp.where(allowed, jnp.exp(scores - log_total[..., None]), 0.0)
        prob_grad = jnp.einsum(
            "rhd,khd->hrk", grads3, values_part, preferred_element_type=jnp.float32
        )
        score_low = (probabilities * (prob_grad - row_delta[..., None])).astype(jnp.bfloat16)
        return (
            running
            + jnp.einsum("hrk,khd->rhd", score_low, keys_part, preferred_element_type=jnp.float32),
            None,
        )

    initial = jnp.zeros(queries3.shape, jnp.float32)
    result, _ = lax.scan(
        query_advance, initial, jnp.arange(keys3.shape[0] // key_block, dtype=jnp.int32)
    )
    return result * HEAD ** (-0.5)


def key_side(queries3, grads3, log_part, delta_part, query_pos, keys3, values3, key_pos, length):
    key_count = keys3.shape[0]
    scores, allowed = block_scores(queries3, keys3, query_pos, key_pos, length)
    probabilities = jnp.where(allowed, jnp.exp(scores - log_part[..., None]), 0.0)
    prob_grad = jnp.einsum("rhd,khd->hrk", grads3, values3, preferred_element_type=jnp.float32)
    score_low = (probabilities * (prob_grad - delta_part[..., None])).astype(jnp.bfloat16)
    value_grad = jnp.einsum(
        "hrk,rhd->khd",
        probabilities.astype(jnp.bfloat16),
        grads3,
        preferred_element_type=jnp.float32,
    )
    key_grad = jnp.einsum(
        "hrk,rhd->khd", score_low, queries3, preferred_element_type=jnp.float32
    ) * HEAD ** (-0.5)
    return jnp.concatenate(
        [key_grad.reshape(key_count, HEADS * HEAD), value_grad.reshape(key_count, HEADS * HEAD)],
        axis=1,
    )


def slot_attention(queries3, keys3, values3, query_pos, length):
    key_pos = jnp.arange(keys3.shape[0], dtype=jnp.int32)
    scores, allowed = block_scores(queries3, keys3, query_pos, key_pos, length)
    masked = jnp.where(allowed, scores, masked_value)
    top = jnp.max(masked, axis=-1)
    kept_terms = jnp.where(allowed, jnp.exp(masked - top[..., None]), 0.0)
    log_total = top + jnp.log(jnp.sum(kept_terms, axis=-1))
    probabilities = jnp.where(allowed, jnp.exp(scores - log_total[..., None]), 0.0)
    probabilities_low = probabilities.astype(jnp.bfloat16)
    attended = jnp.einsum(
        "hrk,khd->rhd", probabilities_low, values3, preferred_element_type=jnp.float32
    )
    return attended, probabilities, probabilities_low


def slot_attention_grads(queries3, keys3, values3, grads3, attended, probabilities, probabilities_low):
    prob_grad = jnp.einsum("rhd,khd->hrk", grads3, values3, preferred_element_type=jnp.float32)
    row_delta = jnp.einsum("rhd,rhd->hr", grads3.astype(jnp.float32), attended)
    score_low = (probabilities * (prob_grad - row_delta[..., None])).astype(jnp.bfloat16)
    query_grad = jnp.einsum(
        "hrk,khd->rhd", score_low, keys3, preferred_element_type=jnp.float32
    ) * HEAD ** (-0.5)
    key_grad = jnp.einsum(
        "hrk,rhd->khd", score_low, queries3, preferred_element_type=jnp.float32
    ) * HEAD ** (-0.5)
    value_grad = jnp.einsum(
        "hrk,rhd->khd", probabilities_low, grads3, preferred_element_type=jnp.float32
    )
    return query_grad, key_grad, value_grad


def _pair_masks(scalars_ref, micro, row_count, key_count):
    length = scalars_ref[micro]
    first_row = scalars_ref[scalars_ref.shape[0] - 1]
    query_pos = first_row + lax.broadcasted_iota(jnp.int32, (row_count, key_count), 0)
    key_pos = lax.broadcasted_iota(jnp.int32, (row_count, key_count), 1)
    return (key_pos <= query_pos) & (key_pos < length)


def _forward_kernel(scalars_ref, q_ref, k_ref, v_ref, out_ref, lse_ref):
    micro = pl.program_id(0)
    row_count = q_ref.shape[0]
    key_count = k_ref.shape[0]
    allowed = _pair_masks(scalars_ref, micro, row_count, key_count)
    for half in range(2):
        lanes = slice(half * HEAD, (half + 1) * HEAD)
        q_head = q_ref[:, lanes]
        k_head = k_ref[:, lanes]
        v_head = v_ref[:, lanes]
        scores = lax.dot_general(
            q_head, k_head, (((1,), (1,)), ((), ())), preferred_element_type=jnp.float32
        ) * HEAD ** (-0.5)
        masked = jnp.where(allowed, scores, masked_value)
        top = jnp.max(masked, axis=1, keepdims=True)
        kept = jnp.where(allowed, jnp.exp(masked - top), 0.0)
        log_total = top + jnp.log(jnp.sum(kept, axis=1, keepdims=True))
        probabilities = jnp.where(allowed, jnp.exp(scores - log_total), 0.0)
        attended = jnp.dot(
            probabilities.astype(jnp.bfloat16), v_head, preferred_element_type=jnp.float32
        )
        out_ref[:, lanes] = attended
        lse_ref[:, lanes] = jnp.broadcast_to(log_total, (row_count, HEAD))


def _backward_kernel(
    scalars_ref, q_ref, k_ref, v_ref, do_ref, o_ref, lse_ref, dq_ref, kv_grad_ref
):
    micro = pl.program_id(0)
    row_count = q_ref.shape[0]
    key_count = k_ref.shape[0]
    allowed = _pair_masks(scalars_ref, micro, row_count, key_count)
    for half in range(2):
        lanes = slice(half * HEAD, (half + 1) * HEAD)
        q_head = q_ref[:, lanes]
        k_head = k_ref[:, lanes]
        v_head = v_ref[:, lanes]
        grad_head = do_ref[:, lanes]
        scores = lax.dot_general(
            q_head, k_head, (((1,), (1,)), ((), ())), preferred_element_type=jnp.float32
        ) * HEAD ** (-0.5)
        log_total = lse_ref[:, half * HEAD : half * HEAD + 1]
        probabilities = jnp.where(allowed, jnp.exp(scores - log_total), 0.0)
        probabilities_low = probabilities.astype(jnp.bfloat16)
        prob_grad = lax.dot_general(
            grad_head, v_head, (((1,), (1,)), ((), ())), preferred_element_type=jnp.float32
        )
        row_delta = jnp.sum(
            grad_head.astype(jnp.float32) * o_ref[:, lanes], axis=1, keepdims=True
        )
        score_low = (probabilities * (prob_grad - row_delta)).astype(jnp.bfloat16)
        dq_ref[:, lanes] = jnp.dot(
            score_low, k_head, preferred_element_type=jnp.float32
        ) * HEAD ** (-0.5)
        key_grad = lax.dot_general(
            score_low, q_head, (((0,), (0,)), ((), ())), preferred_element_type=jnp.float32
        ) * HEAD ** (-0.5)
        value_grad = lax.dot_general(
            probabilities_low, grad_head, (((0,), (0,)), ((), ())),
            preferred_element_type=jnp.float32,
        )
        kv_grad_ref[:, lanes] = key_grad.astype(jnp.bfloat16)
        kv_grad_ref[:, 2 * HEAD + half * HEAD : 2 * HEAD + (half + 1) * HEAD] = value_grad.astype(
            jnp.bfloat16
        )


def attention_forward(scalars, queries, kv_flat, batches):
    all_rows, model_width = queries.shape
    row_count = all_rows // batches
    key_count = kv_flat.shape[0]
    pairs = model_width // (2 * HEAD)
    micro_blocks = kv_flat.shape[1] // batches // (2 * HEAD)
    row_spec = pl.BlockSpec((row_count, 2 * HEAD), lambda m, p, s: (m, p))
    key_spec = pl.BlockSpec((key_count, 2 * HEAD), lambda m, p, s: (0, m * micro_blocks + p))
    value_spec = pl.BlockSpec(
        (key_count, 2 * HEAD), lambda m, p, s: (0, m * micro_blocks + pairs + p)
    )
    return pl.pallas_call(
        _forward_kernel,
        grid_spec=pltpu.PrefetchScalarGridSpec(
            num_scalar_prefetch=1,
            grid=(batches, pairs),
            in_specs=[row_spec, key_spec, value_spec],
            out_specs=[row_spec, row_spec],
        ),
        out_shape=[
            jax.ShapeDtypeStruct((all_rows, model_width), jnp.float32),
            jax.ShapeDtypeStruct((all_rows, model_width), jnp.float32),
        ],
        name="attention_forward",
    )(scalars, queries, kv_flat, kv_flat)


def attention_backward(scalars, queries, kv_flat, grads, attended, log_totals, batches):
    all_rows, model_width = queries.shape
    row_count = all_rows // batches
    key_count = kv_flat.shape[0]
    pairs = model_width // (2 * HEAD)
    micro_blocks = kv_flat.shape[1] // batches // (2 * HEAD)
    row_spec = pl.BlockSpec((row_count, 2 * HEAD), lambda m, p, s: (m, p))
    key_spec = pl.BlockSpec((key_count, 2 * HEAD), lambda m, p, s: (0, m * micro_blocks + p))
    value_spec = pl.BlockSpec(
        (key_count, 2 * HEAD), lambda m, p, s: (0, m * micro_blocks + pairs + p)
    )
    grad_spec = pl.BlockSpec((key_count, 4 * HEAD), lambda m, p, s: (0, m * pairs + p))
    return pl.pallas_call(
        _backward_kernel,
        grid_spec=pltpu.PrefetchScalarGridSpec(
            num_scalar_prefetch=1,
            grid=(batches, pairs),
            in_specs=[row_spec, key_spec, value_spec, row_spec, row_spec, row_spec],
            out_specs=[row_spec, grad_spec],
        ),
        out_shape=[
            jax.ShapeDtypeStruct((all_rows, model_width), jnp.float32),
            jax.ShapeDtypeStruct(kv_flat.shape, jnp.bfloat16),
        ],
        name="attention_backward",
    )(scalars, queries, kv_flat, kv_flat, grads, attended, log_totals)


def local(
    layer_input,
    history,
    cotangent,
    lengths,
    w_qkv,
    w_out,
    w_up,
    w_down,
    ln_gains,
    ln_biases,
    depth_weights,
):
    batches = layer_input.shape[0]
    row_count = layer_input.shape[2]
    model_width = layer_input.shape[3]
    ff_width = w_up.shape[1]
    shard_rows = w_qkv.shape[0]
    all_rows = batches * row_count
    slot_len = row_count * lax.axis_size("seq")
    positions = lax.axis_index("seq") * row_count + jnp.arange(row_count, dtype=jnp.int32)
    cosine_part, sine_part = rotary_tables(jnp.tile(positions, batches))
    gelu_tanh = partial(jax.nn.gelu, approximate=True)
    lane_pad = 128 - 4
    widths = (3 * model_width, 2, 2, lane_pad, model_width, ff_width, ff_width)
    offsets = [0]
    for width in widths:
        offsets.append(offsets[-1] + width)
    late_width = offsets[4]

    def pieces(packed_rows):
        return [packed_rows[:, offsets[i] : offsets[i + 1]] for i in range(len(widths))]

    packed = jnp.concatenate(
        [
            w_qkv,
            ln_gains,
            ln_biases,
            jnp.zeros((shard_rows, lane_pad), w_qkv.dtype),
            w_out,
            w_up,
            w_down.reshape(shard_rows, ff_width),
        ],
        axis=1,
    )
    gathered = lax.all_gather(packed, ("seq", "fsdp"), axis=0, tiled=True)
    full_qkv, gain_rows, bias_rows, _, full_out, full_up, down_rows = pieces(gathered)
    full_down = down_rows.reshape(ff_width, model_width)
    norm_gains = gain_rows.astype(jnp.float32)
    norm_biases = bias_rows.astype(jnp.float32)

    slot_lengths = lengths[:, 0]
    inputs = layer_input[:, 0].reshape(all_rows, model_width).astype(jnp.float32)
    first_low = layer_norm(inputs, norm_gains[:, 0], norm_biases[:, 0]).astype(jnp.bfloat16)
    projected = jnp.dot(first_low, full_qkv, preferred_element_type=jnp.float32)
    queries = rotate(projected[:, :model_width], cosine_part, sine_part).astype(jnp.bfloat16)
    keys_own = rotate(
        projected[:, model_width : 2 * model_width], cosine_part, sine_part
    ).astype(jnp.bfloat16)
    values_own = projected[:, 2 * model_width :].astype(jnp.bfloat16)
    own_kv = jnp.concatenate([keys_own, values_own], axis=1).reshape(
        batches, row_count, 2 * model_width
    )
    earlier = history[:, :, 0].reshape(4, all_rows, model_width).astype(jnp.float32)
    usable = (positions[None, :] < slot_lengths[:, None]).reshape(all_rows, 1)
    grad_next = jnp.where(
        usable, cotangent[:, 0].reshape(all_rows, model_width).astype(jnp.float32), 0.0
    )
    history_part = jnp.einsum("j,jrd->rd", depth_weights[:4], earlier)
    grad_history = (depth_weights[:4, None, None] * grad_next[None]).astype(jnp.bfloat16)
    grad_history = grad_history.reshape(4, batches, 1, row_count, model_width)
    out_grad = depth_weights[4] * grad_next
    out_low = out_grad.astype(jnp.bfloat16)

    kv_all = lax.all_gather(jnp.swapaxes(own_kv, 0, 1), "seq", axis=0, tiled=True)
    kv_flat = kv_all.reshape(slot_len, batches * 2 * model_width)
    scalars = jnp.concatenate(
        [slot_lengths.astype(jnp.int32), (lax.axis_index("seq") * row_count)[None].astype(jnp.int32)]
    )
    attended_rows, log_totals = attention_forward(scalars, queries, kv_flat, batches)
    attended_low = attended_rows.astype(jnp.bfloat16)
    residual = inputs + jnp.dot(attended_low, full_out, preferred_element_type=jnp.float32)
    second_low = layer_norm(residual, norm_gains[:, 1], norm_biases[:, 1]).astype(jnp.bfloat16)
    hidden = jnp.dot(second_low, full_up, preferred_element_type=jnp.float32)
    hidden_low = gelu_tanh(hidden).astype(jnp.bfloat16)
    block_out = residual + jnp.dot(hidden_low, full_down, preferred_element_type=jnp.float32)
    hidden_grad = jnp.einsum("rd,fd->rf", out_low, full_down, preferred_element_type=jnp.float32)
    _, gelu_pullback = jax.vjp(gelu_tanh, hidden)
    up_low = gelu_pullback(hidden_grad)[0].astype(jnp.bfloat16)
    second_grad = jnp.einsum("rf,df->rd", up_low, full_up, preferred_element_type=jnp.float32)
    _, second_pullback = jax.vjp(layer_norm, residual, norm_gains[:, 1], norm_biases[:, 1])
    residual_part, gain_two, bias_two = second_pullback(second_grad)
    residual_grad = out_grad + residual_part
    branch_low = residual_grad.astype(jnp.bfloat16)
    attended_grad = jnp.einsum(
        "rd,cd->rc", branch_low, full_out, preferred_element_type=jnp.float32
    ).astype(jnp.bfloat16)
    query_grad, kv_grad_flat = attention_backward(
        scalars, queries, kv_flat, attended_grad, attended_rows, log_totals, batches
    )
    kv_grad_own = lax.psum_scatter(kv_grad_flat, "seq", scatter_dimension=0, tiled=True)
    pairs = model_width // (2 * HEAD)
    kv_grad_own = kv_grad_own.reshape(row_count, batches, pairs, 2, 2 * HEAD)
    kv_grad_own = jnp.transpose(kv_grad_own, (1, 0, 3, 2, 4)).reshape(
        all_rows, 2 * model_width
    )
    key_value_all = kv_grad_own.astype(jnp.float32)
    combined = depth_weights[4] * block_out + history_part
    next_input = combined.astype(jnp.bfloat16).reshape(batches, 1, row_count, model_width)
    depth_terms = jnp.concatenate(
        [jnp.einsum("jrd,rd->j", earlier, grad_next), jnp.sum(block_out * grad_next)[None]]
    )
    grad_down = jnp.einsum("rf,rd->fd", hidden_low, out_low, preferred_element_type=jnp.float32)
    grad_up = jnp.einsum("rd,rf->df", second_low, up_low, preferred_element_type=jnp.float32)
    grad_outproj = jnp.einsum(
        "rc,rd->cd", attended_low, branch_low, preferred_element_type=jnp.float32
    )
    early_grads = jnp.concatenate(
        [
            jnp.zeros((model_width, late_width), jnp.float32),
            grad_outproj,
            grad_up,
            grad_down.reshape(model_width, ff_width),
        ],
        axis=1,
    ).astype(jnp.bfloat16)
    qkv_low = jnp.concatenate(
        [
            rotate(query_grad, cosine_part, -sine_part),
            rotate(key_value_all[:, :model_width], cosine_part, -sine_part),
            key_value_all[:, model_width:],
        ],
        axis=1,
    ).astype(jnp.bfloat16)
    grad_qkv = jnp.einsum("rd,rc->dc", first_low, qkv_low, preferred_element_type=jnp.float32)
    first_grad = jnp.einsum("rc,dc->rd", qkv_low, full_qkv, preferred_element_type=jnp.float32)
    _, first_pullback = jax.vjp(layer_norm, inputs, norm_gains[:, 0], norm_biases[:, 0])
    input_part, gain_one, bias_one = first_pullback(first_grad)
    grad_input = (residual_grad + input_part).astype(jnp.bfloat16)
    grad_input = grad_input.reshape(batches, 1, row_count, model_width)
    late_grads = jnp.concatenate(
        [
            grad_qkv,
            jnp.stack([gain_one, gain_two], axis=1),
            jnp.stack([bias_one, bias_two], axis=1),
            jnp.zeros((model_width, lane_pad), jnp.float32),
        ],
        axis=1,
    ).astype(jnp.bfloat16)
    packed_grads = lax.dynamic_update_slice(early_grads, late_grads, (0, 0))
    device_count = model_width // shard_rows
    row_major = Layout(major_to_minor=(0, 1, 2))
    scattered = lax.psum_scatter(
        with_layout_constraint(
            packed_grads.reshape(device_count, shard_rows, offsets[-1]), row_major
        ),
        ("seq", "fsdp"),
        scatter_dimension=0,
        tiled=False,
    )
    scattered = with_layout_constraint(scattered, Layout(major_to_minor=(0, 1)))
    full_pieces = pieces(scattered.astype(jnp.float32))
    owned = [
        full_pieces[0],
        full_pieces[4],
        full_pieces[5],
        full_pieces[6].reshape(-1, model_width),
        full_pieces[1],
        full_pieces[2],
    ]
    depth_total = lax.psum(depth_terms, ("seq", "fsdp"))
    return (next_input, grad_input, grad_history, *owned, depth_total)


def solution(mesh):
    in_specs = (
        P(None, "fsdp", "seq", None),
        P(None, None, "fsdp", "seq", None),
        P(None, "fsdp", "seq", None),
        P(None, "fsdp"),
        P(("seq", "fsdp"), None),
        P(("seq", "fsdp"), None),
        P(("seq", "fsdp"), None),
        P(("seq", "fsdp"), None),
        P(("seq", "fsdp"), None),
        P(("seq", "fsdp"), None),
        P(),
    )
    out_specs = (
        P(None, "fsdp", "seq", None),
        P(None, "fsdp", "seq", None),
        P(None, None, "fsdp", "seq", None),
        P(("seq", "fsdp"), None),
        P(("seq", "fsdp"), None),
        P(("seq", "fsdp"), None),
        P(("seq", "fsdp"), None),
        P(("seq", "fsdp"), None),
        P(("seq", "fsdp"), None),
        P(),
    )
    return jax.shard_map(local, mesh=mesh, in_specs=in_specs, out_specs=out_specs, check_vma=False)
```

```python
from functools import partial
import math

import jax
import jax.numpy as jnp
from jax import lax
from jax.sharding import PartitionSpec as P
from jax.experimental.layout import Layout, with_layout_constraint
from jax.experimental import pallas as pl
from jax.experimental.pallas import tpu as pltpu

HEADS = 12
HEAD = 64


epsilon = 1e-05
masked_value = -1e30


def layer_norm(values, gain_vector, bias_vector):
    center = values - jnp.mean(values, axis=-1, keepdims=True)
    spread = jnp.mean(center * center, axis=-1, keepdims=True)
    return center * lax.rsqrt(spread + epsilon) * gain_vector + bias_vector


def rotary_tables(positions):
    half_width = HEAD // 2
    frequencies = 10000.0 ** (-jnp.arange(half_width, dtype=jnp.float32) / half_width)
    angles = positions.astype(jnp.float32)[:, None] * frequencies[None, :]
    return (jnp.cos(angles)[:, None, :], jnp.sin(angles)[:, None, :])


def rotate(values, cosine_part, sine_part):
    row_count = values.shape[0]
    shaped = values.reshape(row_count, HEADS, HEAD)
    half_width = HEAD // 2
    first_half = shaped[..., :half_width]
    second_half = shaped[..., half_width:]
    turned = jnp.concatenate(
        [
            first_half * cosine_part - second_half * sine_part,
            second_half * cosine_part + first_half * sine_part,
        ],
        axis=-1,
    )
    return turned.reshape(row_count, HEADS * HEAD)


def block_scores(queries3, keys3, query_pos, key_pos, length):
    scores = jnp.einsum(
        "rhd,khd->hrk", queries3, keys3, preferred_element_type=jnp.float32
    ) * HEAD ** (-0.5)
    allowed = (key_pos[None, :] <= query_pos[:, None]) & (key_pos[None, :] < length)
    return (scores, allowed[None])


def row_totals(queries3, keys3, query_pos, length, key_block):
    row_count = queries3.shape[0]

    def row_advance(state, block_index):
        running_top, running_sum = state
        first_key = block_index * key_block
        keys_part = lax.dynamic_slice_in_dim(keys3, first_key, key_block, 0)
        key_pos = first_key + jnp.arange(key_block, dtype=jnp.int32)
        scores, allowed = block_scores(queries3, keys_part, query_pos, key_pos, length)
        masked = jnp.where(allowed, scores, masked_value)
        new_top = jnp.maximum(running_top, jnp.max(masked, axis=-1))
        kept_terms = jnp.where(allowed, jnp.exp(masked - new_top[..., None]), 0.0)
        running_sum = running_sum * jnp.exp(running_top - new_top) + jnp.sum(kept_terms, axis=-1)
        return ((new_top, running_sum), None)

    initial = (
        jnp.full((HEADS, row_count), masked_value, jnp.float32),
        jnp.zeros((HEADS, row_count), jnp.float32),
    )
    (row_tops, row_sums), _ = lax.scan(
        row_advance, initial, jnp.arange(keys3.shape[0] // key_block, dtype=jnp.int32)
    )
    return row_tops + jnp.log(row_sums)


def attend(queries3, keys3, values3, query_pos, length, key_block, log_total):

    def attend_advance(running, block_index):
        first_key = block_index * key_block
        keys_part = lax.dynamic_slice_in_dim(keys3, first_key, key_block, 0)
        values_part = lax.dynamic_slice_in_dim(values3, first_key, key_block, 0)
        key_pos = first_key + jnp.arange(key_block, dtype=jnp.int32)
        scores, allowed = block_scores(queries3, keys_part, query_pos, key_pos, length)
        probabilities = jnp.where(allowed, jnp.exp(scores - log_total[..., None]), 0.0).astype(
            jnp.bfloat16
        )
        return (
            running
            + jnp.einsum(
                "hrk,khd->rhd", probabilities, values_part, preferred_element_type=jnp.float32
            ),
            None,
        )

    initial = jnp.zeros(queries3.shape, jnp.float32)
    result, _ = lax.scan(
        attend_advance, initial, jnp.arange(keys3.shape[0] // key_block, dtype=jnp.int32)
    )
    return result


def query_grads(
    queries3, grads3, keys3, values3, query_pos, length, key_block, log_total, row_delta
):

    def query_advance(running, block_index):
        first_key = block_index * key_block
        keys_part = lax.dynamic_slice_in_dim(keys3, first_key, key_block, 0)
        values_part = lax.dynamic_slice_in_dim(values3, first_key, key_block, 0)
        key_pos = first_key + jnp.arange(key_block, dtype=jnp.int32)
        scores, allowed = block_scores(queries3, keys_part, query_pos, key_pos, length)
        probabilities = jnp.where(allowed, jnp.exp(scores - log_total[..., None]), 0.0)
        prob_grad = jnp.einsum(
            "rhd,khd->hrk", grads3, values_part, preferred_element_type=jnp.float32
        )
        score_low = (probabilities * (prob_grad - row_delta[..., None])).astype(jnp.bfloat16)
        return (
            running
            + jnp.einsum("hrk,khd->rhd", score_low, keys_part, preferred_element_type=jnp.float32),
            None,
        )

    initial = jnp.zeros(queries3.shape, jnp.float32)
    result, _ = lax.scan(
        query_advance, initial, jnp.arange(keys3.shape[0] // key_block, dtype=jnp.int32)
    )
    return result * HEAD ** (-0.5)


def key_side(queries3, grads3, log_part, delta_part, query_pos, keys3, values3, key_pos, length):
    key_count = keys3.shape[0]
    scores, allowed = block_scores(queries3, keys3, query_pos, key_pos, length)
    probabilities = jnp.where(allowed, jnp.exp(scores - log_part[..., None]), 0.0)
    prob_grad = jnp.einsum("rhd,khd->hrk", grads3, values3, preferred_element_type=jnp.float32)
    score_low = (probabilities * (prob_grad - delta_part[..., None])).astype(jnp.bfloat16)
    value_grad = jnp.einsum(
        "hrk,rhd->khd",
        probabilities.astype(jnp.bfloat16),
        grads3,
        preferred_element_type=jnp.float32,
    )
    key_grad = jnp.einsum(
        "hrk,rhd->khd", score_low, queries3, preferred_element_type=jnp.float32
    ) * HEAD ** (-0.5)
    return jnp.concatenate(
        [key_grad.reshape(key_count, HEADS * HEAD), value_grad.reshape(key_count, HEADS * HEAD)],
        axis=1,
    )


def slot_attention(queries3, keys3, values3, query_pos, length):
    key_pos = jnp.arange(keys3.shape[0], dtype=jnp.int32)
    scores, allowed = block_scores(queries3, keys3, query_pos, key_pos, length)
    masked = jnp.where(allowed, scores, masked_value)
    top = jnp.max(masked, axis=-1)
    kept_terms = jnp.where(allowed, jnp.exp(masked - top[..., None]), 0.0)
    log_total = top + jnp.log(jnp.sum(kept_terms, axis=-1))
    probabilities = jnp.where(allowed, jnp.exp(scores - log_total[..., None]), 0.0)
    probabilities_low = probabilities.astype(jnp.bfloat16)
    attended = jnp.einsum(
        "hrk,khd->rhd", probabilities_low, values3, preferred_element_type=jnp.float32
    )
    return attended, probabilities, probabilities_low


def slot_attention_grads(queries3, keys3, values3, grads3, attended, probabilities, probabilities_low):
    prob_grad = jnp.einsum("rhd,khd->hrk", grads3, values3, preferred_element_type=jnp.float32)
    row_delta = jnp.einsum("rhd,rhd->hr", grads3.astype(jnp.float32), attended)
    score_low = (probabilities * (prob_grad - row_delta[..., None])).astype(jnp.bfloat16)
    query_grad = jnp.einsum(
        "hrk,khd->rhd", score_low, keys3, preferred_element_type=jnp.float32
    ) * HEAD ** (-0.5)
    key_grad = jnp.einsum(
        "hrk,rhd->khd", score_low, queries3, preferred_element_type=jnp.float32
    ) * HEAD ** (-0.5)
    value_grad = jnp.einsum(
        "hrk,rhd->khd", probabilities_low, grads3, preferred_element_type=jnp.float32
    )
    return query_grad, key_grad, value_grad


def _pair_masks(scalars_ref, micro, row_count, key_count):
    length = scalars_ref[micro]
    first_row = scalars_ref[scalars_ref.shape[0] - 1]
    query_pos = first_row + lax.broadcasted_iota(jnp.int32, (row_count, key_count), 0)
    key_pos = lax.broadcasted_iota(jnp.int32, (row_count, key_count), 1)
    return (key_pos <= query_pos) & (key_pos < length)


def _forward_kernel(scalars_ref, q_ref, k_ref, v_ref, out_ref, lse_ref):
    micro = pl.program_id(0)
    row_count = q_ref.shape[0]
    key_count = k_ref.shape[0]
    allowed = _pair_masks(scalars_ref, micro, row_count, key_count)
    for half in range(2):
        lanes = slice(half * HEAD, (half + 1) * HEAD)
        q_head = q_ref[:, lanes]
        k_head = k_ref[:, lanes]
        v_head = v_ref[:, lanes]
        scores = lax.dot_general(
            q_head, k_head, (((1,), (1,)), ((), ())), preferred_element_type=jnp.float32
        ) * HEAD ** (-0.5)
        masked = jnp.where(allowed, scores, masked_value)
        top = jnp.max(masked, axis=1, keepdims=True)
        kept = jnp.where(allowed, jnp.exp(masked - top), 0.0)
        total = jnp.sum(kept, axis=1, keepdims=True)
        log_total = top + jnp.log(total)
        probabilities = kept * (1.0 / total)
        attended = jnp.dot(
            probabilities.astype(jnp.bfloat16), v_head, preferred_element_type=jnp.float32
        )
        out_ref[:, lanes] = attended
        lse_ref[:, lanes] = jnp.broadcast_to(log_total, (row_count, HEAD))


def _backward_kernel(
    scalars_ref, q_ref, k_ref, v_ref, do_ref, o_ref, lse_ref, dq_ref, kv_grad_ref
):
    micro = pl.program_id(0)
    row_count = q_ref.shape[0]
    key_count = k_ref.shape[0]
    allowed = _pair_masks(scalars_ref, micro, row_count, key_count)
    for half in range(2):
        lanes = slice(half * HEAD, (half + 1) * HEAD)
        q_head = q_ref[:, lanes]
        k_head = k_ref[:, lanes]
        v_head = v_ref[:, lanes]
        grad_head = do_ref[:, lanes]
        scores = lax.dot_general(
            q_head, k_head, (((1,), (1,)), ((), ())), preferred_element_type=jnp.float32
        ) * HEAD ** (-0.5)
        log_total = lse_ref[:, half * HEAD : half * HEAD + 1]
        probabilities = jnp.where(allowed, jnp.exp(scores - log_total), 0.0)
        probabilities_low = probabilities.astype(jnp.bfloat16)
        prob_grad = lax.dot_general(
            grad_head, v_head, (((1,), (1,)), ((), ())), preferred_element_type=jnp.float32
        )
        row_delta = jnp.sum(
            grad_head.astype(jnp.float32) * o_ref[:, lanes], axis=1, keepdims=True
        )
        score_low = (probabilities * (prob_grad - row_delta)).astype(jnp.bfloat16)
        dq_ref[:, lanes] = jnp.dot(
            score_low, k_head, preferred_element_type=jnp.float32
        ) * HEAD ** (-0.5)
        key_grad = lax.dot_general(
            score_low, q_head, (((0,), (0,)), ((), ())), preferred_element_type=jnp.float32
        ) * HEAD ** (-0.5)
        value_grad = lax.dot_general(
            probabilities_low, grad_head, (((0,), (0,)), ((), ())),
            preferred_element_type=jnp.float32,
        )
        kv_grad_ref[:, lanes] = key_grad.astype(jnp.bfloat16)
        kv_grad_ref[:, 2 * HEAD + half * HEAD : 2 * HEAD + (half + 1) * HEAD] = value_grad.astype(
            jnp.bfloat16
        )


def attention_forward(scalars, queries, kv_flat, batches):
    all_rows, model_width = queries.shape
    row_count = all_rows // batches
    key_count = kv_flat.shape[0]
    pairs = model_width // (2 * HEAD)
    micro_blocks = kv_flat.shape[1] // batches // (2 * HEAD)
    row_spec = pl.BlockSpec((row_count, 2 * HEAD), lambda m, p, s: (m, p))
    key_spec = pl.BlockSpec((key_count, 2 * HEAD), lambda m, p, s: (0, m * micro_blocks + p))
    value_spec = pl.BlockSpec(
        (key_count, 2 * HEAD), lambda m, p, s: (0, m * micro_blocks + pairs + p)
    )
    return pl.pallas_call(
        _forward_kernel,
        grid_spec=pltpu.PrefetchScalarGridSpec(
            num_scalar_prefetch=1,
            grid=(batches, pairs),
            in_specs=[row_spec, key_spec, value_spec],
            out_specs=[row_spec, row_spec],
        ),
        out_shape=[
            jax.ShapeDtypeStruct((all_rows, model_width), jnp.float32),
            jax.ShapeDtypeStruct((all_rows, model_width), jnp.float32),
        ],
        name="attention_forward",
    )(scalars, queries, kv_flat, kv_flat)


def attention_backward(scalars, queries, kv_flat, grads, attended, log_totals, batches):
    all_rows, model_width = queries.shape
    row_count = all_rows // batches
    key_count = kv_flat.shape[0]
    pairs = model_width // (2 * HEAD)
    micro_blocks = kv_flat.shape[1] // batches // (2 * HEAD)
    row_spec = pl.BlockSpec((row_count, 2 * HEAD), lambda m, p, s: (m, p))
    key_spec = pl.BlockSpec((key_count, 2 * HEAD), lambda m, p, s: (0, m * micro_blocks + p))
    value_spec = pl.BlockSpec(
        (key_count, 2 * HEAD), lambda m, p, s: (0, m * micro_blocks + pairs + p)
    )
    grad_spec = pl.BlockSpec((key_count, 4 * HEAD), lambda m, p, s: (0, m * pairs + p))
    return pl.pallas_call(
        _backward_kernel,
        grid_spec=pltpu.PrefetchScalarGridSpec(
            num_scalar_prefetch=1,
            grid=(batches, pairs),
            in_specs=[row_spec, key_spec, value_spec, row_spec, row_spec, row_spec],
            out_specs=[row_spec, grad_spec],
        ),
        out_shape=[
            jax.ShapeDtypeStruct((all_rows, model_width), jnp.float32),
            jax.ShapeDtypeStruct(kv_flat.shape, jnp.bfloat16),
        ],
        name="attention_backward",
    )(scalars, queries, kv_flat, kv_flat, grads, attended, log_totals)


def local(
    layer_input,
    history,
    cotangent,
    lengths,
    w_qkv,
    w_out,
    w_up,
    w_down,
    ln_gains,
    ln_biases,
    depth_weights,
):
    batches = layer_input.shape[0]
    row_count = layer_input.shape[2]
    model_width = layer_input.shape[3]
    ff_width = w_up.shape[1]
    shard_rows = w_qkv.shape[0]
    all_rows = batches * row_count
    slot_len = row_count * lax.axis_size("seq")
    positions = lax.axis_index("seq") * row_count + jnp.arange(row_count, dtype=jnp.int32)
    cosine_part, sine_part = rotary_tables(jnp.tile(positions, batches))
    gelu_tanh = partial(jax.nn.gelu, approximate=True)
    lane_pad = 128 - 4
    widths = (3 * model_width, 2, 2, lane_pad, model_width, ff_width, ff_width)
    offsets = [0]
    for width in widths:
        offsets.append(offsets[-1] + width)
    late_width = offsets[4]

    def pieces(packed_rows):
        return [packed_rows[:, offsets[i] : offsets[i + 1]] for i in range(len(widths))]

    packed = jnp.concatenate(
        [
            w_qkv,
            ln_gains,
            ln_biases,
            jnp.zeros((shard_rows, lane_pad), w_qkv.dtype),
            w_out,
            w_up,
            w_down.reshape(shard_rows, ff_width),
        ],
        axis=1,
    )
    gathered = lax.all_gather(packed, ("seq", "fsdp"), axis=0, tiled=True)
    full_qkv, gain_rows, bias_rows, _, full_out, full_up, down_rows = pieces(gathered)
    full_down = down_rows.reshape(ff_width, model_width)
    norm_gains = gain_rows.astype(jnp.float32)
    norm_biases = bias_rows.astype(jnp.float32)

    slot_lengths = lengths[:, 0]
    inputs = layer_input[:, 0].reshape(all_rows, model_width).astype(jnp.float32)
    first_low = layer_norm(inputs, norm_gains[:, 0], norm_biases[:, 0]).astype(jnp.bfloat16)
    projected = jnp.dot(first_low, full_qkv, preferred_element_type=jnp.float32)
    queries = rotate(projected[:, :model_width], cosine_part, sine_part).astype(jnp.bfloat16)
    keys_own = rotate(
        projected[:, model_width : 2 * model_width], cosine_part, sine_part
    ).astype(jnp.bfloat16)
    values_own = projected[:, 2 * model_width :].astype(jnp.bfloat16)
    own_kv = jnp.concatenate([keys_own, values_own], axis=1).reshape(
        batches, row_count, 2 * model_width
    )
    earlier = history[:, :, 0].reshape(4, all_rows, model_width).astype(jnp.float32)
    usable = (positions[None, :] < slot_lengths[:, None]).reshape(all_rows, 1)
    grad_next = jnp.where(
        usable, cotangent[:, 0].reshape(all_rows, model_width).astype(jnp.float32), 0.0
    )
    history_part = jnp.einsum("j,jrd->rd", depth_weights[:4], earlier)
    grad_history = (depth_weights[:4, None, None] * grad_next[None]).astype(jnp.bfloat16)
    grad_history = grad_history.reshape(4, batches, 1, row_count, model_width)
    out_grad = depth_weights[4] * grad_next
    out_low = out_grad.astype(jnp.bfloat16)

    kv_all = lax.all_gather(
        jnp.swapaxes(own_kv, 0, 1).reshape(row_count, batches * 2 * model_width),
        "seq",
        axis=0,
        tiled=False,
    )
    kv_flat = kv_all.reshape(slot_len, batches * 2 * model_width)
    scalars = jnp.concatenate(
        [slot_lengths.astype(jnp.int32), (lax.axis_index("seq") * row_count)[None].astype(jnp.int32)]
    )
    attended_rows, log_totals = attention_forward(scalars, queries, kv_flat, batches)
    attended_low = attended_rows.astype(jnp.bfloat16)
    residual = inputs + jnp.dot(attended_low, full_out, preferred_element_type=jnp.float32)
    second_low = layer_norm(residual, norm_gains[:, 1], norm_biases[:, 1]).astype(jnp.bfloat16)
    hidden = jnp.dot(second_low, full_up, preferred_element_type=jnp.float32)
    hidden_low = gelu_tanh(hidden).astype(jnp.bfloat16)
    block_out = residual + jnp.dot(hidden_low, full_down, preferred_element_type=jnp.float32)
    hidden_grad = jnp.einsum("rd,fd->rf", out_low, full_down, preferred_element_type=jnp.float32)
    _, gelu_pullback = jax.vjp(gelu_tanh, hidden)
    up_low = gelu_pullback(hidden_grad)[0].astype(jnp.bfloat16)
    second_grad = jnp.einsum("rf,df->rd", up_low, full_up, preferred_element_type=jnp.float32)
    _, second_pullback = jax.vjp(layer_norm, residual, norm_gains[:, 1], norm_biases[:, 1])
    residual_part, gain_two, bias_two = second_pullback(second_grad)
    residual_grad = out_grad + residual_part
    branch_low = residual_grad.astype(jnp.bfloat16)
    attended_grad = jnp.einsum(
        "rd,cd->rc", branch_low, full_out, preferred_element_type=jnp.float32
    ).astype(jnp.bfloat16)
    query_grad, kv_grad_flat = attention_backward(
        scalars, queries, kv_flat, attended_grad, attended_rows, log_totals, batches
    )
    kv_grad_own = lax.psum_scatter(kv_grad_flat, "seq", scatter_dimension=0, tiled=True)
    pairs = model_width // (2 * HEAD)
    kv_grad_own = kv_grad_own.reshape(row_count, batches, pairs, 2, 2 * HEAD)
    kv_grad_own = jnp.transpose(kv_grad_own, (1, 0, 3, 2, 4)).reshape(
        all_rows, 2 * model_width
    )
    key_value_all = kv_grad_own.astype(jnp.float32)
    combined = depth_weights[4] * block_out + history_part
    next_input = combined.astype(jnp.bfloat16).reshape(batches, 1, row_count, model_width)
    depth_terms = jnp.concatenate(
        [jnp.einsum("jrd,rd->j", earlier, grad_next), jnp.sum(block_out * grad_next)[None]]
    )
    grad_down = jnp.einsum("rf,rd->fd", hidden_low, out_low, preferred_element_type=jnp.float32)
    grad_up = jnp.einsum("rd,rf->df", second_low, up_low, preferred_element_type=jnp.float32)
    grad_outproj = jnp.einsum(
        "rc,rd->cd", attended_low, branch_low, preferred_element_type=jnp.float32
    )
    early_grads = jnp.concatenate(
        [
            jnp.zeros((model_width, late_width), jnp.float32),
            grad_outproj,
            grad_up,
            grad_down.reshape(model_width, ff_width),
        ],
        axis=1,
    ).astype(jnp.bfloat16)
    qkv_low = jnp.concatenate(
        [
            rotate(query_grad, cosine_part, -sine_part),
            rotate(key_value_all[:, :model_width], cosine_part, -sine_part),
            key_value_all[:, model_width:],
        ],
        axis=1,
    ).astype(jnp.bfloat16)
    grad_qkv = jnp.einsum("rd,rc->dc", first_low, qkv_low, preferred_element_type=jnp.float32)
    first_grad = jnp.einsum("rc,dc->rd", qkv_low, full_qkv, preferred_element_type=jnp.float32)
    _, first_pullback = jax.vjp(layer_norm, inputs, norm_gains[:, 0], norm_biases[:, 0])
    input_part, gain_one, bias_one = first_pullback(first_grad)
    grad_input = (residual_grad + input_part).astype(jnp.bfloat16)
    grad_input = grad_input.reshape(batches, 1, row_count, model_width)
    late_grads = jnp.concatenate(
        [
            grad_qkv,
            jnp.stack([gain_one, gain_two], axis=1),
            jnp.stack([bias_one, bias_two], axis=1),
            jnp.zeros((model_width, lane_pad), jnp.float32),
        ],
        axis=1,
    ).astype(jnp.bfloat16)
    packed_grads = lax.dynamic_update_slice(early_grads, late_grads, (0, 0))
    device_count = model_width // shard_rows
    row_major = Layout(major_to_minor=(0, 1, 2))
    scattered = lax.psum_scatter(
        with_layout_constraint(
            packed_grads.reshape(device_count, shard_rows, offsets[-1]), row_major
        ),
        ("seq", "fsdp"),
        scatter_dimension=0,
        tiled=False,
    )
    scattered = with_layout_constraint(scattered, Layout(major_to_minor=(0, 1)))
    full_pieces = pieces(scattered.astype(jnp.float32))
    owned = [
        full_pieces[0],
        full_pieces[4],
        full_pieces[5],
        full_pieces[6].reshape(-1, model_width),
        full_pieces[1],
        full_pieces[2],
    ]
    depth_total = lax.psum(depth_terms, ("seq", "fsdp"))
    return (next_input, grad_input, grad_history, *owned, depth_total)


def solution(mesh):
    in_specs = (
        P(None, "fsdp", "seq", None),
        P(None, None, "fsdp", "seq", None),
        P(None, "fsdp", "seq", None),
        P(None, "fsdp"),
        P(("seq", "fsdp"), None),
        P(("seq", "fsdp"), None),
        P(("seq", "fsdp"), None),
        P(("seq", "fsdp"), None),
        P(("seq", "fsdp"), None),
        P(("seq", "fsdp"), None),
        P(),
    )
    out_specs = (
        P(None, "fsdp", "seq", None),
        P(None, "fsdp", "seq", None),
        P(None, None, "fsdp", "seq", None),
        P(("seq", "fsdp"), None),
        P(("seq", "fsdp"), None),
        P(("seq", "fsdp"), None),
        P(("seq", "fsdp"), None),
        P(("seq", "fsdp"), None),
        P(("seq", "fsdp"), None),
        P(),
    )
    return jax.shard_map(local, mesh=mesh, in_specs=in_specs, out_specs=out_specs, check_vma=False)
```

```python
from functools import partial
import math

import jax
import jax.numpy as jnp
from jax import lax
from jax.sharding import PartitionSpec as P
from jax.experimental.layout import Layout, with_layout_constraint
from jax.experimental import pallas as pl
from jax.experimental.pallas import tpu as pltpu

HEADS = 12
HEAD = 64


epsilon = 1e-05
masked_value = -1e30


def layer_norm(values, gain_vector, bias_vector):
    center = values - jnp.mean(values, axis=-1, keepdims=True)
    spread = jnp.mean(center * center, axis=-1, keepdims=True)
    return center * lax.rsqrt(spread + epsilon) * gain_vector + bias_vector


def rotary_tables(positions):
    half_width = HEAD // 2
    frequencies = 10000.0 ** (-jnp.arange(half_width, dtype=jnp.float32) / half_width)
    angles = positions.astype(jnp.float32)[:, None] * frequencies[None, :]
    return (jnp.cos(angles)[:, None, :], jnp.sin(angles)[:, None, :])


def rotate(values, cosine_part, sine_part):
    row_count = values.shape[0]
    shaped = values.reshape(row_count, HEADS, HEAD)
    half_width = HEAD // 2
    first_half = shaped[..., :half_width]
    second_half = shaped[..., half_width:]
    turned = jnp.concatenate(
        [
            first_half * cosine_part - second_half * sine_part,
            second_half * cosine_part + first_half * sine_part,
        ],
        axis=-1,
    )
    return turned.reshape(row_count, HEADS * HEAD)


def block_scores(queries3, keys3, query_pos, key_pos, length):
    scores = jnp.einsum(
        "rhd,khd->hrk", queries3, keys3, preferred_element_type=jnp.float32
    ) * HEAD ** (-0.5)
    allowed = (key_pos[None, :] <= query_pos[:, None]) & (key_pos[None, :] < length)
    return (scores, allowed[None])


def row_totals(queries3, keys3, query_pos, length, key_block):
    row_count = queries3.shape[0]

    def row_advance(state, block_index):
        running_top, running_sum = state
        first_key = block_index * key_block
        keys_part = lax.dynamic_slice_in_dim(keys3, first_key, key_block, 0)
        key_pos = first_key + jnp.arange(key_block, dtype=jnp.int32)
        scores, allowed = block_scores(queries3, keys_part, query_pos, key_pos, length)
        masked = jnp.where(allowed, scores, masked_value)
        new_top = jnp.maximum(running_top, jnp.max(masked, axis=-1))
        kept_terms = jnp.where(allowed, jnp.exp(masked - new_top[..., None]), 0.0)
        running_sum = running_sum * jnp.exp(running_top - new_top) + jnp.sum(kept_terms, axis=-1)
        return ((new_top, running_sum), None)

    initial = (
        jnp.full((HEADS, row_count), masked_value, jnp.float32),
        jnp.zeros((HEADS, row_count), jnp.float32),
    )
    (row_tops, row_sums), _ = lax.scan(
        row_advance, initial, jnp.arange(keys3.shape[0] // key_block, dtype=jnp.int32)
    )
    return row_tops + jnp.log(row_sums)


def attend(queries3, keys3, values3, query_pos, length, key_block, log_total):

    def attend_advance(running, block_index):
        first_key = block_index * key_block
        keys_part = lax.dynamic_slice_in_dim(keys3, first_key, key_block, 0)
        values_part = lax.dynamic_slice_in_dim(values3, first_key, key_block, 0)
        key_pos = first_key + jnp.arange(key_block, dtype=jnp.int32)
        scores, allowed = block_scores(queries3, keys_part, query_pos, key_pos, length)
        probabilities = jnp.where(allowed, jnp.exp(scores - log_total[..., None]), 0.0).astype(
            jnp.bfloat16
        )
        return (
            running
            + jnp.einsum(
                "hrk,khd->rhd", probabilities, values_part, preferred_element_type=jnp.float32
            ),
            None,
        )

    initial = jnp.zeros(queries3.shape, jnp.float32)
    result, _ = lax.scan(
        attend_advance, initial, jnp.arange(keys3.shape[0] // key_block, dtype=jnp.int32)
    )
    return result


def query_grads(
    queries3, grads3, keys3, values3, query_pos, length, key_block, log_total, row_delta
):

    def query_advance(running, block_index):
        first_key = block_index * key_block
        keys_part = lax.dynamic_slice_in_dim(keys3, first_key, key_block, 0)
        values_part = lax.dynamic_slice_in_dim(values3, first_key, key_block, 0)
        key_pos = first_key + jnp.arange(key_block, dtype=jnp.int32)
        scores, allowed = block_scores(queries3, keys_part, query_pos, key_pos, length)
        probabilities = jnp.where(allowed, jnp.exp(scores - log_total[..., None]), 0.0)
        prob_grad = jnp.einsum(
            "rhd,khd->hrk", grads3, values_part, preferred_element_type=jnp.float32
        )
        score_low = (probabilities * (prob_grad - row_delta[..., None])).astype(jnp.bfloat16)
        return (
            running
            + jnp.einsum("hrk,khd->rhd", score_low, keys_part, preferred_element_type=jnp.float32),
            None,
        )

    initial = jnp.zeros(queries3.shape, jnp.float32)
    result, _ = lax.scan(
        query_advance, initial, jnp.arange(keys3.shape[0] // key_block, dtype=jnp.int32)
    )
    return result * HEAD ** (-0.5)


def key_side(queries3, grads3, log_part, delta_part, query_pos, keys3, values3, key_pos, length):
    key_count = keys3.shape[0]
    scores, allowed = block_scores(queries3, keys3, query_pos, key_pos, length)
    probabilities = jnp.where(allowed, jnp.exp(scores - log_part[..., None]), 0.0)
    prob_grad = jnp.einsum("rhd,khd->hrk", grads3, values3, preferred_element_type=jnp.float32)
    score_low = (probabilities * (prob_grad - delta_part[..., None])).astype(jnp.bfloat16)
    value_grad = jnp.einsum(
        "hrk,rhd->khd",
        probabilities.astype(jnp.bfloat16),
        grads3,
        preferred_element_type=jnp.float32,
    )
    key_grad = jnp.einsum(
        "hrk,rhd->khd", score_low, queries3, preferred_element_type=jnp.float32
    ) * HEAD ** (-0.5)
    return jnp.concatenate(
        [key_grad.reshape(key_count, HEADS * HEAD), value_grad.reshape(key_count, HEADS * HEAD)],
        axis=1,
    )


def slot_attention(queries3, keys3, values3, query_pos, length):
    key_pos = jnp.arange(keys3.shape[0], dtype=jnp.int32)
    scores, allowed = block_scores(queries3, keys3, query_pos, key_pos, length)
    masked = jnp.where(allowed, scores, masked_value)
    top = jnp.max(masked, axis=-1)
    kept_terms = jnp.where(allowed, jnp.exp(masked - top[..., None]), 0.0)
    log_total = top + jnp.log(jnp.sum(kept_terms, axis=-1))
    probabilities = jnp.where(allowed, jnp.exp(scores - log_total[..., None]), 0.0)
    probabilities_low = probabilities.astype(jnp.bfloat16)
    attended = jnp.einsum(
        "hrk,khd->rhd", probabilities_low, values3, preferred_element_type=jnp.float32
    )
    return attended, probabilities, probabilities_low


def slot_attention_grads(queries3, keys3, values3, grads3, attended, probabilities, probabilities_low):
    prob_grad = jnp.einsum("rhd,khd->hrk", grads3, values3, preferred_element_type=jnp.float32)
    row_delta = jnp.einsum("rhd,rhd->hr", grads3.astype(jnp.float32), attended)
    score_low = (probabilities * (prob_grad - row_delta[..., None])).astype(jnp.bfloat16)
    query_grad = jnp.einsum(
        "hrk,khd->rhd", score_low, keys3, preferred_element_type=jnp.float32
    ) * HEAD ** (-0.5)
    key_grad = jnp.einsum(
        "hrk,rhd->khd", score_low, queries3, preferred_element_type=jnp.float32
    ) * HEAD ** (-0.5)
    value_grad = jnp.einsum(
        "hrk,rhd->khd", probabilities_low, grads3, preferred_element_type=jnp.float32
    )
    return query_grad, key_grad, value_grad


ROW_CHUNK = 32


def _chunk_mask(scalars_ref, micro, chunk, key_count):
    length = scalars_ref[micro]
    first_row = scalars_ref[scalars_ref.shape[0] - 1] + chunk * ROW_CHUNK
    query_pos = first_row + lax.broadcasted_iota(jnp.int32, (ROW_CHUNK, key_count), 0)
    key_pos = lax.broadcasted_iota(jnp.int32, (ROW_CHUNK, key_count), 1)
    return (key_pos <= query_pos) & (key_pos < length)


def _forward_kernel(scalars_ref, q_ref, k_ref, v_ref, out_ref, lse_ref):
    micro = pl.program_id(0)
    row_count = q_ref.shape[0]
    key_count = k_ref.shape[0]

    def chunk_body(chunk, carry):
        rows = pl.ds(pl.multiple_of(chunk * ROW_CHUNK, ROW_CHUNK), ROW_CHUNK)
        allowed = _chunk_mask(scalars_ref, micro, chunk, key_count)
        for half in range(2):
            lanes = slice(half * HEAD, (half + 1) * HEAD)
            scores = lax.dot_general(
                q_ref[rows, lanes],
                k_ref[:, lanes],
                (((1,), (1,)), ((), ())),
                preferred_element_type=jnp.float32,
            ) * HEAD ** (-0.5)
            masked = jnp.where(allowed, scores, masked_value)
            top = jnp.max(masked, axis=1, keepdims=True)
            kept = jnp.where(allowed, jnp.exp(masked - top), 0.0)
            total = jnp.sum(kept, axis=1, keepdims=True)
            log_total = top + jnp.log(total)
            probabilities = kept * (1.0 / total)
            out_ref[rows, lanes] = jnp.dot(
                probabilities.astype(jnp.bfloat16), v_ref[:, lanes],
                preferred_element_type=jnp.float32,
            )
            lse_ref[rows, lanes] = jnp.broadcast_to(log_total, (ROW_CHUNK, HEAD))
        return carry

    lax.fori_loop(0, row_count // ROW_CHUNK, chunk_body, 0)


def _backward_kernel(
    scalars_ref, q_ref, k_ref, v_ref, do_ref, o_ref, lse_ref, dq_ref, kv_grad_ref, acc_ref
):
    micro = pl.program_id(0)
    row_count = q_ref.shape[0]
    key_count = k_ref.shape[0]
    acc_ref[...] = jnp.zeros(acc_ref.shape, jnp.float32)

    def chunk_body(chunk, carry):
        rows = pl.ds(pl.multiple_of(chunk * ROW_CHUNK, ROW_CHUNK), ROW_CHUNK)
        allowed = _chunk_mask(scalars_ref, micro, chunk, key_count)
        for half in range(2):
            lanes = slice(half * HEAD, (half + 1) * HEAD)
            q_head = q_ref[rows, lanes]
            grad_head = do_ref[rows, lanes]
            scores = lax.dot_general(
                q_head, k_ref[:, lanes], (((1,), (1,)), ((), ())),
                preferred_element_type=jnp.float32,
            ) * HEAD ** (-0.5)
            log_total = lse_ref[rows, half * HEAD : half * HEAD + 1]
            probabilities = jnp.where(allowed, jnp.exp(scores - log_total), 0.0)
            prob_grad = lax.dot_general(
                grad_head, v_ref[:, lanes], (((1,), (1,)), ((), ())),
                preferred_element_type=jnp.float32,
            )
            row_delta = jnp.sum(
                grad_head.astype(jnp.float32) * o_ref[rows, lanes], axis=1, keepdims=True
            )
            score_low = (probabilities * (prob_grad - row_delta)).astype(jnp.bfloat16)
            dq_ref[rows, lanes] = jnp.dot(
                score_low, k_ref[:, lanes], preferred_element_type=jnp.float32
            ) * HEAD ** (-0.5)
            acc_ref[0, half] += lax.dot_general(
                score_low, q_head, (((0,), (0,)), ((), ())), preferred_element_type=jnp.float32
            )
            acc_ref[1, half] += lax.dot_general(
                probabilities.astype(jnp.bfloat16), grad_head, (((0,), (0,)), ((), ())),
                preferred_element_type=jnp.float32,
            )
        return carry

    lax.fori_loop(0, row_count // ROW_CHUNK, chunk_body, 0)
    for half in range(2):
        kv_grad_ref[:, half * HEAD : (half + 1) * HEAD] = (
            acc_ref[0, half] * HEAD ** (-0.5)
        ).astype(jnp.bfloat16)
        kv_grad_ref[:, 2 * HEAD + half * HEAD : 2 * HEAD + (half + 1) * HEAD] = acc_ref[
            1, half
        ].astype(jnp.bfloat16)


def attention_forward(scalars, queries, kv_flat, batches):
    all_rows, model_width = queries.shape
    row_count = all_rows // batches
    key_count = kv_flat.shape[0]
    pairs = model_width // (2 * HEAD)
    micro_blocks = kv_flat.shape[1] // batches // (2 * HEAD)
    row_spec = pl.BlockSpec((row_count, 2 * HEAD), lambda m, p, s: (m, p))
    key_spec = pl.BlockSpec((key_count, 2 * HEAD), lambda m, p, s: (0, m * micro_blocks + p))
    value_spec = pl.BlockSpec(
        (key_count, 2 * HEAD), lambda m, p, s: (0, m * micro_blocks + pairs + p)
    )
    return pl.pallas_call(
        _forward_kernel,
        grid_spec=pltpu.PrefetchScalarGridSpec(
            num_scalar_prefetch=1,
            grid=(batches, pairs),
            in_specs=[row_spec, key_spec, value_spec],
            out_specs=[row_spec, row_spec],
        ),
        out_shape=[
            jax.ShapeDtypeStruct((all_rows, model_width), jnp.float32),
            jax.ShapeDtypeStruct((all_rows, model_width), jnp.float32),
        ],
        name="attention_forward",
    )(scalars, queries, kv_flat, kv_flat)


def attention_backward(scalars, queries, kv_flat, grads, attended, log_totals, batches):
    all_rows, model_width = queries.shape
    row_count = all_rows // batches
    key_count = kv_flat.shape[0]
    pairs = model_width // (2 * HEAD)
    micro_blocks = kv_flat.shape[1] // batches // (2 * HEAD)
    row_spec = pl.BlockSpec((row_count, 2 * HEAD), lambda m, p, s: (m, p))
    key_spec = pl.BlockSpec((key_count, 2 * HEAD), lambda m, p, s: (0, m * micro_blocks + p))
    value_spec = pl.BlockSpec(
        (key_count, 2 * HEAD), lambda m, p, s: (0, m * micro_blocks + pairs + p)
    )
    grad_spec = pl.BlockSpec((key_count, 4 * HEAD), lambda m, p, s: (0, m * pairs + p))
    return pl.pallas_call(
        _backward_kernel,
        grid_spec=pltpu.PrefetchScalarGridSpec(
            num_scalar_prefetch=1,
            grid=(batches, pairs),
            in_specs=[row_spec, key_spec, value_spec, row_spec, row_spec, row_spec],
            out_specs=[row_spec, grad_spec],
            scratch_shapes=[pltpu.VMEM((2, 2, key_count, HEAD), jnp.float32)],
        ),
        out_shape=[
            jax.ShapeDtypeStruct((all_rows, model_width), jnp.float32),
            jax.ShapeDtypeStruct(kv_flat.shape, jnp.bfloat16),
        ],
        name="attention_backward",
    )(scalars, queries, kv_flat, kv_flat, grads, attended, log_totals)


def local(
    layer_input,
    history,
    cotangent,
    lengths,
    w_qkv,
    w_out,
    w_up,
    w_down,
    ln_gains,
    ln_biases,
    depth_weights,
):
    batches = layer_input.shape[0]
    row_count = layer_input.shape[2]
    model_width = layer_input.shape[3]
    ff_width = w_up.shape[1]
    shard_rows = w_qkv.shape[0]
    all_rows = batches * row_count
    slot_len = row_count * lax.axis_size("seq")
    positions = lax.axis_index("seq") * row_count + jnp.arange(row_count, dtype=jnp.int32)
    cosine_part, sine_part = rotary_tables(jnp.tile(positions, batches))
    gelu_tanh = partial(jax.nn.gelu, approximate=True)
    lane_pad = 128 - 4
    widths = (3 * model_width, 2, 2, lane_pad, model_width, ff_width, ff_width)
    offsets = [0]
    for width in widths:
        offsets.append(offsets[-1] + width)
    late_width = offsets[4]

    def pieces(packed_rows):
        return [packed_rows[:, offsets[i] : offsets[i + 1]] for i in range(len(widths))]

    packed = jnp.concatenate(
        [
            w_qkv,
            ln_gains,
            ln_biases,
            jnp.zeros((shard_rows, lane_pad), w_qkv.dtype),
            w_out,
            w_up,
            w_down.reshape(shard_rows, ff_width),
        ],
        axis=1,
    )
    gathered = lax.all_gather(packed, ("seq", "fsdp"), axis=0, tiled=True)
    full_qkv, gain_rows, bias_rows, _, full_out, full_up, down_rows = pieces(gathered)
    full_down = down_rows.reshape(ff_width, model_width)
    norm_gains = gain_rows.astype(jnp.float32)
    norm_biases = bias_rows.astype(jnp.float32)

    slot_lengths = lengths[:, 0]
    inputs = layer_input[:, 0].reshape(all_rows, model_width).astype(jnp.float32)
    first_low = layer_norm(inputs, norm_gains[:, 0], norm_biases[:, 0]).astype(jnp.bfloat16)
    projected = jnp.dot(first_low, full_qkv, preferred_element_type=jnp.float32)
    queries = rotate(projected[:, :model_width], cosine_part, sine_part).astype(jnp.bfloat16)
    keys_own = rotate(
        projected[:, model_width : 2 * model_width], cosine_part, sine_part
    ).astype(jnp.bfloat16)
    values_own = projected[:, 2 * model_width :].astype(jnp.bfloat16)
    own_kv = jnp.concatenate([keys_own, values_own], axis=1).reshape(
        batches, row_count, 2 * model_width
    )
    earlier = history[:, :, 0].reshape(4, all_rows, model_width).astype(jnp.float32)
    usable = (positions[None, :] < slot_lengths[:, None]).reshape(all_rows, 1)
    grad_next = jnp.where(
        usable, cotangent[:, 0].reshape(all_rows, model_width).astype(jnp.float32), 0.0
    )
    history_part = jnp.einsum("j,jrd->rd", depth_weights[:4], earlier)
    grad_history = (depth_weights[:4, None, None] * grad_next[None]).astype(jnp.bfloat16)
    grad_history = grad_history.reshape(4, batches, 1, row_count, model_width)
    out_grad = depth_weights[4] * grad_next
    out_low = out_grad.astype(jnp.bfloat16)

    kv_all = lax.all_gather(
        jnp.swapaxes(own_kv, 0, 1).reshape(row_count, batches * 2 * model_width),
        "seq",
        axis=0,
        tiled=False,
    )
    kv_flat = kv_all.reshape(slot_len, batches * 2 * model_width)
    scalars = jnp.concatenate(
        [slot_lengths.astype(jnp.int32), (lax.axis_index("seq") * row_count)[None].astype(jnp.int32)]
    )
    attended_rows, log_totals = attention_forward(scalars, queries, kv_flat, batches)
    attended_low = attended_rows.astype(jnp.bfloat16)
    residual = inputs + jnp.dot(attended_low, full_out, preferred_element_type=jnp.float32)
    second_low = layer_norm(residual, norm_gains[:, 1], norm_biases[:, 1]).astype(jnp.bfloat16)
    hidden = jnp.dot(second_low, full_up, preferred_element_type=jnp.float32)
    hidden_low = gelu_tanh(hidden).astype(jnp.bfloat16)
    block_out = residual + jnp.dot(hidden_low, full_down, preferred_element_type=jnp.float32)
    hidden_grad = jnp.einsum("rd,fd->rf", out_low, full_down, preferred_element_type=jnp.float32)
    _, gelu_pullback = jax.vjp(gelu_tanh, hidden)
    up_low = gelu_pullback(hidden_grad)[0].astype(jnp.bfloat16)
    second_grad = jnp.einsum("rf,df->rd", up_low, full_up, preferred_element_type=jnp.float32)
    _, second_pullback = jax.vjp(layer_norm, residual, norm_gains[:, 1], norm_biases[:, 1])
    residual_part, gain_two, bias_two = second_pullback(second_grad)
    residual_grad = out_grad + residual_part
    branch_low = residual_grad.astype(jnp.bfloat16)
    attended_grad = jnp.einsum(
        "rd,cd->rc", branch_low, full_out, preferred_element_type=jnp.float32
    ).astype(jnp.bfloat16)
    query_grad, kv_grad_flat = attention_backward(
        scalars, queries, kv_flat, attended_grad, attended_rows, log_totals, batches
    )
    kv_grad_own = lax.psum_scatter(kv_grad_flat, "seq", scatter_dimension=0, tiled=True)
    pairs = model_width // (2 * HEAD)
    kv_grad_own = kv_grad_own.reshape(row_count, batches, pairs, 2, 2 * HEAD)
    kv_grad_own = jnp.transpose(kv_grad_own, (1, 0, 3, 2, 4)).reshape(
        all_rows, 2 * model_width
    )
    key_value_all = kv_grad_own.astype(jnp.float32)
    combined = depth_weights[4] * block_out + history_part
    next_input = combined.astype(jnp.bfloat16).reshape(batches, 1, row_count, model_width)
    depth_terms = jnp.concatenate(
        [jnp.einsum("jrd,rd->j", earlier, grad_next), jnp.sum(block_out * grad_next)[None]]
    )
    grad_down = jnp.einsum("rf,rd->fd", hidden_low, out_low, preferred_element_type=jnp.float32)
    grad_up = jnp.einsum("rd,rf->df", second_low, up_low, preferred_element_type=jnp.float32)
    grad_outproj = jnp.einsum(
        "rc,rd->cd", attended_low, branch_low, preferred_element_type=jnp.float32
    )
    early_grads = jnp.concatenate(
        [
            jnp.zeros((model_width, late_width), jnp.float32),
            grad_outproj,
            grad_up,
            grad_down.reshape(model_width, ff_width),
        ],
        axis=1,
    ).astype(jnp.bfloat16)
    qkv_low = jnp.concatenate(
        [
            rotate(query_grad, cosine_part, -sine_part),
            rotate(key_value_all[:, :model_width], cosine_part, -sine_part),
            key_value_all[:, model_width:],
        ],
        axis=1,
    ).astype(jnp.bfloat16)
    grad_qkv = jnp.einsum("rd,rc->dc", first_low, qkv_low, preferred_element_type=jnp.float32)
    first_grad = jnp.einsum("rc,dc->rd", qkv_low, full_qkv, preferred_element_type=jnp.float32)
    _, first_pullback = jax.vjp(layer_norm, inputs, norm_gains[:, 0], norm_biases[:, 0])
    input_part, gain_one, bias_one = first_pullback(first_grad)
    grad_input = (residual_grad + input_part).astype(jnp.bfloat16)
    grad_input = grad_input.reshape(batches, 1, row_count, model_width)
    late_grads = jnp.concatenate(
        [
            grad_qkv,
            jnp.stack([gain_one, gain_two], axis=1),
            jnp.stack([bias_one, bias_two], axis=1),
            jnp.zeros((model_width, lane_pad), jnp.float32),
        ],
        axis=1,
    ).astype(jnp.bfloat16)
    packed_grads = lax.dynamic_update_slice(early_grads, late_grads, (0, 0))
    device_count = model_width // shard_rows
    row_major = Layout(major_to_minor=(0, 1, 2))
    scattered = lax.psum_scatter(
        with_layout_constraint(
            packed_grads.reshape(device_count, shard_rows, offsets[-1]), row_major
        ),
        ("seq", "fsdp"),
        scatter_dimension=0,
        tiled=False,
    )
    scattered = with_layout_constraint(scattered, Layout(major_to_minor=(0, 1)))
    full_pieces = pieces(scattered.astype(jnp.float32))
    owned = [
        full_pieces[0],
        full_pieces[4],
        full_pieces[5],
        full_pieces[6].reshape(-1, model_width),
        full_pieces[1],
        full_pieces[2],
    ]
    depth_total = lax.psum(depth_terms, ("seq", "fsdp"))
    return (next_input, grad_input, grad_history, *owned, depth_total)


def solution(mesh):
    in_specs = (
        P(None, "fsdp", "seq", None),
        P(None, None, "fsdp", "seq", None),
        P(None, "fsdp", "seq", None),
        P(None, "fsdp"),
        P(("seq", "fsdp"), None),
        P(("seq", "fsdp"), None),
        P(("seq", "fsdp"), None),
        P(("seq", "fsdp"), None),
        P(("seq", "fsdp"), None),
        P(("seq", "fsdp"), None),
        P(),
    )
    out_specs = (
        P(None, "fsdp", "seq", None),
        P(None, "fsdp", "seq", None),
        P(None, None, "fsdp", "seq", None),
        P(("seq", "fsdp"), None),
        P(("seq", "fsdp"), None),
        P(("seq", "fsdp"), None),
        P(("seq", "fsdp"), None),
        P(("seq", "fsdp"), None),
        P(("seq", "fsdp"), None),
        P(),
    )
    return jax.shard_map(local, mesh=mesh, in_specs=in_specs, out_specs=out_specs, check_vma=False)
```

```python
from functools import partial
import math

import jax
import jax.numpy as jnp
from jax import lax
from jax.sharding import PartitionSpec as P
from jax.experimental.layout import Layout, with_layout_constraint
from jax.experimental import pallas as pl
from jax.experimental.pallas import tpu as pltpu

HEADS = 12
HEAD = 64


epsilon = 1e-05
masked_value = -1e30


def layer_norm(values, gain_vector, bias_vector):
    center = values - jnp.mean(values, axis=-1, keepdims=True)
    spread = jnp.mean(center * center, axis=-1, keepdims=True)
    return center * lax.rsqrt(spread + epsilon) * gain_vector + bias_vector


def rotary_tables(positions):
    half_width = HEAD // 2
    frequencies = 10000.0 ** (-jnp.arange(half_width, dtype=jnp.float32) / half_width)
    angles = positions.astype(jnp.float32)[:, None] * frequencies[None, :]
    return (jnp.cos(angles)[:, None, :], jnp.sin(angles)[:, None, :])


def rotate(values, cosine_part, sine_part):
    row_count = values.shape[0]
    shaped = values.reshape(row_count, HEADS, HEAD)
    half_width = HEAD // 2
    first_half = shaped[..., :half_width]
    second_half = shaped[..., half_width:]
    turned = jnp.concatenate(
        [
            first_half * cosine_part - second_half * sine_part,
            second_half * cosine_part + first_half * sine_part,
        ],
        axis=-1,
    )
    return turned.reshape(row_count, HEADS * HEAD)


def block_scores(queries3, keys3, query_pos, key_pos, length):
    scores = jnp.einsum(
        "rhd,khd->hrk", queries3, keys3, preferred_element_type=jnp.float32
    ) * HEAD ** (-0.5)
    allowed = (key_pos[None, :] <= query_pos[:, None]) & (key_pos[None, :] < length)
    return (scores, allowed[None])


def row_totals(queries3, keys3, query_pos, length, key_block):
    row_count = queries3.shape[0]

    def row_advance(state, block_index):
        running_top, running_sum = state
        first_key = block_index * key_block
        keys_part = lax.dynamic_slice_in_dim(keys3, first_key, key_block, 0)
        key_pos = first_key + jnp.arange(key_block, dtype=jnp.int32)
        scores, allowed = block_scores(queries3, keys_part, query_pos, key_pos, length)
        masked = jnp.where(allowed, scores, masked_value)
        new_top = jnp.maximum(running_top, jnp.max(masked, axis=-1))
        kept_terms = jnp.where(allowed, jnp.exp(masked - new_top[..., None]), 0.0)
        running_sum = running_sum * jnp.exp(running_top - new_top) + jnp.sum(kept_terms, axis=-1)
        return ((new_top, running_sum), None)

    initial = (
        jnp.full((HEADS, row_count), masked_value, jnp.float32),
        jnp.zeros((HEADS, row_count), jnp.float32),
    )
    (row_tops, row_sums), _ = lax.scan(
        row_advance, initial, jnp.arange(keys3.shape[0] // key_block, dtype=jnp.int32)
    )
    return row_tops + jnp.log(row_sums)


def attend(queries3, keys3, values3, query_pos, length, key_block, log_total):

    def attend_advance(running, block_index):
        first_key = block_index * key_block
        keys_part = lax.dynamic_slice_in_dim(keys3, first_key, key_block, 0)
        values_part = lax.dynamic_slice_in_dim(values3, first_key, key_block, 0)
        key_pos = first_key + jnp.arange(key_block, dtype=jnp.int32)
        scores, allowed = block_scores(queries3, keys_part, query_pos, key_pos, length)
        probabilities = jnp.where(allowed, jnp.exp(scores - log_total[..., None]), 0.0).astype(
            jnp.bfloat16
        )
        return (
            running
            + jnp.einsum(
                "hrk,khd->rhd", probabilities, values_part, preferred_element_type=jnp.float32
            ),
            None,
        )

    initial = jnp.zeros(queries3.shape, jnp.float32)
    result, _ = lax.scan(
        attend_advance, initial, jnp.arange(keys3.shape[0] // key_block, dtype=jnp.int32)
    )
    return result


def query_grads(
    queries3, grads3, keys3, values3, query_pos, length, key_block, log_total, row_delta
):

    def query_advance(running, block_index):
        first_key = block_index * key_block
        keys_part = lax.dynamic_slice_in_dim(keys3, first_key, key_block, 0)
        values_part = lax.dynamic_slice_in_dim(values3, first_key, key_block, 0)
        key_pos = first_key + jnp.arange(key_block, dtype=jnp.int32)
        scores, allowed = block_scores(queries3, keys_part, query_pos, key_pos, length)
        probabilities = jnp.where(allowed, jnp.exp(scores - log_total[..., None]), 0.0)
        prob_grad = jnp.einsum(
            "rhd,khd->hrk", grads3, values_part, preferred_element_type=jnp.float32
        )
        score_low = (probabilities * (prob_grad - row_delta[..., None])).astype(jnp.bfloat16)
        return (
            running
            + jnp.einsum("hrk,khd->rhd", score_low, keys_part, preferred_element_type=jnp.float32),
            None,
        )

    initial = jnp.zeros(queries3.shape, jnp.float32)
    result, _ = lax.scan(
        query_advance, initial, jnp.arange(keys3.shape[0] // key_block, dtype=jnp.int32)
    )
    return result * HEAD ** (-0.5)


def key_side(queries3, grads3, log_part, delta_part, query_pos, keys3, values3, key_pos, length):
    key_count = keys3.shape[0]
    scores, allowed = block_scores(queries3, keys3, query_pos, key_pos, length)
    probabilities = jnp.where(allowed, jnp.exp(scores - log_part[..., None]), 0.0)
    prob_grad = jnp.einsum("rhd,khd->hrk", grads3, values3, preferred_element_type=jnp.float32)
    score_low = (probabilities * (prob_grad - delta_part[..., None])).astype(jnp.bfloat16)
    value_grad = jnp.einsum(
        "hrk,rhd->khd",
        probabilities.astype(jnp.bfloat16),
        grads3,
        preferred_element_type=jnp.float32,
    )
    key_grad = jnp.einsum(
        "hrk,rhd->khd", score_low, queries3, preferred_element_type=jnp.float32
    ) * HEAD ** (-0.5)
    return jnp.concatenate(
        [key_grad.reshape(key_count, HEADS * HEAD), value_grad.reshape(key_count, HEADS * HEAD)],
        axis=1,
    )


def slot_attention(queries3, keys3, values3, query_pos, length):
    key_pos = jnp.arange(keys3.shape[0], dtype=jnp.int32)
    scores, allowed = block_scores(queries3, keys3, query_pos, key_pos, length)
    masked = jnp.where(allowed, scores, masked_value)
    top = jnp.max(masked, axis=-1)
    kept_terms = jnp.where(allowed, jnp.exp(masked - top[..., None]), 0.0)
    log_total = top + jnp.log(jnp.sum(kept_terms, axis=-1))
    probabilities = jnp.where(allowed, jnp.exp(scores - log_total[..., None]), 0.0)
    probabilities_low = probabilities.astype(jnp.bfloat16)
    attended = jnp.einsum(
        "hrk,khd->rhd", probabilities_low, values3, preferred_element_type=jnp.float32
    )
    return attended, probabilities, probabilities_low


def slot_attention_grads(queries3, keys3, values3, grads3, attended, probabilities, probabilities_low):
    prob_grad = jnp.einsum("rhd,khd->hrk", grads3, values3, preferred_element_type=jnp.float32)
    row_delta = jnp.einsum("rhd,rhd->hr", grads3.astype(jnp.float32), attended)
    score_low = (probabilities * (prob_grad - row_delta[..., None])).astype(jnp.bfloat16)
    query_grad = jnp.einsum(
        "hrk,khd->rhd", score_low, keys3, preferred_element_type=jnp.float32
    ) * HEAD ** (-0.5)
    key_grad = jnp.einsum(
        "hrk,rhd->khd", score_low, queries3, preferred_element_type=jnp.float32
    ) * HEAD ** (-0.5)
    value_grad = jnp.einsum(
        "hrk,rhd->khd", probabilities_low, grads3, preferred_element_type=jnp.float32
    )
    return query_grad, key_grad, value_grad


def _pair_masks(scalars_ref, micro, row_count, key_count):
    length = scalars_ref[micro]
    first_row = scalars_ref[scalars_ref.shape[0] - 1]
    query_pos = first_row + lax.broadcasted_iota(jnp.int32, (row_count, key_count), 0)
    key_pos = lax.broadcasted_iota(jnp.int32, (row_count, key_count), 1)
    return (key_pos <= query_pos) & (key_pos < length)


def _forward_kernel(scalars_ref, q_ref, k_ref, v_ref, out_ref, lse_ref):
    micro = pl.program_id(0)
    row_count = q_ref.shape[0]
    key_count = k_ref.shape[0]
    allowed = _pair_masks(scalars_ref, micro, row_count, key_count)
    for half in range(2):
        lanes = slice(half * HEAD, (half + 1) * HEAD)
        q_head = q_ref[:, lanes]
        k_head = k_ref[:, lanes]
        v_head = v_ref[:, lanes]
        scores = lax.dot_general(
            q_head, k_head, (((1,), (1,)), ((), ())), preferred_element_type=jnp.float32
        ) * HEAD ** (-0.5)
        masked = jnp.where(allowed, scores, masked_value)
        top = jnp.max(masked, axis=1, keepdims=True)
        kept = jnp.where(allowed, jnp.exp(masked - top), 0.0)
        total = jnp.sum(kept, axis=1, keepdims=True)
        log_total = top + jnp.log(total)
        probabilities = kept * (1.0 / total)
        attended = jnp.dot(
            probabilities.astype(jnp.bfloat16), v_head, preferred_element_type=jnp.float32
        )
        out_ref[:, lanes] = attended
        lse_ref[:, lanes] = jnp.broadcast_to(log_total, (row_count, HEAD))


def _backward_kernel(
    scalars_ref, q_ref, k_ref, v_ref, do_ref, o_ref, lse_ref, dq_ref, kv_grad_ref
):
    micro = pl.program_id(0)
    row_count = q_ref.shape[0]
    key_count = k_ref.shape[0]
    allowed = _pair_masks(scalars_ref, micro, row_count, key_count)
    for half in range(2):
        lanes = slice(half * HEAD, (half + 1) * HEAD)
        q_head = q_ref[:, lanes]
        k_head = k_ref[:, lanes]
        v_head = v_ref[:, lanes]
        grad_head = do_ref[:, lanes]
        scores = lax.dot_general(
            q_head, k_head, (((1,), (1,)), ((), ())), preferred_element_type=jnp.float32
        ) * HEAD ** (-0.5)
        log_total = lse_ref[:, half * HEAD : half * HEAD + 1]
        probabilities = jnp.where(allowed, jnp.exp(scores - log_total), 0.0)
        probabilities_low = probabilities.astype(jnp.bfloat16)
        prob_grad = lax.dot_general(
            grad_head, v_head, (((1,), (1,)), ((), ())), preferred_element_type=jnp.float32
        )
        row_delta = jnp.sum(
            grad_head.astype(jnp.float32) * o_ref[:, lanes], axis=1, keepdims=True
        )
        score_low = (probabilities * (prob_grad - row_delta)).astype(jnp.bfloat16)
        dq_ref[:, lanes] = jnp.dot(
            score_low, k_head, preferred_element_type=jnp.float32
        ) * HEAD ** (-0.5)
        key_grad = lax.dot_general(
            score_low, q_head, (((0,), (0,)), ((), ())), preferred_element_type=jnp.float32
        ) * HEAD ** (-0.5)
        value_grad = lax.dot_general(
            probabilities_low, grad_head, (((0,), (0,)), ((), ())),
            preferred_element_type=jnp.float32,
        )
        kv_grad_ref[:, lanes] = key_grad.astype(jnp.bfloat16)
        kv_grad_ref[:, 2 * HEAD + half * HEAD : 2 * HEAD + (half + 1) * HEAD] = value_grad.astype(
            jnp.bfloat16
        )


def attention_forward(scalars, queries, kv_flat, batches):
    all_rows, model_width = queries.shape
    row_count = all_rows // batches
    key_count = kv_flat.shape[0]
    pairs = model_width // (2 * HEAD)
    micro_blocks = kv_flat.shape[1] // batches // (2 * HEAD)
    row_spec = pl.BlockSpec((row_count, 2 * HEAD), lambda m, p, s: (m, p))
    key_spec = pl.BlockSpec((key_count, 2 * HEAD), lambda m, p, s: (0, m * micro_blocks + p))
    value_spec = pl.BlockSpec(
        (key_count, 2 * HEAD), lambda m, p, s: (0, m * micro_blocks + pairs + p)
    )
    return pl.pallas_call(
        _forward_kernel,
        grid_spec=pltpu.PrefetchScalarGridSpec(
            num_scalar_prefetch=1,
            grid=(batches, pairs),
            in_specs=[row_spec, key_spec, value_spec],
            out_specs=[row_spec, row_spec],
        ),
        out_shape=[
            jax.ShapeDtypeStruct((all_rows, model_width), jnp.float32),
            jax.ShapeDtypeStruct((all_rows, model_width), jnp.float32),
        ],
        name="attention_forward",
    )(scalars, queries, kv_flat, kv_flat)


def attention_backward(scalars, queries, kv_flat, grads, attended, log_totals, batches):
    all_rows, model_width = queries.shape
    row_count = all_rows // batches
    key_count = kv_flat.shape[0]
    pairs = model_width // (2 * HEAD)
    micro_blocks = kv_flat.shape[1] // batches // (2 * HEAD)
    row_spec = pl.BlockSpec((row_count, 2 * HEAD), lambda m, p, s: (m, p))
    key_spec = pl.BlockSpec((key_count, 2 * HEAD), lambda m, p, s: (0, m * micro_blocks + p))
    value_spec = pl.BlockSpec(
        (key_count, 2 * HEAD), lambda m, p, s: (0, m * micro_blocks + pairs + p)
    )
    grad_spec = pl.BlockSpec((key_count, 4 * HEAD), lambda m, p, s: (0, m * pairs + p))
    return pl.pallas_call(
        _backward_kernel,
        grid_spec=pltpu.PrefetchScalarGridSpec(
            num_scalar_prefetch=1,
            grid=(batches, pairs),
            in_specs=[row_spec, key_spec, value_spec, row_spec, row_spec, row_spec],
            out_specs=[row_spec, grad_spec],
        ),
        out_shape=[
            jax.ShapeDtypeStruct((all_rows, model_width), jnp.float32),
            jax.ShapeDtypeStruct(kv_flat.shape, jnp.bfloat16),
        ],
        name="attention_backward",
    )(scalars, queries, kv_flat, kv_flat, grads, attended, log_totals)


def local(
    layer_input,
    history,
    cotangent,
    lengths,
    w_qkv,
    w_out,
    w_up,
    w_down,
    ln_gains,
    ln_biases,
    depth_weights,
):
    batches = layer_input.shape[0]
    row_count = layer_input.shape[2]
    model_width = layer_input.shape[3]
    ff_width = w_up.shape[1]
    shard_rows = w_qkv.shape[0]
    all_rows = batches * row_count
    slot_len = row_count * lax.axis_size("seq")
    positions = lax.axis_index("seq") * row_count + jnp.arange(row_count, dtype=jnp.int32)
    cosine_part, sine_part = rotary_tables(jnp.tile(positions, batches))
    gelu_tanh = partial(jax.nn.gelu, approximate=True)
    lane_pad = 128 - 4
    widths = (3 * model_width, 2, 2, lane_pad, model_width, ff_width, ff_width)
    offsets = [0]
    for width in widths:
        offsets.append(offsets[-1] + width)
    late_width = offsets[4]

    def pieces(packed_rows):
        return [packed_rows[:, offsets[i] : offsets[i + 1]] for i in range(len(widths))]

    packed = jnp.concatenate(
        [
            w_qkv,
            ln_gains,
            ln_biases,
            jnp.zeros((shard_rows, lane_pad), w_qkv.dtype),
            w_out,
            w_up,
            w_down.reshape(shard_rows, ff_width),
        ],
        axis=1,
    )
    gathered = lax.all_gather(packed, ("seq", "fsdp"), axis=0, tiled=True)
    full_qkv, gain_rows, bias_rows, _, full_out, full_up, down_rows = pieces(gathered)
    full_down = down_rows.reshape(ff_width, model_width)
    norm_gains = gain_rows.astype(jnp.float32)
    norm_biases = bias_rows.astype(jnp.float32)

    slot_lengths = lengths[:, 0]
    inputs = layer_input[:, 0].reshape(all_rows, model_width).astype(jnp.float32)
    first_low = layer_norm(inputs, norm_gains[:, 0], norm_biases[:, 0]).astype(jnp.bfloat16)
    projected = jnp.dot(first_low, full_qkv, preferred_element_type=jnp.float32)
    queries = rotate(projected[:, :model_width], cosine_part, sine_part).astype(jnp.bfloat16)
    keys_own = rotate(
        projected[:, model_width : 2 * model_width], cosine_part, sine_part
    ).astype(jnp.bfloat16)
    values_own = projected[:, 2 * model_width :].astype(jnp.bfloat16)
    own_kv = jnp.concatenate([keys_own, values_own], axis=1).reshape(
        batches, row_count, 2 * model_width
    )
    earlier = history[:, :, 0].reshape(4, all_rows, model_width).astype(jnp.float32)
    usable = (positions[None, :] < slot_lengths[:, None]).reshape(all_rows, 1)
    grad_next = jnp.where(
        usable, cotangent[:, 0].reshape(all_rows, model_width).astype(jnp.float32), 0.0
    )
    history_part = jnp.einsum("j,jrd->rd", depth_weights[:4], earlier)
    grad_history = (depth_weights[:4, None, None] * grad_next[None]).astype(jnp.bfloat16)
    grad_history = grad_history.reshape(4, batches, 1, row_count, model_width)
    out_grad = depth_weights[4] * grad_next
    out_low = out_grad.astype(jnp.bfloat16)

    kv_all = lax.all_gather(
        jnp.swapaxes(own_kv, 0, 1).reshape(row_count, batches * 2 * model_width),
        "seq",
        axis=0,
        tiled=False,
    )
    kv_flat = kv_all.reshape(slot_len, batches * 2 * model_width)
    scalars = jnp.concatenate(
        [slot_lengths.astype(jnp.int32), (lax.axis_index("seq") * row_count)[None].astype(jnp.int32)]
    )
    attended_rows, log_totals = attention_forward(scalars, queries, kv_flat, batches)
    attended_low = attended_rows.astype(jnp.bfloat16)
    residual = inputs + jnp.dot(attended_low, full_out, preferred_element_type=jnp.float32)
    second_low = layer_norm(residual, norm_gains[:, 1], norm_biases[:, 1]).astype(jnp.bfloat16)
    hidden = jnp.dot(second_low, full_up, preferred_element_type=jnp.float32)
    hidden_low = gelu_tanh(hidden).astype(jnp.bfloat16)
    block_out = residual + jnp.dot(hidden_low, full_down, preferred_element_type=jnp.float32)
    hidden_grad = jnp.einsum("rd,fd->rf", out_low, full_down, preferred_element_type=jnp.float32)
    _, gelu_pullback = jax.vjp(gelu_tanh, hidden)
    up_low = gelu_pullback(hidden_grad)[0].astype(jnp.bfloat16)
    second_grad = jnp.einsum("rf,df->rd", up_low, full_up, preferred_element_type=jnp.float32)
    _, second_pullback = jax.vjp(layer_norm, residual, norm_gains[:, 1], norm_biases[:, 1])
    residual_part, gain_two, bias_two = second_pullback(second_grad)
    residual_grad = out_grad + residual_part
    branch_low = residual_grad.astype(jnp.bfloat16)
    attended_grad = jnp.einsum(
        "rd,cd->rc", branch_low, full_out, preferred_element_type=jnp.float32
    ).astype(jnp.bfloat16)
    query_grad, kv_grad_flat = attention_backward(
        scalars, queries, kv_flat, attended_grad, attended_rows, log_totals, batches
    )
    kv_grad_own = lax.psum_scatter(kv_grad_flat, "seq", scatter_dimension=0, tiled=True)
    pairs = model_width // (2 * HEAD)
    kv_grad_own = kv_grad_own.reshape(row_count, batches, pairs, 2, 2 * HEAD)
    kv_grad_own = jnp.transpose(kv_grad_own, (1, 0, 3, 2, 4)).reshape(
        all_rows, 2 * model_width
    )
    key_value_all = kv_grad_own.astype(jnp.float32)
    block_side, _ = lax.optimization_barrier((block_out, kv_grad_flat))
    combined = depth_weights[4] * block_side + history_part
    next_input = combined.astype(jnp.bfloat16).reshape(batches, 1, row_count, model_width)
    depth_terms = jnp.concatenate(
        [jnp.einsum("jrd,rd->j", earlier, grad_next), jnp.sum(block_side * grad_next)[None]]
    )
    grad_down = jnp.einsum("rf,rd->fd", hidden_low, out_low, preferred_element_type=jnp.float32)
    grad_up = jnp.einsum("rd,rf->df", second_low, up_low, preferred_element_type=jnp.float32)
    grad_outproj = jnp.einsum(
        "rc,rd->cd", attended_low, branch_low, preferred_element_type=jnp.float32
    )
    early_grads = jnp.concatenate(
        [
            jnp.zeros((model_width, late_width), jnp.float32),
            grad_outproj,
            grad_up,
            grad_down.reshape(model_width, ff_width),
        ],
        axis=1,
    ).astype(jnp.bfloat16)
    qkv_low = jnp.concatenate(
        [
            rotate(query_grad, cosine_part, -sine_part),
            rotate(key_value_all[:, :model_width], cosine_part, -sine_part),
            key_value_all[:, model_width:],
        ],
        axis=1,
    ).astype(jnp.bfloat16)
    grad_qkv = jnp.einsum("rd,rc->dc", first_low, qkv_low, preferred_element_type=jnp.float32)
    first_grad = jnp.einsum("rc,dc->rd", qkv_low, full_qkv, preferred_element_type=jnp.float32)
    _, first_pullback = jax.vjp(layer_norm, inputs, norm_gains[:, 0], norm_biases[:, 0])
    input_part, gain_one, bias_one = first_pullback(first_grad)
    grad_input = (residual_grad + input_part).astype(jnp.bfloat16)
    grad_input = grad_input.reshape(batches, 1, row_count, model_width)
    norm_grads = jnp.concatenate(
        [
            jnp.stack([gain_one, gain_two], axis=1),
            jnp.stack([bias_one, bias_two], axis=1),
            jnp.zeros((model_width, lane_pad), jnp.float32),
        ],
        axis=1,
    ).astype(jnp.bfloat16)
    packed_grads = lax.dynamic_update_slice(early_grads, grad_qkv.astype(jnp.bfloat16), (0, 0))
    packed_grads = lax.dynamic_update_slice(packed_grads, norm_grads, (0, offsets[1]))
    device_count = model_width // shard_rows
    row_major = Layout(major_to_minor=(0, 1, 2))
    scattered = lax.psum_scatter(
        with_layout_constraint(
            packed_grads.reshape(device_count, shard_rows, offsets[-1]), row_major
        ),
        ("seq", "fsdp"),
        scatter_dimension=0,
        tiled=False,
    )
    scattered = with_layout_constraint(scattered, Layout(major_to_minor=(0, 1)))
    full_pieces = pieces(scattered.astype(jnp.float32))
    owned = [
        full_pieces[0],
        full_pieces[4],
        full_pieces[5],
        full_pieces[6].reshape(-1, model_width),
        full_pieces[1],
        full_pieces[2],
    ]
    depth_total = lax.psum(depth_terms, ("seq", "fsdp"))
    return (next_input, grad_input, grad_history, *owned, depth_total)


def solution(mesh):
    in_specs = (
        P(None, "fsdp", "seq", None),
        P(None, None, "fsdp", "seq", None),
        P(None, "fsdp", "seq", None),
        P(None, "fsdp"),
        P(("seq", "fsdp"), None),
        P(("seq", "fsdp"), None),
        P(("seq", "fsdp"), None),
        P(("seq", "fsdp"), None),
        P(("seq", "fsdp"), None),
        P(("seq", "fsdp"), None),
        P(),
    )
    out_specs = (
        P(None, "fsdp", "seq", None),
        P(None, "fsdp", "seq", None),
        P(None, None, "fsdp", "seq", None),
        P(("seq", "fsdp"), None),
        P(("seq", "fsdp"), None),
        P(("seq", "fsdp"), None),
        P(("seq", "fsdp"), None),
        P(("seq", "fsdp"), None),
        P(("seq", "fsdp"), None),
        P(),
    )
    return jax.shard_map(local, mesh=mesh, in_specs=in_specs, out_specs=out_specs, check_vma=False)
```

```python
from functools import partial
import math

import jax
import jax.numpy as jnp
from jax import lax
from jax.sharding import PartitionSpec as P
from jax.experimental.layout import Layout, with_layout_constraint
from jax.experimental import pallas as pl
from jax.experimental.pallas import tpu as pltpu

HEADS = 12
HEAD = 64


epsilon = 1e-05
masked_value = -1e30


def layer_norm(values, gain_vector, bias_vector):
    center = values - jnp.mean(values, axis=-1, keepdims=True)
    spread = jnp.mean(center * center, axis=-1, keepdims=True)
    return center * lax.rsqrt(spread + epsilon) * gain_vector + bias_vector


def rotary_tables(positions):
    half_width = HEAD // 2
    frequencies = 10000.0 ** (-jnp.arange(half_width, dtype=jnp.float32) / half_width)
    angles = positions.astype(jnp.float32)[:, None] * frequencies[None, :]
    return (jnp.cos(angles)[:, None, :], jnp.sin(angles)[:, None, :])


def rotate(values, cosine_part, sine_part):
    row_count = values.shape[0]
    shaped = values.reshape(row_count, HEADS, HEAD)
    half_width = HEAD // 2
    first_half = shaped[..., :half_width]
    second_half = shaped[..., half_width:]
    turned = jnp.concatenate(
        [
            first_half * cosine_part - second_half * sine_part,
            second_half * cosine_part + first_half * sine_part,
        ],
        axis=-1,
    )
    return turned.reshape(row_count, HEADS * HEAD)


def block_scores(queries3, keys3, query_pos, key_pos, length):
    scores = jnp.einsum(
        "rhd,khd->hrk", queries3, keys3, preferred_element_type=jnp.float32
    ) * HEAD ** (-0.5)
    allowed = (key_pos[None, :] <= query_pos[:, None]) & (key_pos[None, :] < length)
    return (scores, allowed[None])


def row_totals(queries3, keys3, query_pos, length, key_block):
    row_count = queries3.shape[0]

    def row_advance(state, block_index):
        running_top, running_sum = state
        first_key = block_index * key_block
        keys_part = lax.dynamic_slice_in_dim(keys3, first_key, key_block, 0)
        key_pos = first_key + jnp.arange(key_block, dtype=jnp.int32)
        scores, allowed = block_scores(queries3, keys_part, query_pos, key_pos, length)
        masked = jnp.where(allowed, scores, masked_value)
        new_top = jnp.maximum(running_top, jnp.max(masked, axis=-1))
        kept_terms = jnp.where(allowed, jnp.exp(masked - new_top[..., None]), 0.0)
        running_sum = running_sum * jnp.exp(running_top - new_top) + jnp.sum(kept_terms, axis=-1)
        return ((new_top, running_sum), None)

    initial = (
        jnp.full((HEADS, row_count), masked_value, jnp.float32),
        jnp.zeros((HEADS, row_count), jnp.float32),
    )
    (row_tops, row_sums), _ = lax.scan(
        row_advance, initial, jnp.arange(keys3.shape[0] // key_block, dtype=jnp.int32)
    )
    return row_tops + jnp.log(row_sums)


def attend(queries3, keys3, values3, query_pos, length, key_block, log_total):

    def attend_advance(running, block_index):
        first_key = block_index * key_block
        keys_part = lax.dynamic_slice_in_dim(keys3, first_key, key_block, 0)
        values_part = lax.dynamic_slice_in_dim(values3, first_key, key_block, 0)
        key_pos = first_key + jnp.arange(key_block, dtype=jnp.int32)
        scores, allowed = block_scores(queries3, keys_part, query_pos, key_pos, length)
        probabilities = jnp.where(allowed, jnp.exp(scores - log_total[..., None]), 0.0).astype(
            jnp.bfloat16
        )
        return (
            running
            + jnp.einsum(
                "hrk,khd->rhd", probabilities, values_part, preferred_element_type=jnp.float32
            ),
            None,
        )

    initial = jnp.zeros(queries3.shape, jnp.float32)
    result, _ = lax.scan(
        attend_advance, initial, jnp.arange(keys3.shape[0] // key_block, dtype=jnp.int32)
    )
    return result


def query_grads(
    queries3, grads3, keys3, values3, query_pos, length, key_block, log_total, row_delta
):

    def query_advance(running, block_index):
        first_key = block_index * key_block
        keys_part = lax.dynamic_slice_in_dim(keys3, first_key, key_block, 0)
        values_part = lax.dynamic_slice_in_dim(values3, first_key, key_block, 0)
        key_pos = first_key + jnp.arange(key_block, dtype=jnp.int32)
        scores, allowed = block_scores(queries3, keys_part, query_pos, key_pos, length)
        probabilities = jnp.where(allowed, jnp.exp(scores - log_total[..., None]), 0.0)
        prob_grad = jnp.einsum(
            "rhd,khd->hrk", grads3, values_part, preferred_element_type=jnp.float32
        )
        score_low = (probabilities * (prob_grad - row_delta[..., None])).astype(jnp.bfloat16)
        return (
            running
            + jnp.einsum("hrk,khd->rhd", score_low, keys_part, preferred_element_type=jnp.float32),
            None,
        )

    initial = jnp.zeros(queries3.shape, jnp.float32)
    result, _ = lax.scan(
        query_advance, initial, jnp.arange(keys3.shape[0] // key_block, dtype=jnp.int32)
    )
    return result * HEAD ** (-0.5)


def key_side(queries3, grads3, log_part, delta_part, query_pos, keys3, values3, key_pos, length):
    key_count = keys3.shape[0]
    scores, allowed = block_scores(queries3, keys3, query_pos, key_pos, length)
    probabilities = jnp.where(allowed, jnp.exp(scores - log_part[..., None]), 0.0)
    prob_grad = jnp.einsum("rhd,khd->hrk", grads3, values3, preferred_element_type=jnp.float32)
    score_low = (probabilities * (prob_grad - delta_part[..., None])).astype(jnp.bfloat16)
    value_grad = jnp.einsum(
        "hrk,rhd->khd",
        probabilities.astype(jnp.bfloat16),
        grads3,
        preferred_element_type=jnp.float32,
    )
    key_grad = jnp.einsum(
        "hrk,rhd->khd", score_low, queries3, preferred_element_type=jnp.float32
    ) * HEAD ** (-0.5)
    return jnp.concatenate(
        [key_grad.reshape(key_count, HEADS * HEAD), value_grad.reshape(key_count, HEADS * HEAD)],
        axis=1,
    )


def slot_attention(queries3, keys3, values3, query_pos, length):
    key_pos = jnp.arange(keys3.shape[0], dtype=jnp.int32)
    scores, allowed = block_scores(queries3, keys3, query_pos, key_pos, length)
    masked = jnp.where(allowed, scores, masked_value)
    top = jnp.max(masked, axis=-1)
    kept_terms = jnp.where(allowed, jnp.exp(masked - top[..., None]), 0.0)
    log_total = top + jnp.log(jnp.sum(kept_terms, axis=-1))
    probabilities = jnp.where(allowed, jnp.exp(scores - log_total[..., None]), 0.0)
    probabilities_low = probabilities.astype(jnp.bfloat16)
    attended = jnp.einsum(
        "hrk,khd->rhd", probabilities_low, values3, preferred_element_type=jnp.float32
    )
    return attended, probabilities, probabilities_low


def slot_attention_grads(queries3, keys3, values3, grads3, attended, probabilities, probabilities_low):
    prob_grad = jnp.einsum("rhd,khd->hrk", grads3, values3, preferred_element_type=jnp.float32)
    row_delta = jnp.einsum("rhd,rhd->hr", grads3.astype(jnp.float32), attended)
    score_low = (probabilities * (prob_grad - row_delta[..., None])).astype(jnp.bfloat16)
    query_grad = jnp.einsum(
        "hrk,khd->rhd", score_low, keys3, preferred_element_type=jnp.float32
    ) * HEAD ** (-0.5)
    key_grad = jnp.einsum(
        "hrk,rhd->khd", score_low, queries3, preferred_element_type=jnp.float32
    ) * HEAD ** (-0.5)
    value_grad = jnp.einsum(
        "hrk,rhd->khd", probabilities_low, grads3, preferred_element_type=jnp.float32
    )
    return query_grad, key_grad, value_grad


def _pair_masks(scalars_ref, micro, row_count, key_count):
    length = scalars_ref[micro]
    first_row = scalars_ref[scalars_ref.shape[0] - 1]
    query_pos = first_row + lax.broadcasted_iota(jnp.int32, (row_count, key_count), 0)
    key_pos = lax.broadcasted_iota(jnp.int32, (row_count, key_count), 1)
    return (key_pos <= query_pos) & (key_pos < length)


def _forward_kernel(scalars_ref, q_ref, k_ref, v_ref, out_ref, lse_ref):
    micro = pl.program_id(0)
    row_count = q_ref.shape[0]
    key_count = k_ref.shape[0]
    allowed = _pair_masks(scalars_ref, micro, row_count, key_count)
    for half in range(2):
        lanes = slice(half * HEAD, (half + 1) * HEAD)
        q_head = q_ref[:, lanes]
        k_head = k_ref[:, lanes]
        v_head = v_ref[:, lanes]
        scores = lax.dot_general(
            q_head, k_head, (((1,), (1,)), ((), ())), preferred_element_type=jnp.float32
        ) * HEAD ** (-0.5)
        masked = jnp.where(allowed, scores, masked_value)
        top = jnp.max(masked, axis=1, keepdims=True)
        kept = jnp.where(allowed, jnp.exp(masked - top), 0.0)
        total = jnp.sum(kept, axis=1, keepdims=True)
        log_total = top + jnp.log(total)
        probabilities = kept * (1.0 / total)
        attended = jnp.dot(
            probabilities.astype(jnp.bfloat16), v_head, preferred_element_type=jnp.float32
        )
        out_ref[:, lanes] = attended
        lse_ref[:, lanes] = jnp.broadcast_to(log_total, (row_count, HEAD))


def _backward_kernel(
    scalars_ref, q_ref, k_ref, v_ref, do_ref, o_ref, lse_ref, dq_ref, kv_grad_ref
):
    micro = pl.program_id(0)
    row_count = q_ref.shape[0]
    key_count = k_ref.shape[0]
    allowed = _pair_masks(scalars_ref, micro, row_count, key_count)
    for half in range(2):
        lanes = slice(half * HEAD, (half + 1) * HEAD)
        q_head = q_ref[:, lanes]
        k_head = k_ref[:, lanes]
        v_head = v_ref[:, lanes]
        grad_head = do_ref[:, lanes]
        scores = lax.dot_general(
            q_head, k_head, (((1,), (1,)), ((), ())), preferred_element_type=jnp.float32
        ) * HEAD ** (-0.5)
        log_total = lse_ref[:, half * HEAD : half * HEAD + 1]
        probabilities = jnp.where(allowed, jnp.exp(scores - log_total), 0.0)
        probabilities_low = probabilities.astype(jnp.bfloat16)
        prob_grad = lax.dot_general(
            grad_head, v_head, (((1,), (1,)), ((), ())), preferred_element_type=jnp.float32
        )
        row_delta = jnp.sum(
            grad_head.astype(jnp.float32) * o_ref[:, lanes], axis=1, keepdims=True
        )
        score_low = (probabilities * (prob_grad - row_delta)).astype(jnp.bfloat16)
        dq_ref[:, lanes] = jnp.dot(
            score_low, k_head, preferred_element_type=jnp.float32
        ) * HEAD ** (-0.5)
        key_grad = lax.dot_general(
            score_low, q_head, (((0,), (0,)), ((), ())), preferred_element_type=jnp.float32
        ) * HEAD ** (-0.5)
        value_grad = lax.dot_general(
            probabilities_low, grad_head, (((0,), (0,)), ((), ())),
            preferred_element_type=jnp.float32,
        )
        kv_grad_ref[:, lanes] = key_grad.astype(jnp.bfloat16)
        kv_grad_ref[:, 2 * HEAD + half * HEAD : 2 * HEAD + (half + 1) * HEAD] = value_grad.astype(
            jnp.bfloat16
        )


def attention_forward(scalars, queries, kv_flat, batches):
    all_rows, model_width = queries.shape
    row_count = all_rows // batches
    key_count = kv_flat.shape[0]
    pairs = model_width // (2 * HEAD)
    micro_blocks = kv_flat.shape[1] // batches // (2 * HEAD)
    row_spec = pl.BlockSpec((row_count, 2 * HEAD), lambda m, p, s: (m, p))
    key_spec = pl.BlockSpec((key_count, 2 * HEAD), lambda m, p, s: (0, m * micro_blocks + p))
    value_spec = pl.BlockSpec(
        (key_count, 2 * HEAD), lambda m, p, s: (0, m * micro_blocks + pairs + p)
    )
    return pl.pallas_call(
        _forward_kernel,
        grid_spec=pltpu.PrefetchScalarGridSpec(
            num_scalar_prefetch=1,
            grid=(batches, pairs),
            in_specs=[row_spec, key_spec, value_spec],
            out_specs=[row_spec, row_spec],
        ),
        out_shape=[
            jax.ShapeDtypeStruct((all_rows, model_width), jnp.float32),
            jax.ShapeDtypeStruct((all_rows, model_width), jnp.float32),
        ],
        name="attention_forward",
    )(scalars, queries, kv_flat, kv_flat)


def attention_backward(scalars, queries, kv_flat, grads, attended, log_totals, batches):
    all_rows, model_width = queries.shape
    row_count = all_rows // batches
    key_count = kv_flat.shape[0]
    pairs = model_width // (2 * HEAD)
    micro_blocks = kv_flat.shape[1] // batches // (2 * HEAD)
    row_spec = pl.BlockSpec((row_count, 2 * HEAD), lambda m, p, s: (m, p))
    key_spec = pl.BlockSpec((key_count, 2 * HEAD), lambda m, p, s: (0, m * micro_blocks + p))
    value_spec = pl.BlockSpec(
        (key_count, 2 * HEAD), lambda m, p, s: (0, m * micro_blocks + pairs + p)
    )
    grad_spec = pl.BlockSpec((key_count, 4 * HEAD), lambda m, p, s: (0, m * pairs + p))
    return pl.pallas_call(
        _backward_kernel,
        grid_spec=pltpu.PrefetchScalarGridSpec(
            num_scalar_prefetch=1,
            grid=(batches, pairs),
            in_specs=[row_spec, key_spec, value_spec, row_spec, row_spec, row_spec],
            out_specs=[row_spec, grad_spec],
        ),
        out_shape=[
            jax.ShapeDtypeStruct((all_rows, model_width), jnp.float32),
            jax.ShapeDtypeStruct(kv_flat.shape, jnp.bfloat16),
        ],
        name="attention_backward",
    )(scalars, queries, kv_flat, kv_flat, grads, attended, log_totals)


def local(
    layer_input,
    history,
    cotangent,
    lengths,
    w_qkv,
    w_out,
    w_up,
    w_down,
    ln_gains,
    ln_biases,
    depth_weights,
):
    batches = layer_input.shape[0]
    row_count = layer_input.shape[2]
    model_width = layer_input.shape[3]
    ff_width = w_up.shape[1]
    shard_rows = w_qkv.shape[0]
    all_rows = batches * row_count
    slot_len = row_count * lax.axis_size("seq")
    positions = lax.axis_index("seq") * row_count + jnp.arange(row_count, dtype=jnp.int32)
    cosine_part, sine_part = rotary_tables(jnp.tile(positions, batches))
    gelu_tanh = partial(jax.nn.gelu, approximate=True)
    lane_pad = 128 - 4
    widths = (3 * model_width, 2, 2, lane_pad, model_width, ff_width, ff_width)
    offsets = [0]
    for width in widths:
        offsets.append(offsets[-1] + width)

    def pieces(packed_rows):
        return [packed_rows[:, offsets[i] : offsets[i + 1]] for i in range(len(widths))]

    packed = jnp.concatenate(
        [
            w_qkv,
            ln_gains,
            ln_biases,
            jnp.zeros((shard_rows, lane_pad), w_qkv.dtype),
            w_out,
            w_up,
            w_down.reshape(shard_rows, ff_width),
        ],
        axis=1,
    )
    gathered = lax.all_gather(packed, ("seq", "fsdp"), axis=0, tiled=True)
    full_qkv, gain_rows, bias_rows, _, full_out, full_up, down_rows = pieces(gathered)
    full_down = down_rows.reshape(ff_width, model_width)
    norm_gains = gain_rows.astype(jnp.float32)
    norm_biases = bias_rows.astype(jnp.float32)

    slot_lengths = lengths[:, 0]
    inputs = layer_input[:, 0].reshape(all_rows, model_width).astype(jnp.float32)
    first_low = layer_norm(inputs, norm_gains[:, 0], norm_biases[:, 0]).astype(jnp.bfloat16)
    projected = jnp.dot(first_low, full_qkv, preferred_element_type=jnp.float32)
    queries = rotate(projected[:, :model_width], cosine_part, sine_part).astype(jnp.bfloat16)
    keys_own = rotate(
        projected[:, model_width : 2 * model_width], cosine_part, sine_part
    ).astype(jnp.bfloat16)
    values_own = projected[:, 2 * model_width :].astype(jnp.bfloat16)
    own_kv = jnp.concatenate([keys_own, values_own], axis=1).reshape(
        batches, row_count, 2 * model_width
    )
    earlier = history[:, :, 0].reshape(4, all_rows, model_width).astype(jnp.float32)
    usable = (positions[None, :] < slot_lengths[:, None]).reshape(all_rows, 1)
    grad_next = jnp.where(
        usable, cotangent[:, 0].reshape(all_rows, model_width).astype(jnp.float32), 0.0
    )
    history_part = jnp.einsum("j,jrd->rd", depth_weights[:4], earlier)
    grad_history = (depth_weights[:4, None, None] * grad_next[None]).astype(jnp.bfloat16)
    grad_history = grad_history.reshape(4, batches, 1, row_count, model_width)
    out_grad = depth_weights[4] * grad_next
    out_low = out_grad.astype(jnp.bfloat16)

    kv_all = lax.all_gather(
        jnp.swapaxes(own_kv, 0, 1).reshape(row_count, batches * 2 * model_width),
        "seq",
        axis=0,
        tiled=False,
    )
    kv_flat = kv_all.reshape(slot_len, batches * 2 * model_width)
    scalars = jnp.concatenate(
        [slot_lengths.astype(jnp.int32), (lax.axis_index("seq") * row_count)[None].astype(jnp.int32)]
    )
    attended_rows, log_totals = attention_forward(scalars, queries, kv_flat, batches)
    attended_low = attended_rows.astype(jnp.bfloat16)
    residual = inputs + jnp.dot(attended_low, full_out, preferred_element_type=jnp.float32)
    second_low = layer_norm(residual, norm_gains[:, 1], norm_biases[:, 1]).astype(jnp.bfloat16)
    hidden = jnp.dot(second_low, full_up, preferred_element_type=jnp.float32)
    hidden_low = gelu_tanh(hidden).astype(jnp.bfloat16)
    block_out = residual + jnp.dot(hidden_low, full_down, preferred_element_type=jnp.float32)
    hidden_grad = jnp.einsum("rd,fd->rf", out_low, full_down, preferred_element_type=jnp.float32)
    _, gelu_pullback = jax.vjp(gelu_tanh, hidden)
    up_low = gelu_pullback(hidden_grad)[0].astype(jnp.bfloat16)
    second_grad = jnp.einsum("rf,df->rd", up_low, full_up, preferred_element_type=jnp.float32)
    _, second_pullback = jax.vjp(layer_norm, residual, norm_gains[:, 1], norm_biases[:, 1])
    residual_part, gain_two, bias_two = second_pullback(second_grad)
    residual_grad = out_grad + residual_part
    branch_low = residual_grad.astype(jnp.bfloat16)
    attended_grad = jnp.einsum(
        "rd,cd->rc", branch_low, full_out, preferred_element_type=jnp.float32
    ).astype(jnp.bfloat16)
    query_grad, kv_grad_flat = attention_backward(
        scalars, queries, kv_flat, attended_grad, attended_rows, log_totals, batches
    )
    kv_grad_own = lax.psum_scatter(kv_grad_flat, "seq", scatter_dimension=0, tiled=True)
    pairs = model_width // (2 * HEAD)
    kv_grad_own = kv_grad_own.reshape(row_count, batches, pairs, 2, 2 * HEAD)
    kv_grad_own = jnp.transpose(kv_grad_own, (1, 0, 3, 2, 4)).reshape(
        all_rows, 2 * model_width
    )
    key_value_all = kv_grad_own.astype(jnp.float32)
    block_side, _ = lax.optimization_barrier((block_out, kv_grad_flat))
    combined = depth_weights[4] * block_side + history_part
    next_input = combined.astype(jnp.bfloat16).reshape(batches, 1, row_count, model_width)
    depth_terms = jnp.concatenate(
        [jnp.einsum("jrd,rd->j", earlier, grad_next), jnp.sum(block_side * grad_next)[None]]
    )
    grad_down = jnp.einsum("rf,rd->fd", hidden_low, out_low, preferred_element_type=jnp.float32)
    grad_up = jnp.einsum("rd,rf->df", second_low, up_low, preferred_element_type=jnp.float32)
    grad_outproj = jnp.einsum(
        "rc,rd->cd", attended_low, branch_low, preferred_element_type=jnp.float32
    )
    early_grads = jnp.concatenate(
        [
            jnp.zeros((model_width, 3 * model_width), jnp.float32),
            grad_outproj,
            grad_up,
            grad_down.reshape(model_width, ff_width),
        ],
        axis=1,
    ).astype(jnp.bfloat16)
    qkv_low = jnp.concatenate(
        [
            rotate(query_grad, cosine_part, -sine_part),
            rotate(key_value_all[:, :model_width], cosine_part, -sine_part),
            key_value_all[:, model_width:],
        ],
        axis=1,
    ).astype(jnp.bfloat16)
    grad_qkv = jnp.einsum("rd,rc->dc", first_low, qkv_low, preferred_element_type=jnp.float32)
    first_grad = jnp.einsum("rc,dc->rd", qkv_low, full_qkv, preferred_element_type=jnp.float32)
    _, first_pullback = jax.vjp(layer_norm, inputs, norm_gains[:, 0], norm_biases[:, 0])
    input_part, gain_one, bias_one = first_pullback(first_grad)
    grad_input = (residual_grad + input_part).astype(jnp.bfloat16)
    grad_input = grad_input.reshape(batches, 1, row_count, model_width)
    packed_grads = lax.dynamic_update_slice(early_grads, grad_qkv.astype(jnp.bfloat16), (0, 0))
    device_count = model_width // shard_rows
    row_major = Layout(major_to_minor=(0, 1, 2))
    grad_offsets = [0]
    for width in (3 * model_width, model_width, ff_width, ff_width):
        grad_offsets.append(grad_offsets[-1] + width)
    scattered = lax.psum_scatter(
        with_layout_constraint(
            packed_grads.reshape(device_count, shard_rows, grad_offsets[-1]), row_major
        ),
        ("seq", "fsdp"),
        scatter_dimension=0,
        tiled=False,
    )
    scattered = with_layout_constraint(scattered, Layout(major_to_minor=(0, 1)))
    scattered = scattered.astype(jnp.float32)
    full_pieces = [scattered[:, grad_offsets[i] : grad_offsets[i + 1]] for i in range(4)]
    small_sums = lax.psum(
        jnp.concatenate(
            [
                depth_terms,
                jnp.stack([gain_one, gain_two, bias_one, bias_two], axis=1).reshape(-1),
            ]
        ),
        ("seq", "fsdp"),
    )
    depth_total = small_sums[:5]
    device_index = lax.axis_index("seq") * lax.axis_size("fsdp") + lax.axis_index("fsdp")
    norm_owned = lax.dynamic_slice_in_dim(
        small_sums[5:].reshape(model_width, 4), device_index * shard_rows, shard_rows, 0
    )
    owned = [
        full_pieces[0],
        full_pieces[1],
        full_pieces[2],
        full_pieces[3].reshape(-1, model_width),
        norm_owned[:, :2],
        norm_owned[:, 2:],
    ]
    return (next_input, grad_input, grad_history, *owned, depth_total)


def solution(mesh):
    in_specs = (
        P(None, "fsdp", "seq", None),
        P(None, None, "fsdp", "seq", None),
        P(None, "fsdp", "seq", None),
        P(None, "fsdp"),
        P(("seq", "fsdp"), None),
        P(("seq", "fsdp"), None),
        P(("seq", "fsdp"), None),
        P(("seq", "fsdp"), None),
        P(("seq", "fsdp"), None),
        P(("seq", "fsdp"), None),
        P(),
    )
    out_specs = (
        P(None, "fsdp", "seq", None),
        P(None, "fsdp", "seq", None),
        P(None, None, "fsdp", "seq", None),
        P(("seq", "fsdp"), None),
        P(("seq", "fsdp"), None),
        P(("seq", "fsdp"), None),
        P(("seq", "fsdp"), None),
        P(("seq", "fsdp"), None),
        P(("seq", "fsdp"), None),
        P(),
    )
    return jax.shard_map(local, mesh=mesh, in_specs=in_specs, out_specs=out_specs, check_vma=False)
```

```python
from functools import partial
import math

import jax
import jax.numpy as jnp
from jax import lax
from jax.sharding import PartitionSpec as P
from jax.experimental.layout import Layout, with_layout_constraint
from jax.experimental import pallas as pl
from jax.experimental.pallas import tpu as pltpu

HEADS = 12
HEAD = 64
STEP_HEADS = 4


epsilon = 1e-05
masked_value = -1e30


def layer_norm(values, gain_vector, bias_vector):
    center = values - jnp.mean(values, axis=-1, keepdims=True)
    spread = jnp.mean(center * center, axis=-1, keepdims=True)
    return center * lax.rsqrt(spread + epsilon) * gain_vector + bias_vector


def rotary_tables(positions):
    half_width = HEAD // 2
    frequencies = 10000.0 ** (-jnp.arange(half_width, dtype=jnp.float32) / half_width)
    angles = positions.astype(jnp.float32)[:, None] * frequencies[None, :]
    return (jnp.cos(angles)[:, None, :], jnp.sin(angles)[:, None, :])


def rotate(values, cosine_part, sine_part):
    row_count = values.shape[0]
    shaped = values.reshape(row_count, HEADS, HEAD)
    half_width = HEAD // 2
    first_half = shaped[..., :half_width]
    second_half = shaped[..., half_width:]
    turned = jnp.concatenate(
        [
            first_half * cosine_part - second_half * sine_part,
            second_half * cosine_part + first_half * sine_part,
        ],
        axis=-1,
    )
    return turned.reshape(row_count, HEADS * HEAD)


def block_scores(queries3, keys3, query_pos, key_pos, length):
    scores = jnp.einsum(
        "rhd,khd->hrk", queries3, keys3, preferred_element_type=jnp.float32
    ) * HEAD ** (-0.5)
    allowed = (key_pos[None, :] <= query_pos[:, None]) & (key_pos[None, :] < length)
    return (scores, allowed[None])


def row_totals(queries3, keys3, query_pos, length, key_block):
    row_count = queries3.shape[0]

    def row_advance(state, block_index):
        running_top, running_sum = state
        first_key = block_index * key_block
        keys_part = lax.dynamic_slice_in_dim(keys3, first_key, key_block, 0)
        key_pos = first_key + jnp.arange(key_block, dtype=jnp.int32)
        scores, allowed = block_scores(queries3, keys_part, query_pos, key_pos, length)
        masked = jnp.where(allowed, scores, masked_value)
        new_top = jnp.maximum(running_top, jnp.max(masked, axis=-1))
        kept_terms = jnp.where(allowed, jnp.exp(masked - new_top[..., None]), 0.0)
        running_sum = running_sum * jnp.exp(running_top - new_top) + jnp.sum(kept_terms, axis=-1)
        return ((new_top, running_sum), None)

    initial = (
        jnp.full((HEADS, row_count), masked_value, jnp.float32),
        jnp.zeros((HEADS, row_count), jnp.float32),
    )
    (row_tops, row_sums), _ = lax.scan(
        row_advance, initial, jnp.arange(keys3.shape[0] // key_block, dtype=jnp.int32)
    )
    return row_tops + jnp.log(row_sums)


def attend(queries3, keys3, values3, query_pos, length, key_block, log_total):

    def attend_advance(running, block_index):
        first_key = block_index * key_block
        keys_part = lax.dynamic_slice_in_dim(keys3, first_key, key_block, 0)
        values_part = lax.dynamic_slice_in_dim(values3, first_key, key_block, 0)
        key_pos = first_key + jnp.arange(key_block, dtype=jnp.int32)
        scores, allowed = block_scores(queries3, keys_part, query_pos, key_pos, length)
        probabilities = jnp.where(allowed, jnp.exp(scores - log_total[..., None]), 0.0).astype(
            jnp.bfloat16
        )
        return (
            running
            + jnp.einsum(
                "hrk,khd->rhd", probabilities, values_part, preferred_element_type=jnp.float32
            ),
            None,
        )

    initial = jnp.zeros(queries3.shape, jnp.float32)
    result, _ = lax.scan(
        attend_advance, initial, jnp.arange(keys3.shape[0] // key_block, dtype=jnp.int32)
    )
    return result


def query_grads(
    queries3, grads3, keys3, values3, query_pos, length, key_block, log_total, row_delta
):

    def query_advance(running, block_index):
        first_key = block_index * key_block
        keys_part = lax.dynamic_slice_in_dim(keys3, first_key, key_block, 0)
        values_part = lax.dynamic_slice_in_dim(values3, first_key, key_block, 0)
        key_pos = first_key + jnp.arange(key_block, dtype=jnp.int32)
        scores, allowed = block_scores(queries3, keys_part, query_pos, key_pos, length)
        probabilities = jnp.where(allowed, jnp.exp(scores - log_total[..., None]), 0.0)
        prob_grad = jnp.einsum(
            "rhd,khd->hrk", grads3, values_part, preferred_element_type=jnp.float32
        )
        score_low = (probabilities * (prob_grad - row_delta[..., None])).astype(jnp.bfloat16)
        return (
            running
            + jnp.einsum("hrk,khd->rhd", score_low, keys_part, preferred_element_type=jnp.float32),
            None,
        )

    initial = jnp.zeros(queries3.shape, jnp.float32)
    result, _ = lax.scan(
        query_advance, initial, jnp.arange(keys3.shape[0] // key_block, dtype=jnp.int32)
    )
    return result * HEAD ** (-0.5)


def key_side(queries3, grads3, log_part, delta_part, query_pos, keys3, values3, key_pos, length):
    key_count = keys3.shape[0]
    scores, allowed = block_scores(queries3, keys3, query_pos, key_pos, length)
    probabilities = jnp.where(allowed, jnp.exp(scores - log_part[..., None]), 0.0)
    prob_grad = jnp.einsum("rhd,khd->hrk", grads3, values3, preferred_element_type=jnp.float32)
    score_low = (probabilities * (prob_grad - delta_part[..., None])).astype(jnp.bfloat16)
    value_grad = jnp.einsum(
        "hrk,rhd->khd",
        probabilities.astype(jnp.bfloat16),
        grads3,
        preferred_element_type=jnp.float32,
    )
    key_grad = jnp.einsum(
        "hrk,rhd->khd", score_low, queries3, preferred_element_type=jnp.float32
    ) * HEAD ** (-0.5)
    return jnp.concatenate(
        [key_grad.reshape(key_count, HEADS * HEAD), value_grad.reshape(key_count, HEADS * HEAD)],
        axis=1,
    )


def slot_attention(queries3, keys3, values3, query_pos, length):
    key_pos = jnp.arange(keys3.shape[0], dtype=jnp.int32)
    scores, allowed = block_scores(queries3, keys3, query_pos, key_pos, length)
    masked = jnp.where(allowed, scores, masked_value)
    top = jnp.max(masked, axis=-1)
    kept_terms = jnp.where(allowed, jnp.exp(masked - top[..., None]), 0.0)
    log_total = top + jnp.log(jnp.sum(kept_terms, axis=-1))
    probabilities = jnp.where(allowed, jnp.exp(scores - log_total[..., None]), 0.0)
    probabilities_low = probabilities.astype(jnp.bfloat16)
    attended = jnp.einsum(
        "hrk,khd->rhd", probabilities_low, values3, preferred_element_type=jnp.float32
    )
    return attended, probabilities, probabilities_low


def slot_attention_grads(queries3, keys3, values3, grads3, attended, probabilities, probabilities_low):
    prob_grad = jnp.einsum("rhd,khd->hrk", grads3, values3, preferred_element_type=jnp.float32)
    row_delta = jnp.einsum("rhd,rhd->hr", grads3.astype(jnp.float32), attended)
    score_low = (probabilities * (prob_grad - row_delta[..., None])).astype(jnp.bfloat16)
    query_grad = jnp.einsum(
        "hrk,khd->rhd", score_low, keys3, preferred_element_type=jnp.float32
    ) * HEAD ** (-0.5)
    key_grad = jnp.einsum(
        "hrk,rhd->khd", score_low, queries3, preferred_element_type=jnp.float32
    ) * HEAD ** (-0.5)
    value_grad = jnp.einsum(
        "hrk,rhd->khd", probabilities_low, grads3, preferred_element_type=jnp.float32
    )
    return query_grad, key_grad, value_grad


def _pair_masks(scalars_ref, micro, row_count, key_count):
    length = scalars_ref[micro]
    first_row = scalars_ref[scalars_ref.shape[0] - 1]
    query_pos = first_row + lax.broadcasted_iota(jnp.int32, (row_count, key_count), 0)
    key_pos = lax.broadcasted_iota(jnp.int32, (row_count, key_count), 1)
    return (key_pos <= query_pos) & (key_pos < length)


def _forward_kernel(scalars_ref, q_ref, k_ref, v_ref, out_ref, lse_ref):
    micro = pl.program_id(0)
    row_count = q_ref.shape[0]
    key_count = k_ref.shape[0]
    allowed = _pair_masks(scalars_ref, micro, row_count, key_count)
    for half in range(STEP_HEADS):
        lanes = slice(half * HEAD, (half + 1) * HEAD)
        q_head = q_ref[:, lanes]
        k_head = k_ref[:, lanes]
        v_head = v_ref[:, lanes]
        scores = lax.dot_general(
            q_head, k_head, (((1,), (1,)), ((), ())), preferred_element_type=jnp.float32
        ) * HEAD ** (-0.5)
        masked = jnp.where(allowed, scores, masked_value)
        top = jnp.max(masked, axis=1, keepdims=True)
        kept = jnp.where(allowed, jnp.exp(masked - top), 0.0)
        total = jnp.sum(kept, axis=1, keepdims=True)
        log_total = top + jnp.log(total)
        probabilities = kept * (1.0 / total)
        attended = jnp.dot(
            probabilities.astype(jnp.bfloat16), v_head, preferred_element_type=jnp.float32
        )
        out_ref[:, lanes] = attended
        lse_ref[:, lanes] = jnp.broadcast_to(log_total, (row_count, HEAD))


def _backward_kernel(
    scalars_ref, q_ref, k_ref, v_ref, do_ref, o_ref, lse_ref, dq_ref, kv_grad_ref
):
    micro = pl.program_id(0)
    row_count = q_ref.shape[0]
    key_count = k_ref.shape[0]
    allowed = _pair_masks(scalars_ref, micro, row_count, key_count)
    for half in range(STEP_HEADS):
        lanes = slice(half * HEAD, (half + 1) * HEAD)
        q_head = q_ref[:, lanes]
        k_head = k_ref[:, lanes]
        v_head = v_ref[:, lanes]
        grad_head = do_ref[:, lanes]
        scores = lax.dot_general(
            q_head, k_head, (((1,), (1,)), ((), ())), preferred_element_type=jnp.float32
        ) * HEAD ** (-0.5)
        log_total = lse_ref[:, half * HEAD : half * HEAD + 1]
        probabilities = jnp.where(allowed, jnp.exp(scores - log_total), 0.0)
        probabilities_low = probabilities.astype(jnp.bfloat16)
        prob_grad = lax.dot_general(
            grad_head, v_head, (((1,), (1,)), ((), ())), preferred_element_type=jnp.float32
        )
        row_delta = jnp.sum(
            grad_head.astype(jnp.float32) * o_ref[:, lanes], axis=1, keepdims=True
        )
        score_low = (probabilities * (prob_grad - row_delta)).astype(jnp.bfloat16)
        dq_ref[:, lanes] = jnp.dot(
            score_low, k_head, preferred_element_type=jnp.float32
        ) * HEAD ** (-0.5)
        key_grad = lax.dot_general(
            score_low, q_head, (((0,), (0,)), ((), ())), preferred_element_type=jnp.float32
        ) * HEAD ** (-0.5)
        value_grad = lax.dot_general(
            probabilities_low, grad_head, (((0,), (0,)), ((), ())),
            preferred_element_type=jnp.float32,
        )
        kv_grad_ref[:, lanes] = key_grad.astype(jnp.bfloat16)
        kv_grad_ref[:, STEP_HEADS * HEAD + half * HEAD : STEP_HEADS * HEAD + (half + 1) * HEAD] = value_grad.astype(
            jnp.bfloat16
        )


def attention_forward(scalars, queries, kv_flat, batches):
    all_rows, model_width = queries.shape
    row_count = all_rows // batches
    key_count = kv_flat.shape[0]
    pairs = model_width // (STEP_HEADS * HEAD)
    micro_blocks = kv_flat.shape[1] // batches // (STEP_HEADS * HEAD)
    row_spec = pl.BlockSpec((row_count, STEP_HEADS * HEAD), lambda m, p, s: (m, p))
    key_spec = pl.BlockSpec((key_count, STEP_HEADS * HEAD), lambda m, p, s: (0, m * micro_blocks + p))
    value_spec = pl.BlockSpec(
        (key_count, STEP_HEADS * HEAD), lambda m, p, s: (0, m * micro_blocks + pairs + p)
    )
    return pl.pallas_call(
        _forward_kernel,
        grid_spec=pltpu.PrefetchScalarGridSpec(
            num_scalar_prefetch=1,
            grid=(batches, pairs),
            in_specs=[row_spec, key_spec, value_spec],
            out_specs=[row_spec, row_spec],
        ),
        out_shape=[
            jax.ShapeDtypeStruct((all_rows, model_width), jnp.float32),
            jax.ShapeDtypeStruct((all_rows, model_width), jnp.float32),
        ],
        name="attention_forward",
    )(scalars, queries, kv_flat, kv_flat)


def attention_backward(scalars, queries, kv_flat, grads, attended, log_totals, batches):
    all_rows, model_width = queries.shape
    row_count = all_rows // batches
    key_count = kv_flat.shape[0]
    pairs = model_width // (STEP_HEADS * HEAD)
    micro_blocks = kv_flat.shape[1] // batches // (STEP_HEADS * HEAD)
    row_spec = pl.BlockSpec((row_count, STEP_HEADS * HEAD), lambda m, p, s: (m, p))
    key_spec = pl.BlockSpec((key_count, STEP_HEADS * HEAD), lambda m, p, s: (0, m * micro_blocks + p))
    value_spec = pl.BlockSpec(
        (key_count, STEP_HEADS * HEAD), lambda m, p, s: (0, m * micro_blocks + pairs + p)
    )
    grad_spec = pl.BlockSpec((key_count, 2 * STEP_HEADS * HEAD), lambda m, p, s: (0, m * pairs + p))
    return pl.pallas_call(
        _backward_kernel,
        grid_spec=pltpu.PrefetchScalarGridSpec(
            num_scalar_prefetch=1,
            grid=(batches, pairs),
            in_specs=[row_spec, key_spec, value_spec, row_spec, row_spec, row_spec],
            out_specs=[row_spec, grad_spec],
        ),
        out_shape=[
            jax.ShapeDtypeStruct((all_rows, model_width), jnp.float32),
            jax.ShapeDtypeStruct(kv_flat.shape, jnp.bfloat16),
        ],
        name="attention_backward",
    )(scalars, queries, kv_flat, kv_flat, grads, attended, log_totals)


def local(
    layer_input,
    history,
    cotangent,
    lengths,
    w_qkv,
    w_out,
    w_up,
    w_down,
    ln_gains,
    ln_biases,
    depth_weights,
):
    batches = layer_input.shape[0]
    row_count = layer_input.shape[2]
    model_width = layer_input.shape[3]
    ff_width = w_up.shape[1]
    shard_rows = w_qkv.shape[0]
    all_rows = batches * row_count
    slot_len = row_count * lax.axis_size("seq")
    positions = lax.axis_index("seq") * row_count + jnp.arange(row_count, dtype=jnp.int32)
    cosine_part, sine_part = rotary_tables(jnp.tile(positions, batches))
    gelu_tanh = partial(jax.nn.gelu, approximate=True)
    lane_pad = 128 - 4
    widths = (3 * model_width, 2, 2, lane_pad, model_width, ff_width, ff_width)
    offsets = [0]
    for width in widths:
        offsets.append(offsets[-1] + width)

    def pieces(packed_rows):
        return [packed_rows[:, offsets[i] : offsets[i + 1]] for i in range(len(widths))]

    packed = jnp.concatenate(
        [
            w_qkv,
            ln_gains,
            ln_biases,
            jnp.zeros((shard_rows, lane_pad), w_qkv.dtype),
            w_out,
            w_up,
            w_down.reshape(shard_rows, ff_width),
        ],
        axis=1,
    )
    gathered = lax.all_gather(packed, ("seq", "fsdp"), axis=0, tiled=True)
    full_qkv, gain_rows, bias_rows, _, full_out, full_up, down_rows = pieces(gathered)
    full_down = down_rows.reshape(ff_width, model_width)
    norm_gains = gain_rows.astype(jnp.float32)
    norm_biases = bias_rows.astype(jnp.float32)

    slot_lengths = lengths[:, 0]
    inputs = layer_input[:, 0].reshape(all_rows, model_width).astype(jnp.float32)
    first_low = layer_norm(inputs, norm_gains[:, 0], norm_biases[:, 0]).astype(jnp.bfloat16)
    projected = jnp.dot(first_low, full_qkv, preferred_element_type=jnp.float32)
    queries = rotate(projected[:, :model_width], cosine_part, sine_part).astype(jnp.bfloat16)
    keys_own = rotate(
        projected[:, model_width : 2 * model_width], cosine_part, sine_part
    ).astype(jnp.bfloat16)
    values_own = projected[:, 2 * model_width :].astype(jnp.bfloat16)
    own_kv = jnp.concatenate([keys_own, values_own], axis=1).reshape(
        batches, row_count, 2 * model_width
    )
    earlier = history[:, :, 0].reshape(4, all_rows, model_width).astype(jnp.float32)
    usable = (positions[None, :] < slot_lengths[:, None]).reshape(all_rows, 1)
    grad_next = jnp.where(
        usable, cotangent[:, 0].reshape(all_rows, model_width).astype(jnp.float32), 0.0
    )
    history_part = jnp.einsum("j,jrd->rd", depth_weights[:4], earlier)
    grad_history = (depth_weights[:4, None, None] * grad_next[None]).astype(jnp.bfloat16)
    grad_history = grad_history.reshape(4, batches, 1, row_count, model_width)
    out_grad = depth_weights[4] * grad_next
    out_low = out_grad.astype(jnp.bfloat16)

    kv_all = lax.all_gather(
        jnp.swapaxes(own_kv, 0, 1).reshape(row_count, batches * 2 * model_width),
        "seq",
        axis=0,
        tiled=False,
    )
    kv_flat = kv_all.reshape(slot_len, batches * 2 * model_width)
    scalars = jnp.concatenate(
        [slot_lengths.astype(jnp.int32), (lax.axis_index("seq") * row_count)[None].astype(jnp.int32)]
    )
    attended_rows, log_totals = attention_forward(scalars, queries, kv_flat, batches)
    attended_low = attended_rows.astype(jnp.bfloat16)
    residual = inputs + jnp.dot(attended_low, full_out, preferred_element_type=jnp.float32)
    second_low = layer_norm(residual, norm_gains[:, 1], norm_biases[:, 1]).astype(jnp.bfloat16)
    hidden = jnp.dot(second_low, full_up, preferred_element_type=jnp.float32)
    hidden_low = gelu_tanh(hidden).astype(jnp.bfloat16)
    block_out = residual + jnp.dot(hidden_low, full_down, preferred_element_type=jnp.float32)
    hidden_grad = jnp.einsum("rd,fd->rf", out_low, full_down, preferred_element_type=jnp.float32)
    _, gelu_pullback = jax.vjp(gelu_tanh, hidden)
    up_low = gelu_pullback(hidden_grad)[0].astype(jnp.bfloat16)
    second_grad = jnp.einsum("rf,df->rd", up_low, full_up, preferred_element_type=jnp.float32)
    _, second_pullback = jax.vjp(layer_norm, residual, norm_gains[:, 1], norm_biases[:, 1])
    residual_part, gain_two, bias_two = second_pullback(second_grad)
    residual_grad = out_grad + residual_part
    branch_low = residual_grad.astype(jnp.bfloat16)
    attended_grad = jnp.einsum(
        "rd,cd->rc", branch_low, full_out, preferred_element_type=jnp.float32
    ).astype(jnp.bfloat16)
    query_grad, kv_grad_flat = attention_backward(
        scalars, queries, kv_flat, attended_grad, attended_rows, log_totals, batches
    )
    kv_grad_own = lax.psum_scatter(kv_grad_flat, "seq", scatter_dimension=0, tiled=True)
    pairs = model_width // (STEP_HEADS * HEAD)
    kv_grad_own = kv_grad_own.reshape(row_count, batches, pairs, 2, STEP_HEADS * HEAD)
    kv_grad_own = jnp.transpose(kv_grad_own, (1, 0, 3, 2, 4)).reshape(
        all_rows, 2 * model_width
    )
    key_value_all = kv_grad_own.astype(jnp.float32)
    block_side, _ = lax.optimization_barrier((block_out, kv_grad_flat))
    combined = depth_weights[4] * block_side + history_part
    next_input = combined.astype(jnp.bfloat16).reshape(batches, 1, row_count, model_width)
    depth_terms = jnp.concatenate(
        [jnp.einsum("jrd,rd->j", earlier, grad_next), jnp.sum(block_side * grad_next)[None]]
    )
    grad_down = jnp.einsum("rf,rd->fd", hidden_low, out_low, preferred_element_type=jnp.float32)
    grad_up = jnp.einsum("rd,rf->df", second_low, up_low, preferred_element_type=jnp.float32)
    grad_outproj = jnp.einsum(
        "rc,rd->cd", attended_low, branch_low, preferred_element_type=jnp.float32
    )
    early_grads = jnp.concatenate(
        [
            jnp.zeros((model_width, 3 * model_width), jnp.float32),
            grad_outproj,
            grad_up,
            grad_down.reshape(model_width, ff_width),
        ],
        axis=1,
    ).astype(jnp.bfloat16)
    qkv_low = jnp.concatenate(
        [
            rotate(query_grad, cosine_part, -sine_part),
            rotate(key_value_all[:, :model_width], cosine_part, -sine_part),
            key_value_all[:, model_width:],
        ],
        axis=1,
    ).astype(jnp.bfloat16)
    grad_qkv = jnp.einsum("rd,rc->dc", first_low, qkv_low, preferred_element_type=jnp.float32)
    first_grad = jnp.einsum("rc,dc->rd", qkv_low, full_qkv, preferred_element_type=jnp.float32)
    _, first_pullback = jax.vjp(layer_norm, inputs, norm_gains[:, 0], norm_biases[:, 0])
    input_part, gain_one, bias_one = first_pullback(first_grad)
    grad_input = (residual_grad + input_part).astype(jnp.bfloat16)
    grad_input = grad_input.reshape(batches, 1, row_count, model_width)
    packed_grads = lax.dynamic_update_slice(early_grads, grad_qkv.astype(jnp.bfloat16), (0, 0))
    device_count = model_width // shard_rows
    row_major = Layout(major_to_minor=(0, 1, 2))
    grad_offsets = [0]
    for width in (3 * model_width, model_width, ff_width, ff_width):
        grad_offsets.append(grad_offsets[-1] + width)
    scattered = lax.psum_scatter(
        with_layout_constraint(
            packed_grads.reshape(device_count, shard_rows, grad_offsets[-1]), row_major
        ),
        ("seq", "fsdp"),
        scatter_dimension=0,
        tiled=False,
    )
    scattered = with_layout_constraint(scattered, Layout(major_to_minor=(0, 1)))
    scattered = scattered.astype(jnp.float32)
    full_pieces = [scattered[:, grad_offsets[i] : grad_offsets[i + 1]] for i in range(4)]
    small_sums = lax.psum(
        jnp.concatenate(
            [
                depth_terms,
                jnp.stack([gain_one, gain_two, bias_one, bias_two], axis=1).reshape(-1),
            ]
        ),
        ("seq", "fsdp"),
    )
    depth_total = small_sums[:5]
    device_index = lax.axis_index("seq") * lax.axis_size("fsdp") + lax.axis_index("fsdp")
    norm_owned = lax.dynamic_slice_in_dim(
        small_sums[5:].reshape(model_width, 4), device_index * shard_rows, shard_rows, 0
    )
    owned = [
        full_pieces[0],
        full_pieces[1],
        full_pieces[2],
        full_pieces[3].reshape(-1, model_width),
        norm_owned[:, :2],
        norm_owned[:, 2:],
    ]
    return (next_input, grad_input, grad_history, *owned, depth_total)


def solution(mesh):
    in_specs = (
        P(None, "fsdp", "seq", None),
        P(None, None, "fsdp", "seq", None),
        P(None, "fsdp", "seq", None),
        P(None, "fsdp"),
        P(("seq", "fsdp"), None),
        P(("seq", "fsdp"), None),
        P(("seq", "fsdp"), None),
        P(("seq", "fsdp"), None),
        P(("seq", "fsdp"), None),
        P(("seq", "fsdp"), None),
        P(),
    )
    out_specs = (
        P(None, "fsdp", "seq", None),
        P(None, "fsdp", "seq", None),
        P(None, None, "fsdp", "seq", None),
        P(("seq", "fsdp"), None),
        P(("seq", "fsdp"), None),
        P(("seq", "fsdp"), None),
        P(("seq", "fsdp"), None),
        P(("seq", "fsdp"), None),
        P(("seq", "fsdp"), None),
        P(),
    )
    return jax.shard_map(local, mesh=mesh, in_specs=in_specs, out_specs=out_specs, check_vma=False)
```

```python
from functools import partial
import math

import jax
import jax.numpy as jnp
from jax import lax
from jax.sharding import PartitionSpec as P
from jax.experimental.layout import Layout, with_layout_constraint
from jax.experimental import pallas as pl
from jax.experimental.pallas import tpu as pltpu

HEADS = 12
HEAD = 64
STEP_HEADS = 4


epsilon = 1e-05
masked_value = -1e30


def layer_norm(values, gain_vector, bias_vector):
    center = values - jnp.mean(values, axis=-1, keepdims=True)
    spread = jnp.mean(center * center, axis=-1, keepdims=True)
    return center * lax.rsqrt(spread + epsilon) * gain_vector + bias_vector


def rotary_tables(positions):
    half_width = HEAD // 2
    frequencies = 10000.0 ** (-jnp.arange(half_width, dtype=jnp.float32) / half_width)
    angles = positions.astype(jnp.float32)[:, None] * frequencies[None, :]
    return (jnp.cos(angles)[:, None, :], jnp.sin(angles)[:, None, :])


def rotate(values, cosine_part, sine_part):
    row_count = values.shape[0]
    shaped = values.reshape(row_count, HEADS, HEAD)
    half_width = HEAD // 2
    first_half = shaped[..., :half_width]
    second_half = shaped[..., half_width:]
    turned = jnp.concatenate(
        [
            first_half * cosine_part - second_half * sine_part,
            second_half * cosine_part + first_half * sine_part,
        ],
        axis=-1,
    )
    return turned.reshape(row_count, HEADS * HEAD)


def block_scores(queries3, keys3, query_pos, key_pos, length):
    scores = jnp.einsum(
        "rhd,khd->hrk", queries3, keys3, preferred_element_type=jnp.float32
    ) * HEAD ** (-0.5)
    allowed = (key_pos[None, :] <= query_pos[:, None]) & (key_pos[None, :] < length)
    return (scores, allowed[None])


def row_totals(queries3, keys3, query_pos, length, key_block):
    row_count = queries3.shape[0]

    def row_advance(state, block_index):
        running_top, running_sum = state
        first_key = block_index * key_block
        keys_part = lax.dynamic_slice_in_dim(keys3, first_key, key_block, 0)
        key_pos = first_key + jnp.arange(key_block, dtype=jnp.int32)
        scores, allowed = block_scores(queries3, keys_part, query_pos, key_pos, length)
        masked = jnp.where(allowed, scores, masked_value)
        new_top = jnp.maximum(running_top, jnp.max(masked, axis=-1))
        kept_terms = jnp.where(allowed, jnp.exp(masked - new_top[..., None]), 0.0)
        running_sum = running_sum * jnp.exp(running_top - new_top) + jnp.sum(kept_terms, axis=-1)
        return ((new_top, running_sum), None)

    initial = (
        jnp.full((HEADS, row_count), masked_value, jnp.float32),
        jnp.zeros((HEADS, row_count), jnp.float32),
    )
    (row_tops, row_sums), _ = lax.scan(
        row_advance, initial, jnp.arange(keys3.shape[0] // key_block, dtype=jnp.int32)
    )
    return row_tops + jnp.log(row_sums)


def attend(queries3, keys3, values3, query_pos, length, key_block, log_total):

    def attend_advance(running, block_index):
        first_key = block_index * key_block
        keys_part = lax.dynamic_slice_in_dim(keys3, first_key, key_block, 0)
        values_part = lax.dynamic_slice_in_dim(values3, first_key, key_block, 0)
        key_pos = first_key + jnp.arange(key_block, dtype=jnp.int32)
        scores, allowed = block_scores(queries3, keys_part, query_pos, key_pos, length)
        probabilities = jnp.where(allowed, jnp.exp(scores - log_total[..., None]), 0.0).astype(
            jnp.bfloat16
        )
        return (
            running
            + jnp.einsum(
                "hrk,khd->rhd", probabilities, values_part, preferred_element_type=jnp.float32
            ),
            None,
        )

    initial = jnp.zeros(queries3.shape, jnp.float32)
    result, _ = lax.scan(
        attend_advance, initial, jnp.arange(keys3.shape[0] // key_block, dtype=jnp.int32)
    )
    return result


def query_grads(
    queries3, grads3, keys3, values3, query_pos, length, key_block, log_total, row_delta
):

    def query_advance(running, block_index):
        first_key = block_index * key_block
        keys_part = lax.dynamic_slice_in_dim(keys3, first_key, key_block, 0)
        values_part = lax.dynamic_slice_in_dim(values3, first_key, key_block, 0)
        key_pos = first_key + jnp.arange(key_block, dtype=jnp.int32)
        scores, allowed = block_scores(queries3, keys_part, query_pos, key_pos, length)
        probabilities = jnp.where(allowed, jnp.exp(scores - log_total[..., None]), 0.0)
        prob_grad = jnp.einsum(
            "rhd,khd->hrk", grads3, values_part, preferred_element_type=jnp.float32
        )
        score_low = (probabilities * (prob_grad - row_delta[..., None])).astype(jnp.bfloat16)
        return (
            running
            + jnp.einsum("hrk,khd->rhd", score_low, keys_part, preferred_element_type=jnp.float32),
            None,
        )

    initial = jnp.zeros(queries3.shape, jnp.float32)
    result, _ = lax.scan(
        query_advance, initial, jnp.arange(keys3.shape[0] // key_block, dtype=jnp.int32)
    )
    return result * HEAD ** (-0.5)


def key_side(queries3, grads3, log_part, delta_part, query_pos, keys3, values3, key_pos, length):
    key_count = keys3.shape[0]
    scores, allowed = block_scores(queries3, keys3, query_pos, key_pos, length)
    probabilities = jnp.where(allowed, jnp.exp(scores - log_part[..., None]), 0.0)
    prob_grad = jnp.einsum("rhd,khd->hrk", grads3, values3, preferred_element_type=jnp.float32)
    score_low = (probabilities * (prob_grad - delta_part[..., None])).astype(jnp.bfloat16)
    value_grad = jnp.einsum(
        "hrk,rhd->khd",
        probabilities.astype(jnp.bfloat16),
        grads3,
        preferred_element_type=jnp.float32,
    )
    key_grad = jnp.einsum(
        "hrk,rhd->khd", score_low, queries3, preferred_element_type=jnp.float32
    ) * HEAD ** (-0.5)
    return jnp.concatenate(
        [key_grad.reshape(key_count, HEADS * HEAD), value_grad.reshape(key_count, HEADS * HEAD)],
        axis=1,
    )


def slot_attention(queries3, keys3, values3, query_pos, length):
    key_pos = jnp.arange(keys3.shape[0], dtype=jnp.int32)
    scores, allowed = block_scores(queries3, keys3, query_pos, key_pos, length)
    masked = jnp.where(allowed, scores, masked_value)
    top = jnp.max(masked, axis=-1)
    kept_terms = jnp.where(allowed, jnp.exp(masked - top[..., None]), 0.0)
    log_total = top + jnp.log(jnp.sum(kept_terms, axis=-1))
    probabilities = jnp.where(allowed, jnp.exp(scores - log_total[..., None]), 0.0)
    probabilities_low = probabilities.astype(jnp.bfloat16)
    attended = jnp.einsum(
        "hrk,khd->rhd", probabilities_low, values3, preferred_element_type=jnp.float32
    )
    return attended, probabilities, probabilities_low


def slot_attention_grads(queries3, keys3, values3, grads3, attended, probabilities, probabilities_low):
    prob_grad = jnp.einsum("rhd,khd->hrk", grads3, values3, preferred_element_type=jnp.float32)
    row_delta = jnp.einsum("rhd,rhd->hr", grads3.astype(jnp.float32), attended)
    score_low = (probabilities * (prob_grad - row_delta[..., None])).astype(jnp.bfloat16)
    query_grad = jnp.einsum(
        "hrk,khd->rhd", score_low, keys3, preferred_element_type=jnp.float32
    ) * HEAD ** (-0.5)
    key_grad = jnp.einsum(
        "hrk,rhd->khd", score_low, queries3, preferred_element_type=jnp.float32
    ) * HEAD ** (-0.5)
    value_grad = jnp.einsum(
        "hrk,rhd->khd", probabilities_low, grads3, preferred_element_type=jnp.float32
    )
    return query_grad, key_grad, value_grad


def _pair_masks(scalars_ref, micro, row_count, key_count):
    length = scalars_ref[micro]
    first_row = scalars_ref[scalars_ref.shape[0] - 1]
    query_pos = first_row + lax.broadcasted_iota(jnp.int32, (row_count, key_count), 0)
    key_pos = lax.broadcasted_iota(jnp.int32, (row_count, key_count), 1)
    return (key_pos <= query_pos) & (key_pos < length)


def _forward_kernel(scalars_ref, q_ref, k_ref, v_ref, out_ref, prob_ref):
    micro = pl.program_id(0)
    row_count = q_ref.shape[0]
    key_count = k_ref.shape[0]
    allowed = _pair_masks(scalars_ref, micro, row_count, key_count)
    for half in range(STEP_HEADS):
        lanes = slice(half * HEAD, (half + 1) * HEAD)
        q_head = q_ref[:, lanes]
        k_head = k_ref[:, lanes]
        v_head = v_ref[:, lanes]
        scores = lax.dot_general(
            q_head, k_head, (((1,), (1,)), ((), ())), preferred_element_type=jnp.float32
        ) * HEAD ** (-0.5)
        masked = jnp.where(allowed, scores, masked_value)
        top = jnp.max(masked, axis=1, keepdims=True)
        kept = jnp.where(allowed, jnp.exp(masked - top), 0.0)
        total = jnp.sum(kept, axis=1, keepdims=True)
        probabilities = kept * (1.0 / total)
        prob_ref[half] = probabilities
        attended = jnp.dot(
            probabilities.astype(jnp.bfloat16), v_head, preferred_element_type=jnp.float32
        )
        out_ref[:, lanes] = attended


def _backward_kernel(
    scalars_ref, q_ref, k_ref, v_ref, do_ref, o_ref, prob_ref, dq_ref, kv_grad_ref
):
    for half in range(STEP_HEADS):
        lanes = slice(half * HEAD, (half + 1) * HEAD)
        q_head = q_ref[:, lanes]
        k_head = k_ref[:, lanes]
        v_head = v_ref[:, lanes]
        grad_head = do_ref[:, lanes]
        probabilities = prob_ref[half]
        probabilities_low = probabilities.astype(jnp.bfloat16)
        prob_grad = lax.dot_general(
            grad_head, v_head, (((1,), (1,)), ((), ())), preferred_element_type=jnp.float32
        )
        row_delta = jnp.sum(
            grad_head.astype(jnp.float32) * o_ref[:, lanes], axis=1, keepdims=True
        )
        score_low = (probabilities * (prob_grad - row_delta)).astype(jnp.bfloat16)
        dq_ref[:, lanes] = jnp.dot(
            score_low, k_head, preferred_element_type=jnp.float32
        ) * HEAD ** (-0.5)
        key_grad = lax.dot_general(
            score_low, q_head, (((0,), (0,)), ((), ())), preferred_element_type=jnp.float32
        ) * HEAD ** (-0.5)
        value_grad = lax.dot_general(
            probabilities_low, grad_head, (((0,), (0,)), ((), ())),
            preferred_element_type=jnp.float32,
        )
        kv_grad_ref[:, lanes] = key_grad.astype(jnp.bfloat16)
        kv_grad_ref[:, STEP_HEADS * HEAD + half * HEAD : STEP_HEADS * HEAD + (half + 1) * HEAD] = value_grad.astype(
            jnp.bfloat16
        )


def attention_forward(scalars, queries, kv_flat, batches):
    all_rows, model_width = queries.shape
    row_count = all_rows // batches
    key_count = kv_flat.shape[0]
    pairs = model_width // (STEP_HEADS * HEAD)
    micro_blocks = kv_flat.shape[1] // batches // (STEP_HEADS * HEAD)
    row_spec = pl.BlockSpec((row_count, STEP_HEADS * HEAD), lambda m, p, s: (m, p))
    key_spec = pl.BlockSpec((key_count, STEP_HEADS * HEAD), lambda m, p, s: (0, m * micro_blocks + p))
    value_spec = pl.BlockSpec(
        (key_count, STEP_HEADS * HEAD), lambda m, p, s: (0, m * micro_blocks + pairs + p)
    )
    prob_spec = pl.BlockSpec(
        (STEP_HEADS, row_count, key_count), lambda m, p, s: (m * pairs + p, 0, 0)
    )
    return pl.pallas_call(
        _forward_kernel,
        grid_spec=pltpu.PrefetchScalarGridSpec(
            num_scalar_prefetch=1,
            grid=(batches, pairs),
            in_specs=[row_spec, key_spec, value_spec],
            out_specs=[row_spec, prob_spec],
        ),
        out_shape=[
            jax.ShapeDtypeStruct((all_rows, model_width), jnp.float32),
            jax.ShapeDtypeStruct((batches * HEADS, row_count, key_count), jnp.float32),
        ],
        name="attention_forward",
    )(scalars, queries, kv_flat, kv_flat)


def attention_backward(scalars, queries, kv_flat, grads, attended, probabilities, batches):
    all_rows, model_width = queries.shape
    row_count = all_rows // batches
    key_count = kv_flat.shape[0]
    pairs = model_width // (STEP_HEADS * HEAD)
    micro_blocks = kv_flat.shape[1] // batches // (STEP_HEADS * HEAD)
    row_spec = pl.BlockSpec((row_count, STEP_HEADS * HEAD), lambda m, p, s: (m, p))
    key_spec = pl.BlockSpec((key_count, STEP_HEADS * HEAD), lambda m, p, s: (0, m * micro_blocks + p))
    value_spec = pl.BlockSpec(
        (key_count, STEP_HEADS * HEAD), lambda m, p, s: (0, m * micro_blocks + pairs + p)
    )
    grad_spec = pl.BlockSpec((key_count, 2 * STEP_HEADS * HEAD), lambda m, p, s: (0, m * pairs + p))
    prob_spec = pl.BlockSpec(
        (STEP_HEADS, row_count, key_count), lambda m, p, s: (m * pairs + p, 0, 0)
    )
    return pl.pallas_call(
        _backward_kernel,
        grid_spec=pltpu.PrefetchScalarGridSpec(
            num_scalar_prefetch=1,
            grid=(batches, pairs),
            in_specs=[row_spec, key_spec, value_spec, row_spec, row_spec, prob_spec],
            out_specs=[row_spec, grad_spec],
        ),
        out_shape=[
            jax.ShapeDtypeStruct((all_rows, model_width), jnp.float32),
            jax.ShapeDtypeStruct(kv_flat.shape, jnp.bfloat16),
        ],
        name="attention_backward",
    )(scalars, queries, kv_flat, kv_flat, grads, attended, probabilities)


def local(
    layer_input,
    history,
    cotangent,
    lengths,
    w_qkv,
    w_out,
    w_up,
    w_down,
    ln_gains,
    ln_biases,
    depth_weights,
):
    batches = layer_input.shape[0]
    row_count = layer_input.shape[2]
    model_width = layer_input.shape[3]
    ff_width = w_up.shape[1]
    shard_rows = w_qkv.shape[0]
    all_rows = batches * row_count
    slot_len = row_count * lax.axis_size("seq")
    positions = lax.axis_index("seq") * row_count + jnp.arange(row_count, dtype=jnp.int32)
    cosine_part, sine_part = rotary_tables(jnp.tile(positions, batches))
    gelu_tanh = partial(jax.nn.gelu, approximate=True)
    lane_pad = 128 - 4
    widths = (3 * model_width, 2, 2, lane_pad, model_width, ff_width, ff_width)
    offsets = [0]
    for width in widths:
        offsets.append(offsets[-1] + width)

    def pieces(packed_rows):
        return [packed_rows[:, offsets[i] : offsets[i + 1]] for i in range(len(widths))]

    packed = jnp.concatenate(
        [
            w_qkv,
            ln_gains,
            ln_biases,
            jnp.zeros((shard_rows, lane_pad), w_qkv.dtype),
            w_out,
            w_up,
            w_down.reshape(shard_rows, ff_width),
        ],
        axis=1,
    )
    gathered = lax.all_gather(packed, ("seq", "fsdp"), axis=0, tiled=True)
    full_qkv, gain_rows, bias_rows, _, full_out, full_up, down_rows = pieces(gathered)
    full_down = down_rows.reshape(ff_width, model_width)
    norm_gains = gain_rows.astype(jnp.float32)
    norm_biases = bias_rows.astype(jnp.float32)

    slot_lengths = lengths[:, 0]
    inputs = layer_input[:, 0].reshape(all_rows, model_width).astype(jnp.float32)
    first_low = layer_norm(inputs, norm_gains[:, 0], norm_biases[:, 0]).astype(jnp.bfloat16)
    projected = jnp.dot(first_low, full_qkv, preferred_element_type=jnp.float32)
    queries = rotate(projected[:, :model_width], cosine_part, sine_part).astype(jnp.bfloat16)
    keys_own = rotate(
        projected[:, model_width : 2 * model_width], cosine_part, sine_part
    ).astype(jnp.bfloat16)
    values_own = projected[:, 2 * model_width :].astype(jnp.bfloat16)
    own_kv = jnp.concatenate([keys_own, values_own], axis=1).reshape(
        batches, row_count, 2 * model_width
    )
    earlier = history[:, :, 0].reshape(4, all_rows, model_width).astype(jnp.float32)
    usable = (positions[None, :] < slot_lengths[:, None]).reshape(all_rows, 1)
    grad_next = jnp.where(
        usable, cotangent[:, 0].reshape(all_rows, model_width).astype(jnp.float32), 0.0
    )
    history_part = jnp.einsum("j,jrd->rd", depth_weights[:4], earlier)
    grad_history = (depth_weights[:4, None, None] * grad_next[None]).astype(jnp.bfloat16)
    grad_history = grad_history.reshape(4, batches, 1, row_count, model_width)
    out_grad = depth_weights[4] * grad_next
    out_low = out_grad.astype(jnp.bfloat16)

    kv_all = lax.all_gather(
        jnp.swapaxes(own_kv, 0, 1).reshape(row_count, batches * 2 * model_width),
        "seq",
        axis=0,
        tiled=False,
    )
    kv_flat = kv_all.reshape(slot_len, batches * 2 * model_width)
    scalars = jnp.concatenate(
        [slot_lengths.astype(jnp.int32), (lax.axis_index("seq") * row_count)[None].astype(jnp.int32)]
    )
    attended_rows, probabilities = attention_forward(scalars, queries, kv_flat, batches)
    attended_low = attended_rows.astype(jnp.bfloat16)
    residual = inputs + jnp.dot(attended_low, full_out, preferred_element_type=jnp.float32)
    second_low = layer_norm(residual, norm_gains[:, 1], norm_biases[:, 1]).astype(jnp.bfloat16)
    hidden = jnp.dot(second_low, full_up, preferred_element_type=jnp.float32)
    hidden_low = gelu_tanh(hidden).astype(jnp.bfloat16)
    block_out = residual + jnp.dot(hidden_low, full_down, preferred_element_type=jnp.float32)
    hidden_grad = jnp.einsum("rd,fd->rf", out_low, full_down, preferred_element_type=jnp.float32)
    _, gelu_pullback = jax.vjp(gelu_tanh, hidden)
    up_low = gelu_pullback(hidden_grad)[0].astype(jnp.bfloat16)
    second_grad = jnp.einsum("rf,df->rd", up_low, full_up, preferred_element_type=jnp.float32)
    _, second_pullback = jax.vjp(layer_norm, residual, norm_gains[:, 1], norm_biases[:, 1])
    residual_part, gain_two, bias_two = second_pullback(second_grad)
    residual_grad = out_grad + residual_part
    branch_low = residual_grad.astype(jnp.bfloat16)
    attended_grad = jnp.einsum(
        "rd,cd->rc", branch_low, full_out, preferred_element_type=jnp.float32
    ).astype(jnp.bfloat16)
    query_grad, kv_grad_flat = attention_backward(
        scalars, queries, kv_flat, attended_grad, attended_rows, probabilities, batches
    )
    kv_grad_own = lax.psum_scatter(kv_grad_flat, "seq", scatter_dimension=0, tiled=True)
    pairs = model_width // (STEP_HEADS * HEAD)
    kv_grad_own = kv_grad_own.reshape(row_count, batches, pairs, 2, STEP_HEADS * HEAD)
    kv_grad_own = jnp.transpose(kv_grad_own, (1, 0, 3, 2, 4)).reshape(
        all_rows, 2 * model_width
    )
    key_value_all = kv_grad_own.astype(jnp.float32)
    block_side, _ = lax.optimization_barrier((block_out, kv_grad_flat))
    combined = depth_weights[4] * block_side + history_part
    next_input = combined.astype(jnp.bfloat16).reshape(batches, 1, row_count, model_width)
    depth_terms = jnp.concatenate(
        [jnp.einsum("jrd,rd->j", earlier, grad_next), jnp.sum(block_side * grad_next)[None]]
    )
    grad_down = jnp.einsum("rf,rd->fd", hidden_low, out_low, preferred_element_type=jnp.float32)
    grad_up = jnp.einsum("rd,rf->df", second_low, up_low, preferred_element_type=jnp.float32)
    grad_outproj = jnp.einsum(
        "rc,rd->cd", attended_low, branch_low, preferred_element_type=jnp.float32
    )
    early_grads = jnp.concatenate(
        [
            jnp.zeros((model_width, 3 * model_width), jnp.float32),
            grad_outproj,
            grad_up,
            grad_down.reshape(model_width, ff_width),
        ],
        axis=1,
    ).astype(jnp.bfloat16)
    qkv_low = jnp.concatenate(
        [
            rotate(query_grad, cosine_part, -sine_part),
            rotate(key_value_all[:, :model_width], cosine_part, -sine_part),
            key_value_all[:, model_width:],
        ],
        axis=1,
    ).astype(jnp.bfloat16)
    grad_qkv = jnp.einsum("rd,rc->dc", first_low, qkv_low, preferred_element_type=jnp.float32)
    first_grad = jnp.einsum("rc,dc->rd", qkv_low, full_qkv, preferred_element_type=jnp.float32)
    _, first_pullback = jax.vjp(layer_norm, inputs, norm_gains[:, 0], norm_biases[:, 0])
    input_part, gain_one, bias_one = first_pullback(first_grad)
    grad_input = (residual_grad + input_part).astype(jnp.bfloat16)
    grad_input = grad_input.reshape(batches, 1, row_count, model_width)
    packed_grads = lax.dynamic_update_slice(early_grads, grad_qkv.astype(jnp.bfloat16), (0, 0))
    device_count = model_width // shard_rows
    row_major = Layout(major_to_minor=(0, 1, 2))
    grad_offsets = [0]
    for width in (3 * model_width, model_width, ff_width, ff_width):
        grad_offsets.append(grad_offsets[-1] + width)
    scattered = lax.psum_scatter(
        with_layout_constraint(
            packed_grads.reshape(device_count, shard_rows, grad_offsets[-1]), row_major
        ),
        ("seq", "fsdp"),
        scatter_dimension=0,
        tiled=False,
    )
    scattered = with_layout_constraint(scattered, Layout(major_to_minor=(0, 1)))
    scattered = scattered.astype(jnp.float32)
    full_pieces = [scattered[:, grad_offsets[i] : grad_offsets[i + 1]] for i in range(4)]
    small_sums = lax.psum(
        jnp.concatenate(
            [
                depth_terms,
                jnp.stack([gain_one, gain_two, bias_one, bias_two], axis=1).reshape(-1),
            ]
        ),
        ("seq", "fsdp"),
    )
    depth_total = small_sums[:5]
    device_index = lax.axis_index("seq") * lax.axis_size("fsdp") + lax.axis_index("fsdp")
    norm_owned = lax.dynamic_slice_in_dim(
        small_sums[5:].reshape(model_width, 4), device_index * shard_rows, shard_rows, 0
    )
    owned = [
        full_pieces[0],
        full_pieces[1],
        full_pieces[2],
        full_pieces[3].reshape(-1, model_width),
        norm_owned[:, :2],
        norm_owned[:, 2:],
    ]
    return (next_input, grad_input, grad_history, *owned, depth_total)


def solution(mesh):
    in_specs = (
        P(None, "fsdp", "seq", None),
        P(None, None, "fsdp", "seq", None),
        P(None, "fsdp", "seq", None),
        P(None, "fsdp"),
        P(("seq", "fsdp"), None),
        P(("seq", "fsdp"), None),
        P(("seq", "fsdp"), None),
        P(("seq", "fsdp"), None),
        P(("seq", "fsdp"), None),
        P(("seq", "fsdp"), None),
        P(),
    )
    out_specs = (
        P(None, "fsdp", "seq", None),
        P(None, "fsdp", "seq", None),
        P(None, None, "fsdp", "seq", None),
        P(("seq", "fsdp"), None),
        P(("seq", "fsdp"), None),
        P(("seq", "fsdp"), None),
        P(("seq", "fsdp"), None),
        P(("seq", "fsdp"), None),
        P(("seq", "fsdp"), None),
        P(),
    )
    return jax.shard_map(local, mesh=mesh, in_specs=in_specs, out_specs=out_specs, check_vma=False)
```

```python
from functools import partial
import math

import jax
import jax.numpy as jnp
from jax import lax
from jax.sharding import PartitionSpec as P
from jax.experimental.layout import Layout, with_layout_constraint
from jax.experimental import pallas as pl
from jax.experimental.pallas import tpu as pltpu

HEADS = 12
HEAD = 64


epsilon = 1e-05
masked_value = -1e30


def layer_norm(values, gain_vector, bias_vector):
    center = values - jnp.mean(values, axis=-1, keepdims=True)
    spread = jnp.mean(center * center, axis=-1, keepdims=True)
    return center * lax.rsqrt(spread + epsilon) * gain_vector + bias_vector


def rotary_tables(positions):
    half_width = HEAD // 2
    frequencies = 10000.0 ** (-jnp.arange(half_width, dtype=jnp.float32) / half_width)
    angles = positions.astype(jnp.float32)[:, None] * frequencies[None, :]
    return (jnp.cos(angles)[:, None, :], jnp.sin(angles)[:, None, :])


def rotate(values, cosine_part, sine_part):
    row_count = values.shape[0]
    shaped = values.reshape(row_count, HEADS, HEAD)
    half_width = HEAD // 2
    first_half = shaped[..., :half_width]
    second_half = shaped[..., half_width:]
    turned = jnp.concatenate(
        [
            first_half * cosine_part - second_half * sine_part,
            second_half * cosine_part + first_half * sine_part,
        ],
        axis=-1,
    )
    return turned.reshape(row_count, HEADS * HEAD)


def block_scores(queries3, keys3, query_pos, key_pos, length):
    scores = jnp.einsum(
        "rhd,khd->hrk", queries3, keys3, preferred_element_type=jnp.float32
    ) * HEAD ** (-0.5)
    allowed = (key_pos[None, :] <= query_pos[:, None]) & (key_pos[None, :] < length)
    return (scores, allowed[None])


def row_totals(queries3, keys3, query_pos, length, key_block):
    row_count = queries3.shape[0]

    def row_advance(state, block_index):
        running_top, running_sum = state
        first_key = block_index * key_block
        keys_part = lax.dynamic_slice_in_dim(keys3, first_key, key_block, 0)
        key_pos = first_key + jnp.arange(key_block, dtype=jnp.int32)
        scores, allowed = block_scores(queries3, keys_part, query_pos, key_pos, length)
        masked = jnp.where(allowed, scores, masked_value)
        new_top = jnp.maximum(running_top, jnp.max(masked, axis=-1))
        kept_terms = jnp.where(allowed, jnp.exp(masked - new_top[..., None]), 0.0)
        running_sum = running_sum * jnp.exp(running_top - new_top) + jnp.sum(kept_terms, axis=-1)
        return ((new_top, running_sum), None)

    initial = (
        jnp.full((HEADS, row_count), masked_value, jnp.float32),
        jnp.zeros((HEADS, row_count), jnp.float32),
    )
    (row_tops, row_sums), _ = lax.scan(
        row_advance, initial, jnp.arange(keys3.shape[0] // key_block, dtype=jnp.int32)
    )
    return row_tops + jnp.log(row_sums)


def attend(queries3, keys3, values3, query_pos, length, key_block, log_total):

    def attend_advance(running, block_index):
        first_key = block_index * key_block
        keys_part = lax.dynamic_slice_in_dim(keys3, first_key, key_block, 0)
        values_part = lax.dynamic_slice_in_dim(values3, first_key, key_block, 0)
        key_pos = first_key + jnp.arange(key_block, dtype=jnp.int32)
        scores, allowed = block_scores(queries3, keys_part, query_pos, key_pos, length)
        probabilities = jnp.where(allowed, jnp.exp(scores - log_total[..., None]), 0.0).astype(
            jnp.bfloat16
        )
        return (
            running
            + jnp.einsum(
                "hrk,khd->rhd", probabilities, values_part, preferred_element_type=jnp.float32
            ),
            None,
        )

    initial = jnp.zeros(queries3.shape, jnp.float32)
    result, _ = lax.scan(
        attend_advance, initial, jnp.arange(keys3.shape[0] // key_block, dtype=jnp.int32)
    )
    return result


def query_grads(
    queries3, grads3, keys3, values3, query_pos, length, key_block, log_total, row_delta
):

    def query_advance(running, block_index):
        first_key = block_index * key_block
        keys_part = lax.dynamic_slice_in_dim(keys3, first_key, key_block, 0)
        values_part = lax.dynamic_slice_in_dim(values3, first_key, key_block, 0)
        key_pos = first_key + jnp.arange(key_block, dtype=jnp.int32)
        scores, allowed = block_scores(queries3, keys_part, query_pos, key_pos, length)
        probabilities = jnp.where(allowed, jnp.exp(scores - log_total[..., None]), 0.0)
        prob_grad = jnp.einsum(
            "rhd,khd->hrk", grads3, values_part, preferred_element_type=jnp.float32
        )
        score_low = (probabilities * (prob_grad - row_delta[..., None])).astype(jnp.bfloat16)
        return (
            running
            + jnp.einsum("hrk,khd->rhd", score_low, keys_part, preferred_element_type=jnp.float32),
            None,
        )

    initial = jnp.zeros(queries3.shape, jnp.float32)
    result, _ = lax.scan(
        query_advance, initial, jnp.arange(keys3.shape[0] // key_block, dtype=jnp.int32)
    )
    return result * HEAD ** (-0.5)


def key_side(queries3, grads3, log_part, delta_part, query_pos, keys3, values3, key_pos, length):
    key_count = keys3.shape[0]
    scores, allowed = block_scores(queries3, keys3, query_pos, key_pos, length)
    probabilities = jnp.where(allowed, jnp.exp(scores - log_part[..., None]), 0.0)
    prob_grad = jnp.einsum("rhd,khd->hrk", grads3, values3, preferred_element_type=jnp.float32)
    score_low = (probabilities * (prob_grad - delta_part[..., None])).astype(jnp.bfloat16)
    value_grad = jnp.einsum(
        "hrk,rhd->khd",
        probabilities.astype(jnp.bfloat16),
        grads3,
        preferred_element_type=jnp.float32,
    )
    key_grad = jnp.einsum(
        "hrk,rhd->khd", score_low, queries3, preferred_element_type=jnp.float32
    ) * HEAD ** (-0.5)
    return jnp.concatenate(
        [key_grad.reshape(key_count, HEADS * HEAD), value_grad.reshape(key_count, HEADS * HEAD)],
        axis=1,
    )


def slot_attention(queries3, keys3, values3, query_pos, length):
    key_pos = jnp.arange(keys3.shape[0], dtype=jnp.int32)
    scores, allowed = block_scores(queries3, keys3, query_pos, key_pos, length)
    masked = jnp.where(allowed, scores, masked_value)
    top = jnp.max(masked, axis=-1)
    kept_terms = jnp.where(allowed, jnp.exp(masked - top[..., None]), 0.0)
    log_total = top + jnp.log(jnp.sum(kept_terms, axis=-1))
    probabilities = jnp.where(allowed, jnp.exp(scores - log_total[..., None]), 0.0)
    probabilities_low = probabilities.astype(jnp.bfloat16)
    attended = jnp.einsum(
        "hrk,khd->rhd", probabilities_low, values3, preferred_element_type=jnp.float32
    )
    return attended, probabilities, probabilities_low


def slot_attention_grads(queries3, keys3, values3, grads3, attended, probabilities, probabilities_low):
    prob_grad = jnp.einsum("rhd,khd->hrk", grads3, values3, preferred_element_type=jnp.float32)
    row_delta = jnp.einsum("rhd,rhd->hr", grads3.astype(jnp.float32), attended)
    score_low = (probabilities * (prob_grad - row_delta[..., None])).astype(jnp.bfloat16)
    query_grad = jnp.einsum(
        "hrk,khd->rhd", score_low, keys3, preferred_element_type=jnp.float32
    ) * HEAD ** (-0.5)
    key_grad = jnp.einsum(
        "hrk,rhd->khd", score_low, queries3, preferred_element_type=jnp.float32
    ) * HEAD ** (-0.5)
    value_grad = jnp.einsum(
        "hrk,rhd->khd", probabilities_low, grads3, preferred_element_type=jnp.float32
    )
    return query_grad, key_grad, value_grad


def _pair_masks(scalars_ref, micro, row_count, key_count):
    length = scalars_ref[micro]
    first_row = scalars_ref[scalars_ref.shape[0] - 1]
    query_pos = first_row + lax.broadcasted_iota(jnp.int32, (row_count, key_count), 0)
    key_pos = lax.broadcasted_iota(jnp.int32, (row_count, key_count), 1)
    return (key_pos <= query_pos) & (key_pos < length)


def _forward_kernel(scalars_ref, q_ref, k_ref, v_ref, out_ref, lse_ref):
    micro = pl.program_id(0)
    row_count = q_ref.shape[0]
    key_count = k_ref.shape[0] * k_ref.shape[2]
    allowed = _pair_masks(scalars_ref, micro, row_count, key_count)
    k_all = k_ref[...].reshape(key_count, k_ref.shape[3])
    v_all = v_ref[...].reshape(key_count, v_ref.shape[3])
    for half in range(2):
        lanes = slice(half * HEAD, (half + 1) * HEAD)
        q_head = q_ref[:, lanes]
        k_head = k_all[:, lanes]
        v_head = v_all[:, lanes]
        scores = lax.dot_general(
            q_head, k_head, (((1,), (1,)), ((), ())), preferred_element_type=jnp.float32
        ) * HEAD ** (-0.5)
        masked = jnp.where(allowed, scores, masked_value)
        top = jnp.max(masked, axis=1, keepdims=True)
        kept = jnp.where(allowed, jnp.exp(masked - top), 0.0)
        total = jnp.sum(kept, axis=1, keepdims=True)
        log_total = top + jnp.log(total)
        probabilities = kept * (1.0 / total)
        attended = jnp.dot(
            probabilities.astype(jnp.bfloat16), v_head, preferred_element_type=jnp.float32
        )
        out_ref[:, lanes] = attended
        lse_ref[:, lanes] = jnp.broadcast_to(log_total, (row_count, HEAD))


def _backward_kernel(
    scalars_ref, q_ref, k_ref, v_ref, do_ref, o_ref, lse_ref, dq_ref, kv_grad_ref
):
    micro = pl.program_id(0)
    row_count = q_ref.shape[0]
    key_count = k_ref.shape[0] * k_ref.shape[2]
    allowed = _pair_masks(scalars_ref, micro, row_count, key_count)
    k_all = k_ref[...].reshape(key_count, k_ref.shape[3])
    v_all = v_ref[...].reshape(key_count, v_ref.shape[3])
    for half in range(2):
        lanes = slice(half * HEAD, (half + 1) * HEAD)
        q_head = q_ref[:, lanes]
        k_head = k_all[:, lanes]
        v_head = v_all[:, lanes]
        grad_head = do_ref[:, lanes]
        scores = lax.dot_general(
            q_head, k_head, (((1,), (1,)), ((), ())), preferred_element_type=jnp.float32
        ) * HEAD ** (-0.5)
        log_total = lse_ref[:, half * HEAD : half * HEAD + 1]
        probabilities = jnp.where(allowed, jnp.exp(scores - log_total), 0.0)
        probabilities_low = probabilities.astype(jnp.bfloat16)
        prob_grad = lax.dot_general(
            grad_head, v_head, (((1,), (1,)), ((), ())), preferred_element_type=jnp.float32
        )
        row_delta = jnp.sum(
            grad_head.astype(jnp.float32) * o_ref[:, lanes], axis=1, keepdims=True
        )
        score_low = (probabilities * (prob_grad - row_delta)).astype(jnp.bfloat16)
        dq_ref[:, lanes] = jnp.dot(
            score_low, k_head, preferred_element_type=jnp.float32
        ) * HEAD ** (-0.5)
        key_grad = lax.dot_general(
            score_low, q_head, (((0,), (0,)), ((), ())), preferred_element_type=jnp.float32
        ) * HEAD ** (-0.5)
        value_grad = lax.dot_general(
            probabilities_low, grad_head, (((0,), (0,)), ((), ())),
            preferred_element_type=jnp.float32,
        )
        kv_grad_ref[:, lanes] = key_grad.astype(jnp.bfloat16)
        kv_grad_ref[:, 2 * HEAD + half * HEAD : 2 * HEAD + (half + 1) * HEAD] = value_grad.astype(
            jnp.bfloat16
        )


def attention_forward(scalars, queries, kv_flat, batches):
    all_rows, model_width = queries.shape
    row_count = all_rows // batches
    devices = kv_flat.shape[0]
    key_count = devices * row_count
    pairs = model_width // (2 * HEAD)
    row_spec = pl.BlockSpec((row_count, 2 * HEAD), lambda m, p, s: (m, p))
    key_spec = pl.BlockSpec((devices, 1, row_count, 2 * HEAD), lambda m, p, s: (0, m, 0, p))
    value_spec = pl.BlockSpec(
        (devices, 1, row_count, 2 * HEAD), lambda m, p, s: (0, m, 0, pairs + p)
    )
    return pl.pallas_call(
        _forward_kernel,
        grid_spec=pltpu.PrefetchScalarGridSpec(
            num_scalar_prefetch=1,
            grid=(batches, pairs),
            in_specs=[row_spec, key_spec, value_spec],
            out_specs=[row_spec, row_spec],
        ),
        out_shape=[
            jax.ShapeDtypeStruct((all_rows, model_width), jnp.float32),
            jax.ShapeDtypeStruct((all_rows, model_width), jnp.float32),
        ],
        name="attention_forward",
    )(scalars, queries, kv_flat, kv_flat)


def attention_backward(scalars, queries, kv_flat, grads, attended, log_totals, batches):
    all_rows, model_width = queries.shape
    row_count = all_rows // batches
    devices = kv_flat.shape[0]
    key_count = devices * row_count
    pairs = model_width // (2 * HEAD)
    row_spec = pl.BlockSpec((row_count, 2 * HEAD), lambda m, p, s: (m, p))
    key_spec = pl.BlockSpec((devices, 1, row_count, 2 * HEAD), lambda m, p, s: (0, m, 0, p))
    value_spec = pl.BlockSpec(
        (devices, 1, row_count, 2 * HEAD), lambda m, p, s: (0, m, 0, pairs + p)
    )
    grad_spec = pl.BlockSpec((key_count, 4 * HEAD), lambda m, p, s: (0, m * pairs + p))
    return pl.pallas_call(
        _backward_kernel,
        grid_spec=pltpu.PrefetchScalarGridSpec(
            num_scalar_prefetch=1,
            grid=(batches, pairs),
            in_specs=[row_spec, key_spec, value_spec, row_spec, row_spec, row_spec],
            out_specs=[row_spec, grad_spec],
        ),
        out_shape=[
            jax.ShapeDtypeStruct((all_rows, model_width), jnp.float32),
            jax.ShapeDtypeStruct((key_count, batches * 2 * model_width), jnp.bfloat16),
        ],
        name="attention_backward",
    )(scalars, queries, kv_flat, kv_flat, grads, attended, log_totals)


def local(
    layer_input,
    history,
    cotangent,
    lengths,
    w_qkv,
    w_out,
    w_up,
    w_down,
    ln_gains,
    ln_biases,
    depth_weights,
):
    batches = layer_input.shape[0]
    row_count = layer_input.shape[2]
    model_width = layer_input.shape[3]
    ff_width = w_up.shape[1]
    shard_rows = w_qkv.shape[0]
    all_rows = batches * row_count
    slot_len = row_count * lax.axis_size("seq")
    positions = lax.axis_index("seq") * row_count + jnp.arange(row_count, dtype=jnp.int32)
    cosine_part, sine_part = rotary_tables(jnp.tile(positions, batches))
    gelu_tanh = partial(jax.nn.gelu, approximate=True)
    lane_pad = 128 - 4
    widths = (3 * model_width, 2, 2, lane_pad, model_width, ff_width, ff_width)
    offsets = [0]
    for width in widths:
        offsets.append(offsets[-1] + width)

    def pieces(packed_rows):
        return [packed_rows[:, offsets[i] : offsets[i + 1]] for i in range(len(widths))]

    packed = jnp.concatenate(
        [
            w_qkv,
            ln_gains,
            ln_biases,
            jnp.zeros((shard_rows, lane_pad), w_qkv.dtype),
            w_out,
            w_up,
            w_down.reshape(shard_rows, ff_width),
        ],
        axis=1,
    )
    gathered = lax.all_gather(packed, ("seq", "fsdp"), axis=0, tiled=True)
    full_qkv, gain_rows, bias_rows, _, full_out, full_up, down_rows = pieces(gathered)
    full_down = down_rows.reshape(ff_width, model_width)
    norm_gains = gain_rows.astype(jnp.float32)
    norm_biases = bias_rows.astype(jnp.float32)

    slot_lengths = lengths[:, 0]
    inputs = layer_input[:, 0].reshape(all_rows, model_width).astype(jnp.float32)
    first_low = layer_norm(inputs, norm_gains[:, 0], norm_biases[:, 0]).astype(jnp.bfloat16)
    projected = jnp.dot(first_low, full_qkv, preferred_element_type=jnp.float32)
    queries = rotate(projected[:, :model_width], cosine_part, sine_part).astype(jnp.bfloat16)
    keys_own = rotate(
        projected[:, model_width : 2 * model_width], cosine_part, sine_part
    ).astype(jnp.bfloat16)
    values_own = projected[:, 2 * model_width :].astype(jnp.bfloat16)
    own_kv = jnp.concatenate([keys_own, values_own], axis=1).reshape(
        batches, row_count, 2 * model_width
    )
    earlier = history[:, :, 0].reshape(4, all_rows, model_width).astype(jnp.float32)
    usable = (positions[None, :] < slot_lengths[:, None]).reshape(all_rows, 1)
    grad_next = jnp.where(
        usable, cotangent[:, 0].reshape(all_rows, model_width).astype(jnp.float32), 0.0
    )
    history_part = (
        depth_weights[0] * earlier[0]
        + depth_weights[1] * earlier[1]
        + depth_weights[2] * earlier[2]
        + depth_weights[3] * earlier[3]
    )
    grad_history = (depth_weights[:4, None, None] * grad_next[None]).astype(jnp.bfloat16)
    grad_history = grad_history.reshape(4, batches, 1, row_count, model_width)
    out_grad = depth_weights[4] * grad_next
    out_low = out_grad.astype(jnp.bfloat16)

    kv_flat = lax.all_gather(own_kv, "seq", axis=0, tiled=False)
    scalars = jnp.concatenate(
        [slot_lengths.astype(jnp.int32), (lax.axis_index("seq") * row_count)[None].astype(jnp.int32)]
    )
    attended_rows, log_totals = attention_forward(scalars, queries, kv_flat, batches)
    attended_low = attended_rows.astype(jnp.bfloat16)
    residual = inputs + jnp.dot(attended_low, full_out, preferred_element_type=jnp.float32)
    second_low = layer_norm(residual, norm_gains[:, 1], norm_biases[:, 1]).astype(jnp.bfloat16)
    hidden = jnp.dot(second_low, full_up, preferred_element_type=jnp.float32)
    hidden_low = gelu_tanh(hidden).astype(jnp.bfloat16)
    block_out = residual + jnp.dot(hidden_low, full_down, preferred_element_type=jnp.float32)
    hidden_grad = jnp.einsum("rd,fd->rf", out_low, full_down, preferred_element_type=jnp.float32)
    _, gelu_pullback = jax.vjp(gelu_tanh, hidden)
    up_low = gelu_pullback(hidden_grad)[0].astype(jnp.bfloat16)
    second_grad = jnp.einsum("rf,df->rd", up_low, full_up, preferred_element_type=jnp.float32)
    _, second_pullback = jax.vjp(layer_norm, residual, norm_gains[:, 1], norm_biases[:, 1])
    residual_part, gain_two, bias_two = second_pullback(second_grad)
    residual_grad = out_grad + residual_part
    branch_low = residual_grad.astype(jnp.bfloat16)
    attended_grad = jnp.einsum(
        "rd,cd->rc", branch_low, full_out, preferred_element_type=jnp.float32
    ).astype(jnp.bfloat16)
    query_grad, kv_grad_flat = attention_backward(
        scalars, queries, kv_flat, attended_grad, attended_rows, log_totals, batches
    )
    kv_grad_own = lax.psum_scatter(kv_grad_flat, "seq", scatter_dimension=0, tiled=True)
    pairs = model_width // (2 * HEAD)
    kv_grad_own = kv_grad_own.reshape(row_count, batches, pairs, 2, 2 * HEAD)
    kv_grad_own = jnp.transpose(kv_grad_own, (1, 0, 3, 2, 4)).reshape(
        all_rows, 2 * model_width
    )
    key_value_all = kv_grad_own.astype(jnp.float32)
    block_side, _ = lax.optimization_barrier((block_out, kv_grad_flat))
    combined = depth_weights[4] * block_side + history_part
    next_input = combined.astype(jnp.bfloat16).reshape(batches, 1, row_count, model_width)
    depth_terms = jnp.concatenate(
        [jnp.sum(earlier * grad_next[None], axis=(1, 2)), jnp.sum(block_side * grad_next)[None]]
    )
    grad_down = jnp.einsum("rf,rd->fd", hidden_low, out_low, preferred_element_type=jnp.float32)
    grad_up = jnp.einsum("rd,rf->df", second_low, up_low, preferred_element_type=jnp.float32)
    grad_outproj = jnp.einsum(
        "rc,rd->cd", attended_low, branch_low, preferred_element_type=jnp.float32
    )
    early_grads = jnp.concatenate(
        [
            jnp.zeros((model_width, 3 * model_width), jnp.float32),
            grad_outproj,
            grad_up,
            grad_down.reshape(model_width, ff_width),
        ],
        axis=1,
    ).astype(jnp.bfloat16)
    qkv_low = jnp.concatenate(
        [
            rotate(query_grad, cosine_part, -sine_part),
            rotate(key_value_all[:, :model_width], cosine_part, -sine_part),
            key_value_all[:, model_width:],
        ],
        axis=1,
    ).astype(jnp.bfloat16)
    grad_qkv = jnp.einsum("rd,rc->dc", first_low, qkv_low, preferred_element_type=jnp.float32)
    first_grad = jnp.einsum("rc,dc->rd", qkv_low, full_qkv, preferred_element_type=jnp.float32)
    _, first_pullback = jax.vjp(layer_norm, inputs, norm_gains[:, 0], norm_biases[:, 0])
    input_part, gain_one, bias_one = first_pullback(first_grad)
    grad_input = (residual_grad + input_part).astype(jnp.bfloat16)
    grad_input = grad_input.reshape(batches, 1, row_count, model_width)
    packed_grads = lax.dynamic_update_slice(early_grads, grad_qkv.astype(jnp.bfloat16), (0, 0))
    device_count = model_width // shard_rows
    row_major = Layout(major_to_minor=(0, 1, 2))
    grad_offsets = [0]
    for width in (3 * model_width, model_width, ff_width, ff_width):
        grad_offsets.append(grad_offsets[-1] + width)
    scattered = lax.psum_scatter(
        with_layout_constraint(
            packed_grads.reshape(device_count, shard_rows, grad_offsets[-1]), row_major
        ),
        ("seq", "fsdp"),
        scatter_dimension=0,
        tiled=False,
    )
    scattered = with_layout_constraint(scattered, Layout(major_to_minor=(0, 1)))
    scattered = scattered.astype(jnp.float32)
    full_pieces = [scattered[:, grad_offsets[i] : grad_offsets[i + 1]] for i in range(4)]
    small_sums = lax.psum(
        jnp.concatenate(
            [
                depth_terms,
                jnp.stack([gain_one, gain_two, bias_one, bias_two], axis=1).reshape(-1),
            ]
        ),
        ("seq", "fsdp"),
    )
    depth_total = small_sums[:5]
    device_index = lax.axis_index("seq") * lax.axis_size("fsdp") + lax.axis_index("fsdp")
    norm_owned = lax.dynamic_slice_in_dim(
        small_sums[5:].reshape(model_width, 4), device_index * shard_rows, shard_rows, 0
    )
    owned = [
        full_pieces[0],
        full_pieces[1],
        full_pieces[2],
        full_pieces[3].reshape(-1, model_width),
        norm_owned[:, :2],
        norm_owned[:, 2:],
    ]
    return (next_input, grad_input, grad_history, *owned, depth_total)


def solution(mesh):
    in_specs = (
        P(None, "fsdp", "seq", None),
        P(None, None, "fsdp", "seq", None),
        P(None, "fsdp", "seq", None),
        P(None, "fsdp"),
        P(("seq", "fsdp"), None),
        P(("seq", "fsdp"), None),
        P(("seq", "fsdp"), None),
        P(("seq", "fsdp"), None),
        P(("seq", "fsdp"), None),
        P(("seq", "fsdp"), None),
        P(),
    )
    out_specs = (
        P(None, "fsdp", "seq", None),
        P(None, "fsdp", "seq", None),
        P(None, None, "fsdp", "seq", None),
        P(("seq", "fsdp"), None),
        P(("seq", "fsdp"), None),
        P(("seq", "fsdp"), None),
        P(("seq", "fsdp"), None),
        P(("seq", "fsdp"), None),
        P(("seq", "fsdp"), None),
        P(),
    )
    return jax.shard_map(local, mesh=mesh, in_specs=in_specs, out_specs=out_specs, check_vma=False)
```

```python
from functools import partial
import math

import jax
import jax.numpy as jnp
from jax import lax
from jax.sharding import PartitionSpec as P
from jax.experimental.layout import Layout, with_layout_constraint
from jax.experimental import pallas as pl
from jax.experimental.pallas import tpu as pltpu

HEADS = 12
HEAD = 64


epsilon = 1e-05
masked_value = -1e30


def layer_norm(values, gain_vector, bias_vector):
    center = values - jnp.mean(values, axis=-1, keepdims=True)
    spread = jnp.mean(center * center, axis=-1, keepdims=True)
    return center * lax.rsqrt(spread + epsilon) * gain_vector + bias_vector


def rotary_tables(positions):
    half_width = HEAD // 2
    frequencies = 10000.0 ** (-jnp.arange(half_width, dtype=jnp.float32) / half_width)
    angles = positions.astype(jnp.float32)[:, None] * frequencies[None, :]
    return (jnp.cos(angles)[:, None, :], jnp.sin(angles)[:, None, :])


def rotate(values, cosine_part, sine_part):
    row_count = values.shape[0]
    shaped = values.reshape(row_count, HEADS, HEAD)
    half_width = HEAD // 2
    first_half = shaped[..., :half_width]
    second_half = shaped[..., half_width:]
    turned = jnp.concatenate(
        [
            first_half * cosine_part - second_half * sine_part,
            second_half * cosine_part + first_half * sine_part,
        ],
        axis=-1,
    )
    return turned.reshape(row_count, HEADS * HEAD)


def block_scores(queries3, keys3, query_pos, key_pos, length):
    scores = jnp.einsum(
        "rhd,khd->hrk", queries3, keys3, preferred_element_type=jnp.float32
    ) * HEAD ** (-0.5)
    allowed = (key_pos[None, :] <= query_pos[:, None]) & (key_pos[None, :] < length)
    return (scores, allowed[None])


def row_totals(queries3, keys3, query_pos, length, key_block):
    row_count = queries3.shape[0]

    def row_advance(state, block_index):
        running_top, running_sum = state
        first_key = block_index * key_block
        keys_part = lax.dynamic_slice_in_dim(keys3, first_key, key_block, 0)
        key_pos = first_key + jnp.arange(key_block, dtype=jnp.int32)
        scores, allowed = block_scores(queries3, keys_part, query_pos, key_pos, length)
        masked = jnp.where(allowed, scores, masked_value)
        new_top = jnp.maximum(running_top, jnp.max(masked, axis=-1))
        kept_terms = jnp.where(allowed, jnp.exp(masked - new_top[..., None]), 0.0)
        running_sum = running_sum * jnp.exp(running_top - new_top) + jnp.sum(kept_terms, axis=-1)
        return ((new_top, running_sum), None)

    initial = (
        jnp.full((HEADS, row_count), masked_value, jnp.float32),
        jnp.zeros((HEADS, row_count), jnp.float32),
    )
    (row_tops, row_sums), _ = lax.scan(
        row_advance, initial, jnp.arange(keys3.shape[0] // key_block, dtype=jnp.int32)
    )
    return row_tops + jnp.log(row_sums)


def attend(queries3, keys3, values3, query_pos, length, key_block, log_total):

    def attend_advance(running, block_index):
        first_key = block_index * key_block
        keys_part = lax.dynamic_slice_in_dim(keys3, first_key, key_block, 0)
        values_part = lax.dynamic_slice_in_dim(values3, first_key, key_block, 0)
        key_pos = first_key + jnp.arange(key_block, dtype=jnp.int32)
        scores, allowed = block_scores(queries3, keys_part, query_pos, key_pos, length)
        probabilities = jnp.where(allowed, jnp.exp(scores - log_total[..., None]), 0.0).astype(
            jnp.bfloat16
        )
        return (
            running
            + jnp.einsum(
                "hrk,khd->rhd", probabilities, values_part, preferred_element_type=jnp.float32
            ),
            None,
        )

    initial = jnp.zeros(queries3.shape, jnp.float32)
    result, _ = lax.scan(
        attend_advance, initial, jnp.arange(keys3.shape[0] // key_block, dtype=jnp.int32)
    )
    return result


def query_grads(
    queries3, grads3, keys3, values3, query_pos, length, key_block, log_total, row_delta
):

    def query_advance(running, block_index):
        first_key = block_index * key_block
        keys_part = lax.dynamic_slice_in_dim(keys3, first_key, key_block, 0)
        values_part = lax.dynamic_slice_in_dim(values3, first_key, key_block, 0)
        key_pos = first_key + jnp.arange(key_block, dtype=jnp.int32)
        scores, allowed = block_scores(queries3, keys_part, query_pos, key_pos, length)
        probabilities = jnp.where(allowed, jnp.exp(scores - log_total[..., None]), 0.0)
        prob_grad = jnp.einsum(
            "rhd,khd->hrk", grads3, values_part, preferred_element_type=jnp.float32
        )
        score_low = (probabilities * (prob_grad - row_delta[..., None])).astype(jnp.bfloat16)
        return (
            running
            + jnp.einsum("hrk,khd->rhd", score_low, keys_part, preferred_element_type=jnp.float32),
            None,
        )

    initial = jnp.zeros(queries3.shape, jnp.float32)
    result, _ = lax.scan(
        query_advance, initial, jnp.arange(keys3.shape[0] // key_block, dtype=jnp.int32)
    )
    return result * HEAD ** (-0.5)


def key_side(queries3, grads3, log_part, delta_part, query_pos, keys3, values3, key_pos, length):
    key_count = keys3.shape[0]
    scores, allowed = block_scores(queries3, keys3, query_pos, key_pos, length)
    probabilities = jnp.where(allowed, jnp.exp(scores - log_part[..., None]), 0.0)
    prob_grad = jnp.einsum("rhd,khd->hrk", grads3, values3, preferred_element_type=jnp.float32)
    score_low = (probabilities * (prob_grad - delta_part[..., None])).astype(jnp.bfloat16)
    value_grad = jnp.einsum(
        "hrk,rhd->khd",
        probabilities.astype(jnp.bfloat16),
        grads3,
        preferred_element_type=jnp.float32,
    )
    key_grad = jnp.einsum(
        "hrk,rhd->khd", score_low, queries3, preferred_element_type=jnp.float32
    ) * HEAD ** (-0.5)
    return jnp.concatenate(
        [key_grad.reshape(key_count, HEADS * HEAD), value_grad.reshape(key_count, HEADS * HEAD)],
        axis=1,
    )


def slot_attention(queries3, keys3, values3, query_pos, length):
    key_pos = jnp.arange(keys3.shape[0], dtype=jnp.int32)
    scores, allowed = block_scores(queries3, keys3, query_pos, key_pos, length)
    masked = jnp.where(allowed, scores, masked_value)
    top = jnp.max(masked, axis=-1)
    kept_terms = jnp.where(allowed, jnp.exp(masked - top[..., None]), 0.0)
    log_total = top + jnp.log(jnp.sum(kept_terms, axis=-1))
    probabilities = jnp.where(allowed, jnp.exp(scores - log_total[..., None]), 0.0)
    probabilities_low = probabilities.astype(jnp.bfloat16)
    attended = jnp.einsum(
        "hrk,khd->rhd", probabilities_low, values3, preferred_element_type=jnp.float32
    )
    return attended, probabilities, probabilities_low


def slot_attention_grads(queries3, keys3, values3, grads3, attended, probabilities, probabilities_low):
    prob_grad = jnp.einsum("rhd,khd->hrk", grads3, values3, preferred_element_type=jnp.float32)
    row_delta = jnp.einsum("rhd,rhd->hr", grads3.astype(jnp.float32), attended)
    score_low = (probabilities * (prob_grad - row_delta[..., None])).astype(jnp.bfloat16)
    query_grad = jnp.einsum(
        "hrk,khd->rhd", score_low, keys3, preferred_element_type=jnp.float32
    ) * HEAD ** (-0.5)
    key_grad = jnp.einsum(
        "hrk,rhd->khd", score_low, queries3, preferred_element_type=jnp.float32
    ) * HEAD ** (-0.5)
    value_grad = jnp.einsum(
        "hrk,rhd->khd", probabilities_low, grads3, preferred_element_type=jnp.float32
    )
    return query_grad, key_grad, value_grad


def _pair_masks(scalars_ref, micro, row_count, key_count):
    length = scalars_ref[micro]
    first_row = scalars_ref[scalars_ref.shape[0] - 1]
    query_pos = first_row + lax.broadcasted_iota(jnp.int32, (row_count, key_count), 0)
    key_pos = lax.broadcasted_iota(jnp.int32, (row_count, key_count), 1)
    return (key_pos <= query_pos) & (key_pos < length)


def _forward_kernel(scalars_ref, q_ref, k_ref, v_ref, out_ref, lse_ref):
    micro = pl.program_id(0)
    row_count = q_ref.shape[0]
    key_count = k_ref.shape[0] * k_ref.shape[2]
    allowed = _pair_masks(scalars_ref, micro, row_count, key_count)
    k_all = k_ref[...].reshape(key_count, k_ref.shape[3])
    v_all = v_ref[...].reshape(key_count, v_ref.shape[3])
    for half in range(2):
        lanes = slice(half * HEAD, (half + 1) * HEAD)
        q_head = q_ref[:, lanes]
        k_head = k_all[:, lanes]
        v_head = v_all[:, lanes]
        scores = lax.dot_general(
            q_head, k_head, (((1,), (1,)), ((), ())), preferred_element_type=jnp.float32
        ) * HEAD ** (-0.5)
        masked = jnp.where(allowed, scores, masked_value)
        top = jnp.max(masked, axis=1, keepdims=True)
        kept = jnp.where(allowed, jnp.exp(masked - top), 0.0)
        total = jnp.sum(kept, axis=1, keepdims=True)
        log_total = top + jnp.log(total)
        probabilities = kept * (1.0 / total)
        attended = jnp.dot(
            probabilities.astype(jnp.bfloat16), v_head, preferred_element_type=jnp.float32
        )
        out_ref[:, lanes] = attended
        lse_ref[:, lanes] = jnp.broadcast_to(log_total, (row_count, HEAD))


def _backward_kernel(
    scalars_ref, q_ref, k_ref, v_ref, do_ref, o_ref, lse_ref, dq_ref, kv_grad_ref
):
    micro = pl.program_id(0)
    row_count = q_ref.shape[0]
    key_count = k_ref.shape[0] * k_ref.shape[2]
    allowed = _pair_masks(scalars_ref, micro, row_count, key_count)
    k_all = k_ref[...].reshape(key_count, k_ref.shape[3])
    v_all = v_ref[...].reshape(key_count, v_ref.shape[3])
    for half in range(2):
        lanes = slice(half * HEAD, (half + 1) * HEAD)
        q_head = q_ref[:, lanes]
        k_head = k_all[:, lanes]
        v_head = v_all[:, lanes]
        grad_head = do_ref[:, lanes]
        scores = lax.dot_general(
            q_head, k_head, (((1,), (1,)), ((), ())), preferred_element_type=jnp.float32
        ) * HEAD ** (-0.5)
        log_total = lse_ref[:, half * HEAD : half * HEAD + 1]
        probabilities = jnp.where(allowed, jnp.exp(scores - log_total), 0.0)
        probabilities_low = probabilities.astype(jnp.bfloat16)
        prob_grad = lax.dot_general(
            grad_head, v_head, (((1,), (1,)), ((), ())), preferred_element_type=jnp.float32
        )
        row_delta = jnp.sum(
            grad_head.astype(jnp.float32) * o_ref[:, lanes], axis=1, keepdims=True
        )
        score_low = (probabilities * (prob_grad - row_delta)).astype(jnp.bfloat16)
        dq_ref[:, lanes] = jnp.dot(
            score_low, k_head, preferred_element_type=jnp.float32
        ) * HEAD ** (-0.5)
        key_grad = lax.dot_general(
            score_low, q_head, (((0,), (0,)), ((), ())), preferred_element_type=jnp.float32
        ) * HEAD ** (-0.5)
        value_grad = lax.dot_general(
            probabilities_low, grad_head, (((0,), (0,)), ((), ())),
            preferred_element_type=jnp.float32,
        )
        kv_grad_ref[:, lanes] = key_grad.astype(jnp.bfloat16)
        kv_grad_ref[:, 2 * HEAD + half * HEAD : 2 * HEAD + (half + 1) * HEAD] = value_grad.astype(
            jnp.bfloat16
        )


def attention_forward(scalars, queries, kv_flat, batches):
    all_rows, model_width = queries.shape
    row_count = all_rows // batches
    devices = kv_flat.shape[0]
    key_count = devices * row_count
    pairs = model_width // (2 * HEAD)
    row_spec = pl.BlockSpec((row_count, 2 * HEAD), lambda m, p, s: (m, p))
    key_spec = pl.BlockSpec((devices, 1, row_count, 2 * HEAD), lambda m, p, s: (0, m, 0, p))
    value_spec = pl.BlockSpec(
        (devices, 1, row_count, 2 * HEAD), lambda m, p, s: (0, m, 0, pairs + p)
    )
    return pl.pallas_call(
        _forward_kernel,
        grid_spec=pltpu.PrefetchScalarGridSpec(
            num_scalar_prefetch=1,
            grid=(batches, pairs),
            in_specs=[row_spec, key_spec, value_spec],
            out_specs=[row_spec, row_spec],
        ),
        out_shape=[
            jax.ShapeDtypeStruct((all_rows, model_width), jnp.float32),
            jax.ShapeDtypeStruct((all_rows, model_width), jnp.float32),
        ],
        name="attention_forward",
    )(scalars, queries, kv_flat, kv_flat)


def attention_backward(scalars, queries, kv_flat, grads, attended, log_totals, batches):
    all_rows, model_width = queries.shape
    row_count = all_rows // batches
    devices = kv_flat.shape[0]
    key_count = devices * row_count
    pairs = model_width // (2 * HEAD)
    row_spec = pl.BlockSpec((row_count, 2 * HEAD), lambda m, p, s: (m, p))
    key_spec = pl.BlockSpec((devices, 1, row_count, 2 * HEAD), lambda m, p, s: (0, m, 0, p))
    value_spec = pl.BlockSpec(
        (devices, 1, row_count, 2 * HEAD), lambda m, p, s: (0, m, 0, pairs + p)
    )
    grad_spec = pl.BlockSpec((key_count, 4 * HEAD), lambda m, p, s: (0, m * pairs + p))
    return pl.pallas_call(
        _backward_kernel,
        grid_spec=pltpu.PrefetchScalarGridSpec(
            num_scalar_prefetch=1,
            grid=(batches, pairs),
            in_specs=[row_spec, key_spec, value_spec, row_spec, row_spec, row_spec],
            out_specs=[row_spec, grad_spec],
        ),
        out_shape=[
            jax.ShapeDtypeStruct((all_rows, model_width), jnp.float32),
            jax.ShapeDtypeStruct((key_count, batches * 2 * model_width), jnp.bfloat16),
        ],
        name="attention_backward",
    )(scalars, queries, kv_flat, kv_flat, grads, attended, log_totals)


def local(
    layer_input,
    history,
    cotangent,
    lengths,
    w_qkv,
    w_out,
    w_up,
    w_down,
    ln_gains,
    ln_biases,
    depth_weights,
):
    batches = layer_input.shape[0]
    row_count = layer_input.shape[2]
    model_width = layer_input.shape[3]
    ff_width = w_up.shape[1]
    shard_rows = w_qkv.shape[0]
    all_rows = batches * row_count
    slot_len = row_count * lax.axis_size("seq")
    positions = lax.axis_index("seq") * row_count + jnp.arange(row_count, dtype=jnp.int32)
    cosine_part, sine_part = rotary_tables(jnp.tile(positions, batches))
    gelu_tanh = partial(jax.nn.gelu, approximate=True)
    lane_pad = 128 - 4
    widths = (3 * model_width, 2, 2, lane_pad, model_width, ff_width, ff_width)
    offsets = [0]
    for width in widths:
        offsets.append(offsets[-1] + width)

    def pieces(packed_rows):
        return [packed_rows[:, offsets[i] : offsets[i + 1]] for i in range(len(widths))]

    packed = jnp.concatenate(
        [
            w_qkv,
            ln_gains,
            ln_biases,
            jnp.zeros((shard_rows, lane_pad), w_qkv.dtype),
            w_out,
            w_up,
            w_down.reshape(shard_rows, ff_width),
        ],
        axis=1,
    )
    gathered = lax.all_gather(packed, ("seq", "fsdp"), axis=0, tiled=True)
    full_qkv, gain_rows, bias_rows, _, full_out, full_up, down_rows = pieces(gathered)
    full_down = down_rows.reshape(ff_width, model_width)
    norm_gains = gain_rows.astype(jnp.float32)
    norm_biases = bias_rows.astype(jnp.float32)

    slot_lengths = lengths[:, 0]
    inputs = layer_input[:, 0].reshape(all_rows, model_width).astype(jnp.float32)
    first_low = layer_norm(inputs, norm_gains[:, 0], norm_biases[:, 0]).astype(jnp.bfloat16)
    projected = jnp.dot(first_low, full_qkv, preferred_element_type=jnp.float32)
    queries = rotate(projected[:, :model_width], cosine_part, sine_part).astype(jnp.bfloat16)
    keys_own = rotate(
        projected[:, model_width : 2 * model_width], cosine_part, sine_part
    ).astype(jnp.bfloat16)
    values_own = projected[:, 2 * model_width :].astype(jnp.bfloat16)
    own_kv = jnp.concatenate([keys_own, values_own], axis=1).reshape(
        batches, row_count, 2 * model_width
    )
    earlier = history[:, :, 0].reshape(4, all_rows, model_width).astype(jnp.float32)
    usable = (positions[None, :] < slot_lengths[:, None]).reshape(all_rows, 1)
    grad_next = jnp.where(
        usable, cotangent[:, 0].reshape(all_rows, model_width).astype(jnp.float32), 0.0
    )
    history_part = (
        depth_weights[0] * earlier[0]
        + depth_weights[1] * earlier[1]
        + depth_weights[2] * earlier[2]
        + depth_weights[3] * earlier[3]
    )
    grad_history = (depth_weights[:4, None, None] * grad_next[None]).astype(jnp.bfloat16)
    grad_history = grad_history.reshape(4, batches, 1, row_count, model_width)
    out_grad = depth_weights[4] * grad_next
    out_low = out_grad.astype(jnp.bfloat16)

    kv_flat = lax.all_gather(own_kv, "seq", axis=0, tiled=False)
    scalars = jnp.concatenate(
        [slot_lengths.astype(jnp.int32), (lax.axis_index("seq") * row_count)[None].astype(jnp.int32)]
    )
    attended_rows, log_totals = attention_forward(scalars, queries, kv_flat, batches)
    attended_low = attended_rows.astype(jnp.bfloat16)
    residual = inputs + jnp.dot(attended_low, full_out, preferred_element_type=jnp.float32)
    second_low = layer_norm(residual, norm_gains[:, 1], norm_biases[:, 1]).astype(jnp.bfloat16)
    hidden = jnp.dot(second_low, full_up, preferred_element_type=jnp.float32)
    hidden_low = gelu_tanh(hidden).astype(jnp.bfloat16)
    block_out = residual + jnp.dot(hidden_low, full_down, preferred_element_type=jnp.float32)
    hidden_grad = jnp.einsum("rd,fd->rf", out_low, full_down, preferred_element_type=jnp.float32)
    _, gelu_pullback = jax.vjp(gelu_tanh, hidden)
    up_low = gelu_pullback(hidden_grad)[0].astype(jnp.bfloat16)
    second_grad = jnp.einsum("rf,df->rd", up_low, full_up, preferred_element_type=jnp.float32)
    _, second_pullback = jax.vjp(layer_norm, residual, norm_gains[:, 1], norm_biases[:, 1])
    residual_part, gain_two, bias_two = second_pullback(second_grad)
    residual_grad = out_grad + residual_part
    branch_low = residual_grad.astype(jnp.bfloat16)
    attended_grad = jnp.einsum(
        "rd,cd->rc", branch_low, full_out, preferred_element_type=jnp.float32
    ).astype(jnp.bfloat16)
    query_grad, kv_grad_flat = attention_backward(
        scalars, queries, kv_flat, attended_grad, attended_rows, log_totals, batches
    )
    kv_grad_own = lax.psum_scatter(kv_grad_flat, "seq", scatter_dimension=0, tiled=True)
    block_side, _ = lax.optimization_barrier((block_out, kv_grad_flat))
    combined = depth_weights[4] * block_side + history_part
    next_input = combined.astype(jnp.bfloat16).reshape(batches, 1, row_count, model_width)
    depth_terms = jnp.concatenate(
        [jnp.sum(earlier * grad_next[None], axis=(1, 2)), jnp.sum(block_side * grad_next)[None]]
    )
    grad_down = jnp.einsum("rf,rd->fd", hidden_low, out_low, preferred_element_type=jnp.float32)
    grad_up = jnp.einsum("rd,rf->df", second_low, up_low, preferred_element_type=jnp.float32)
    grad_outproj = jnp.einsum(
        "rc,rd->cd", attended_low, branch_low, preferred_element_type=jnp.float32
    )
    early_grads = jnp.concatenate(
        [
            jnp.zeros((model_width, 3 * model_width), jnp.float32),
            grad_outproj,
            grad_up,
            grad_down.reshape(model_width, ff_width),
        ],
        axis=1,
    ).astype(jnp.bfloat16)
    kv_grad_own, early_grads = lax.optimization_barrier((kv_grad_own, early_grads))
    pairs = model_width // (2 * HEAD)
    kv_grad_own = kv_grad_own.reshape(row_count, batches, pairs, 2, 2 * HEAD)
    kv_grad_own = jnp.transpose(kv_grad_own, (1, 0, 3, 2, 4)).reshape(
        all_rows, 2 * model_width
    )
    key_value_all = kv_grad_own.astype(jnp.float32)
    qkv_low = jnp.concatenate(
        [
            rotate(query_grad, cosine_part, -sine_part),
            rotate(key_value_all[:, :model_width], cosine_part, -sine_part),
            key_value_all[:, model_width:],
        ],
        axis=1,
    ).astype(jnp.bfloat16)
    grad_qkv = jnp.einsum("rd,rc->dc", first_low, qkv_low, preferred_element_type=jnp.float32)
    first_grad = jnp.einsum("rc,dc->rd", qkv_low, full_qkv, preferred_element_type=jnp.float32)
    _, first_pullback = jax.vjp(layer_norm, inputs, norm_gains[:, 0], norm_biases[:, 0])
    input_part, gain_one, bias_one = first_pullback(first_grad)
    grad_input = (residual_grad + input_part).astype(jnp.bfloat16)
    grad_input = grad_input.reshape(batches, 1, row_count, model_width)
    packed_grads = lax.dynamic_update_slice(early_grads, grad_qkv.astype(jnp.bfloat16), (0, 0))
    device_count = model_width // shard_rows
    row_major = Layout(major_to_minor=(0, 1, 2))
    grad_offsets = [0]
    for width in (3 * model_width, model_width, ff_width, ff_width):
        grad_offsets.append(grad_offsets[-1] + width)
    scattered = lax.psum_scatter(
        with_layout_constraint(
            packed_grads.reshape(device_count, shard_rows, grad_offsets[-1]), row_major
        ),
        ("seq", "fsdp"),
        scatter_dimension=0,
        tiled=False,
    )
    scattered = with_layout_constraint(scattered, Layout(major_to_minor=(0, 1)))
    scattered = scattered.astype(jnp.float32)
    full_pieces = [scattered[:, grad_offsets[i] : grad_offsets[i + 1]] for i in range(4)]
    small_sums = lax.psum(
        jnp.concatenate(
            [
                depth_terms,
                jnp.stack([gain_one, gain_two, bias_one, bias_two], axis=1).reshape(-1),
            ]
        ),
        ("seq", "fsdp"),
    )
    depth_total = small_sums[:5]
    device_index = lax.axis_index("seq") * lax.axis_size("fsdp") + lax.axis_index("fsdp")
    norm_owned = lax.dynamic_slice_in_dim(
        small_sums[5:].reshape(model_width, 4), device_index * shard_rows, shard_rows, 0
    )
    owned = [
        full_pieces[0],
        full_pieces[1],
        full_pieces[2],
        full_pieces[3].reshape(-1, model_width),
        norm_owned[:, :2],
        norm_owned[:, 2:],
    ]
    return (next_input, grad_input, grad_history, *owned, depth_total)


def solution(mesh):
    in_specs = (
        P(None, "fsdp", "seq", None),
        P(None, None, "fsdp", "seq", None),
        P(None, "fsdp", "seq", None),
        P(None, "fsdp"),
        P(("seq", "fsdp"), None),
        P(("seq", "fsdp"), None),
        P(("seq", "fsdp"), None),
        P(("seq", "fsdp"), None),
        P(("seq", "fsdp"), None),
        P(("seq", "fsdp"), None),
        P(),
    )
    out_specs = (
        P(None, "fsdp", "seq", None),
        P(None, "fsdp", "seq", None),
        P(None, None, "fsdp", "seq", None),
        P(("seq", "fsdp"), None),
        P(("seq", "fsdp"), None),
        P(("seq", "fsdp"), None),
        P(("seq", "fsdp"), None),
        P(("seq", "fsdp"), None),
        P(("seq", "fsdp"), None),
        P(),
    )
    return jax.shard_map(local, mesh=mesh, in_specs=in_specs, out_specs=out_specs, check_vma=False)
```

```python
from functools import partial
import math

import jax
import jax.numpy as jnp
from jax import lax
from jax.sharding import PartitionSpec as P
from jax.experimental.layout import Layout, with_layout_constraint
from jax.experimental import pallas as pl
from jax.experimental.pallas import tpu as pltpu

HEADS = 12
HEAD = 64


epsilon = 1e-05
masked_value = -1e30


def layer_norm(values, gain_vector, bias_vector):
    center = values - jnp.mean(values, axis=-1, keepdims=True)
    spread = jnp.mean(center * center, axis=-1, keepdims=True)
    return center * lax.rsqrt(spread + epsilon) * gain_vector + bias_vector


def rotary_tables(positions):
    half_width = HEAD // 2
    frequencies = 10000.0 ** (-jnp.arange(half_width, dtype=jnp.float32) / half_width)
    angles = positions.astype(jnp.float32)[:, None] * frequencies[None, :]
    return (jnp.cos(angles)[:, None, :], jnp.sin(angles)[:, None, :])


def rotate(values, cosine_part, sine_part):
    row_count = values.shape[0]
    shaped = values.reshape(row_count, HEADS, HEAD)
    half_width = HEAD // 2
    first_half = shaped[..., :half_width]
    second_half = shaped[..., half_width:]
    turned = jnp.concatenate(
        [
            first_half * cosine_part - second_half * sine_part,
            second_half * cosine_part + first_half * sine_part,
        ],
        axis=-1,
    )
    return turned.reshape(row_count, HEADS * HEAD)


def block_scores(queries3, keys3, query_pos, key_pos, length):
    scores = jnp.einsum(
        "rhd,khd->hrk", queries3, keys3, preferred_element_type=jnp.float32
    ) * HEAD ** (-0.5)
    allowed = (key_pos[None, :] <= query_pos[:, None]) & (key_pos[None, :] < length)
    return (scores, allowed[None])


def row_totals(queries3, keys3, query_pos, length, key_block):
    row_count = queries3.shape[0]

    def row_advance(state, block_index):
        running_top, running_sum = state
        first_key = block_index * key_block
        keys_part = lax.dynamic_slice_in_dim(keys3, first_key, key_block, 0)
        key_pos = first_key + jnp.arange(key_block, dtype=jnp.int32)
        scores, allowed = block_scores(queries3, keys_part, query_pos, key_pos, length)
        masked = jnp.where(allowed, scores, masked_value)
        new_top = jnp.maximum(running_top, jnp.max(masked, axis=-1))
        kept_terms = jnp.where(allowed, jnp.exp(masked - new_top[..., None]), 0.0)
        running_sum = running_sum * jnp.exp(running_top - new_top) + jnp.sum(kept_terms, axis=-1)
        return ((new_top, running_sum), None)

    initial = (
        jnp.full((HEADS, row_count), masked_value, jnp.float32),
        jnp.zeros((HEADS, row_count), jnp.float32),
    )
    (row_tops, row_sums), _ = lax.scan(
        row_advance, initial, jnp.arange(keys3.shape[0] // key_block, dtype=jnp.int32)
    )
    return row_tops + jnp.log(row_sums)


def attend(queries3, keys3, values3, query_pos, length, key_block, log_total):

    def attend_advance(running, block_index):
        first_key = block_index * key_block
        keys_part = lax.dynamic_slice_in_dim(keys3, first_key, key_block, 0)
        values_part = lax.dynamic_slice_in_dim(values3, first_key, key_block, 0)
        key_pos = first_key + jnp.arange(key_block, dtype=jnp.int32)
        scores, allowed = block_scores(queries3, keys_part, query_pos, key_pos, length)
        probabilities = jnp.where(allowed, jnp.exp(scores - log_total[..., None]), 0.0).astype(
            jnp.bfloat16
        )
        return (
            running
            + jnp.einsum(
                "hrk,khd->rhd", probabilities, values_part, preferred_element_type=jnp.float32
            ),
            None,
        )

    initial = jnp.zeros(queries3.shape, jnp.float32)
    result, _ = lax.scan(
        attend_advance, initial, jnp.arange(keys3.shape[0] // key_block, dtype=jnp.int32)
    )
    return result


def query_grads(
    queries3, grads3, keys3, values3, query_pos, length, key_block, log_total, row_delta
):

    def query_advance(running, block_index):
        first_key = block_index * key_block
        keys_part = lax.dynamic_slice_in_dim(keys3, first_key, key_block, 0)
        values_part = lax.dynamic_slice_in_dim(values3, first_key, key_block, 0)
        key_pos = first_key + jnp.arange(key_block, dtype=jnp.int32)
        scores, allowed = block_scores(queries3, keys_part, query_pos, key_pos, length)
        probabilities = jnp.where(allowed, jnp.exp(scores - log_total[..., None]), 0.0)
        prob_grad = jnp.einsum(
            "rhd,khd->hrk", grads3, values_part, preferred_element_type=jnp.float32
        )
        score_low = (probabilities * (prob_grad - row_delta[..., None])).astype(jnp.bfloat16)
        return (
            running
            + jnp.einsum("hrk,khd->rhd", score_low, keys_part, preferred_element_type=jnp.float32),
            None,
        )

    initial = jnp.zeros(queries3.shape, jnp.float32)
    result, _ = lax.scan(
        query_advance, initial, jnp.arange(keys3.shape[0] // key_block, dtype=jnp.int32)
    )
    return result * HEAD ** (-0.5)


def key_side(queries3, grads3, log_part, delta_part, query_pos, keys3, values3, key_pos, length):
    key_count = keys3.shape[0]
    scores, allowed = block_scores(queries3, keys3, query_pos, key_pos, length)
    probabilities = jnp.where(allowed, jnp.exp(scores - log_part[..., None]), 0.0)
    prob_grad = jnp.einsum("rhd,khd->hrk", grads3, values3, preferred_element_type=jnp.float32)
    score_low = (probabilities * (prob_grad - delta_part[..., None])).astype(jnp.bfloat16)
    value_grad = jnp.einsum(
        "hrk,rhd->khd",
        probabilities.astype(jnp.bfloat16),
        grads3,
        preferred_element_type=jnp.float32,
    )
    key_grad = jnp.einsum(
        "hrk,rhd->khd", score_low, queries3, preferred_element_type=jnp.float32
    ) * HEAD ** (-0.5)
    return jnp.concatenate(
        [key_grad.reshape(key_count, HEADS * HEAD), value_grad.reshape(key_count, HEADS * HEAD)],
        axis=1,
    )


def slot_attention(queries3, keys3, values3, query_pos, length):
    key_pos = jnp.arange(keys3.shape[0], dtype=jnp.int32)
    scores, allowed = block_scores(queries3, keys3, query_pos, key_pos, length)
    masked = jnp.where(allowed, scores, masked_value)
    top = jnp.max(masked, axis=-1)
    kept_terms = jnp.where(allowed, jnp.exp(masked - top[..., None]), 0.0)
    log_total = top + jnp.log(jnp.sum(kept_terms, axis=-1))
    probabilities = jnp.where(allowed, jnp.exp(scores - log_total[..., None]), 0.0)
    probabilities_low = probabilities.astype(jnp.bfloat16)
    attended = jnp.einsum(
        "hrk,khd->rhd", probabilities_low, values3, preferred_element_type=jnp.float32
    )
    return attended, probabilities, probabilities_low


def slot_attention_grads(queries3, keys3, values3, grads3, attended, probabilities, probabilities_low):
    prob_grad = jnp.einsum("rhd,khd->hrk", grads3, values3, preferred_element_type=jnp.float32)
    row_delta = jnp.einsum("rhd,rhd->hr", grads3.astype(jnp.float32), attended)
    score_low = (probabilities * (prob_grad - row_delta[..., None])).astype(jnp.bfloat16)
    query_grad = jnp.einsum(
        "hrk,khd->rhd", score_low, keys3, preferred_element_type=jnp.float32
    ) * HEAD ** (-0.5)
    key_grad = jnp.einsum(
        "hrk,rhd->khd", score_low, queries3, preferred_element_type=jnp.float32
    ) * HEAD ** (-0.5)
    value_grad = jnp.einsum(
        "hrk,rhd->khd", probabilities_low, grads3, preferred_element_type=jnp.float32
    )
    return query_grad, key_grad, value_grad


def _pair_masks(scalars_ref, micro, row_count, key_count):
    length = scalars_ref[micro]
    first_row = scalars_ref[scalars_ref.shape[0] - 1]
    query_pos = first_row + lax.broadcasted_iota(jnp.int32, (row_count, key_count), 0)
    key_pos = lax.broadcasted_iota(jnp.int32, (row_count, key_count), 1)
    return (key_pos <= query_pos) & (key_pos < length)


def _forward_kernel(scalars_ref, q_ref, k_ref, v_ref, out_ref, lse_ref):
    micro = pl.program_id(0)
    row_count = q_ref.shape[0]
    key_count = k_ref.shape[0] * k_ref.shape[2]
    allowed = _pair_masks(scalars_ref, micro, row_count, key_count)
    k_all = k_ref[...].reshape(key_count, k_ref.shape[3])
    v_all = v_ref[...].reshape(key_count, v_ref.shape[3])
    for half in range(2):
        lanes = slice(half * HEAD, (half + 1) * HEAD)
        q_head = q_ref[:, lanes]
        k_head = k_all[:, lanes]
        v_head = v_all[:, lanes]
        scores = lax.dot_general(
            q_head, k_head, (((1,), (1,)), ((), ())), preferred_element_type=jnp.float32
        ) * HEAD ** (-0.5)
        masked = jnp.where(allowed, scores, masked_value)
        top = jnp.max(masked, axis=1, keepdims=True)
        kept = jnp.where(allowed, jnp.exp(masked - top), 0.0)
        total = jnp.sum(kept, axis=1, keepdims=True)
        log_total = top + jnp.log(total)
        probabilities = kept * (1.0 / total)
        attended = jnp.dot(
            probabilities.astype(jnp.bfloat16), v_head, preferred_element_type=jnp.float32
        )
        out_ref[:, lanes] = attended
        lse_ref[:, lanes] = jnp.broadcast_to(log_total, (row_count, HEAD))


def _backward_kernel(
    scalars_ref, q_ref, k_ref, v_ref, do_ref, o_ref, lse_ref, dq_ref, kv_grad_ref
):
    micro = pl.program_id(0)
    row_count = q_ref.shape[0]
    key_count = k_ref.shape[0] * k_ref.shape[2]
    allowed = _pair_masks(scalars_ref, micro, row_count, key_count)
    k_all = k_ref[...].reshape(key_count, k_ref.shape[3])
    v_all = v_ref[...].reshape(key_count, v_ref.shape[3])
    for half in range(2):
        lanes = slice(half * HEAD, (half + 1) * HEAD)
        q_head = q_ref[:, lanes]
        k_head = k_all[:, lanes]
        v_head = v_all[:, lanes]
        grad_head = do_ref[:, lanes]
        scores = lax.dot_general(
            q_head, k_head, (((1,), (1,)), ((), ())), preferred_element_type=jnp.float32
        ) * HEAD ** (-0.5)
        log_total = lse_ref[:, half * HEAD : half * HEAD + 1]
        probabilities = jnp.where(allowed, jnp.exp(scores - log_total), 0.0)
        probabilities_low = probabilities.astype(jnp.bfloat16)
        prob_grad = lax.dot_general(
            grad_head, v_head, (((1,), (1,)), ((), ())), preferred_element_type=jnp.float32
        )
        row_delta = jnp.sum(
            grad_head.astype(jnp.float32) * o_ref[:, lanes], axis=1, keepdims=True
        )
        score_low = (probabilities * (prob_grad - row_delta)).astype(jnp.bfloat16)
        dq_ref[:, lanes] = jnp.dot(
            score_low, k_head, preferred_element_type=jnp.float32
        ) * HEAD ** (-0.5)
        key_grad = lax.dot_general(
            score_low, q_head, (((0,), (0,)), ((), ())), preferred_element_type=jnp.float32
        ) * HEAD ** (-0.5)
        value_grad = lax.dot_general(
            probabilities_low, grad_head, (((0,), (0,)), ((), ())),
            preferred_element_type=jnp.float32,
        )
        kv_grad_ref[:, lanes] = key_grad.astype(jnp.bfloat16)
        kv_grad_ref[:, 2 * HEAD + half * HEAD : 2 * HEAD + (half + 1) * HEAD] = value_grad.astype(
            jnp.bfloat16
        )


def attention_forward(scalars, queries, kv_flat, batches):
    all_rows, model_width = queries.shape
    row_count = all_rows // batches
    devices = kv_flat.shape[0]
    key_count = devices * row_count
    pairs = model_width // (2 * HEAD)
    row_spec = pl.BlockSpec((row_count, 2 * HEAD), lambda m, p, s: (m, p))
    key_spec = pl.BlockSpec((devices, 1, row_count, 2 * HEAD), lambda m, p, s: (0, m, 0, p))
    value_spec = pl.BlockSpec(
        (devices, 1, row_count, 2 * HEAD), lambda m, p, s: (0, m, 0, pairs + p)
    )
    return pl.pallas_call(
        _forward_kernel,
        grid_spec=pltpu.PrefetchScalarGridSpec(
            num_scalar_prefetch=1,
            grid=(batches, pairs),
            in_specs=[row_spec, key_spec, value_spec],
            out_specs=[row_spec, row_spec],
        ),
        out_shape=[
            jax.ShapeDtypeStruct((all_rows, model_width), jnp.float32),
            jax.ShapeDtypeStruct((all_rows, model_width), jnp.float32),
        ],
        name="attention_forward",
    )(scalars, queries, kv_flat, kv_flat)


def attention_backward(scalars, queries, kv_flat, grads, attended, log_totals, batches):
    all_rows, model_width = queries.shape
    row_count = all_rows // batches
    devices = kv_flat.shape[0]
    key_count = devices * row_count
    pairs = model_width // (2 * HEAD)
    row_spec = pl.BlockSpec((row_count, 2 * HEAD), lambda m, p, s: (m, p))
    key_spec = pl.BlockSpec((devices, 1, row_count, 2 * HEAD), lambda m, p, s: (0, m, 0, p))
    value_spec = pl.BlockSpec(
        (devices, 1, row_count, 2 * HEAD), lambda m, p, s: (0, m, 0, pairs + p)
    )
    grad_spec = pl.BlockSpec((key_count, 4 * HEAD), lambda m, p, s: (0, m * pairs + p))
    return pl.pallas_call(
        _backward_kernel,
        grid_spec=pltpu.PrefetchScalarGridSpec(
            num_scalar_prefetch=1,
            grid=(batches, pairs),
            in_specs=[row_spec, key_spec, value_spec, row_spec, row_spec, row_spec],
            out_specs=[row_spec, grad_spec],
        ),
        out_shape=[
            jax.ShapeDtypeStruct((all_rows, model_width), jnp.float32),
            jax.ShapeDtypeStruct((key_count, batches * 2 * model_width), jnp.bfloat16),
        ],
        name="attention_backward",
    )(scalars, queries, kv_flat, kv_flat, grads, attended, log_totals)


def local(
    layer_input,
    history,
    cotangent,
    lengths,
    w_qkv,
    w_out,
    w_up,
    w_down,
    ln_gains,
    ln_biases,
    depth_weights,
):
    batches = layer_input.shape[0]
    row_count = layer_input.shape[2]
    model_width = layer_input.shape[3]
    ff_width = w_up.shape[1]
    shard_rows = w_qkv.shape[0]
    all_rows = batches * row_count
    slot_len = row_count * lax.axis_size("seq")
    positions = lax.axis_index("seq") * row_count + jnp.arange(row_count, dtype=jnp.int32)
    cosine_part, sine_part = rotary_tables(jnp.tile(positions, batches))
    gelu_tanh = partial(jax.nn.gelu, approximate=True)
    lane_pad = 128 - 4
    widths = (3 * model_width, 2, 2, lane_pad, model_width, ff_width, ff_width)
    offsets = [0]
    for width in widths:
        offsets.append(offsets[-1] + width)

    def pieces(packed_rows):
        return [packed_rows[:, offsets[i] : offsets[i + 1]] for i in range(len(widths))]

    packed = jnp.concatenate(
        [
            w_qkv,
            ln_gains,
            ln_biases,
            jnp.zeros((shard_rows, lane_pad), w_qkv.dtype),
            w_out,
            w_up,
            w_down.reshape(shard_rows, ff_width),
        ],
        axis=1,
    )
    gathered = lax.all_gather(packed, ("seq", "fsdp"), axis=0, tiled=True)
    full_qkv, gain_rows, bias_rows, _, full_out, full_up, down_rows = pieces(gathered)
    full_down = down_rows.reshape(ff_width, model_width)
    norm_gains = gain_rows.astype(jnp.float32)
    norm_biases = bias_rows.astype(jnp.float32)

    slot_lengths = lengths[:, 0]
    inputs = layer_input[:, 0].reshape(all_rows, model_width).astype(jnp.float32)
    first_low = layer_norm(inputs, norm_gains[:, 0], norm_biases[:, 0]).astype(jnp.bfloat16)
    projected = jnp.dot(first_low, full_qkv, preferred_element_type=jnp.float32)
    queries = rotate(projected[:, :model_width], cosine_part, sine_part).astype(jnp.bfloat16)
    keys_own = rotate(
        projected[:, model_width : 2 * model_width], cosine_part, sine_part
    ).astype(jnp.bfloat16)
    values_own = projected[:, 2 * model_width :].astype(jnp.bfloat16)
    own_kv = jnp.concatenate([keys_own, values_own], axis=1).reshape(
        batches, row_count, 2 * model_width
    )
    earlier = history[:, :, 0].reshape(4, all_rows, model_width).astype(jnp.float32)
    usable = (positions[None, :] < slot_lengths[:, None]).reshape(all_rows, 1)
    grad_next = jnp.where(
        usable, cotangent[:, 0].reshape(all_rows, model_width).astype(jnp.float32), 0.0
    )
    history_part = (
        depth_weights[0] * earlier[0]
        + depth_weights[1] * earlier[1]
        + depth_weights[2] * earlier[2]
        + depth_weights[3] * earlier[3]
    )
    grad_history = (depth_weights[:4, None, None] * grad_next[None]).astype(jnp.bfloat16)
    grad_history = grad_history.reshape(4, batches, 1, row_count, model_width)
    out_grad = depth_weights[4] * grad_next
    out_low = out_grad.astype(jnp.bfloat16)

    kv_flat = lax.all_gather(own_kv, "seq", axis=0, tiled=False)
    scalars = jnp.concatenate(
        [slot_lengths.astype(jnp.int32), (lax.axis_index("seq") * row_count)[None].astype(jnp.int32)]
    )
    attended_rows, log_totals = attention_forward(scalars, queries, kv_flat, batches)
    attended_low = attended_rows.astype(jnp.bfloat16)
    residual = inputs + jnp.dot(attended_low, full_out, preferred_element_type=jnp.float32)
    second_low = layer_norm(residual, norm_gains[:, 1], norm_biases[:, 1]).astype(jnp.bfloat16)
    hidden = jnp.dot(second_low, full_up, preferred_element_type=jnp.float32)
    hidden_low = gelu_tanh(hidden).astype(jnp.bfloat16)
    block_out = residual + jnp.dot(hidden_low, full_down, preferred_element_type=jnp.float32)
    hidden_grad = jnp.einsum("rd,fd->rf", out_low, full_down, preferred_element_type=jnp.float32)
    _, gelu_pullback = jax.vjp(gelu_tanh, hidden)
    up_low = gelu_pullback(hidden_grad)[0].astype(jnp.bfloat16)
    second_grad = jnp.einsum("rf,df->rd", up_low, full_up, preferred_element_type=jnp.float32)
    _, second_pullback = jax.vjp(layer_norm, residual, norm_gains[:, 1], norm_biases[:, 1])
    residual_part, gain_two, bias_two = second_pullback(second_grad)
    residual_grad = out_grad + residual_part
    branch_low = residual_grad.astype(jnp.bfloat16)
    attended_grad = jnp.einsum(
        "rd,cd->rc", branch_low, full_out, preferred_element_type=jnp.float32
    ).astype(jnp.bfloat16)
    query_grad, kv_grad_flat = attention_backward(
        scalars, queries, kv_flat, attended_grad, attended_rows, log_totals, batches
    )
    kv_grad_own = lax.psum_scatter(kv_grad_flat, "seq", scatter_dimension=0, tiled=True)
    block_side = block_out
    combined = depth_weights[4] * block_side + history_part
    next_input = combined.astype(jnp.bfloat16).reshape(batches, 1, row_count, model_width)
    depth_terms = jnp.concatenate(
        [jnp.sum(earlier * grad_next[None], axis=(1, 2)), jnp.sum(block_side * grad_next)[None]]
    )
    grad_down = jnp.einsum("rf,rd->fd", hidden_low, out_low, preferred_element_type=jnp.float32)
    grad_up = jnp.einsum("rd,rf->df", second_low, up_low, preferred_element_type=jnp.float32)
    grad_outproj = jnp.einsum(
        "rc,rd->cd", attended_low, branch_low, preferred_element_type=jnp.float32
    )
    early_grads = jnp.concatenate(
        [
            jnp.zeros((model_width, 3 * model_width), jnp.float32),
            grad_outproj,
            grad_up,
            grad_down.reshape(model_width, ff_width),
        ],
        axis=1,
    ).astype(jnp.bfloat16)
    kv_grad_own, early_grads = lax.optimization_barrier((kv_grad_own, early_grads))
    pairs = model_width // (2 * HEAD)
    kv_grad_own = kv_grad_own.reshape(row_count, batches, pairs, 2, 2 * HEAD)
    kv_grad_own = jnp.transpose(kv_grad_own, (1, 0, 3, 2, 4)).reshape(
        all_rows, 2 * model_width
    )
    key_value_all = kv_grad_own.astype(jnp.float32)
    qkv_low = jnp.concatenate(
        [
            rotate(query_grad, cosine_part, -sine_part),
            rotate(key_value_all[:, :model_width], cosine_part, -sine_part),
            key_value_all[:, model_width:],
        ],
        axis=1,
    ).astype(jnp.bfloat16)
    grad_qkv = jnp.einsum("rd,rc->dc", first_low, qkv_low, preferred_element_type=jnp.float32)
    first_grad = jnp.einsum("rc,dc->rd", qkv_low, full_qkv, preferred_element_type=jnp.float32)
    _, first_pullback = jax.vjp(layer_norm, inputs, norm_gains[:, 0], norm_biases[:, 0])
    input_part, gain_one, bias_one = first_pullback(first_grad)
    grad_input = (residual_grad + input_part).astype(jnp.bfloat16)
    grad_input = grad_input.reshape(batches, 1, row_count, model_width)
    packed_grads = lax.dynamic_update_slice(early_grads, grad_qkv.astype(jnp.bfloat16), (0, 0))
    device_count = model_width // shard_rows
    row_major = Layout(major_to_minor=(0, 1, 2))
    grad_offsets = [0]
    for width in (3 * model_width, model_width, ff_width, ff_width):
        grad_offsets.append(grad_offsets[-1] + width)
    scattered = lax.psum_scatter(
        with_layout_constraint(
            packed_grads.reshape(device_count, shard_rows, grad_offsets[-1]), row_major
        ),
        ("seq", "fsdp"),
        scatter_dimension=0,
        tiled=False,
    )
    scattered = with_layout_constraint(scattered, Layout(major_to_minor=(0, 1)))
    scattered = scattered.astype(jnp.float32)
    full_pieces = [scattered[:, grad_offsets[i] : grad_offsets[i + 1]] for i in range(4)]
    small_sums = lax.psum(
        jnp.concatenate(
            [
                depth_terms,
                jnp.stack([gain_one, gain_two, bias_one, bias_two], axis=1).reshape(-1),
            ]
        ),
        ("seq", "fsdp"),
    )
    depth_total = small_sums[:5]
    device_index = lax.axis_index("seq") * lax.axis_size("fsdp") + lax.axis_index("fsdp")
    norm_owned = lax.dynamic_slice_in_dim(
        small_sums[5:].reshape(model_width, 4), device_index * shard_rows, shard_rows, 0
    )
    owned = [
        full_pieces[0],
        full_pieces[1],
        full_pieces[2],
        full_pieces[3].reshape(-1, model_width),
        norm_owned[:, :2],
        norm_owned[:, 2:],
    ]
    return (next_input, grad_input, grad_history, *owned, depth_total)


def solution(mesh):
    in_specs = (
        P(None, "fsdp", "seq", None),
        P(None, None, "fsdp", "seq", None),
        P(None, "fsdp", "seq", None),
        P(None, "fsdp"),
        P(("seq", "fsdp"), None),
        P(("seq", "fsdp"), None),
        P(("seq", "fsdp"), None),
        P(("seq", "fsdp"), None),
        P(("seq", "fsdp"), None),
        P(("seq", "fsdp"), None),
        P(),
    )
    out_specs = (
        P(None, "fsdp", "seq", None),
        P(None, "fsdp", "seq", None),
        P(None, None, "fsdp", "seq", None),
        P(("seq", "fsdp"), None),
        P(("seq", "fsdp"), None),
        P(("seq", "fsdp"), None),
        P(("seq", "fsdp"), None),
        P(("seq", "fsdp"), None),
        P(("seq", "fsdp"), None),
        P(),
    )
    return jax.shard_map(local, mesh=mesh, in_specs=in_specs, out_specs=out_specs, check_vma=False)
```

```python
from functools import partial
import math

import jax
import jax.numpy as jnp
from jax import lax
from jax.sharding import PartitionSpec as P
from jax.experimental.layout import Layout, with_layout_constraint
from jax.experimental import pallas as pl
from jax.experimental.pallas import tpu as pltpu

HEADS = 12
HEAD = 64


epsilon = 1e-05
masked_value = -1e30


def layer_norm(values, gain_vector, bias_vector):
    center = values - jnp.mean(values, axis=-1, keepdims=True)
    spread = jnp.mean(center * center, axis=-1, keepdims=True)
    return center * lax.rsqrt(spread + epsilon) * gain_vector + bias_vector


def rotary_tables(positions):
    half_width = HEAD // 2
    frequencies = 10000.0 ** (-jnp.arange(half_width, dtype=jnp.float32) / half_width)
    angles = positions.astype(jnp.float32)[:, None] * frequencies[None, :]
    return (jnp.cos(angles)[:, None, :], jnp.sin(angles)[:, None, :])


def rotate(values, cosine_part, sine_part):
    row_count = values.shape[0]
    shaped = values.reshape(row_count, HEADS, HEAD)
    half_width = HEAD // 2
    first_half = shaped[..., :half_width]
    second_half = shaped[..., half_width:]
    turned = jnp.concatenate(
        [
            first_half * cosine_part - second_half * sine_part,
            second_half * cosine_part + first_half * sine_part,
        ],
        axis=-1,
    )
    return turned.reshape(row_count, HEADS * HEAD)


def block_scores(queries3, keys3, query_pos, key_pos, length):
    scores = jnp.einsum(
        "rhd,khd->hrk", queries3, keys3, preferred_element_type=jnp.float32
    ) * HEAD ** (-0.5)
    allowed = (key_pos[None, :] <= query_pos[:, None]) & (key_pos[None, :] < length)
    return (scores, allowed[None])


def row_totals(queries3, keys3, query_pos, length, key_block):
    row_count = queries3.shape[0]

    def row_advance(state, block_index):
        running_top, running_sum = state
        first_key = block_index * key_block
        keys_part = lax.dynamic_slice_in_dim(keys3, first_key, key_block, 0)
        key_pos = first_key + jnp.arange(key_block, dtype=jnp.int32)
        scores, allowed = block_scores(queries3, keys_part, query_pos, key_pos, length)
        masked = jnp.where(allowed, scores, masked_value)
        new_top = jnp.maximum(running_top, jnp.max(masked, axis=-1))
        kept_terms = jnp.where(allowed, jnp.exp(masked - new_top[..., None]), 0.0)
        running_sum = running_sum * jnp.exp(running_top - new_top) + jnp.sum(kept_terms, axis=-1)
        return ((new_top, running_sum), None)

    initial = (
        jnp.full((HEADS, row_count), masked_value, jnp.float32),
        jnp.zeros((HEADS, row_count), jnp.float32),
    )
    (row_tops, row_sums), _ = lax.scan(
        row_advance, initial, jnp.arange(keys3.shape[0] // key_block, dtype=jnp.int32)
    )
    return row_tops + jnp.log(row_sums)


def attend(queries3, keys3, values3, query_pos, length, key_block, log_total):

    def attend_advance(running, block_index):
        first_key = block_index * key_block
        keys_part = lax.dynamic_slice_in_dim(keys3, first_key, key_block, 0)
        values_part = lax.dynamic_slice_in_dim(values3, first_key, key_block, 0)
        key_pos = first_key + jnp.arange(key_block, dtype=jnp.int32)
        scores, allowed = block_scores(queries3, keys_part, query_pos, key_pos, length)
        probabilities = jnp.where(allowed, jnp.exp(scores - log_total[..., None]), 0.0).astype(
            jnp.bfloat16
        )
        return (
            running
            + jnp.einsum(
                "hrk,khd->rhd", probabilities, values_part, preferred_element_type=jnp.float32
            ),
            None,
        )

    initial = jnp.zeros(queries3.shape, jnp.float32)
    result, _ = lax.scan(
        attend_advance, initial, jnp.arange(keys3.shape[0] // key_block, dtype=jnp.int32)
    )
    return result


def query_grads(
    queries3, grads3, keys3, values3, query_pos, length, key_block, log_total, row_delta
):

    def query_advance(running, block_index):
        first_key = block_index * key_block
        keys_part = lax.dynamic_slice_in_dim(keys3, first_key, key_block, 0)
        values_part = lax.dynamic_slice_in_dim(values3, first_key, key_block, 0)
        key_pos = first_key + jnp.arange(key_block, dtype=jnp.int32)
        scores, allowed = block_scores(queries3, keys_part, query_pos, key_pos, length)
        probabilities = jnp.where(allowed, jnp.exp(scores - log_total[..., None]), 0.0)
        prob_grad = jnp.einsum(
            "rhd,khd->hrk", grads3, values_part, preferred_element_type=jnp.float32
        )
        score_low = (probabilities * (prob_grad - row_delta[..., None])).astype(jnp.bfloat16)
        return (
            running
            + jnp.einsum("hrk,khd->rhd", score_low, keys_part, preferred_element_type=jnp.float32),
            None,
        )

    initial = jnp.zeros(queries3.shape, jnp.float32)
    result, _ = lax.scan(
        query_advance, initial, jnp.arange(keys3.shape[0] // key_block, dtype=jnp.int32)
    )
    return result * HEAD ** (-0.5)


def key_side(queries3, grads3, log_part, delta_part, query_pos, keys3, values3, key_pos, length):
    key_count = keys3.shape[0]
    scores, allowed = block_scores(queries3, keys3, query_pos, key_pos, length)
    probabilities = jnp.where(allowed, jnp.exp(scores - log_part[..., None]), 0.0)
    prob_grad = jnp.einsum("rhd,khd->hrk", grads3, values3, preferred_element_type=jnp.float32)
    score_low = (probabilities * (prob_grad - delta_part[..., None])).astype(jnp.bfloat16)
    value_grad = jnp.einsum(
        "hrk,rhd->khd",
        probabilities.astype(jnp.bfloat16),
        grads3,
        preferred_element_type=jnp.float32,
    )
    key_grad = jnp.einsum(
        "hrk,rhd->khd", score_low, queries3, preferred_element_type=jnp.float32
    ) * HEAD ** (-0.5)
    return jnp.concatenate(
        [key_grad.reshape(key_count, HEADS * HEAD), value_grad.reshape(key_count, HEADS * HEAD)],
        axis=1,
    )


def slot_attention(queries3, keys3, values3, query_pos, length):
    key_pos = jnp.arange(keys3.shape[0], dtype=jnp.int32)
    scores, allowed = block_scores(queries3, keys3, query_pos, key_pos, length)
    masked = jnp.where(allowed, scores, masked_value)
    top = jnp.max(masked, axis=-1)
    kept_terms = jnp.where(allowed, jnp.exp(masked - top[..., None]), 0.0)
    log_total = top + jnp.log(jnp.sum(kept_terms, axis=-1))
    probabilities = jnp.where(allowed, jnp.exp(scores - log_total[..., None]), 0.0)
    probabilities_low = probabilities.astype(jnp.bfloat16)
    attended = jnp.einsum(
        "hrk,khd->rhd", probabilities_low, values3, preferred_element_type=jnp.float32
    )
    return attended, probabilities, probabilities_low


def slot_attention_grads(queries3, keys3, values3, grads3, attended, probabilities, probabilities_low):
    prob_grad = jnp.einsum("rhd,khd->hrk", grads3, values3, preferred_element_type=jnp.float32)
    row_delta = jnp.einsum("rhd,rhd->hr", grads3.astype(jnp.float32), attended)
    score_low = (probabilities * (prob_grad - row_delta[..., None])).astype(jnp.bfloat16)
    query_grad = jnp.einsum(
        "hrk,khd->rhd", score_low, keys3, preferred_element_type=jnp.float32
    ) * HEAD ** (-0.5)
    key_grad = jnp.einsum(
        "hrk,rhd->khd", score_low, queries3, preferred_element_type=jnp.float32
    ) * HEAD ** (-0.5)
    value_grad = jnp.einsum(
        "hrk,rhd->khd", probabilities_low, grads3, preferred_element_type=jnp.float32
    )
    return query_grad, key_grad, value_grad


def _pair_masks(scalars_ref, micro, row_count, key_count):
    length = scalars_ref[micro]
    first_row = scalars_ref[scalars_ref.shape[0] - 1]
    query_pos = first_row + lax.broadcasted_iota(jnp.int32, (row_count, key_count), 0)
    key_pos = lax.broadcasted_iota(jnp.int32, (row_count, key_count), 1)
    return (key_pos <= query_pos) & (key_pos < length)


def _forward_kernel(scalars_ref, q_ref, k_ref, v_ref, out_ref, lse_ref):
    micro = pl.program_id(0)
    row_count = q_ref.shape[0]
    key_count = k_ref.shape[0] * k_ref.shape[2]
    allowed = _pair_masks(scalars_ref, micro, row_count, key_count)
    k_all = k_ref[...].reshape(key_count, k_ref.shape[3])
    v_all = v_ref[...].reshape(key_count, v_ref.shape[3])
    for half in range(2):
        lanes = slice(half * HEAD, (half + 1) * HEAD)
        q_head = q_ref[:, lanes]
        k_head = k_all[:, lanes]
        v_head = v_all[:, lanes]
        scores = lax.dot_general(
            q_head, k_head, (((1,), (1,)), ((), ())), preferred_element_type=jnp.float32
        ) * HEAD ** (-0.5)
        masked = jnp.where(allowed, scores, masked_value)
        top = jnp.max(masked, axis=1, keepdims=True)
        kept = jnp.where(allowed, jnp.exp(masked - top), 0.0)
        total = jnp.sum(kept, axis=1, keepdims=True)
        log_total = top + jnp.log(total)
        probabilities = kept * (1.0 / total)
        attended = jnp.dot(
            probabilities.astype(jnp.bfloat16), v_head, preferred_element_type=jnp.float32
        )
        out_ref[:, lanes] = attended
        lse_ref[:, lanes] = jnp.broadcast_to(log_total, (row_count, HEAD))


def _backward_kernel(
    scalars_ref, q_ref, k_ref, v_ref, do_ref, o_ref, lse_ref, dq_ref, kv_grad_ref, pair_ref
):
    micro = pl.program_id(0)
    pair = pl.program_id(1)
    row_count = q_ref.shape[0]
    key_count = k_ref.shape[0] * k_ref.shape[2]
    allowed = _pair_masks(scalars_ref, micro, row_count, key_count)
    k_all = k_ref[...].reshape(key_count, k_ref.shape[3])
    v_all = v_ref[...].reshape(key_count, v_ref.shape[3])
    for half in range(2):
        lanes = slice(half * HEAD, (half + 1) * HEAD)
        q_head = q_ref[:, lanes]
        k_head = k_all[:, lanes]
        v_head = v_all[:, lanes]
        grad_head = do_ref[:, lanes]
        scores = lax.dot_general(
            q_head, k_head, (((1,), (1,)), ((), ())), preferred_element_type=jnp.float32
        ) * HEAD ** (-0.5)
        log_total = lse_ref[:, half * HEAD : half * HEAD + 1]
        probabilities = jnp.where(allowed, jnp.exp(scores - log_total), 0.0)
        probabilities_low = probabilities.astype(jnp.bfloat16)
        prob_grad = lax.dot_general(
            grad_head, v_head, (((1,), (1,)), ((), ())), preferred_element_type=jnp.float32
        )
        row_delta = jnp.sum(
            grad_head.astype(jnp.float32) * o_ref[:, lanes], axis=1, keepdims=True
        )
        score_low = (probabilities * (prob_grad - row_delta)).astype(jnp.bfloat16)
        dq_ref[:, lanes] = jnp.dot(
            score_low, k_head, preferred_element_type=jnp.float32
        ) * HEAD ** (-0.5)
        key_grad = lax.dot_general(
            score_low, q_head, (((0,), (0,)), ((), ())), preferred_element_type=jnp.float32
        ) * HEAD ** (-0.5)
        value_grad = lax.dot_general(
            probabilities_low, grad_head, (((0,), (0,)), ((), ())),
            preferred_element_type=jnp.float32,
        )
        pair_ref[0, :, lanes] = key_grad.astype(jnp.bfloat16)
        pair_ref[1, :, lanes] = value_grad.astype(jnp.bfloat16)
    half_width = kv_grad_ref.shape[1] // 2
    first_col = pl.multiple_of(pair * 2 * HEAD, 2 * HEAD)
    kv_grad_ref[:, pl.ds(first_col, 2 * HEAD)] = pair_ref[0]
    kv_grad_ref[:, pl.ds(first_col + half_width, 2 * HEAD)] = pair_ref[1]


def attention_forward(scalars, queries, kv_flat, batches):
    all_rows, model_width = queries.shape
    row_count = all_rows // batches
    devices = kv_flat.shape[0]
    key_count = devices * row_count
    pairs = model_width // (2 * HEAD)
    row_spec = pl.BlockSpec((row_count, 2 * HEAD), lambda m, p, s: (m, p))
    key_spec = pl.BlockSpec((devices, 1, row_count, 2 * HEAD), lambda m, p, s: (0, m, 0, p))
    value_spec = pl.BlockSpec(
        (devices, 1, row_count, 2 * HEAD), lambda m, p, s: (0, m, 0, pairs + p)
    )
    return pl.pallas_call(
        _forward_kernel,
        grid_spec=pltpu.PrefetchScalarGridSpec(
            num_scalar_prefetch=1,
            grid=(batches, pairs),
            in_specs=[row_spec, key_spec, value_spec],
            out_specs=[row_spec, row_spec],
        ),
        out_shape=[
            jax.ShapeDtypeStruct((all_rows, model_width), jnp.float32),
            jax.ShapeDtypeStruct((all_rows, model_width), jnp.float32),
        ],
        name="attention_forward",
    )(scalars, queries, kv_flat, kv_flat)


def attention_backward(scalars, queries, kv_flat, grads, attended, log_totals, batches):
    all_rows, model_width = queries.shape
    row_count = all_rows // batches
    devices = kv_flat.shape[0]
    key_count = devices * row_count
    pairs = model_width // (2 * HEAD)
    row_spec = pl.BlockSpec((row_count, 2 * HEAD), lambda m, p, s: (m, p))
    key_spec = pl.BlockSpec((devices, 1, row_count, 2 * HEAD), lambda m, p, s: (0, m, 0, p))
    value_spec = pl.BlockSpec(
        (devices, 1, row_count, 2 * HEAD), lambda m, p, s: (0, m, 0, pairs + p)
    )
    grad_spec = pl.BlockSpec((key_count, 2 * model_width), lambda m, p, s: (0, m))
    return pl.pallas_call(
        _backward_kernel,
        grid_spec=pltpu.PrefetchScalarGridSpec(
            num_scalar_prefetch=1,
            grid=(batches, pairs),
            in_specs=[row_spec, key_spec, value_spec, row_spec, row_spec, row_spec],
            out_specs=[row_spec, grad_spec],
            scratch_shapes=[pltpu.VMEM((2, key_count, 2 * HEAD), jnp.bfloat16)],
        ),
        out_shape=[
            jax.ShapeDtypeStruct((all_rows, model_width), jnp.float32),
            jax.ShapeDtypeStruct((key_count, batches * 2 * model_width), jnp.bfloat16),
        ],
        name="attention_backward",
    )(scalars, queries, kv_flat, kv_flat, grads, attended, log_totals)


def local(
    layer_input,
    history,
    cotangent,
    lengths,
    w_qkv,
    w_out,
    w_up,
    w_down,
    ln_gains,
    ln_biases,
    depth_weights,
):
    batches = layer_input.shape[0]
    row_count = layer_input.shape[2]
    model_width = layer_input.shape[3]
    ff_width = w_up.shape[1]
    shard_rows = w_qkv.shape[0]
    all_rows = batches * row_count
    slot_len = row_count * lax.axis_size("seq")
    positions = lax.axis_index("seq") * row_count + jnp.arange(row_count, dtype=jnp.int32)
    cosine_part, sine_part = rotary_tables(jnp.tile(positions, batches))
    gelu_tanh = partial(jax.nn.gelu, approximate=True)
    lane_pad = 128 - 4
    widths = (3 * model_width, 2, 2, lane_pad, model_width, ff_width, ff_width)
    offsets = [0]
    for width in widths:
        offsets.append(offsets[-1] + width)

    def pieces(packed_rows):
        return [packed_rows[:, offsets[i] : offsets[i + 1]] for i in range(len(widths))]

    packed = jnp.concatenate(
        [
            w_qkv,
            ln_gains,
            ln_biases,
            jnp.zeros((shard_rows, lane_pad), w_qkv.dtype),
            w_out,
            w_up,
            w_down.reshape(shard_rows, ff_width),
        ],
        axis=1,
    )
    gathered = lax.all_gather(packed, ("seq", "fsdp"), axis=0, tiled=True)
    full_qkv, gain_rows, bias_rows, _, full_out, full_up, down_rows = pieces(gathered)
    full_down = down_rows.reshape(ff_width, model_width)
    norm_gains = gain_rows.astype(jnp.float32)
    norm_biases = bias_rows.astype(jnp.float32)

    slot_lengths = lengths[:, 0]
    inputs = layer_input[:, 0].reshape(all_rows, model_width).astype(jnp.float32)
    first_low = layer_norm(inputs, norm_gains[:, 0], norm_biases[:, 0]).astype(jnp.bfloat16)
    projected = jnp.dot(first_low, full_qkv, preferred_element_type=jnp.float32)
    queries = rotate(projected[:, :model_width], cosine_part, sine_part).astype(jnp.bfloat16)
    keys_own = rotate(
        projected[:, model_width : 2 * model_width], cosine_part, sine_part
    ).astype(jnp.bfloat16)
    values_own = projected[:, 2 * model_width :].astype(jnp.bfloat16)
    own_kv = jnp.concatenate([keys_own, values_own], axis=1).reshape(
        batches, row_count, 2 * model_width
    )
    earlier = history[:, :, 0].reshape(4, all_rows, model_width).astype(jnp.float32)
    usable = (positions[None, :] < slot_lengths[:, None]).reshape(all_rows, 1)
    grad_next = jnp.where(
        usable, cotangent[:, 0].reshape(all_rows, model_width).astype(jnp.float32), 0.0
    )
    history_part = (
        depth_weights[0] * earlier[0]
        + depth_weights[1] * earlier[1]
        + depth_weights[2] * earlier[2]
        + depth_weights[3] * earlier[3]
    )
    grad_history = (depth_weights[:4, None, None] * grad_next[None]).astype(jnp.bfloat16)
    grad_history = grad_history.reshape(4, batches, 1, row_count, model_width)
    out_grad = depth_weights[4] * grad_next
    out_low = out_grad.astype(jnp.bfloat16)

    kv_flat = lax.all_gather(own_kv, "seq", axis=0, tiled=False)
    scalars = jnp.concatenate(
        [slot_lengths.astype(jnp.int32), (lax.axis_index("seq") * row_count)[None].astype(jnp.int32)]
    )
    attended_rows, log_totals = attention_forward(scalars, queries, kv_flat, batches)
    attended_low = attended_rows.astype(jnp.bfloat16)
    residual = inputs + jnp.dot(attended_low, full_out, preferred_element_type=jnp.float32)
    second_low = layer_norm(residual, norm_gains[:, 1], norm_biases[:, 1]).astype(jnp.bfloat16)
    hidden = jnp.dot(second_low, full_up, preferred_element_type=jnp.float32)
    hidden_low = gelu_tanh(hidden).astype(jnp.bfloat16)
    block_out = residual + jnp.dot(hidden_low, full_down, preferred_element_type=jnp.float32)
    hidden_grad = jnp.einsum("rd,fd->rf", out_low, full_down, preferred_element_type=jnp.float32)
    _, gelu_pullback = jax.vjp(gelu_tanh, hidden)
    up_low = gelu_pullback(hidden_grad)[0].astype(jnp.bfloat16)
    second_grad = jnp.einsum("rf,df->rd", up_low, full_up, preferred_element_type=jnp.float32)
    _, second_pullback = jax.vjp(layer_norm, residual, norm_gains[:, 1], norm_biases[:, 1])
    residual_part, gain_two, bias_two = second_pullback(second_grad)
    residual_grad = out_grad + residual_part
    branch_low = residual_grad.astype(jnp.bfloat16)
    attended_grad = jnp.einsum(
        "rd,cd->rc", branch_low, full_out, preferred_element_type=jnp.float32
    ).astype(jnp.bfloat16)
    query_grad, kv_grad_flat = attention_backward(
        scalars, queries, kv_flat, attended_grad, attended_rows, log_totals, batches
    )
    kv_grad_own = lax.psum_scatter(kv_grad_flat, "seq", scatter_dimension=0, tiled=True)
    block_side = block_out
    combined = depth_weights[4] * block_side + history_part
    next_input = combined.astype(jnp.bfloat16).reshape(batches, 1, row_count, model_width)
    depth_terms = jnp.concatenate(
        [jnp.sum(earlier * grad_next[None], axis=(1, 2)), jnp.sum(block_side * grad_next)[None]]
    )
    grad_down = jnp.einsum("rf,rd->fd", hidden_low, out_low, preferred_element_type=jnp.float32)
    grad_up = jnp.einsum("rd,rf->df", second_low, up_low, preferred_element_type=jnp.float32)
    grad_outproj = jnp.einsum(
        "rc,rd->cd", attended_low, branch_low, preferred_element_type=jnp.float32
    )
    early_grads = jnp.concatenate(
        [
            jnp.zeros((model_width, 3 * model_width), jnp.float32),
            grad_outproj,
            grad_up,
            grad_down.reshape(model_width, ff_width),
        ],
        axis=1,
    ).astype(jnp.bfloat16)
    kv_grad_own, early_grads = lax.optimization_barrier((kv_grad_own, early_grads))
    kv_grad_own = jnp.swapaxes(
        kv_grad_own.reshape(row_count, batches, 2 * model_width), 0, 1
    ).reshape(all_rows, 2 * model_width)
    key_value_all = kv_grad_own.astype(jnp.float32)
    qkv_low = jnp.concatenate(
        [
            rotate(query_grad, cosine_part, -sine_part),
            rotate(key_value_all[:, :model_width], cosine_part, -sine_part),
            key_value_all[:, model_width:],
        ],
        axis=1,
    ).astype(jnp.bfloat16)
    grad_qkv = jnp.einsum("rd,rc->dc", first_low, qkv_low, preferred_element_type=jnp.float32)
    first_grad = jnp.einsum("rc,dc->rd", qkv_low, full_qkv, preferred_element_type=jnp.float32)
    _, first_pullback = jax.vjp(layer_norm, inputs, norm_gains[:, 0], norm_biases[:, 0])
    input_part, gain_one, bias_one = first_pullback(first_grad)
    grad_input = (residual_grad + input_part).astype(jnp.bfloat16)
    grad_input = grad_input.reshape(batches, 1, row_count, model_width)
    packed_grads = lax.dynamic_update_slice(early_grads, grad_qkv.astype(jnp.bfloat16), (0, 0))
    device_count = model_width // shard_rows
    row_major = Layout(major_to_minor=(0, 1, 2))
    grad_offsets = [0]
    for width in (3 * model_width, model_width, ff_width, ff_width):
        grad_offsets.append(grad_offsets[-1] + width)
    scattered = lax.psum_scatter(
        with_layout_constraint(
            packed_grads.reshape(device_count, shard_rows, grad_offsets[-1]), row_major
        ),
        ("seq", "fsdp"),
        scatter_dimension=0,
        tiled=False,
    )
    scattered = with_layout_constraint(scattered, Layout(major_to_minor=(0, 1)))
    scattered = scattered.astype(jnp.float32)
    full_pieces = [scattered[:, grad_offsets[i] : grad_offsets[i + 1]] for i in range(4)]
    small_sums = lax.psum(
        jnp.concatenate(
            [
                depth_terms,
                jnp.stack([gain_one, gain_two, bias_one, bias_two], axis=1).reshape(-1),
            ]
        ),
        ("seq", "fsdp"),
    )
    depth_total = small_sums[:5]
    device_index = lax.axis_index("seq") * lax.axis_size("fsdp") + lax.axis_index("fsdp")
    norm_owned = lax.dynamic_slice_in_dim(
        small_sums[5:].reshape(model_width, 4), device_index * shard_rows, shard_rows, 0
    )
    owned = [
        full_pieces[0],
        full_pieces[1],
        full_pieces[2],
        full_pieces[3].reshape(-1, model_width),
        norm_owned[:, :2],
        norm_owned[:, 2:],
    ]
    return (next_input, grad_input, grad_history, *owned, depth_total)


def solution(mesh):
    in_specs = (
        P(None, "fsdp", "seq", None),
        P(None, None, "fsdp", "seq", None),
        P(None, "fsdp", "seq", None),
        P(None, "fsdp"),
        P(("seq", "fsdp"), None),
        P(("seq", "fsdp"), None),
        P(("seq", "fsdp"), None),
        P(("seq", "fsdp"), None),
        P(("seq", "fsdp"), None),
        P(("seq", "fsdp"), None),
        P(),
    )
    out_specs = (
        P(None, "fsdp", "seq", None),
        P(None, "fsdp", "seq", None),
        P(None, None, "fsdp", "seq", None),
        P(("seq", "fsdp"), None),
        P(("seq", "fsdp"), None),
        P(("seq", "fsdp"), None),
        P(("seq", "fsdp"), None),
        P(("seq", "fsdp"), None),
        P(("seq", "fsdp"), None),
        P(),
    )
    return jax.shard_map(local, mesh=mesh, in_specs=in_specs, out_specs=out_specs, check_vma=False)
```

```python
from functools import partial
import math

import jax
import jax.numpy as jnp
from jax import lax
from jax.sharding import PartitionSpec as P
from jax.experimental.layout import Layout, with_layout_constraint
from jax.experimental import pallas as pl
from jax.experimental.pallas import tpu as pltpu

HEADS = 12
HEAD = 64


epsilon = 1e-05
masked_value = -1e30


def layer_norm(values, gain_vector, bias_vector):
    center = values - jnp.mean(values, axis=-1, keepdims=True)
    spread = jnp.mean(center * center, axis=-1, keepdims=True)
    return center * lax.rsqrt(spread + epsilon) * gain_vector + bias_vector


def rotary_tables(positions):
    half_width = HEAD // 2
    frequencies = 10000.0 ** (-jnp.arange(half_width, dtype=jnp.float32) / half_width)
    angles = positions.astype(jnp.float32)[:, None] * frequencies[None, :]
    return (jnp.cos(angles)[:, None, :], jnp.sin(angles)[:, None, :])


def rotate(values, cosine_part, sine_part):
    row_count = values.shape[0]
    shaped = values.reshape(row_count, HEADS, HEAD)
    half_width = HEAD // 2
    first_half = shaped[..., :half_width]
    second_half = shaped[..., half_width:]
    turned = jnp.concatenate(
        [
            first_half * cosine_part - second_half * sine_part,
            second_half * cosine_part + first_half * sine_part,
        ],
        axis=-1,
    )
    return turned.reshape(row_count, HEADS * HEAD)


def block_scores(queries3, keys3, query_pos, key_pos, length):
    scores = jnp.einsum(
        "rhd,khd->hrk", queries3, keys3, preferred_element_type=jnp.float32
    ) * HEAD ** (-0.5)
    allowed = (key_pos[None, :] <= query_pos[:, None]) & (key_pos[None, :] < length)
    return (scores, allowed[None])


def row_totals(queries3, keys3, query_pos, length, key_block):
    row_count = queries3.shape[0]

    def row_advance(state, block_index):
        running_top, running_sum = state
        first_key = block_index * key_block
        keys_part = lax.dynamic_slice_in_dim(keys3, first_key, key_block, 0)
        key_pos = first_key + jnp.arange(key_block, dtype=jnp.int32)
        scores, allowed = block_scores(queries3, keys_part, query_pos, key_pos, length)
        masked = jnp.where(allowed, scores, masked_value)
        new_top = jnp.maximum(running_top, jnp.max(masked, axis=-1))
        kept_terms = jnp.where(allowed, jnp.exp(masked - new_top[..., None]), 0.0)
        running_sum = running_sum * jnp.exp(running_top - new_top) + jnp.sum(kept_terms, axis=-1)
        return ((new_top, running_sum), None)

    initial = (
        jnp.full((HEADS, row_count), masked_value, jnp.float32),
        jnp.zeros((HEADS, row_count), jnp.float32),
    )
    (row_tops, row_sums), _ = lax.scan(
        row_advance, initial, jnp.arange(keys3.shape[0] // key_block, dtype=jnp.int32)
    )
    return row_tops + jnp.log(row_sums)


def attend(queries3, keys3, values3, query_pos, length, key_block, log_total):

    def attend_advance(running, block_index):
        first_key = block_index * key_block
        keys_part = lax.dynamic_slice_in_dim(keys3, first_key, key_block, 0)
        values_part = lax.dynamic_slice_in_dim(values3, first_key, key_block, 0)
        key_pos = first_key + jnp.arange(key_block, dtype=jnp.int32)
        scores, allowed = block_scores(queries3, keys_part, query_pos, key_pos, length)
        probabilities = jnp.where(allowed, jnp.exp(scores - log_total[..., None]), 0.0).astype(
            jnp.bfloat16
        )
        return (
            running
            + jnp.einsum(
                "hrk,khd->rhd", probabilities, values_part, preferred_element_type=jnp.float32
            ),
            None,
        )

    initial = jnp.zeros(queries3.shape, jnp.float32)
    result, _ = lax.scan(
        attend_advance, initial, jnp.arange(keys3.shape[0] // key_block, dtype=jnp.int32)
    )
    return result


def query_grads(
    queries3, grads3, keys3, values3, query_pos, length, key_block, log_total, row_delta
):

    def query_advance(running, block_index):
        first_key = block_index * key_block
        keys_part = lax.dynamic_slice_in_dim(keys3, first_key, key_block, 0)
        values_part = lax.dynamic_slice_in_dim(values3, first_key, key_block, 0)
        key_pos = first_key + jnp.arange(key_block, dtype=jnp.int32)
        scores, allowed = block_scores(queries3, keys_part, query_pos, key_pos, length)
        probabilities = jnp.where(allowed, jnp.exp(scores - log_total[..., None]), 0.0)
        prob_grad = jnp.einsum(
            "rhd,khd->hrk", grads3, values_part, preferred_element_type=jnp.float32
        )
        score_low = (probabilities * (prob_grad - row_delta[..., None])).astype(jnp.bfloat16)
        return (
            running
            + jnp.einsum("hrk,khd->rhd", score_low, keys_part, preferred_element_type=jnp.float32),
            None,
        )

    initial = jnp.zeros(queries3.shape, jnp.float32)
    result, _ = lax.scan(
        query_advance, initial, jnp.arange(keys3.shape[0] // key_block, dtype=jnp.int32)
    )
    return result * HEAD ** (-0.5)


def key_side(queries3, grads3, log_part, delta_part, query_pos, keys3, values3, key_pos, length):
    key_count = keys3.shape[0]
    scores, allowed = block_scores(queries3, keys3, query_pos, key_pos, length)
    probabilities = jnp.where(allowed, jnp.exp(scores - log_part[..., None]), 0.0)
    prob_grad = jnp.einsum("rhd,khd->hrk", grads3, values3, preferred_element_type=jnp.float32)
    score_low = (probabilities * (prob_grad - delta_part[..., None])).astype(jnp.bfloat16)
    value_grad = jnp.einsum(
        "hrk,rhd->khd",
        probabilities.astype(jnp.bfloat16),
        grads3,
        preferred_element_type=jnp.float32,
    )
    key_grad = jnp.einsum(
        "hrk,rhd->khd", score_low, queries3, preferred_element_type=jnp.float32
    ) * HEAD ** (-0.5)
    return jnp.concatenate(
        [key_grad.reshape(key_count, HEADS * HEAD), value_grad.reshape(key_count, HEADS * HEAD)],
        axis=1,
    )


def slot_attention(queries3, keys3, values3, query_pos, length):
    key_pos = jnp.arange(keys3.shape[0], dtype=jnp.int32)
    scores, allowed = block_scores(queries3, keys3, query_pos, key_pos, length)
    masked = jnp.where(allowed, scores, masked_value)
    top = jnp.max(masked, axis=-1)
    kept_terms = jnp.where(allowed, jnp.exp(masked - top[..., None]), 0.0)
    log_total = top + jnp.log(jnp.sum(kept_terms, axis=-1))
    probabilities = jnp.where(allowed, jnp.exp(scores - log_total[..., None]), 0.0)
    probabilities_low = probabilities.astype(jnp.bfloat16)
    attended = jnp.einsum(
        "hrk,khd->rhd", probabilities_low, values3, preferred_element_type=jnp.float32
    )
    return attended, probabilities, probabilities_low


def slot_attention_grads(queries3, keys3, values3, grads3, attended, probabilities, probabilities_low):
    prob_grad = jnp.einsum("rhd,khd->hrk", grads3, values3, preferred_element_type=jnp.float32)
    row_delta = jnp.einsum("rhd,rhd->hr", grads3.astype(jnp.float32), attended)
    score_low = (probabilities * (prob_grad - row_delta[..., None])).astype(jnp.bfloat16)
    query_grad = jnp.einsum(
        "hrk,khd->rhd", score_low, keys3, preferred_element_type=jnp.float32
    ) * HEAD ** (-0.5)
    key_grad = jnp.einsum(
        "hrk,rhd->khd", score_low, queries3, preferred_element_type=jnp.float32
    ) * HEAD ** (-0.5)
    value_grad = jnp.einsum(
        "hrk,rhd->khd", probabilities_low, grads3, preferred_element_type=jnp.float32
    )
    return query_grad, key_grad, value_grad


def _pair_masks(scalars_ref, micro, row_count, key_count):
    length = scalars_ref[micro]
    first_row = scalars_ref[scalars_ref.shape[0] - 1]
    query_pos = first_row + lax.broadcasted_iota(jnp.int32, (row_count, key_count), 0)
    key_pos = lax.broadcasted_iota(jnp.int32, (row_count, key_count), 1)
    return (key_pos <= query_pos) & (key_pos < length)


def _forward_kernel(scalars_ref, q_ref, k_ref, v_ref, out_ref, lse_ref):
    micro = pl.program_id(0)
    row_count = q_ref.shape[0]
    key_count = k_ref.shape[0] * k_ref.shape[2]
    allowed = _pair_masks(scalars_ref, micro, row_count, key_count)
    k_all = k_ref[...].reshape(key_count, k_ref.shape[3])
    v_all = v_ref[...].reshape(key_count, v_ref.shape[3])
    for half in range(2):
        lanes = slice(half * HEAD, (half + 1) * HEAD)
        q_head = q_ref[:, lanes]
        k_head = k_all[:, lanes]
        v_head = v_all[:, lanes]
        scores = lax.dot_general(
            q_head, k_head, (((1,), (1,)), ((), ())), preferred_element_type=jnp.float32
        ) * HEAD ** (-0.5)
        masked = jnp.where(allowed, scores, masked_value)
        top = jnp.max(masked, axis=1, keepdims=True)
        kept = jnp.where(allowed, jnp.exp(masked - top), 0.0)
        total = jnp.sum(kept, axis=1, keepdims=True)
        log_total = top + jnp.log(total)
        probabilities = kept * (1.0 / total)
        attended = jnp.dot(
            probabilities.astype(jnp.bfloat16), v_head, preferred_element_type=jnp.float32
        )
        out_ref[:, lanes] = attended
        lse_ref[:, lanes] = jnp.broadcast_to(log_total, (row_count, HEAD))


def _backward_kernel(
    scalars_ref, q_ref, k_ref, v_ref, do_ref, o_ref, lse_ref, dq_ref, kv_grad_ref, pair_ref
):
    micro = pl.program_id(0)
    pair = pl.program_id(1)
    row_count = q_ref.shape[0]
    key_count = k_ref.shape[0] * k_ref.shape[2]
    allowed = _pair_masks(scalars_ref, micro, row_count, key_count)
    k_all = k_ref[...].reshape(key_count, k_ref.shape[3])
    v_all = v_ref[...].reshape(key_count, v_ref.shape[3])
    for half in range(2):
        lanes = slice(half * HEAD, (half + 1) * HEAD)
        q_head = q_ref[:, lanes]
        k_head = k_all[:, lanes]
        v_head = v_all[:, lanes]
        grad_head = do_ref[:, lanes]
        scores = lax.dot_general(
            q_head, k_head, (((1,), (1,)), ((), ())), preferred_element_type=jnp.float32
        ) * HEAD ** (-0.5)
        log_total = lse_ref[:, half * HEAD : half * HEAD + 1]
        probabilities = jnp.where(allowed, jnp.exp(scores - log_total), 0.0)
        probabilities_low = probabilities.astype(jnp.bfloat16)
        prob_grad = lax.dot_general(
            grad_head, v_head, (((1,), (1,)), ((), ())), preferred_element_type=jnp.float32
        )
        row_delta = jnp.sum(
            grad_head.astype(jnp.float32) * o_ref[:, lanes], axis=1, keepdims=True
        )
        score_low = (probabilities * (prob_grad - row_delta)).astype(jnp.bfloat16)
        dq_ref[:, lanes] = jnp.dot(
            score_low, k_head, preferred_element_type=jnp.float32
        ) * HEAD ** (-0.5)
        key_grad = lax.dot_general(
            score_low, q_head, (((0,), (0,)), ((), ())), preferred_element_type=jnp.float32
        ) * HEAD ** (-0.5)
        value_grad = lax.dot_general(
            probabilities_low, grad_head, (((0,), (0,)), ((), ())),
            preferred_element_type=jnp.float32,
        )
        pair_ref[0, :, lanes] = key_grad.astype(jnp.bfloat16)
        pair_ref[1, :, lanes] = value_grad.astype(jnp.bfloat16)
    half_width = kv_grad_ref.shape[1] // 2
    first_col = pl.multiple_of(pair * 2 * HEAD, 2 * HEAD)
    kv_grad_ref[:, pl.ds(first_col, 2 * HEAD)] = pair_ref[0]
    kv_grad_ref[:, pl.ds(first_col + half_width, 2 * HEAD)] = pair_ref[1]


def attention_forward(scalars, queries, kv_flat, batches):
    all_rows, model_width = queries.shape
    row_count = all_rows // batches
    devices = kv_flat.shape[0]
    key_count = devices * row_count
    pairs = model_width // (2 * HEAD)
    row_spec = pl.BlockSpec((row_count, 2 * HEAD), lambda m, p, s: (m, p))
    key_spec = pl.BlockSpec((devices, 1, row_count, 2 * HEAD), lambda m, p, s: (0, m, 0, p))
    value_spec = pl.BlockSpec(
        (devices, 1, row_count, 2 * HEAD), lambda m, p, s: (0, m, 0, pairs + p)
    )
    return pl.pallas_call(
        _forward_kernel,
        grid_spec=pltpu.PrefetchScalarGridSpec(
            num_scalar_prefetch=1,
            grid=(batches, pairs),
            in_specs=[row_spec, key_spec, value_spec],
            out_specs=[row_spec, row_spec],
        ),
        out_shape=[
            jax.ShapeDtypeStruct((all_rows, model_width), jnp.float32),
            jax.ShapeDtypeStruct((all_rows, model_width), jnp.float32),
        ],
        name="attention_forward",
    )(scalars, queries, kv_flat, kv_flat)


def attention_backward(scalars, queries, kv_flat, grads, attended, log_totals, batches):
    all_rows, model_width = queries.shape
    row_count = all_rows // batches
    devices = kv_flat.shape[0]
    key_count = devices * row_count
    pairs = model_width // (2 * HEAD)
    row_spec = pl.BlockSpec((row_count, 2 * HEAD), lambda m, p, s: (m, p))
    key_spec = pl.BlockSpec((devices, 1, row_count, 2 * HEAD), lambda m, p, s: (0, m, 0, p))
    value_spec = pl.BlockSpec(
        (devices, 1, row_count, 2 * HEAD), lambda m, p, s: (0, m, 0, pairs + p)
    )
    grad_spec = pl.BlockSpec((None, key_count, 2 * model_width), lambda m, p, s: (m, 0, 0))
    return pl.pallas_call(
        _backward_kernel,
        grid_spec=pltpu.PrefetchScalarGridSpec(
            num_scalar_prefetch=1,
            grid=(batches, pairs),
            in_specs=[row_spec, key_spec, value_spec, row_spec, row_spec, row_spec],
            out_specs=[row_spec, grad_spec],
            scratch_shapes=[pltpu.VMEM((2, key_count, 2 * HEAD), jnp.bfloat16)],
        ),
        out_shape=[
            jax.ShapeDtypeStruct((all_rows, model_width), jnp.float32),
            jax.ShapeDtypeStruct((batches, key_count, 2 * model_width), jnp.bfloat16),
        ],
        name="attention_backward",
    )(scalars, queries, kv_flat, kv_flat, grads, attended, log_totals)


def local(
    layer_input,
    history,
    cotangent,
    lengths,
    w_qkv,
    w_out,
    w_up,
    w_down,
    ln_gains,
    ln_biases,
    depth_weights,
):
    batches = layer_input.shape[0]
    row_count = layer_input.shape[2]
    model_width = layer_input.shape[3]
    ff_width = w_up.shape[1]
    shard_rows = w_qkv.shape[0]
    all_rows = batches * row_count
    slot_len = row_count * lax.axis_size("seq")
    positions = lax.axis_index("seq") * row_count + jnp.arange(row_count, dtype=jnp.int32)
    cosine_part, sine_part = rotary_tables(jnp.tile(positions, batches))
    gelu_tanh = partial(jax.nn.gelu, approximate=True)
    lane_pad = 128 - 4
    widths = (3 * model_width, 2, 2, lane_pad, model_width, ff_width, ff_width)
    offsets = [0]
    for width in widths:
        offsets.append(offsets[-1] + width)

    def pieces(packed_rows):
        return [packed_rows[:, offsets[i] : offsets[i + 1]] for i in range(len(widths))]

    packed = jnp.concatenate(
        [
            w_qkv,
            ln_gains,
            ln_biases,
            jnp.zeros((shard_rows, lane_pad), w_qkv.dtype),
            w_out,
            w_up,
            w_down.reshape(shard_rows, ff_width),
        ],
        axis=1,
    )
    gathered = lax.all_gather(packed, ("seq", "fsdp"), axis=0, tiled=True)
    full_qkv, gain_rows, bias_rows, _, full_out, full_up, down_rows = pieces(gathered)
    full_down = down_rows.reshape(ff_width, model_width)
    norm_gains = gain_rows.astype(jnp.float32)
    norm_biases = bias_rows.astype(jnp.float32)

    slot_lengths = lengths[:, 0]
    inputs = layer_input[:, 0].reshape(all_rows, model_width).astype(jnp.float32)
    first_low = layer_norm(inputs, norm_gains[:, 0], norm_biases[:, 0]).astype(jnp.bfloat16)
    projected = jnp.dot(first_low, full_qkv, preferred_element_type=jnp.float32)
    queries = rotate(projected[:, :model_width], cosine_part, sine_part).astype(jnp.bfloat16)
    keys_own = rotate(
        projected[:, model_width : 2 * model_width], cosine_part, sine_part
    ).astype(jnp.bfloat16)
    values_own = projected[:, 2 * model_width :].astype(jnp.bfloat16)
    own_kv = jnp.concatenate([keys_own, values_own], axis=1).reshape(
        batches, row_count, 2 * model_width
    )
    earlier = history[:, :, 0].reshape(4, all_rows, model_width).astype(jnp.float32)
    usable = (positions[None, :] < slot_lengths[:, None]).reshape(all_rows, 1)
    grad_next = jnp.where(
        usable, cotangent[:, 0].reshape(all_rows, model_width).astype(jnp.float32), 0.0
    )
    history_part = (
        depth_weights[0] * earlier[0]
        + depth_weights[1] * earlier[1]
        + depth_weights[2] * earlier[2]
        + depth_weights[3] * earlier[3]
    )
    grad_history = (depth_weights[:4, None, None] * grad_next[None]).astype(jnp.bfloat16)
    grad_history = grad_history.reshape(4, batches, 1, row_count, model_width)
    out_grad = depth_weights[4] * grad_next
    out_low = out_grad.astype(jnp.bfloat16)

    kv_flat = lax.all_gather(own_kv, "seq", axis=0, tiled=False)
    scalars = jnp.concatenate(
        [slot_lengths.astype(jnp.int32), (lax.axis_index("seq") * row_count)[None].astype(jnp.int32)]
    )
    attended_rows, log_totals = attention_forward(scalars, queries, kv_flat, batches)
    attended_low = attended_rows.astype(jnp.bfloat16)
    residual = inputs + jnp.dot(attended_low, full_out, preferred_element_type=jnp.float32)
    second_low = layer_norm(residual, norm_gains[:, 1], norm_biases[:, 1]).astype(jnp.bfloat16)
    hidden = jnp.dot(second_low, full_up, preferred_element_type=jnp.float32)
    hidden_low = gelu_tanh(hidden).astype(jnp.bfloat16)
    block_out = residual + jnp.dot(hidden_low, full_down, preferred_element_type=jnp.float32)
    hidden_grad = jnp.einsum("rd,fd->rf", out_low, full_down, preferred_element_type=jnp.float32)
    _, gelu_pullback = jax.vjp(gelu_tanh, hidden)
    up_low = gelu_pullback(hidden_grad)[0].astype(jnp.bfloat16)
    second_grad = jnp.einsum("rf,df->rd", up_low, full_up, preferred_element_type=jnp.float32)
    _, second_pullback = jax.vjp(layer_norm, residual, norm_gains[:, 1], norm_biases[:, 1])
    residual_part, gain_two, bias_two = second_pullback(second_grad)
    residual_grad = out_grad + residual_part
    branch_low = residual_grad.astype(jnp.bfloat16)
    attended_grad = jnp.einsum(
        "rd,cd->rc", branch_low, full_out, preferred_element_type=jnp.float32
    ).astype(jnp.bfloat16)
    query_grad, kv_grad_flat = attention_backward(
        scalars, queries, kv_flat, attended_grad, attended_rows, log_totals, batches
    )
    micro_major = Layout(major_to_minor=(1, 0, 2))
    kv_grad_own = lax.psum_scatter(
        with_layout_constraint(jnp.swapaxes(kv_grad_flat, 0, 1), micro_major),
        "seq",
        scatter_dimension=0,
        tiled=True,
    )
    kv_grad_own = with_layout_constraint(kv_grad_own, micro_major)
    block_side = block_out
    combined = depth_weights[4] * block_side + history_part
    next_input = combined.astype(jnp.bfloat16).reshape(batches, 1, row_count, model_width)
    depth_terms = jnp.concatenate(
        [jnp.sum(earlier * grad_next[None], axis=(1, 2)), jnp.sum(block_side * grad_next)[None]]
    )
    grad_down = jnp.einsum("rf,rd->fd", hidden_low, out_low, preferred_element_type=jnp.float32)
    grad_up = jnp.einsum("rd,rf->df", second_low, up_low, preferred_element_type=jnp.float32)
    grad_outproj = jnp.einsum(
        "rc,rd->cd", attended_low, branch_low, preferred_element_type=jnp.float32
    )
    early_grads = jnp.concatenate(
        [
            jnp.zeros((model_width, 3 * model_width), jnp.float32),
            grad_outproj,
            grad_up,
            grad_down.reshape(model_width, ff_width),
        ],
        axis=1,
    ).astype(jnp.bfloat16)
    kv_grad_own, early_grads = lax.optimization_barrier((kv_grad_own, early_grads))
    kv_grad_own = jnp.swapaxes(kv_grad_own, 0, 1).reshape(all_rows, 2 * model_width)
    key_value_all = kv_grad_own.astype(jnp.float32)
    qkv_low = jnp.concatenate(
        [
            rotate(query_grad, cosine_part, -sine_part),
            rotate(key_value_all[:, :model_width], cosine_part, -sine_part),
            key_value_all[:, model_width:],
        ],
        axis=1,
    ).astype(jnp.bfloat16)
    grad_qkv = jnp.einsum("rd,rc->dc", first_low, qkv_low, preferred_element_type=jnp.float32)
    first_grad = jnp.einsum("rc,dc->rd", qkv_low, full_qkv, preferred_element_type=jnp.float32)
    _, first_pullback = jax.vjp(layer_norm, inputs, norm_gains[:, 0], norm_biases[:, 0])
    input_part, gain_one, bias_one = first_pullback(first_grad)
    grad_input = (residual_grad + input_part).astype(jnp.bfloat16)
    grad_input = grad_input.reshape(batches, 1, row_count, model_width)
    packed_grads = lax.dynamic_update_slice(early_grads, grad_qkv.astype(jnp.bfloat16), (0, 0))
    device_count = model_width // shard_rows
    row_major = Layout(major_to_minor=(0, 1, 2))
    grad_offsets = [0]
    for width in (3 * model_width, model_width, ff_width, ff_width):
        grad_offsets.append(grad_offsets[-1] + width)
    scattered = lax.psum_scatter(
        with_layout_constraint(
            packed_grads.reshape(device_count, shard_rows, grad_offsets[-1]), row_major
        ),
        ("seq", "fsdp"),
        scatter_dimension=0,
        tiled=False,
    )
    scattered = with_layout_constraint(scattered, Layout(major_to_minor=(0, 1)))
    scattered = scattered.astype(jnp.float32)
    full_pieces = [scattered[:, grad_offsets[i] : grad_offsets[i + 1]] for i in range(4)]
    small_sums = lax.psum(
        jnp.concatenate(
            [
                depth_terms,
                jnp.stack([gain_one, gain_two, bias_one, bias_two], axis=1).reshape(-1),
            ]
        ),
        ("seq", "fsdp"),
    )
    depth_total = small_sums[:5]
    device_index = lax.axis_index("seq") * lax.axis_size("fsdp") + lax.axis_index("fsdp")
    norm_owned = lax.dynamic_slice_in_dim(
        small_sums[5:].reshape(model_width, 4), device_index * shard_rows, shard_rows, 0
    )
    owned = [
        full_pieces[0],
        full_pieces[1],
        full_pieces[2],
        full_pieces[3].reshape(-1, model_width),
        norm_owned[:, :2],
        norm_owned[:, 2:],
    ]
    return (next_input, grad_input, grad_history, *owned, depth_total)


def solution(mesh):
    in_specs = (
        P(None, "fsdp", "seq", None),
        P(None, None, "fsdp", "seq", None),
        P(None, "fsdp", "seq", None),
        P(None, "fsdp"),
        P(("seq", "fsdp"), None),
        P(("seq", "fsdp"), None),
        P(("seq", "fsdp"), None),
        P(("seq", "fsdp"), None),
        P(("seq", "fsdp"), None),
        P(("seq", "fsdp"), None),
        P(),
    )
    out_specs = (
        P(None, "fsdp", "seq", None),
        P(None, "fsdp", "seq", None),
        P(None, None, "fsdp", "seq", None),
        P(("seq", "fsdp"), None),
        P(("seq", "fsdp"), None),
        P(("seq", "fsdp"), None),
        P(("seq", "fsdp"), None),
        P(("seq", "fsdp"), None),
        P(("seq", "fsdp"), None),
        P(),
    )
    return jax.shard_map(local, mesh=mesh, in_specs=in_specs, out_specs=out_specs, check_vma=False)
```

```python
from functools import partial
import math

import jax
import jax.numpy as jnp
from jax import lax
from jax.sharding import PartitionSpec as P
from jax.experimental.layout import Layout, with_layout_constraint
from jax.experimental import pallas as pl
from jax.experimental.pallas import tpu as pltpu

HEADS = 12
HEAD = 64


epsilon = 1e-05
masked_value = -1e30


def layer_norm(values, gain_vector, bias_vector):
    center = values - jnp.mean(values, axis=-1, keepdims=True)
    spread = jnp.mean(center * center, axis=-1, keepdims=True)
    return center * lax.rsqrt(spread + epsilon) * gain_vector + bias_vector


def rotary_tables(positions):
    half_width = HEAD // 2
    frequencies = 10000.0 ** (-jnp.arange(half_width, dtype=jnp.float32) / half_width)
    angles = positions.astype(jnp.float32)[:, None] * frequencies[None, :]
    return (jnp.cos(angles)[:, None, :], jnp.sin(angles)[:, None, :])


def rotate(values, cosine_part, sine_part):
    row_count = values.shape[0]
    shaped = values.reshape(row_count, HEADS, HEAD)
    half_width = HEAD // 2
    first_half = shaped[..., :half_width]
    second_half = shaped[..., half_width:]
    turned = jnp.concatenate(
        [
            first_half * cosine_part - second_half * sine_part,
            second_half * cosine_part + first_half * sine_part,
        ],
        axis=-1,
    )
    return turned.reshape(row_count, HEADS * HEAD)


def block_scores(queries3, keys3, query_pos, key_pos, length):
    scores = jnp.einsum(
        "rhd,khd->hrk", queries3, keys3, preferred_element_type=jnp.float32
    ) * HEAD ** (-0.5)
    allowed = (key_pos[None, :] <= query_pos[:, None]) & (key_pos[None, :] < length)
    return (scores, allowed[None])


def row_totals(queries3, keys3, query_pos, length, key_block):
    row_count = queries3.shape[0]

    def row_advance(state, block_index):
        running_top, running_sum = state
        first_key = block_index * key_block
        keys_part = lax.dynamic_slice_in_dim(keys3, first_key, key_block, 0)
        key_pos = first_key + jnp.arange(key_block, dtype=jnp.int32)
        scores, allowed = block_scores(queries3, keys_part, query_pos, key_pos, length)
        masked = jnp.where(allowed, scores, masked_value)
        new_top = jnp.maximum(running_top, jnp.max(masked, axis=-1))
        kept_terms = jnp.where(allowed, jnp.exp(masked - new_top[..., None]), 0.0)
        running_sum = running_sum * jnp.exp(running_top - new_top) + jnp.sum(kept_terms, axis=-1)
        return ((new_top, running_sum), None)

    initial = (
        jnp.full((HEADS, row_count), masked_value, jnp.float32),
        jnp.zeros((HEADS, row_count), jnp.float32),
    )
    (row_tops, row_sums), _ = lax.scan(
        row_advance, initial, jnp.arange(keys3.shape[0] // key_block, dtype=jnp.int32)
    )
    return row_tops + jnp.log(row_sums)


def attend(queries3, keys3, values3, query_pos, length, key_block, log_total):

    def attend_advance(running, block_index):
        first_key = block_index * key_block
        keys_part = lax.dynamic_slice_in_dim(keys3, first_key, key_block, 0)
        values_part = lax.dynamic_slice_in_dim(values3, first_key, key_block, 0)
        key_pos = first_key + jnp.arange(key_block, dtype=jnp.int32)
        scores, allowed = block_scores(queries3, keys_part, query_pos, key_pos, length)
        probabilities = jnp.where(allowed, jnp.exp(scores - log_total[..., None]), 0.0).astype(
            jnp.bfloat16
        )
        return (
            running
            + jnp.einsum(
                "hrk,khd->rhd", probabilities, values_part, preferred_element_type=jnp.float32
            ),
            None,
        )

    initial = jnp.zeros(queries3.shape, jnp.float32)
    result, _ = lax.scan(
        attend_advance, initial, jnp.arange(keys3.shape[0] // key_block, dtype=jnp.int32)
    )
    return result


def query_grads(
    queries3, grads3, keys3, values3, query_pos, length, key_block, log_total, row_delta
):

    def query_advance(running, block_index):
        first_key = block_index * key_block
        keys_part = lax.dynamic_slice_in_dim(keys3, first_key, key_block, 0)
        values_part = lax.dynamic_slice_in_dim(values3, first_key, key_block, 0)
        key_pos = first_key + jnp.arange(key_block, dtype=jnp.int32)
        scores, allowed = block_scores(queries3, keys_part, query_pos, key_pos, length)
        probabilities = jnp.where(allowed, jnp.exp(scores - log_total[..., None]), 0.0)
        prob_grad = jnp.einsum(
            "rhd,khd->hrk", grads3, values_part, preferred_element_type=jnp.float32
        )
        score_low = (probabilities * (prob_grad - row_delta[..., None])).astype(jnp.bfloat16)
        return (
            running
            + jnp.einsum("hrk,khd->rhd", score_low, keys_part, preferred_element_type=jnp.float32),
            None,
        )

    initial = jnp.zeros(queries3.shape, jnp.float32)
    result, _ = lax.scan(
        query_advance, initial, jnp.arange(keys3.shape[0] // key_block, dtype=jnp.int32)
    )
    return result * HEAD ** (-0.5)


def key_side(queries3, grads3, log_part, delta_part, query_pos, keys3, values3, key_pos, length):
    key_count = keys3.shape[0]
    scores, allowed = block_scores(queries3, keys3, query_pos, key_pos, length)
    probabilities = jnp.where(allowed, jnp.exp(scores - log_part[..., None]), 0.0)
    prob_grad = jnp.einsum("rhd,khd->hrk", grads3, values3, preferred_element_type=jnp.float32)
    score_low = (probabilities * (prob_grad - delta_part[..., None])).astype(jnp.bfloat16)
    value_grad = jnp.einsum(
        "hrk,rhd->khd",
        probabilities.astype(jnp.bfloat16),
        grads3,
        preferred_element_type=jnp.float32,
    )
    key_grad = jnp.einsum(
        "hrk,rhd->khd", score_low, queries3, preferred_element_type=jnp.float32
    ) * HEAD ** (-0.5)
    return jnp.concatenate(
        [key_grad.reshape(key_count, HEADS * HEAD), value_grad.reshape(key_count, HEADS * HEAD)],
        axis=1,
    )


def slot_attention(queries3, keys3, values3, query_pos, length):
    key_pos = jnp.arange(keys3.shape[0], dtype=jnp.int32)
    scores, allowed = block_scores(queries3, keys3, query_pos, key_pos, length)
    masked = jnp.where(allowed, scores, masked_value)
    top = jnp.max(masked, axis=-1)
    kept_terms = jnp.where(allowed, jnp.exp(masked - top[..., None]), 0.0)
    log_total = top + jnp.log(jnp.sum(kept_terms, axis=-1))
    probabilities = jnp.where(allowed, jnp.exp(scores - log_total[..., None]), 0.0)
    probabilities_low = probabilities.astype(jnp.bfloat16)
    attended = jnp.einsum(
        "hrk,khd->rhd", probabilities_low, values3, preferred_element_type=jnp.float32
    )
    return attended, probabilities, probabilities_low


def slot_attention_grads(queries3, keys3, values3, grads3, attended, probabilities, probabilities_low):
    prob_grad = jnp.einsum("rhd,khd->hrk", grads3, values3, preferred_element_type=jnp.float32)
    row_delta = jnp.einsum("rhd,rhd->hr", grads3.astype(jnp.float32), attended)
    score_low = (probabilities * (prob_grad - row_delta[..., None])).astype(jnp.bfloat16)
    query_grad = jnp.einsum(
        "hrk,khd->rhd", score_low, keys3, preferred_element_type=jnp.float32
    ) * HEAD ** (-0.5)
    key_grad = jnp.einsum(
        "hrk,rhd->khd", score_low, queries3, preferred_element_type=jnp.float32
    ) * HEAD ** (-0.5)
    value_grad = jnp.einsum(
        "hrk,rhd->khd", probabilities_low, grads3, preferred_element_type=jnp.float32
    )
    return query_grad, key_grad, value_grad


def _pair_masks(scalars_ref, micro, row_count, key_count):
    length = scalars_ref[micro]
    first_row = scalars_ref[scalars_ref.shape[0] - 1]
    query_pos = first_row + lax.broadcasted_iota(jnp.int32, (row_count, key_count), 0)
    key_pos = lax.broadcasted_iota(jnp.int32, (row_count, key_count), 1)
    return (key_pos <= query_pos) & (key_pos < length)


def _forward_kernel(scalars_ref, q_ref, k_ref, v_ref, out_ref, lse_ref):
    micro = pl.program_id(0)
    row_count = q_ref.shape[0]
    key_count = k_ref.shape[0] * k_ref.shape[2]
    allowed = _pair_masks(scalars_ref, micro, row_count, key_count)
    k_all = k_ref[...].reshape(key_count, k_ref.shape[3])
    v_all = v_ref[...].reshape(key_count, v_ref.shape[3])
    for half in range(2):
        lanes = slice(half * HEAD, (half + 1) * HEAD)
        q_head = q_ref[:, lanes]
        k_head = k_all[:, lanes]
        v_head = v_all[:, lanes]
        scores = lax.dot_general(
            q_head, k_head, (((1,), (1,)), ((), ())), preferred_element_type=jnp.float32
        ) * HEAD ** (-0.5)
        masked = jnp.where(allowed, scores, masked_value)
        top = jnp.max(masked, axis=1, keepdims=True)
        kept = jnp.exp(masked - top)
        total = jnp.sum(kept, axis=1, keepdims=True)
        log_total = top + jnp.log(total)
        probabilities = kept * (1.0 / total)
        attended = jnp.dot(
            probabilities.astype(jnp.bfloat16), v_head, preferred_element_type=jnp.float32
        )
        out_ref[:, lanes] = attended
        lse_ref[:, lanes] = jnp.broadcast_to(log_total, (row_count, HEAD))


def _backward_kernel(
    scalars_ref, q_ref, k_ref, v_ref, do_ref, o_ref, lse_ref, dq_ref, kv_grad_ref, pair_ref
):
    micro = pl.program_id(0)
    pair = pl.program_id(1)
    row_count = q_ref.shape[0]
    key_count = k_ref.shape[0] * k_ref.shape[2]
    allowed = _pair_masks(scalars_ref, micro, row_count, key_count)
    k_all = k_ref[...].reshape(key_count, k_ref.shape[3])
    v_all = v_ref[...].reshape(key_count, v_ref.shape[3])
    for half in range(2):
        lanes = slice(half * HEAD, (half + 1) * HEAD)
        q_head = q_ref[:, lanes]
        k_head = k_all[:, lanes]
        v_head = v_all[:, lanes]
        grad_head = do_ref[:, lanes]
        scores = lax.dot_general(
            q_head, k_head, (((1,), (1,)), ((), ())), preferred_element_type=jnp.float32
        ) * HEAD ** (-0.5)
        log_total = lse_ref[:, half * HEAD : half * HEAD + 1]
        probabilities = jnp.where(allowed, jnp.exp(scores - log_total), 0.0)
        probabilities_low = probabilities.astype(jnp.bfloat16)
        prob_grad = lax.dot_general(
            grad_head, v_head, (((1,), (1,)), ((), ())), preferred_element_type=jnp.float32
        )
        row_delta = jnp.sum(
            grad_head.astype(jnp.float32) * o_ref[:, lanes], axis=1, keepdims=True
        )
        score_low = (probabilities * (prob_grad - row_delta)).astype(jnp.bfloat16)
        dq_ref[:, lanes] = jnp.dot(
            score_low, k_head, preferred_element_type=jnp.float32
        ) * HEAD ** (-0.5)
        key_grad = lax.dot_general(
            score_low, q_head, (((0,), (0,)), ((), ())), preferred_element_type=jnp.float32
        ) * HEAD ** (-0.5)
        value_grad = lax.dot_general(
            probabilities_low, grad_head, (((0,), (0,)), ((), ())),
            preferred_element_type=jnp.float32,
        )
        pair_ref[0, :, lanes] = key_grad.astype(jnp.bfloat16)
        pair_ref[1, :, lanes] = value_grad.astype(jnp.bfloat16)
    half_width = kv_grad_ref.shape[1] // 2
    first_col = pl.multiple_of(pair * 2 * HEAD, 2 * HEAD)
    kv_grad_ref[:, pl.ds(first_col, 2 * HEAD)] = pair_ref[0]
    kv_grad_ref[:, pl.ds(first_col + half_width, 2 * HEAD)] = pair_ref[1]


def attention_forward(scalars, queries, kv_flat, batches):
    all_rows, model_width = queries.shape
    row_count = all_rows // batches
    devices = kv_flat.shape[0]
    key_count = devices * row_count
    pairs = model_width // (2 * HEAD)
    row_spec = pl.BlockSpec((row_count, 2 * HEAD), lambda m, p, s: (m, p))
    key_spec = pl.BlockSpec((devices, 1, row_count, 2 * HEAD), lambda m, p, s: (0, m, 0, p))
    value_spec = pl.BlockSpec(
        (devices, 1, row_count, 2 * HEAD), lambda m, p, s: (0, m, 0, pairs + p)
    )
    return pl.pallas_call(
        _forward_kernel,
        grid_spec=pltpu.PrefetchScalarGridSpec(
            num_scalar_prefetch=1,
            grid=(batches, pairs),
            in_specs=[row_spec, key_spec, value_spec],
            out_specs=[row_spec, row_spec],
        ),
        out_shape=[
            jax.ShapeDtypeStruct((all_rows, model_width), jnp.float32),
            jax.ShapeDtypeStruct((all_rows, model_width), jnp.float32),
        ],
        name="attention_forward",
    )(scalars, queries, kv_flat, kv_flat)


def attention_backward(scalars, queries, kv_flat, grads, attended, log_totals, batches):
    all_rows, model_width = queries.shape
    row_count = all_rows // batches
    devices = kv_flat.shape[0]
    key_count = devices * row_count
    pairs = model_width // (2 * HEAD)
    row_spec = pl.BlockSpec((row_count, 2 * HEAD), lambda m, p, s: (m, p))
    key_spec = pl.BlockSpec((devices, 1, row_count, 2 * HEAD), lambda m, p, s: (0, m, 0, p))
    value_spec = pl.BlockSpec(
        (devices, 1, row_count, 2 * HEAD), lambda m, p, s: (0, m, 0, pairs + p)
    )
    grad_spec = pl.BlockSpec((None, key_count, 2 * model_width), lambda m, p, s: (m, 0, 0))
    return pl.pallas_call(
        _backward_kernel,
        grid_spec=pltpu.PrefetchScalarGridSpec(
            num_scalar_prefetch=1,
            grid=(batches, pairs),
            in_specs=[row_spec, key_spec, value_spec, row_spec, row_spec, row_spec],
            out_specs=[row_spec, grad_spec],
            scratch_shapes=[pltpu.VMEM((2, key_count, 2 * HEAD), jnp.bfloat16)],
        ),
        out_shape=[
            jax.ShapeDtypeStruct((all_rows, model_width), jnp.float32),
            jax.ShapeDtypeStruct((batches, key_count, 2 * model_width), jnp.bfloat16),
        ],
        name="attention_backward",
    )(scalars, queries, kv_flat, kv_flat, grads, attended, log_totals)


def local(
    layer_input,
    history,
    cotangent,
    lengths,
    w_qkv,
    w_out,
    w_up,
    w_down,
    ln_gains,
    ln_biases,
    depth_weights,
):
    batches = layer_input.shape[0]
    row_count = layer_input.shape[2]
    model_width = layer_input.shape[3]
    ff_width = w_up.shape[1]
    shard_rows = w_qkv.shape[0]
    all_rows = batches * row_count
    slot_len = row_count * lax.axis_size("seq")
    positions = lax.axis_index("seq") * row_count + jnp.arange(row_count, dtype=jnp.int32)
    cosine_part, sine_part = rotary_tables(jnp.tile(positions, batches))
    gelu_tanh = partial(jax.nn.gelu, approximate=True)
    lane_pad = 128 - 4
    widths = (3 * model_width, 2, 2, lane_pad, model_width, ff_width, ff_width)
    offsets = [0]
    for width in widths:
        offsets.append(offsets[-1] + width)

    def pieces(packed_rows):
        return [packed_rows[:, offsets[i] : offsets[i + 1]] for i in range(len(widths))]

    packed = jnp.concatenate(
        [
            w_qkv,
            ln_gains,
            ln_biases,
            jnp.zeros((shard_rows, lane_pad), w_qkv.dtype),
            w_out,
            w_up,
            w_down.reshape(shard_rows, ff_width),
        ],
        axis=1,
    )
    gathered = lax.all_gather(packed, ("seq", "fsdp"), axis=0, tiled=True)
    full_qkv, gain_rows, bias_rows, _, full_out, full_up, down_rows = pieces(gathered)
    full_down = down_rows.reshape(ff_width, model_width)
    norm_gains = gain_rows.astype(jnp.float32)
    norm_biases = bias_rows.astype(jnp.float32)

    slot_lengths = lengths[:, 0]
    inputs = layer_input[:, 0].reshape(all_rows, model_width).astype(jnp.float32)
    first_low = layer_norm(inputs, norm_gains[:, 0], norm_biases[:, 0]).astype(jnp.bfloat16)
    projected = jnp.dot(first_low, full_qkv, preferred_element_type=jnp.float32)
    queries = rotate(projected[:, :model_width], cosine_part, sine_part).astype(jnp.bfloat16)
    keys_own = rotate(
        projected[:, model_width : 2 * model_width], cosine_part, sine_part
    ).astype(jnp.bfloat16)
    values_own = projected[:, 2 * model_width :].astype(jnp.bfloat16)
    own_kv = jnp.concatenate([keys_own, values_own], axis=1).reshape(
        batches, row_count, 2 * model_width
    )
    earlier = history[:, :, 0].reshape(4, all_rows, model_width).astype(jnp.float32)
    usable = (positions[None, :] < slot_lengths[:, None]).reshape(all_rows, 1)
    grad_next = jnp.where(
        usable, cotangent[:, 0].reshape(all_rows, model_width).astype(jnp.float32), 0.0
    )
    history_part = (
        depth_weights[0] * earlier[0]
        + depth_weights[1] * earlier[1]
        + depth_weights[2] * earlier[2]
        + depth_weights[3] * earlier[3]
    )
    grad_history = (depth_weights[:4, None, None] * grad_next[None]).astype(jnp.bfloat16)
    grad_history = grad_history.reshape(4, batches, 1, row_count, model_width)
    out_grad = depth_weights[4] * grad_next
    out_low = out_grad.astype(jnp.bfloat16)

    kv_flat = lax.all_gather(own_kv, "seq", axis=0, tiled=False)
    scalars = jnp.concatenate(
        [slot_lengths.astype(jnp.int32), (lax.axis_index("seq") * row_count)[None].astype(jnp.int32)]
    )
    attended_rows, log_totals = attention_forward(scalars, queries, kv_flat, batches)
    attended_low = attended_rows.astype(jnp.bfloat16)
    residual = inputs + jnp.dot(attended_low, full_out, preferred_element_type=jnp.float32)
    second_low = layer_norm(residual, norm_gains[:, 1], norm_biases[:, 1]).astype(jnp.bfloat16)
    hidden = jnp.dot(second_low, full_up, preferred_element_type=jnp.float32)
    hidden_low = gelu_tanh(hidden).astype(jnp.bfloat16)
    block_out = residual + jnp.dot(hidden_low, full_down, preferred_element_type=jnp.float32)
    hidden_grad = jnp.einsum("rd,fd->rf", out_low, full_down, preferred_element_type=jnp.float32)
    _, gelu_pullback = jax.vjp(gelu_tanh, hidden)
    up_low = gelu_pullback(hidden_grad)[0].astype(jnp.bfloat16)
    second_grad = jnp.einsum("rf,df->rd", up_low, full_up, preferred_element_type=jnp.float32)
    _, second_pullback = jax.vjp(layer_norm, residual, norm_gains[:, 1], norm_biases[:, 1])
    residual_part, gain_two, bias_two = second_pullback(second_grad)
    residual_grad = out_grad + residual_part
    branch_low = residual_grad.astype(jnp.bfloat16)
    attended_grad = jnp.einsum(
        "rd,cd->rc", branch_low, full_out, preferred_element_type=jnp.float32
    ).astype(jnp.bfloat16)
    query_grad, kv_grad_flat = attention_backward(
        scalars, queries, kv_flat, attended_grad, attended_rows, log_totals, batches
    )
    micro_major = Layout(major_to_minor=(1, 0, 2))
    kv_grad_own = lax.psum_scatter(
        with_layout_constraint(jnp.swapaxes(kv_grad_flat, 0, 1), micro_major),
        "seq",
        scatter_dimension=0,
        tiled=True,
    )
    kv_grad_own = with_layout_constraint(kv_grad_own, micro_major)
    block_side = block_out
    combined = depth_weights[4] * block_side + history_part
    next_input = combined.astype(jnp.bfloat16).reshape(batches, 1, row_count, model_width)
    depth_terms = jnp.concatenate(
        [jnp.sum(earlier * grad_next[None], axis=(1, 2)), jnp.sum(block_side * grad_next)[None]]
    )
    grad_down = jnp.einsum("rf,rd->fd", hidden_low, out_low, preferred_element_type=jnp.float32)
    grad_up = jnp.einsum("rd,rf->df", second_low, up_low, preferred_element_type=jnp.float32)
    grad_outproj = jnp.einsum(
        "rc,rd->cd", attended_low, branch_low, preferred_element_type=jnp.float32
    )
    early_grads = jnp.concatenate(
        [
            jnp.zeros((model_width, 3 * model_width), jnp.float32),
            grad_outproj,
            grad_up,
            grad_down.reshape(model_width, ff_width),
        ],
        axis=1,
    ).astype(jnp.bfloat16)
    kv_grad_own, early_grads = lax.optimization_barrier((kv_grad_own, early_grads))
    kv_grad_own = jnp.swapaxes(kv_grad_own, 0, 1).reshape(all_rows, 2 * model_width)
    key_value_all = kv_grad_own.astype(jnp.float32)
    qkv_low = jnp.concatenate(
        [
            rotate(query_grad, cosine_part, -sine_part),
            rotate(key_value_all[:, :model_width], cosine_part, -sine_part),
            key_value_all[:, model_width:],
        ],
        axis=1,
    ).astype(jnp.bfloat16)
    grad_qkv = jnp.einsum("rd,rc->dc", first_low, qkv_low, preferred_element_type=jnp.float32)
    first_grad = jnp.einsum("rc,dc->rd", qkv_low, full_qkv, preferred_element_type=jnp.float32)
    _, first_pullback = jax.vjp(layer_norm, inputs, norm_gains[:, 0], norm_biases[:, 0])
    input_part, gain_one, bias_one = first_pullback(first_grad)
    grad_input = (residual_grad + input_part).astype(jnp.bfloat16)
    grad_input = grad_input.reshape(batches, 1, row_count, model_width)
    packed_grads = lax.dynamic_update_slice(early_grads, grad_qkv.astype(jnp.bfloat16), (0, 0))
    device_count = model_width // shard_rows
    row_major = Layout(major_to_minor=(0, 1, 2))
    grad_offsets = [0]
    for width in (3 * model_width, model_width, ff_width, ff_width):
        grad_offsets.append(grad_offsets[-1] + width)
    scattered = lax.psum_scatter(
        with_layout_constraint(
            packed_grads.reshape(device_count, shard_rows, grad_offsets[-1]), row_major
        ),
        ("seq", "fsdp"),
        scatter_dimension=0,
        tiled=False,
    )
    scattered = with_layout_constraint(scattered, Layout(major_to_minor=(0, 1)))
    scattered = scattered.astype(jnp.float32)
    full_pieces = [scattered[:, grad_offsets[i] : grad_offsets[i + 1]] for i in range(4)]
    small_sums = lax.psum(
        jnp.concatenate(
            [
                depth_terms,
                jnp.stack([gain_one, gain_two, bias_one, bias_two], axis=1).reshape(-1),
            ]
        ),
        ("seq", "fsdp"),
    )
    depth_total = small_sums[:5]
    device_index = lax.axis_index("seq") * lax.axis_size("fsdp") + lax.axis_index("fsdp")
    norm_owned = lax.dynamic_slice_in_dim(
        small_sums[5:].reshape(model_width, 4), device_index * shard_rows, shard_rows, 0
    )
    owned = [
        full_pieces[0],
        full_pieces[1],
        full_pieces[2],
        full_pieces[3].reshape(-1, model_width),
        norm_owned[:, :2],
        norm_owned[:, 2:],
    ]
    return (next_input, grad_input, grad_history, *owned, depth_total)


def solution(mesh):
    in_specs = (
        P(None, "fsdp", "seq", None),
        P(None, None, "fsdp", "seq", None),
        P(None, "fsdp", "seq", None),
        P(None, "fsdp"),
        P(("seq", "fsdp"), None),
        P(("seq", "fsdp"), None),
        P(("seq", "fsdp"), None),
        P(("seq", "fsdp"), None),
        P(("seq", "fsdp"), None),
        P(("seq", "fsdp"), None),
        P(),
    )
    out_specs = (
        P(None, "fsdp", "seq", None),
        P(None, "fsdp", "seq", None),
        P(None, None, "fsdp", "seq", None),
        P(("seq", "fsdp"), None),
        P(("seq", "fsdp"), None),
        P(("seq", "fsdp"), None),
        P(("seq", "fsdp"), None),
        P(("seq", "fsdp"), None),
        P(("seq", "fsdp"), None),
        P(),
    )
    return jax.shard_map(local, mesh=mesh, in_specs=in_specs, out_specs=out_specs, check_vma=False)
```

```python
from functools import partial
import math

import jax
import jax.numpy as jnp
from jax import lax
from jax.sharding import PartitionSpec as P
from jax.experimental.layout import Layout, with_layout_constraint
from jax.experimental import pallas as pl
from jax.experimental.pallas import tpu as pltpu

HEADS = 12
HEAD = 64


epsilon = 1e-05
masked_value = -1e30


def layer_norm(values, gain_vector, bias_vector):
    center = values - jnp.mean(values, axis=-1, keepdims=True)
    spread = jnp.mean(center * center, axis=-1, keepdims=True)
    return center * lax.rsqrt(spread + epsilon) * gain_vector + bias_vector


def rotary_tables(positions):
    half_width = HEAD // 2
    frequencies = 10000.0 ** (-jnp.arange(half_width, dtype=jnp.float32) / half_width)
    angles = positions.astype(jnp.float32)[:, None] * frequencies[None, :]
    return (jnp.cos(angles)[:, None, :], jnp.sin(angles)[:, None, :])


def rotate(values, cosine_part, sine_part):
    row_count = values.shape[0]
    shaped = values.reshape(row_count, HEADS, HEAD)
    half_width = HEAD // 2
    first_half = shaped[..., :half_width]
    second_half = shaped[..., half_width:]
    turned = jnp.concatenate(
        [
            first_half * cosine_part - second_half * sine_part,
            second_half * cosine_part + first_half * sine_part,
        ],
        axis=-1,
    )
    return turned.reshape(row_count, HEADS * HEAD)


def block_scores(queries3, keys3, query_pos, key_pos, length):
    scores = jnp.einsum(
        "rhd,khd->hrk", queries3, keys3, preferred_element_type=jnp.float32
    ) * HEAD ** (-0.5)
    allowed = (key_pos[None, :] <= query_pos[:, None]) & (key_pos[None, :] < length)
    return (scores, allowed[None])


def row_totals(queries3, keys3, query_pos, length, key_block):
    row_count = queries3.shape[0]

    def row_advance(state, block_index):
        running_top, running_sum = state
        first_key = block_index * key_block
        keys_part = lax.dynamic_slice_in_dim(keys3, first_key, key_block, 0)
        key_pos = first_key + jnp.arange(key_block, dtype=jnp.int32)
        scores, allowed = block_scores(queries3, keys_part, query_pos, key_pos, length)
        masked = jnp.where(allowed, scores, masked_value)
        new_top = jnp.maximum(running_top, jnp.max(masked, axis=-1))
        kept_terms = jnp.where(allowed, jnp.exp(masked - new_top[..., None]), 0.0)
        running_sum = running_sum * jnp.exp(running_top - new_top) + jnp.sum(kept_terms, axis=-1)
        return ((new_top, running_sum), None)

    initial = (
        jnp.full((HEADS, row_count), masked_value, jnp.float32),
        jnp.zeros((HEADS, row_count), jnp.float32),
    )
    (row_tops, row_sums), _ = lax.scan(
        row_advance, initial, jnp.arange(keys3.shape[0] // key_block, dtype=jnp.int32)
    )
    return row_tops + jnp.log(row_sums)


def attend(queries3, keys3, values3, query_pos, length, key_block, log_total):

    def attend_advance(running, block_index):
        first_key = block_index * key_block
        keys_part = lax.dynamic_slice_in_dim(keys3, first_key, key_block, 0)
        values_part = lax.dynamic_slice_in_dim(values3, first_key, key_block, 0)
        key_pos = first_key + jnp.arange(key_block, dtype=jnp.int32)
        scores, allowed = block_scores(queries3, keys_part, query_pos, key_pos, length)
        probabilities = jnp.where(allowed, jnp.exp(scores - log_total[..., None]), 0.0).astype(
            jnp.bfloat16
        )
        return (
            running
            + jnp.einsum(
                "hrk,khd->rhd", probabilities, values_part, preferred_element_type=jnp.float32
            ),
            None,
        )

    initial = jnp.zeros(queries3.shape, jnp.float32)
    result, _ = lax.scan(
        attend_advance, initial, jnp.arange(keys3.shape[0] // key_block, dtype=jnp.int32)
    )
    return result


def query_grads(
    queries3, grads3, keys3, values3, query_pos, length, key_block, log_total, row_delta
):

    def query_advance(running, block_index):
        first_key = block_index * key_block
        keys_part = lax.dynamic_slice_in_dim(keys3, first_key, key_block, 0)
        values_part = lax.dynamic_slice_in_dim(values3, first_key, key_block, 0)
        key_pos = first_key + jnp.arange(key_block, dtype=jnp.int32)
        scores, allowed = block_scores(queries3, keys_part, query_pos, key_pos, length)
        probabilities = jnp.where(allowed, jnp.exp(scores - log_total[..., None]), 0.0)
        prob_grad = jnp.einsum(
            "rhd,khd->hrk", grads3, values_part, preferred_element_type=jnp.float32
        )
        score_low = (probabilities * (prob_grad - row_delta[..., None])).astype(jnp.bfloat16)
        return (
            running
            + jnp.einsum("hrk,khd->rhd", score_low, keys_part, preferred_element_type=jnp.float32),
            None,
        )

    initial = jnp.zeros(queries3.shape, jnp.float32)
    result, _ = lax.scan(
        query_advance, initial, jnp.arange(keys3.shape[0] // key_block, dtype=jnp.int32)
    )
    return result * HEAD ** (-0.5)


def key_side(queries3, grads3, log_part, delta_part, query_pos, keys3, values3, key_pos, length):
    key_count = keys3.shape[0]
    scores, allowed = block_scores(queries3, keys3, query_pos, key_pos, length)
    probabilities = jnp.where(allowed, jnp.exp(scores - log_part[..., None]), 0.0)
    prob_grad = jnp.einsum("rhd,khd->hrk", grads3, values3, preferred_element_type=jnp.float32)
    score_low = (probabilities * (prob_grad - delta_part[..., None])).astype(jnp.bfloat16)
    value_grad = jnp.einsum(
        "hrk,rhd->khd",
        probabilities.astype(jnp.bfloat16),
        grads3,
        preferred_element_type=jnp.float32,
    )
    key_grad = jnp.einsum(
        "hrk,rhd->khd", score_low, queries3, preferred_element_type=jnp.float32
    ) * HEAD ** (-0.5)
    return jnp.concatenate(
        [key_grad.reshape(key_count, HEADS * HEAD), value_grad.reshape(key_count, HEADS * HEAD)],
        axis=1,
    )


def slot_attention(queries3, keys3, values3, query_pos, length):
    key_pos = jnp.arange(keys3.shape[0], dtype=jnp.int32)
    scores, allowed = block_scores(queries3, keys3, query_pos, key_pos, length)
    masked = jnp.where(allowed, scores, masked_value)
    top = jnp.max(masked, axis=-1)
    kept_terms = jnp.where(allowed, jnp.exp(masked - top[..., None]), 0.0)
    log_total = top + jnp.log(jnp.sum(kept_terms, axis=-1))
    probabilities = jnp.where(allowed, jnp.exp(scores - log_total[..., None]), 0.0)
    probabilities_low = probabilities.astype(jnp.bfloat16)
    attended = jnp.einsum(
        "hrk,khd->rhd", probabilities_low, values3, preferred_element_type=jnp.float32
    )
    return attended, probabilities, probabilities_low


def slot_attention_grads(queries3, keys3, values3, grads3, attended, probabilities, probabilities_low):
    prob_grad = jnp.einsum("rhd,khd->hrk", grads3, values3, preferred_element_type=jnp.float32)
    row_delta = jnp.einsum("rhd,rhd->hr", grads3.astype(jnp.float32), attended)
    score_low = (probabilities * (prob_grad - row_delta[..., None])).astype(jnp.bfloat16)
    query_grad = jnp.einsum(
        "hrk,khd->rhd", score_low, keys3, preferred_element_type=jnp.float32
    ) * HEAD ** (-0.5)
    key_grad = jnp.einsum(
        "hrk,rhd->khd", score_low, queries3, preferred_element_type=jnp.float32
    ) * HEAD ** (-0.5)
    value_grad = jnp.einsum(
        "hrk,rhd->khd", probabilities_low, grads3, preferred_element_type=jnp.float32
    )
    return query_grad, key_grad, value_grad


def _pair_masks(scalars_ref, micro, row_count, key_count):
    length = scalars_ref[micro]
    first_row = scalars_ref[scalars_ref.shape[0] - 1]
    query_pos = first_row + lax.broadcasted_iota(jnp.int32, (row_count, key_count), 0)
    key_pos = lax.broadcasted_iota(jnp.int32, (row_count, key_count), 1)
    return (key_pos <= query_pos) & (key_pos < length)


def _forward_kernel(scalars_ref, q_ref, k_ref, v_ref, out_ref, lse_ref):
    micro = pl.program_id(0)
    row_count = q_ref.shape[0]
    key_count = k_ref.shape[0] * k_ref.shape[2]
    allowed = _pair_masks(scalars_ref, micro, row_count, key_count)
    k_all = k_ref[...].reshape(key_count, k_ref.shape[3])
    v_all = v_ref[...].reshape(key_count, v_ref.shape[3])
    for half in range(2):
        lanes = slice(half * HEAD, (half + 1) * HEAD)
        q_head = q_ref[:, lanes]
        k_head = k_all[:, lanes]
        v_head = v_all[:, lanes]
        scores = lax.dot_general(
            q_head, k_head, (((1,), (1,)), ((), ())), preferred_element_type=jnp.float32
        ) * HEAD ** (-0.5)
        masked = jnp.where(allowed, scores, masked_value)
        top = jnp.max(masked, axis=1, keepdims=True)
        kept = jnp.where(allowed, jnp.exp(masked - top), 0.0)
        total = jnp.sum(kept, axis=1, keepdims=True)
        log_total = top + jnp.log(total)
        probabilities = kept * (1.0 / total)
        attended = jnp.dot(
            probabilities.astype(jnp.bfloat16), v_head, preferred_element_type=jnp.float32
        )
        out_ref[:, lanes] = attended
        lse_ref[:, lanes] = jnp.broadcast_to(log_total, (row_count, HEAD))


def _backward_kernel(
    scalars_ref, q_ref, k_ref, v_ref, do_ref, o_ref, lse_ref, dq_ref, kv_grad_ref, pair_ref
):
    micro = pl.program_id(0)
    pair = pl.program_id(1)
    row_count = q_ref.shape[0]
    key_count = k_ref.shape[0] * k_ref.shape[2]
    allowed = _pair_masks(scalars_ref, micro, row_count, key_count)
    k_all = k_ref[...].reshape(key_count, k_ref.shape[3])
    v_all = v_ref[...].reshape(key_count, v_ref.shape[3])
    for half in range(2):
        lanes = slice(half * HEAD, (half + 1) * HEAD)
        q_head = q_ref[:, lanes]
        k_head = k_all[:, lanes]
        v_head = v_all[:, lanes]
        grad_head = do_ref[:, lanes]
        scores = lax.dot_general(
            q_head, k_head, (((1,), (1,)), ((), ())), preferred_element_type=jnp.float32
        ) * HEAD ** (-0.5)
        log_total = lse_ref[:, half * HEAD : half * HEAD + 1]
        probabilities = jnp.where(allowed, jnp.exp(scores - log_total), 0.0)
        probabilities_low = probabilities.astype(jnp.bfloat16)
        prob_grad = lax.dot_general(
            grad_head, v_head, (((1,), (1,)), ((), ())), preferred_element_type=jnp.float32
        )
        row_delta = jnp.sum(
            grad_head.astype(jnp.float32) * o_ref[:, lanes], axis=1, keepdims=True
        )
        score_low = (probabilities * (prob_grad - row_delta)).astype(jnp.bfloat16)
        dq_ref[:, lanes] = jnp.dot(
            score_low, k_head, preferred_element_type=jnp.float32
        ) * HEAD ** (-0.5)
        key_grad = lax.dot_general(
            score_low, q_head, (((0,), (0,)), ((), ())), preferred_element_type=jnp.float32
        ) * HEAD ** (-0.5)
        value_grad = lax.dot_general(
            probabilities_low, grad_head, (((0,), (0,)), ((), ())),
            preferred_element_type=jnp.float32,
        )
        pair_ref[0, :, lanes] = key_grad.astype(jnp.bfloat16)
        pair_ref[1, :, lanes] = value_grad.astype(jnp.bfloat16)
    half_width = kv_grad_ref.shape[1] // 2
    first_col = pl.multiple_of(pair * 2 * HEAD, 2 * HEAD)
    kv_grad_ref[:, pl.ds(first_col, 2 * HEAD)] = pair_ref[0]
    kv_grad_ref[:, pl.ds(first_col + half_width, 2 * HEAD)] = pair_ref[1]


def attention_forward(scalars, queries, kv_flat, batches):
    all_rows, model_width = queries.shape
    row_count = all_rows // batches
    devices = kv_flat.shape[0]
    key_count = devices * row_count
    pairs = model_width // (2 * HEAD)
    row_spec = pl.BlockSpec((row_count, 2 * HEAD), lambda m, p, s: (m, p))
    key_spec = pl.BlockSpec((devices, 1, row_count, 2 * HEAD), lambda m, p, s: (0, m, 0, p))
    value_spec = pl.BlockSpec(
        (devices, 1, row_count, 2 * HEAD), lambda m, p, s: (0, m, 0, pairs + p)
    )
    return pl.pallas_call(
        _forward_kernel,
        grid_spec=pltpu.PrefetchScalarGridSpec(
            num_scalar_prefetch=1,
            grid=(batches, pairs),
            in_specs=[row_spec, key_spec, value_spec],
            out_specs=[row_spec, row_spec],
        ),
        out_shape=[
            jax.ShapeDtypeStruct((all_rows, model_width), jnp.float32),
            jax.ShapeDtypeStruct((all_rows, model_width), jnp.float32),
        ],
        name="attention_forward",
    )(scalars, queries, kv_flat, kv_flat)


def attention_backward(scalars, queries, kv_flat, grads, attended, log_totals, batches):
    all_rows, model_width = queries.shape
    row_count = all_rows // batches
    devices = kv_flat.shape[0]
    key_count = devices * row_count
    pairs = model_width // (2 * HEAD)
    row_spec = pl.BlockSpec((row_count, 2 * HEAD), lambda m, p, s: (m, p))
    key_spec = pl.BlockSpec((devices, 1, row_count, 2 * HEAD), lambda m, p, s: (0, m, 0, p))
    value_spec = pl.BlockSpec(
        (devices, 1, row_count, 2 * HEAD), lambda m, p, s: (0, m, 0, pairs + p)
    )
    grad_spec = pl.BlockSpec((None, key_count, 2 * model_width), lambda m, p, s: (m, 0, 0))
    return pl.pallas_call(
        _backward_kernel,
        grid_spec=pltpu.PrefetchScalarGridSpec(
            num_scalar_prefetch=1,
            grid=(batches, pairs),
            in_specs=[row_spec, key_spec, value_spec, row_spec, row_spec, row_spec],
            out_specs=[row_spec, grad_spec],
            scratch_shapes=[pltpu.VMEM((2, key_count, 2 * HEAD), jnp.bfloat16)],
        ),
        out_shape=[
            jax.ShapeDtypeStruct((all_rows, model_width), jnp.float32),
            jax.ShapeDtypeStruct((batches, key_count, 2 * model_width), jnp.bfloat16),
        ],
        name="attention_backward",
    )(scalars, queries, kv_flat, kv_flat, grads, attended, log_totals)


def local(
    layer_input,
    history,
    cotangent,
    lengths,
    w_qkv,
    w_out,
    w_up,
    w_down,
    ln_gains,
    ln_biases,
    depth_weights,
):
    batches = layer_input.shape[0]
    row_count = layer_input.shape[2]
    model_width = layer_input.shape[3]
    ff_width = w_up.shape[1]
    shard_rows = w_qkv.shape[0]
    all_rows = batches * row_count
    slot_len = row_count * lax.axis_size("seq")
    positions = lax.axis_index("seq") * row_count + jnp.arange(row_count, dtype=jnp.int32)
    cosine_part, sine_part = rotary_tables(jnp.tile(positions, batches))
    gelu_tanh = partial(jax.nn.gelu, approximate=True)
    lane_pad = 128 - 4
    widths = (3 * model_width, 2, 2, lane_pad, model_width, ff_width, ff_width)
    offsets = [0]
    for width in widths:
        offsets.append(offsets[-1] + width)

    def pieces(packed_rows):
        return [packed_rows[:, offsets[i] : offsets[i + 1]] for i in range(len(widths))]

    packed = jnp.concatenate(
        [
            w_qkv,
            ln_gains,
            ln_biases,
            jnp.zeros((shard_rows, lane_pad), w_qkv.dtype),
            w_out,
            w_up,
            w_down.reshape(shard_rows, ff_width),
        ],
        axis=1,
    )
    gathered = lax.all_gather(packed, ("seq", "fsdp"), axis=0, tiled=True)
    full_qkv, gain_rows, bias_rows, _, full_out, full_up, down_rows = pieces(gathered)
    full_down = down_rows.reshape(ff_width, model_width)
    norm_gains = gain_rows.astype(jnp.float32)
    norm_biases = bias_rows.astype(jnp.float32)

    slot_lengths = lengths[:, 0]
    inputs = layer_input[:, 0].reshape(all_rows, model_width).astype(jnp.float32)
    first_low = layer_norm(inputs, norm_gains[:, 0], norm_biases[:, 0]).astype(jnp.bfloat16)
    projected = jnp.dot(first_low, full_qkv, preferred_element_type=jnp.float32)
    queries = rotate(projected[:, :model_width], cosine_part, sine_part).astype(jnp.bfloat16)
    keys_own = rotate(
        projected[:, model_width : 2 * model_width], cosine_part, sine_part
    ).astype(jnp.bfloat16)
    values_own = projected[:, 2 * model_width :].astype(jnp.bfloat16)
    own_kv = jnp.concatenate([keys_own, values_own], axis=1).reshape(
        batches, row_count, 2 * model_width
    )
    earlier = history[:, :, 0].reshape(4, all_rows, model_width).astype(jnp.float32)
    usable = (positions[None, :] < slot_lengths[:, None]).reshape(all_rows, 1)
    grad_next = jnp.where(
        usable, cotangent[:, 0].reshape(all_rows, model_width).astype(jnp.float32), 0.0
    )
    history_part = (
        depth_weights[0] * earlier[0]
        + depth_weights[1] * earlier[1]
        + depth_weights[2] * earlier[2]
        + depth_weights[3] * earlier[3]
    )
    grad_history = (depth_weights[:4, None, None] * grad_next[None]).astype(jnp.bfloat16)
    grad_history = grad_history.reshape(4, batches, 1, row_count, model_width)
    out_grad = depth_weights[4] * grad_next
    out_low = out_grad.astype(jnp.bfloat16)

    kv_flat = lax.all_gather(own_kv, "seq", axis=0, tiled=False)
    scalars = jnp.concatenate(
        [slot_lengths.astype(jnp.int32), (lax.axis_index("seq") * row_count)[None].astype(jnp.int32)]
    )
    attended_rows, log_totals = attention_forward(scalars, queries, kv_flat, batches)
    attended_low = attended_rows.astype(jnp.bfloat16)
    residual = inputs + jnp.dot(attended_low, full_out, preferred_element_type=jnp.float32)
    second_low = layer_norm(residual, norm_gains[:, 1], norm_biases[:, 1]).astype(jnp.bfloat16)
    hidden = jnp.dot(second_low, full_up, preferred_element_type=jnp.float32)
    hidden_low = gelu_tanh(hidden).astype(jnp.bfloat16)
    block_out = residual + jnp.dot(hidden_low, full_down, preferred_element_type=jnp.float32)
    hidden_grad = jnp.einsum("rd,fd->rf", out_low, full_down, preferred_element_type=jnp.float32)
    _, gelu_pullback = jax.vjp(gelu_tanh, hidden)
    up_low = gelu_pullback(hidden_grad)[0].astype(jnp.bfloat16)
    second_grad = jnp.einsum("rf,df->rd", up_low, full_up, preferred_element_type=jnp.float32)
    _, second_pullback = jax.vjp(layer_norm, residual, norm_gains[:, 1], norm_biases[:, 1])
    residual_part, gain_two, bias_two = second_pullback(second_grad)
    residual_grad = out_grad + residual_part
    branch_low = residual_grad.astype(jnp.bfloat16)
    attended_grad = jnp.einsum(
        "rd,cd->rc", branch_low, full_out, preferred_element_type=jnp.float32
    ).astype(jnp.bfloat16)
    query_grad, kv_grad_flat = attention_backward(
        scalars, queries, kv_flat, attended_grad, attended_rows, log_totals, batches
    )
    micro_major = Layout(major_to_minor=(1, 0, 2))
    kv_grad_own = lax.psum_scatter(
        with_layout_constraint(jnp.swapaxes(kv_grad_flat, 0, 1), micro_major),
        "seq",
        scatter_dimension=0,
        tiled=True,
    )
    kv_grad_own = with_layout_constraint(kv_grad_own, micro_major)
    block_side = block_out
    combined = depth_weights[4] * block_side + history_part
    next_input = combined.astype(jnp.bfloat16).reshape(batches, 1, row_count, model_width)
    depth_terms = jnp.concatenate(
        [jnp.sum(earlier * grad_next[None], axis=(1, 2)), jnp.sum(block_side * grad_next)[None]]
    )
    grad_down = jnp.einsum("rf,rd->fd", hidden_low, out_low, preferred_element_type=jnp.float32)
    grad_up = jnp.einsum("rd,rf->df", second_low, up_low, preferred_element_type=jnp.float32)
    grad_outproj = jnp.einsum(
        "rc,rd->cd", attended_low, branch_low, preferred_element_type=jnp.float32
    )
    early_grads = jnp.concatenate(
        [
            jnp.zeros((model_width, 3 * model_width), jnp.float32),
            grad_outproj,
            grad_up,
            grad_down.reshape(model_width, ff_width),
        ],
        axis=1,
    ).astype(jnp.bfloat16)
    kv_grad_own, early_grads = lax.optimization_barrier((kv_grad_own, early_grads))
    kv_grad_own = jnp.swapaxes(kv_grad_own, 0, 1).reshape(all_rows, 2 * model_width)
    key_value_all = kv_grad_own.astype(jnp.float32)
    qkv_low = jnp.concatenate(
        [
            rotate(query_grad, cosine_part, -sine_part),
            rotate(key_value_all[:, :model_width], cosine_part, -sine_part),
            key_value_all[:, model_width:],
        ],
        axis=1,
    ).astype(jnp.bfloat16)
    grad_qkv = jnp.einsum("rd,rc->dc", first_low, qkv_low, preferred_element_type=jnp.float32)
    first_grad = jnp.einsum("rc,dc->rd", qkv_low, full_qkv, preferred_element_type=jnp.float32)
    _, first_pullback = jax.vjp(layer_norm, inputs, norm_gains[:, 0], norm_biases[:, 0])
    input_part, gain_one, bias_one = first_pullback(first_grad)
    grad_input = (residual_grad + input_part).astype(jnp.bfloat16)
    grad_input = grad_input.reshape(batches, 1, row_count, model_width)
    packed_grads = lax.dynamic_update_slice(early_grads, grad_qkv.astype(jnp.bfloat16), (0, 0))
    device_count = model_width // shard_rows
    row_major = Layout(major_to_minor=(0, 1, 2))
    grad_offsets = [0]
    for width in (3 * model_width, model_width, ff_width, ff_width):
        grad_offsets.append(grad_offsets[-1] + width)
    scattered = lax.psum_scatter(
        with_layout_constraint(
            packed_grads.reshape(device_count, shard_rows, grad_offsets[-1]), row_major
        ),
        ("seq", "fsdp"),
        scatter_dimension=0,
        tiled=False,
    )
    scattered = with_layout_constraint(scattered, Layout(major_to_minor=(0, 1)))
    full_pieces = [
        scattered[:, grad_offsets[i] : grad_offsets[i + 1]].astype(jnp.float32) for i in range(4)
    ]
    small_sums = lax.psum(
        jnp.concatenate(
            [
                depth_terms,
                jnp.stack([gain_one, gain_two, bias_one, bias_two], axis=1).reshape(-1),
            ]
        ),
        ("seq", "fsdp"),
    )
    depth_total = small_sums[:5]
    device_index = lax.axis_index("seq") * lax.axis_size("fsdp") + lax.axis_index("fsdp")
    norm_owned = lax.dynamic_slice_in_dim(
        small_sums[5:].reshape(model_width, 4), device_index * shard_rows, shard_rows, 0
    )
    owned = [
        full_pieces[0],
        full_pieces[1],
        full_pieces[2],
        full_pieces[3].reshape(-1, model_width),
        norm_owned[:, :2],
        norm_owned[:, 2:],
    ]
    return (next_input, grad_input, grad_history, *owned, depth_total)


def solution(mesh):
    in_specs = (
        P(None, "fsdp", "seq", None),
        P(None, None, "fsdp", "seq", None),
        P(None, "fsdp", "seq", None),
        P(None, "fsdp"),
        P(("seq", "fsdp"), None),
        P(("seq", "fsdp"), None),
        P(("seq", "fsdp"), None),
        P(("seq", "fsdp"), None),
        P(("seq", "fsdp"), None),
        P(("seq", "fsdp"), None),
        P(),
    )
    out_specs = (
        P(None, "fsdp", "seq", None),
        P(None, "fsdp", "seq", None),
        P(None, None, "fsdp", "seq", None),
        P(("seq", "fsdp"), None),
        P(("seq", "fsdp"), None),
        P(("seq", "fsdp"), None),
        P(("seq", "fsdp"), None),
        P(("seq", "fsdp"), None),
        P(("seq", "fsdp"), None),
        P(),
    )
    return jax.shard_map(local, mesh=mesh, in_specs=in_specs, out_specs=out_specs, check_vma=False)
```
